32 devices in a mesh: groups: 2 (over y), tile: 4 (over z), depth: 2 (over x), batch: 2 (over core).
Axes of the slice: x: 2, y: 2, z: 4, core: 2. Of those that a mesh axis runs over, the one named last changes fastest.
Arguments:
- object_field: float32 [4, 2, 1024, 512], P(('groups', 'depth'), None, 'tile'), parts along dimension 0, may hold values from -1 to 1, as said below
- probe: bfloat16 [4, 256, 256], P('groups'), parts along dimension 0, may hold values from -6 to 6
- positions: int32 [32, 2], P(('groups', 'tile', 'batch')), parts along dimension 0, may hold values from 0 to 768, as said below
- counts: int32 [16], P(('groups', 'tile', 'batch')), parts along dimension 0, may hold values from 0 to 2, as said below
- measured: float32 [32, 256, 256], P(('groups', 'tile', 'batch')), parts along dimension 0, may hold values from 0.1 to 8
Outputs:
- object_grad: float32 [4, 2, 1024, 512], P(('groups', 'depth'), None, 'tile'), parts along dimension 0
The draws below stay inside these ranges and needn't reach their ends.
There are 2 independent parts, one for each index of `groups`. The reference program is written for one: setup_inputs(seed, part) draws one part's arguments, and reference() takes and returns one part's arrays. A program takes and returns all parts, laid end to end along the dimension named above; each array names one. Nothing has to cross between parts.
Inputs may be any that keep to these rules, and one draw needn't show every extreme that they name: `positions`: slot i belongs to tile (i // 2) // 2; its row offset lies within that tile's rows, from its first row to 255 rows later, and its patch ends inside the object; its column offset is at most 256. Some slot starts at row 768. counts[2 t] and counts[2 t + 1] are the live first slots of the two devices of tile t along the batch axis; their sum is at least 1 and at most 2, and equals 2 for some tile. `object_field`: each entry pair is a complex number of magnitude at most 1.
All inputs are finite; a program needn't handle non-finite values.
Results may differ from the reference program's by a relative error of at most 0.03.
Values may be sent and summed in bfloat16 or wider, within the bound.
No kernel may reach another device: no remote copies, remote signals or barrier semaphores. Data moves between devices by JAX's collectives and lax.ppermute only.
A program may use at most 64 MiB of HBM per device.

```python
import math
import jax
import jax.numpy as jnp
from jax import lax

P_SIZE = 256
TROW = 256
OC = 512
CAP = 2
SLICES = 2
ROWS = 1024
SLOTS = 16
N_TILE = 4
N_BATCH = 2


def draw_object_field(key, part):
    first, second = jax.random.split(key)
    shape = (SLICES, ROWS, OC)
    amplitude = jax.random.uniform(first, shape, jnp.float32, 0.7, 1.0)
    phase = jax.random.uniform(second, shape, jnp.float32, -0.8, 0.8)
    return jnp.stack([amplitude * jnp.cos(phase), amplitude * jnp.sin(phase)], axis=1).astype(jnp.float32)


def draw_positions(key, part):
    slot_total = N_TILE * N_BATCH * CAP
    index = jnp.arange(slot_total, dtype=jnp.int32)
    tile = index // (N_BATCH * CAP)
    first, second = jax.random.split(key)
    span = jnp.where(tile == N_TILE - 1, TROW - P_SIZE + 1, TROW)
    offsets = jax.random.randint(first, (slot_total,), 0, 1 << 20, dtype=jnp.int32) % span
    offsets = jnp.where(index == slot_total - 1, TROW - P_SIZE, offsets)
    rows = tile * TROW + offsets
    columns = jax.random.randint(second, (slot_total,), 0, OC - P_SIZE + 1, dtype=jnp.int32)
    return jnp.stack([rows, columns], axis=1).astype(jnp.int32)


def draw_counts(key, part):
    first, second, third = jax.random.split(key, 3)
    tiles = jnp.arange(N_TILE, dtype=jnp.int32)
    totals = jax.random.randint(first, (N_TILE,), CAP // 2, CAP + 1, dtype=jnp.int32)
    busiest = jax.random.randint(second, (), 0, N_TILE, dtype=jnp.int32)
    totals = jnp.where(tiles == busiest, CAP, totals)
    later = jax.random.randint(third, (N_TILE,), 0, 1 << 20, dtype=jnp.int32) % (totals // 2 + 1)
    later = jnp.where(tiles == busiest, 0, later)
    earlier = totals - later
    return jnp.stack([earlier, later], axis=1).reshape(-1).astype(jnp.int32)


def steps_of(stream_key, extent, shards, least, top_value):
    factor_of, own = 1.0, jax.random.fold_in(stream_key, 6)
    for position, parts in shards:
        heights = jnp.exp(jax.random.uniform(jax.random.fold_in(own, position), (parts,), jnp.float32, least / len(shards), top_value / len(shards)))
        factor_of = factor_of * jnp.repeat(heights, extent[position] // parts).reshape([-1 if axis == position else 1 for axis in range(len(extent))])
    return factor_of


def centred(stream_key, dims, deviation, limit, kind=jnp.bfloat16):
    drawn = jax.random.normal(stream_key, dims, jnp.float32) * deviation
    return jnp.minimum(jnp.maximum(drawn, -limit), limit).astype(kind)


def setup_inputs(seed: int = 0, part: int = 0) -> dict:
    arg_keys = jax.random.split(jax.random.key(seed), 6)
    own_keys = jax.random.split(jax.random.fold_in(arg_keys[5], part), 6)
    return {
        "object_field": draw_object_field(jax.random.fold_in(jax.random.fold_in(arg_keys[5], part), 71), part),
        "probe": centred(own_keys[1], (2, P_SIZE, P_SIZE), 1.0, 6.0),
        "positions": draw_positions(jax.random.fold_in(jax.random.fold_in(arg_keys[5], part), 71), part),
        "counts": draw_counts(jax.random.fold_in(jax.random.fold_in(arg_keys[5], part), 71), part),
        "measured": jnp.clip(jnp.exp(math.log(8.0) - 4.3820266 * jax.random.uniform(own_keys[4], (SLOTS, P_SIZE, P_SIZE), jnp.float32) ** steps_of(own_keys[4], (SLOTS, P_SIZE, P_SIZE), ((0, 8),), -0.2, 0.2)), 0.1, 8.0),
    }


SLICE_COEF = 0.002
DETECTOR_COEF = 0.006
RESIDUAL_SCALE = 0.125

def dft_block(width, sign):
    freq = jnp.arange(width, dtype=jnp.int32)
    product = freq[:, None] * freq[None, :] % width
    angle = 2.0 * math.pi / width * product.astype(jnp.float32)
    scale = 1.0 / math.sqrt(width)
    real_part = (jnp.cos(angle) * scale).astype(jnp.bfloat16)
    imag_part = (sign * jnp.sin(angle) * scale).astype(jnp.bfloat16)
    upper = jnp.concatenate([real_part, -imag_part], axis=1)
    lower = jnp.concatenate([imag_part, real_part], axis=1)
    return jnp.concatenate([upper, lower], axis=0)

def chirp_parts(width, coef):
    freq = jnp.arange(width, dtype=jnp.int32)
    shifted = (freq + width // 2) % width - width // 2
    square = shifted * shifted
    total = (square[:, None] + square[None, :]).astype(jnp.float32)
    phase = -coef * total
    return (jnp.cos(phase), jnp.sin(phase))

def left_apply(block, wave):
    width = wave.shape[1]
    stacked = wave.reshape(2 * width, width)
    return jnp.dot(block, stacked, preferred_element_type=jnp.float32).reshape(2, width, width)

def propagate(wave, forward_block, inverse_block, chirp_re, chirp_im):
    first = left_apply(forward_block, wave).astype(jnp.bfloat16)
    spectrum = left_apply(forward_block, jnp.swapaxes(first, -1, -2))
    spec_re = spectrum[0]
    spec_im = spectrum[1]
    filtered = jnp.stack([spec_re * chirp_re - spec_im * chirp_im, spec_re * chirp_im + spec_im * chirp_re], axis=0).astype(jnp.bfloat16)
    back = left_apply(inverse_block, filtered).astype(jnp.bfloat16)
    return left_apply(inverse_block, jnp.swapaxes(back, -1, -2)).astype(jnp.bfloat16)

def transmit(wave, patch):
    values = wave.astype(jnp.float32)
    wave_re = values[0]
    wave_im = values[1]
    return jnp.stack([patch[0] * wave_re - patch[1] * wave_im, patch[0] * wave_im + patch[1] * wave_re], axis=0).astype(jnp.bfloat16)

def residual_wave(wave, measured):
    values = wave.astype(jnp.float32)
    intensity = values[0] * values[0] + values[1] * values[1]
    weight = RESIDUAL_SCALE * (intensity - measured)
    return jnp.stack([weight * values[0], weight * values[1]], axis=0).astype(jnp.bfloat16)

def adjoint_terms(incoming, forward_block, inverse_block, chirp_re, chirp_im, inputs, patch):
    spread = propagate(incoming, forward_block, inverse_block, chirp_re, -chirp_im).astype(jnp.float32)
    source = inputs.astype(jnp.float32)
    term = jnp.stack([source[0] * spread[0] + source[1] * spread[1], source[0] * spread[1] - source[1] * spread[0]], axis=0)
    passed = jnp.stack([patch[0] * spread[0] + patch[1] * spread[1], patch[0] * spread[1] - patch[1] * spread[0]], axis=0).astype(jnp.bfloat16)
    return (passed, term)

def reference(object_field, probe, positions, counts, measured):
    slices = object_field.shape[0]
    width = probe.shape[1]
    forward_block = dft_block(width, -1.0)
    inverse_block = dft_block(width, 1.0)
    chirps = [chirp_parts(width, SLICE_COEF if layer < slices - 1 else DETECTOR_COEF) for layer in range(slices)]
    slot_total = positions.shape[0]
    capacity = slot_total // counts.shape[0]
    live = jnp.arange(slot_total, dtype=jnp.int32) % capacity < jnp.repeat(counts, capacity)
    anchor = jnp.zeros((), jnp.int32)

    def one_position(place, intensity):
        patches = lax.dynamic_slice(object_field, (anchor, anchor, place[0].astype(jnp.int32), place[1].astype(jnp.int32)), (slices, 2, width, width))
        inputs = []
        wave = probe
        for layer in range(slices):
            inputs.append(wave)
            wave = propagate(transmit(wave, patches[layer]), forward_block, inverse_block, chirps[layer][0], chirps[layer][1])
        carried = residual_wave(wave, intensity)
        terms = [None] * slices
        for layer in reversed(range(slices)):
            carried, term = adjoint_terms(carried, forward_block, inverse_block, chirps[layer][0], chirps[layer][1], inputs[layer], patches[layer])
            terms[layer] = term
        return jnp.stack(terms, axis=0)

    def nothing(place, intensity):
        return jnp.zeros((slices, 2, width, width), jnp.float32)

    def accumulate(total, item):
        place, intensity, alive = item
        term = lax.cond(alive, one_position, nothing, place, intensity)
        start = (anchor, anchor, place[0].astype(jnp.int32), place[1].astype(jnp.int32))
        current = lax.dynamic_slice(total, start, (slices, 2, width, width))
        return (lax.dynamic_update_slice(total, current + term, start), anchor)
    gradient, unused = lax.scan(accumulate, jnp.zeros(object_field.shape, jnp.float32), (positions, measured, live))
    return gradient
```

```python
import math

import jax
import jax.numpy as jnp
from jax import lax
from jax.sharding import PartitionSpec as P

SLICE_COEF = 0.002
DETECTOR_COEF = 0.006
RESIDUAL_SCALE = 0.125


def from_behind(block, axis, distance):
    devices = range(lax.axis_size(axis))
    route = [(i - distance, i) for i in devices if i - distance in devices]
    return lax.ppermute(block, axis, route)


def dft_block(width, sign):
    freq = jnp.arange(width, dtype=jnp.int32)
    product = freq[:, None] * freq[None, :] % width
    angle = 2.0 * math.pi / width * product.astype(jnp.float32)
    scale = 1.0 / math.sqrt(width)
    real_part = (jnp.cos(angle) * scale).astype(jnp.bfloat16)
    imag_part = (sign * jnp.sin(angle) * scale).astype(jnp.bfloat16)
    upper = jnp.concatenate([real_part, -imag_part], axis=1)
    lower = jnp.concatenate([imag_part, real_part], axis=1)
    return jnp.concatenate([upper, lower], axis=0)


def chirp_parts(width, coef):
    freq = jnp.arange(width, dtype=jnp.int32)
    shifted = (freq + width // 2) % width - width // 2
    square = shifted * shifted
    total = (square[:, None] + square[None, :]).astype(jnp.float32)
    phase = -coef * total
    return (jnp.cos(phase), jnp.sin(phase))


def left_apply(block, waves):
    number = waves.shape[0]
    width = waves.shape[2]
    stacked = waves.reshape(number, 2 * width, width)
    result = jnp.einsum("ij,gjk->gik", block, stacked, preferred_element_type=jnp.float32)
    return result.reshape(number, 2, width, width)


def propagate(waves, forward_block, inverse_block, chirp_re, chirp_im):
    first = left_apply(forward_block, waves).astype(jnp.bfloat16)
    spectrum = left_apply(forward_block, jnp.swapaxes(first, -1, -2))
    spec_re = spectrum[:, 0]
    spec_im = spectrum[:, 1]
    filtered = jnp.stack(
        [spec_re * chirp_re - spec_im * chirp_im, spec_re * chirp_im + spec_im * chirp_re], axis=1
    ).astype(jnp.bfloat16)
    back = left_apply(inverse_block, filtered).astype(jnp.bfloat16)
    return left_apply(inverse_block, jnp.swapaxes(back, -1, -2)).astype(jnp.bfloat16)


def transmit(waves, patch):
    values = waves.astype(jnp.float32)
    wave_re = values[:, 0]
    wave_im = values[:, 1]
    return jnp.stack(
        [
            patch[:, 0] * wave_re - patch[:, 1] * wave_im,
            patch[:, 0] * wave_im + patch[:, 1] * wave_re,
        ],
        axis=1,
    ).astype(jnp.bfloat16)


def residual_wave(waves, measured):
    values = waves.astype(jnp.float32)
    intensity = values[:, 0] * values[:, 0] + values[:, 1] * values[:, 1]
    weight = RESIDUAL_SCALE * (intensity - measured)
    return jnp.stack([weight * values[:, 0], weight * values[:, 1]], axis=1).astype(jnp.bfloat16)


def adjoint_terms(incoming, forward_block, inverse_block, chirp_re, chirp_im, inputs, patch):
    spread = propagate(incoming, forward_block, inverse_block, chirp_re, -chirp_im).astype(
        jnp.float32
    )
    source = inputs.astype(jnp.float32)
    term = jnp.stack(
        [
            source[:, 0] * spread[:, 0] + source[:, 1] * spread[:, 1],
            source[:, 0] * spread[:, 1] - source[:, 1] * spread[:, 0],
        ],
        axis=1,
    )
    passed = jnp.stack(
        [
            patch[:, 0] * spread[:, 0] + patch[:, 1] * spread[:, 1],
            patch[:, 0] * spread[:, 1] - patch[:, 1] * spread[:, 0],
        ],
        axis=1,
    ).astype(jnp.bfloat16)
    return (passed, term)


def local(object_field, probe, positions, counts, measured):
    width = probe.shape[1]
    tile_rows = object_field.shape[2]
    columns_all = object_field.shape[3]
    tile_index = lax.axis_index("tile")
    tile_count = lax.axis_size("tile")
    segment = lax.axis_index("depth")
    depth_count = lax.axis_size("depth")
    batch_index = lax.axis_index("batch")
    batch_count = lax.axis_size("batch")
    rim = from_behind(object_field[:, :, :width, :], "tile", -1)
    extended = jnp.concatenate([object_field, rim], axis=2)[0]
    capacity = positions.shape[0]
    live = jnp.arange(capacity, dtype=jnp.int32) < counts[0]
    local_rows = positions[:, 0] - tile_index * tile_rows
    local_columns = positions[:, 1]
    anchor = jnp.zeros((), jnp.int32)

    def cut_patch(row, column):
        return lax.dynamic_slice(extended, (anchor, row, column), (2, width, width))

    patches = jax.vmap(cut_patch)(local_rows, local_columns)
    number = patches.shape[0]
    forward_block = dft_block(width, -1.0)
    inverse_block = dft_block(width, 1.0)
    coef = jnp.where(
        segment == depth_count - 1, jnp.float32(DETECTOR_COEF), jnp.float32(SLICE_COEF)
    )
    chirp_re, chirp_im = chirp_parts(width, coef)
    start = jnp.broadcast_to(probe[None], (number, 2, width, width))

    def forward_all(waves):
        return propagate(transmit(waves, patches), forward_block, inverse_block, chirp_re, chirp_im)

    def forward_last(waves):
        return residual_wave(forward_all(waves), measured)

    def silent(waves):
        return jnp.zeros_like(waves)

    carry = start
    inputs = start
    for turn in range(depth_count):
        if turn > 0:
            carry = lax.ppermute(carry, "depth", [(turn - 1, turn)])
            inputs = jnp.where(segment == turn, carry, inputs)
        step = forward_last if turn == depth_count - 1 else forward_all
        carry = lax.cond(segment == turn, step, silent, carry)

    def spread_of(incoming):
        return propagate(incoming, forward_block, inverse_block, chirp_re, -chirp_im)

    def back_pass(incoming):
        spread = spread_of(incoming)
        values = spread.astype(jnp.float32)
        passed = jnp.stack(
            [
                patches[:, 0] * values[:, 0] + patches[:, 1] * values[:, 1],
                patches[:, 0] * values[:, 1] - patches[:, 1] * values[:, 0],
            ],
            axis=1,
        ).astype(jnp.bfloat16)
        return (passed, spread)

    def back_silent(incoming):
        return (jnp.zeros_like(incoming), jnp.zeros_like(incoming))

    spread = jnp.zeros_like(start)
    for turn in reversed(range(depth_count)):
        if turn < depth_count - 1:
            carry = lax.ppermute(carry, "depth", [(turn + 1, turn)])
        if turn > 0:
            passed, got = lax.cond(segment == turn, back_pass, back_silent, carry)
        else:
            passed = carry
            got = lax.cond(segment == turn, spread_of, silent, carry)
        spread = jnp.where(segment == turn, got, spread)
        carry = passed

    source = inputs.astype(jnp.float32)
    values = spread.astype(jnp.float32)
    terms = jnp.stack(
        [
            source[:, 0] * values[:, 0] + source[:, 1] * values[:, 1],
            source[:, 0] * values[:, 1] - source[:, 1] * values[:, 0],
        ],
        axis=1,
    )
    weighted = jnp.where(live[:, None, None, None], terms, 0.0)
    gradient = jnp.zeros((2, tile_rows + width, columns_all), jnp.float32)
    for index in range(number):
        place = (anchor, local_rows[index], local_columns[index])
        current = lax.dynamic_slice(gradient, place, (2, width, width))
        gradient = lax.dynamic_update_slice(gradient, current + weighted[index], place)

    own = gradient[:, :tile_rows, :].astype(jnp.bfloat16)
    spill = gradient[:, tile_rows:, :].astype(jnp.bfloat16)
    pairs = [(b, (b + 1) % batch_count) for b in range(batch_count)]
    partner = lax.ppermute(own, "batch", pairs)
    same_core = lax.ppermute(
        spill, "tile", [(t, t + 1) for t in range(tile_count - 1)]
    )
    diagonal = lax.ppermute(
        spill,
        ("tile", "batch"),
        [
            (t * batch_count + b, (t + 1) * batch_count + (b + 1) % batch_count)
            for t in range(tile_count - 1)
            for b in range(batch_count)
        ],
    )
    summed = own.astype(jnp.float32) + partner.astype(jnp.float32)
    spilled = same_core.astype(jnp.float32) + diagonal.astype(jnp.float32)
    summed = summed.at[:, :width, :].add(spilled)
    return summed[None]


def solution(mesh):
    placed = (
        P(("groups", "depth"), None, "tile", None),
        P("groups", None, None),
        P(("groups", "tile", "batch"), None),
        P(("groups", "tile", "batch")),
        P(("groups", "tile", "batch"), None, None),
    )
    return jax.shard_map(
        local,
        mesh=mesh,
        in_specs=placed,
        out_specs=P(("groups", "depth"), None, "tile", None),
        check_vma=False,
    )
```

```python
import math

import jax
import jax.numpy as jnp
from jax import lax
from jax.sharding import PartitionSpec as P
from jax.experimental import pallas as pl

SLICE_COEF = 0.002
DETECTOR_COEF = 0.006
RESIDUAL_SCALE = 0.125


def from_behind(block, axis, distance):
    devices = range(lax.axis_size(axis))
    route = [(i - distance, i) for i in devices if i - distance in devices]
    return lax.ppermute(block, axis, route)


def dft_block(width, sign):
    freq = jnp.arange(width, dtype=jnp.int32)
    product = freq[:, None] * freq[None, :] % width
    angle = 2.0 * math.pi / width * product.astype(jnp.float32)
    scale = 1.0 / math.sqrt(width)
    real_part = (jnp.cos(angle) * scale).astype(jnp.bfloat16)
    imag_part = (sign * jnp.sin(angle) * scale).astype(jnp.bfloat16)
    upper = jnp.concatenate([real_part, -imag_part], axis=1)
    lower = jnp.concatenate([imag_part, real_part], axis=1)
    return jnp.concatenate([upper, lower], axis=0)


def chirp_parts(width, coef):
    freq = jnp.arange(width, dtype=jnp.int32)
    shifted = (freq + width // 2) % width - width // 2
    square = shifted * shifted
    total = (square[:, None] + square[None, :]).astype(jnp.float32)
    phase = -coef * total
    return (jnp.cos(phase), jnp.sin(phase))


def left_apply(block, waves):
    number = waves.shape[0]
    width = waves.shape[2]
    stacked = waves.reshape(number, 2 * width, width)
    result = jnp.einsum("ij,gjk->gik", block, stacked, preferred_element_type=jnp.float32)
    return result.reshape(number, 2, width, width)


def propagate(waves, forward_block, inverse_block, chirp_re, chirp_im):
    first = left_apply(forward_block, waves).astype(jnp.bfloat16)
    spectrum = left_apply(forward_block, jnp.swapaxes(first, -1, -2))
    spec_re = spectrum[:, 0]
    spec_im = spectrum[:, 1]
    filtered = jnp.stack(
        [spec_re * chirp_re - spec_im * chirp_im, spec_re * chirp_im + spec_im * chirp_re], axis=1
    ).astype(jnp.bfloat16)
    back = left_apply(inverse_block, filtered).astype(jnp.bfloat16)
    return left_apply(inverse_block, jnp.swapaxes(back, -1, -2)).astype(jnp.bfloat16)


def transmit(waves, patch):
    values = waves.astype(jnp.float32)
    wave_re = values[:, 0]
    wave_im = values[:, 1]
    return jnp.stack(
        [
            patch[:, 0] * wave_re - patch[:, 1] * wave_im,
            patch[:, 0] * wave_im + patch[:, 1] * wave_re,
        ],
        axis=1,
    ).astype(jnp.bfloat16)


def residual_wave(waves, measured):
    values = waves.astype(jnp.float32)
    intensity = values[:, 0] * values[:, 0] + values[:, 1] * values[:, 1]
    weight = RESIDUAL_SCALE * (intensity - measured)
    return jnp.stack([weight * values[:, 0], weight * values[:, 1]], axis=1).astype(jnp.bfloat16)


def adjoint_terms(incoming, forward_block, inverse_block, chirp_re, chirp_im, inputs, patch):
    spread = propagate(incoming, forward_block, inverse_block, chirp_re, -chirp_im).astype(
        jnp.float32
    )
    source = inputs.astype(jnp.float32)
    term = jnp.stack(
        [
            source[:, 0] * spread[:, 0] + source[:, 1] * spread[:, 1],
            source[:, 0] * spread[:, 1] - source[:, 1] * spread[:, 0],
        ],
        axis=1,
    )
    passed = jnp.stack(
        [
            patch[:, 0] * spread[:, 0] + patch[:, 1] * spread[:, 1],
            patch[:, 0] * spread[:, 1] - patch[:, 1] * spread[:, 0],
        ],
        axis=1,
    ).astype(jnp.bfloat16)
    return (passed, term)


def wave_kernel(transmit_first, residual_after, backward):
    def kernel(*refs):
        refs = list(refs)
        wave_ref = refs.pop(0)
        patch_ref = refs.pop(0)
        chirp_ref = refs.pop(0)
        fl_ref, fr_ref, gl_ref, gr_ref = refs[:4]
        refs = refs[4:]
        extra_ref = refs.pop(0) if (residual_after or backward) else None
        width = wave_ref.shape[2]
        wave = wave_ref[0].astype(jnp.float32)
        patch_re = patch_ref[0, 0]
        patch_im = patch_ref[0, 1]
        if transmit_first:
            wave_re = patch_re * wave[0] - patch_im * wave[1]
            wave_im = patch_re * wave[1] + patch_im * wave[0]
        else:
            wave_re = wave[0]
            wave_im = wave[1]
        stacked = jnp.concatenate([wave_re, wave_im], axis=0).astype(jnp.bfloat16)
        first = jnp.dot(fl_ref[...], stacked, preferred_element_type=jnp.float32).astype(jnp.bfloat16)
        rowwise = jnp.concatenate([first[:width], first[width:]], axis=1)
        spectrum = jnp.dot(rowwise, fr_ref[...], preferred_element_type=jnp.float32)
        spec_re = spectrum[:, :width]
        spec_im = spectrum[:, width:]
        chirp_re = chirp_ref[0]
        chirp_im = chirp_ref[1]
        if backward:
            chirp_im = -chirp_im
        filtered = jnp.concatenate(
            [spec_re * chirp_re - spec_im * chirp_im, spec_re * chirp_im + spec_im * chirp_re],
            axis=1,
        ).astype(jnp.bfloat16)
        back = jnp.dot(filtered, gr_ref[...], preferred_element_type=jnp.float32).astype(jnp.bfloat16)
        columnwise = jnp.concatenate([back[:, :width], back[:, width:]], axis=0)
        out = jnp.dot(gl_ref[...], columnwise, preferred_element_type=jnp.float32).astype(jnp.bfloat16)
        values = out.astype(jnp.float32)
        out_re = values[:width]
        out_im = values[width:]
        if residual_after:
            measured = extra_ref[0]
            weight = RESIDUAL_SCALE * (out_re * out_re + out_im * out_im - measured)
            result_ref = refs[0]
            result_ref[0, 0] = (weight * out_re).astype(jnp.bfloat16)
            result_ref[0, 1] = (weight * out_im).astype(jnp.bfloat16)
        elif backward:
            source = extra_ref[0].astype(jnp.float32)
            passed_ref, term_ref = refs[0], refs[1]
            passed_ref[0, 0] = (patch_re * out_re + patch_im * out_im).astype(jnp.bfloat16)
            passed_ref[0, 1] = (patch_re * out_im - patch_im * out_re).astype(jnp.bfloat16)
            term_ref[0, 0] = source[0] * out_re + source[1] * out_im
            term_ref[0, 1] = source[0] * out_im - source[1] * out_re
        else:
            result_ref = refs[0]
            result_ref[0, 0] = out[:width]
            result_ref[0, 1] = out[width:]

    return kernel


def run_waves(waves, patches, chirps, blocks, extra=None, transmit_first=True, residual_after=False, backward=False):
    number, _, width, _ = waves.shape
    wave_spec = pl.BlockSpec((1, 2, width, width), lambda i: (i, 0, 0, 0))
    chirp_spec = pl.BlockSpec((2, width, width), lambda i: (0, 0, 0))
    block_spec = pl.BlockSpec((2 * width, 2 * width), lambda i: (0, 0))
    in_specs = [wave_spec, wave_spec, chirp_spec] + [block_spec] * 4
    args = [waves, patches, chirps] + list(blocks)
    if residual_after:
        in_specs.append(pl.BlockSpec((1, width, width), lambda i: (i, 0, 0)))
        args.append(extra)
    if backward:
        in_specs.append(wave_spec)
        args.append(extra)
        out_shape = (
            jax.ShapeDtypeStruct(waves.shape, jnp.bfloat16),
            jax.ShapeDtypeStruct(waves.shape, jnp.float32),
        )
        out_specs = (wave_spec, wave_spec)
    else:
        out_shape = jax.ShapeDtypeStruct(waves.shape, jnp.bfloat16)
        out_specs = wave_spec
    return pl.pallas_call(
        wave_kernel(transmit_first, residual_after, backward),
        grid=(number,),
        in_specs=in_specs,
        out_specs=out_specs,
        out_shape=out_shape,
    )(*args)


def local(object_field, probe, positions, counts, measured):
    width = probe.shape[1]
    tile_rows = object_field.shape[2]
    columns_all = object_field.shape[3]
    tile_index = lax.axis_index("tile")
    tile_count = lax.axis_size("tile")
    segment = lax.axis_index("depth")
    depth_count = lax.axis_size("depth")
    batch_index = lax.axis_index("batch")
    batch_count = lax.axis_size("batch")
    rim = from_behind(object_field[:, :, :width, :], "tile", -1)
    extended = jnp.concatenate([object_field, rim], axis=2)[0]
    capacity = positions.shape[0]
    live = jnp.arange(capacity, dtype=jnp.int32) < counts[0]
    local_rows = positions[:, 0] - tile_index * tile_rows
    local_columns = positions[:, 1]
    anchor = jnp.zeros((), jnp.int32)

    def cut_patch(row, column):
        return lax.dynamic_slice(extended, (anchor, row, column), (2, width, width))

    patches = jax.vmap(cut_patch)(local_rows, local_columns)
    number = patches.shape[0]
    forward_block = dft_block(width, -1.0)
    inverse_block = dft_block(width, 1.0)
    coef = jnp.where(
        segment == depth_count - 1, jnp.float32(DETECTOR_COEF), jnp.float32(SLICE_COEF)
    )
    chirp_re, chirp_im = chirp_parts(width, coef)
    start = jnp.broadcast_to(probe[None], (number, 2, width, width))

    chirps = jnp.stack([chirp_re, chirp_im])
    blocks = (forward_block, forward_block.T, inverse_block, inverse_block.T)

    def forward_all(waves):
        return run_waves(waves, patches, chirps, blocks)

    def forward_last(waves):
        return run_waves(waves, patches, chirps, blocks, measured, residual_after=True)

    def silent(waves):
        return jnp.zeros_like(waves)

    carry = start
    inputs = start
    for turn in range(depth_count):
        if turn > 0:
            carry = lax.ppermute(carry, "depth", [(turn - 1, turn)])
            inputs = jnp.where(segment == turn, carry, inputs)
        step = forward_last if turn == depth_count - 1 else forward_all
        carry = lax.cond(segment == turn, step, silent, carry)

    def back_pass(incoming):
        return run_waves(
            incoming, patches, chirps, blocks, inputs, transmit_first=False, backward=True
        )

    def back_silent(incoming):
        return (jnp.zeros_like(incoming), jnp.zeros(incoming.shape, jnp.float32))

    terms = jnp.zeros(start.shape, jnp.float32)
    for turn in reversed(range(depth_count)):
        if turn < depth_count - 1:
            carry = lax.ppermute(carry, "depth", [(turn + 1, turn)])
        carry, got = lax.cond(segment == turn, back_pass, back_silent, carry)
        terms = jnp.where(segment == turn, got, terms)

    weighted = jnp.where(live[:, None, None, None], terms, 0.0)
    gradient = jnp.zeros((2, tile_rows + width, columns_all), jnp.float32)
    for index in range(number):
        place = (anchor, local_rows[index], local_columns[index])
        current = lax.dynamic_slice(gradient, place, (2, width, width))
        gradient = lax.dynamic_update_slice(gradient, current + weighted[index], place)

    own = gradient[:, :tile_rows, :].astype(jnp.bfloat16)
    spill = gradient[:, tile_rows:, :].astype(jnp.bfloat16)
    pairs = [(b, (b + 1) % batch_count) for b in range(batch_count)]
    partner = lax.ppermute(own, "batch", pairs)
    same_core = lax.ppermute(
        spill, "tile", [(t, t + 1) for t in range(tile_count - 1)]
    )
    diagonal = lax.ppermute(
        spill,
        ("tile", "batch"),
        [
            (t * batch_count + b, (t + 1) * batch_count + (b + 1) % batch_count)
            for t in range(tile_count - 1)
            for b in range(batch_count)
        ],
    )
    summed = own.astype(jnp.float32) + partner.astype(jnp.float32)
    spilled = same_core.astype(jnp.float32) + diagonal.astype(jnp.float32)
    summed = summed.at[:, :width, :].add(spilled)
    return summed[None]


def solution(mesh):
    placed = (
        P(("groups", "depth"), None, "tile", None),
        P("groups", None, None),
        P(("groups", "tile", "batch"), None),
        P(("groups", "tile", "batch")),
        P(("groups", "tile", "batch"), None, None),
    )
    return jax.shard_map(
        local,
        mesh=mesh,
        in_specs=placed,
        out_specs=P(("groups", "depth"), None, "tile", None),
        check_vma=False,
    )
```

```python
import math

import jax
import jax.numpy as jnp
from jax import lax
from jax.sharding import PartitionSpec as P
from jax.experimental import pallas as pl
from jax.experimental.pallas import tpu as pltpu

SLICE_COEF = 0.002
DETECTOR_COEF = 0.006
RESIDUAL_SCALE = 0.125


def from_behind(block, axis, distance):
    devices = range(lax.axis_size(axis))
    route = [(i - distance, i) for i in devices if i - distance in devices]
    return lax.ppermute(block, axis, route)


def dft_block(width, sign):
    freq = jnp.arange(width, dtype=jnp.int32)
    product = freq[:, None] * freq[None, :] % width
    angle = 2.0 * math.pi / width * product.astype(jnp.float32)
    scale = 1.0 / math.sqrt(width)
    real_part = (jnp.cos(angle) * scale).astype(jnp.bfloat16)
    imag_part = (sign * jnp.sin(angle) * scale).astype(jnp.bfloat16)
    upper = jnp.concatenate([real_part, -imag_part], axis=1)
    lower = jnp.concatenate([imag_part, real_part], axis=1)
    return jnp.concatenate([upper, lower], axis=0)


def dft_right(width, sign):
    freq = jnp.arange(width, dtype=jnp.int32)
    product = freq[:, None] * freq[None, :] % width
    angle = 2.0 * math.pi / width * product.astype(jnp.float32)
    scale = 1.0 / math.sqrt(width)
    real_part = (jnp.cos(angle) * scale).astype(jnp.bfloat16)
    imag_part = (sign * jnp.sin(angle) * scale).astype(jnp.bfloat16)
    upper = jnp.concatenate([real_part, imag_part], axis=1)
    lower = jnp.concatenate([-imag_part, real_part], axis=1)
    return jnp.concatenate([upper, lower], axis=0)


def chirp_parts(width, coef):
    freq = jnp.arange(width, dtype=jnp.int32)
    shifted = (freq + width // 2) % width - width // 2
    square = shifted * shifted
    total = (square[:, None] + square[None, :]).astype(jnp.float32)
    phase = -coef * total
    return (jnp.cos(phase), jnp.sin(phase))


def left_apply(block, waves):
    number = waves.shape[0]
    width = waves.shape[2]
    stacked = waves.reshape(number, 2 * width, width)
    result = jnp.einsum("ij,gjk->gik", block, stacked, preferred_element_type=jnp.float32)
    return result.reshape(number, 2, width, width)


def propagate(waves, forward_block, inverse_block, chirp_re, chirp_im):
    first = left_apply(forward_block, waves).astype(jnp.bfloat16)
    spectrum = left_apply(forward_block, jnp.swapaxes(first, -1, -2))
    spec_re = spectrum[:, 0]
    spec_im = spectrum[:, 1]
    filtered = jnp.stack(
        [spec_re * chirp_re - spec_im * chirp_im, spec_re * chirp_im + spec_im * chirp_re], axis=1
    ).astype(jnp.bfloat16)
    back = left_apply(inverse_block, filtered).astype(jnp.bfloat16)
    return left_apply(inverse_block, jnp.swapaxes(back, -1, -2)).astype(jnp.bfloat16)


def transmit(waves, patch):
    values = waves.astype(jnp.float32)
    wave_re = values[:, 0]
    wave_im = values[:, 1]
    return jnp.stack(
        [
            patch[:, 0] * wave_re - patch[:, 1] * wave_im,
            patch[:, 0] * wave_im + patch[:, 1] * wave_re,
        ],
        axis=1,
    ).astype(jnp.bfloat16)


def residual_wave(waves, measured):
    values = waves.astype(jnp.float32)
    intensity = values[:, 0] * values[:, 0] + values[:, 1] * values[:, 1]
    weight = RESIDUAL_SCALE * (intensity - measured)
    return jnp.stack([weight * values[:, 0], weight * values[:, 1]], axis=1).astype(jnp.bfloat16)


def adjoint_terms(incoming, forward_block, inverse_block, chirp_re, chirp_im, inputs, patch):
    spread = propagate(incoming, forward_block, inverse_block, chirp_re, -chirp_im).astype(
        jnp.float32
    )
    source = inputs.astype(jnp.float32)
    term = jnp.stack(
        [
            source[:, 0] * spread[:, 0] + source[:, 1] * spread[:, 1],
            source[:, 0] * spread[:, 1] - source[:, 1] * spread[:, 0],
        ],
        axis=1,
    )
    passed = jnp.stack(
        [
            patch[:, 0] * spread[:, 0] + patch[:, 1] * spread[:, 1],
            patch[:, 0] * spread[:, 1] - patch[:, 1] * spread[:, 0],
        ],
        axis=1,
    ).astype(jnp.bfloat16)
    return (passed, term)


def wave_kernel(transmit_first, residual_after, backward):
    def kernel(*refs):
        refs = list(refs)
        wave_ref = refs.pop(0)
        patch_ref = refs.pop(0)
        chirp_ref = refs.pop(0)
        fl_ref, fr_ref, gl_ref, gr_ref = refs[:4]
        refs = refs[4:]
        extra_ref = refs.pop(0) if (residual_after or backward) else None
        width = wave_ref.shape[2]
        wave = wave_ref[0].astype(jnp.float32)
        patch_re = patch_ref[0, 0]
        patch_im = patch_ref[0, 1]
        if transmit_first:
            wave_re = patch_re * wave[0] - patch_im * wave[1]
            wave_im = patch_re * wave[1] + patch_im * wave[0]
        else:
            wave_re = wave[0]
            wave_im = wave[1]
        stacked = jnp.concatenate([wave_re, wave_im], axis=0).astype(jnp.bfloat16)
        first = jnp.dot(fl_ref[...], stacked, preferred_element_type=jnp.float32).astype(jnp.bfloat16)
        rowwise = jnp.concatenate([first[:width], first[width:]], axis=1)
        spectrum = jnp.dot(rowwise, fr_ref[...], preferred_element_type=jnp.float32)
        spec_re = spectrum[:, :width]
        spec_im = spectrum[:, width:]
        chirp_re = chirp_ref[0]
        chirp_im = chirp_ref[1]
        if backward:
            chirp_im = -chirp_im
        filtered = jnp.concatenate(
            [spec_re * chirp_re - spec_im * chirp_im, spec_re * chirp_im + spec_im * chirp_re],
            axis=1,
        ).astype(jnp.bfloat16)
        back = jnp.dot(filtered, gr_ref[...], preferred_element_type=jnp.float32).astype(jnp.bfloat16)
        columnwise = jnp.concatenate([back[:, :width], back[:, width:]], axis=0)
        out = jnp.dot(gl_ref[...], columnwise, preferred_element_type=jnp.float32).astype(jnp.bfloat16)
        values = out.astype(jnp.float32)
        out_re = values[:width]
        out_im = values[width:]
        if residual_after:
            measured = extra_ref[0]
            weight = RESIDUAL_SCALE * (out_re * out_re + out_im * out_im - measured)
            result_ref = refs[0]
            result_ref[0, 0] = (weight * out_re).astype(jnp.bfloat16)
            result_ref[0, 1] = (weight * out_im).astype(jnp.bfloat16)
        elif backward:
            source = extra_ref[0].astype(jnp.float32)
            passed_ref, term_ref = refs[0], refs[1]
            passed_ref[0, 0] = (patch_re * out_re + patch_im * out_im).astype(jnp.bfloat16)
            passed_ref[0, 1] = (patch_re * out_im - patch_im * out_re).astype(jnp.bfloat16)
            term_ref[0, 0] = source[0] * out_re + source[1] * out_im
            term_ref[0, 1] = source[0] * out_im - source[1] * out_re
        else:
            result_ref = refs[0]
            result_ref[0, 0] = out[:width]
            result_ref[0, 1] = out[width:]

    return kernel


def run_waves(waves, patches, chirps, blocks, extra=None, transmit_first=True, residual_after=False, backward=False):
    number, _, width, _ = waves.shape
    wave_spec = pl.BlockSpec((1, 2, width, width), lambda i: (i, 0, 0, 0))
    chirp_spec = pl.BlockSpec((2, width, width), lambda i: (0, 0, 0))
    block_spec = pl.BlockSpec((2 * width, 2 * width), lambda i: (0, 0))
    in_specs = [wave_spec, wave_spec, chirp_spec] + [block_spec] * 4
    args = [waves, patches, chirps] + list(blocks)
    if residual_after:
        in_specs.append(pl.BlockSpec((1, width, width), lambda i: (i, 0, 0)))
        args.append(extra)
    if backward:
        in_specs.append(wave_spec)
        args.append(extra)
        out_shape = (
            jax.ShapeDtypeStruct(waves.shape, jnp.bfloat16),
            jax.ShapeDtypeStruct(waves.shape, jnp.float32),
        )
        out_specs = (wave_spec, wave_spec)
    else:
        out_shape = jax.ShapeDtypeStruct(waves.shape, jnp.bfloat16)
        out_specs = wave_spec
    return pl.pallas_call(
        wave_kernel(transmit_first, residual_after, backward),
        grid=(number,),
        in_specs=in_specs,
        out_specs=out_specs,
        out_shape=out_shape,
    )(*args)


def scatter_kernel(rows_ref, columns_ref, live_ref, terms_ref, out_ref):
    index = pl.program_id(0)

    @pl.when(index == 0)
    def _():
        out_ref[...] = jnp.zeros(out_ref.shape, out_ref.dtype)

    width = terms_ref.shape[2]
    height = out_ref.shape[1]
    columns_all = out_ref.shape[2]
    row = rows_ref[index]
    column = columns_ref[index]
    alive = live_ref[index] > 0
    for part in range(2):
        term = jnp.where(alive, terms_ref[0, part], 0.0)
        wide = jnp.concatenate(
            [term, jnp.zeros((width, columns_all - width), jnp.float32)], axis=1
        )
        wide = pltpu.roll(wide, column, 1)
        tall = jnp.concatenate(
            [wide, jnp.zeros((height - width, columns_all), jnp.float32)], axis=0
        )
        tall = pltpu.roll(tall, row, 0)
        out_ref[part] = out_ref[part] + tall


def scatter_terms(terms, rows, columns, live, height, columns_all):
    number, _, width, _ = terms.shape
    grid_spec = pltpu.PrefetchScalarGridSpec(
        num_scalar_prefetch=3,
        grid=(number,),
        in_specs=[pl.BlockSpec((1, 2, width, width), lambda i, r, c, a: (i, 0, 0, 0))],
        out_specs=pl.BlockSpec((2, height, columns_all), lambda i, r, c, a: (0, 0, 0)),
    )
    return pl.pallas_call(
        scatter_kernel,
        grid_spec=grid_spec,
        out_shape=jax.ShapeDtypeStruct((2, height, columns_all), jnp.float32),
    )(rows, columns, live.astype(jnp.int32), terms)


def local(object_field, probe, positions, counts, measured):
    width = probe.shape[1]
    tile_rows = object_field.shape[2]
    columns_all = object_field.shape[3]
    tile_index = lax.axis_index("tile")
    tile_count = lax.axis_size("tile")
    segment = lax.axis_index("depth")
    depth_count = lax.axis_size("depth")
    batch_index = lax.axis_index("batch")
    batch_count = lax.axis_size("batch")
    rim = from_behind(object_field[:, :, :width, :], "tile", -1)
    extended = jnp.concatenate([object_field, rim], axis=2)[0]
    capacity = positions.shape[0]
    live = jnp.arange(capacity, dtype=jnp.int32) < counts[0]
    local_rows = positions[:, 0] - tile_index * tile_rows
    local_columns = positions[:, 1]
    anchor = jnp.zeros((), jnp.int32)

    def cut_patch(row, column):
        return lax.dynamic_slice(extended, (anchor, row, column), (2, width, width))

    patches = jax.vmap(cut_patch)(local_rows, local_columns)
    number = patches.shape[0]
    forward_block = dft_block(width, -1.0)
    inverse_block = dft_block(width, 1.0)
    coef = jnp.where(
        segment == depth_count - 1, jnp.float32(DETECTOR_COEF), jnp.float32(SLICE_COEF)
    )
    chirp_re, chirp_im = chirp_parts(width, coef)
    start = jnp.broadcast_to(probe[None], (number, 2, width, width))

    chirps = jnp.stack([chirp_re, chirp_im])
    blocks = (forward_block, dft_right(width, -1.0), inverse_block, dft_right(width, 1.0))

    def forward_all(waves):
        return run_waves(waves, patches, chirps, blocks)

    def forward_last(waves):
        return run_waves(waves, patches, chirps, blocks, measured, residual_after=True)

    def silent(waves):
        return jnp.zeros_like(waves)

    carry = start
    inputs = start
    for turn in range(depth_count):
        if turn > 0:
            carry = lax.ppermute(carry, "depth", [(turn - 1, turn)])
            inputs = jnp.where(segment == turn, carry, inputs)
        step = forward_last if turn == depth_count - 1 else forward_all
        carry = lax.cond(segment == turn, step, silent, carry)

    def back_pass(incoming):
        return run_waves(
            incoming, patches, chirps, blocks, inputs, transmit_first=False, backward=True
        )

    def back_silent(incoming):
        return (jnp.zeros_like(incoming), jnp.zeros(incoming.shape, jnp.float32))

    terms = jnp.zeros(start.shape, jnp.float32)
    for turn in reversed(range(depth_count)):
        if turn < depth_count - 1:
            carry = lax.ppermute(carry, "depth", [(turn + 1, turn)])
        carry, got = lax.cond(segment == turn, back_pass, back_silent, carry)
        terms = jnp.where(segment == turn, got, terms)

    gradient = scatter_terms(
        terms, local_rows, local_columns, live, tile_rows + width, columns_all
    )
    spill = gradient[:, tile_rows:, :].astype(jnp.bfloat16)
    arrived = lax.ppermute(spill, "tile", [(t, t + 1) for t in range(tile_count - 1)])
    own = gradient[:, :tile_rows, :]
    own = own.at[:, :width, :].add(arrived.astype(jnp.float32)).astype(jnp.bfloat16)
    pairs = [(b, (b + 1) % batch_count) for b in range(batch_count)]
    partner = lax.ppermute(own, "batch", pairs)
    summed = own.astype(jnp.float32) + partner.astype(jnp.float32)
    return summed[None]


def solution(mesh):
    placed = (
        P(("groups", "depth"), None, "tile", None),
        P("groups", None, None),
        P(("groups", "tile", "batch"), None),
        P(("groups", "tile", "batch")),
        P(("groups", "tile", "batch"), None, None),
    )
    return jax.shard_map(
        local,
        mesh=mesh,
        in_specs=placed,
        out_specs=P(("groups", "depth"), None, "tile", None),
        check_vma=False,
    )
```

```python
import math

import jax
import jax.numpy as jnp
from jax import lax
from jax.sharding import PartitionSpec as P
from jax.experimental import pallas as pl
from jax.experimental.pallas import tpu as pltpu

SLICE_COEF = 0.002
DETECTOR_COEF = 0.006
RESIDUAL_SCALE = 0.125


def from_behind(block, axis, distance):
    devices = range(lax.axis_size(axis))
    route = [(i - distance, i) for i in devices if i - distance in devices]
    return lax.ppermute(block, axis, route)


def dft_block(width, sign):
    freq = jnp.arange(width, dtype=jnp.int32)
    product = freq[:, None] * freq[None, :] % width
    angle = 2.0 * math.pi / width * product.astype(jnp.float32)
    scale = 1.0 / math.sqrt(width)
    real_part = (jnp.cos(angle) * scale).astype(jnp.bfloat16)
    imag_part = (sign * jnp.sin(angle) * scale).astype(jnp.bfloat16)
    upper = jnp.concatenate([real_part, -imag_part], axis=1)
    lower = jnp.concatenate([imag_part, real_part], axis=1)
    return jnp.concatenate([upper, lower], axis=0)


def dft_right(width, sign):
    freq = jnp.arange(width, dtype=jnp.int32)
    product = freq[:, None] * freq[None, :] % width
    angle = 2.0 * math.pi / width * product.astype(jnp.float32)
    scale = 1.0 / math.sqrt(width)
    real_part = (jnp.cos(angle) * scale).astype(jnp.bfloat16)
    imag_part = (sign * jnp.sin(angle) * scale).astype(jnp.bfloat16)
    upper = jnp.concatenate([real_part, imag_part], axis=1)
    lower = jnp.concatenate([-imag_part, real_part], axis=1)
    return jnp.concatenate([upper, lower], axis=0)


def chirp_parts(width, coef):
    freq = jnp.arange(width, dtype=jnp.int32)
    shifted = (freq + width // 2) % width - width // 2
    square = shifted * shifted
    total = (square[:, None] + square[None, :]).astype(jnp.float32)
    phase = -coef * total
    return (jnp.cos(phase), jnp.sin(phase))


def left_apply(block, waves):
    number = waves.shape[0]
    width = waves.shape[2]
    stacked = waves.reshape(number, 2 * width, width)
    result = jnp.einsum("ij,gjk->gik", block, stacked, preferred_element_type=jnp.float32)
    return result.reshape(number, 2, width, width)


def propagate(waves, forward_block, inverse_block, chirp_re, chirp_im):
    first = left_apply(forward_block, waves).astype(jnp.bfloat16)
    spectrum = left_apply(forward_block, jnp.swapaxes(first, -1, -2))
    spec_re = spectrum[:, 0]
    spec_im = spectrum[:, 1]
    filtered = jnp.stack(
        [spec_re * chirp_re - spec_im * chirp_im, spec_re * chirp_im + spec_im * chirp_re], axis=1
    ).astype(jnp.bfloat16)
    back = left_apply(inverse_block, filtered).astype(jnp.bfloat16)
    return left_apply(inverse_block, jnp.swapaxes(back, -1, -2)).astype(jnp.bfloat16)


def transmit(waves, patch):
    values = waves.astype(jnp.float32)
    wave_re = values[:, 0]
    wave_im = values[:, 1]
    return jnp.stack(
        [
            patch[:, 0] * wave_re - patch[:, 1] * wave_im,
            patch[:, 0] * wave_im + patch[:, 1] * wave_re,
        ],
        axis=1,
    ).astype(jnp.bfloat16)


def residual_wave(waves, measured):
    values = waves.astype(jnp.float32)
    intensity = values[:, 0] * values[:, 0] + values[:, 1] * values[:, 1]
    weight = RESIDUAL_SCALE * (intensity - measured)
    return jnp.stack([weight * values[:, 0], weight * values[:, 1]], axis=1).astype(jnp.bfloat16)


def adjoint_terms(incoming, forward_block, inverse_block, chirp_re, chirp_im, inputs, patch):
    spread = propagate(incoming, forward_block, inverse_block, chirp_re, -chirp_im).astype(
        jnp.float32
    )
    source = inputs.astype(jnp.float32)
    term = jnp.stack(
        [
            source[:, 0] * spread[:, 0] + source[:, 1] * spread[:, 1],
            source[:, 0] * spread[:, 1] - source[:, 1] * spread[:, 0],
        ],
        axis=1,
    )
    passed = jnp.stack(
        [
            patch[:, 0] * spread[:, 0] + patch[:, 1] * spread[:, 1],
            patch[:, 0] * spread[:, 1] - patch[:, 1] * spread[:, 0],
        ],
        axis=1,
    ).astype(jnp.bfloat16)
    return (passed, term)


def wave_kernel(transmit_first, residual_after, backward):
    def kernel(*refs):
        refs = list(refs)
        wave_ref = refs.pop(0)
        patch_ref = refs.pop(0)
        chirp_ref = refs.pop(0)
        fl_ref, fr_ref, gl_ref, gr_ref = refs[:4]
        refs = refs[4:]
        extra_ref = refs.pop(0) if (residual_after or backward) else None
        width = wave_ref.shape[2]
        wave = wave_ref[0].astype(jnp.float32)
        patch_re = patch_ref[0, 0]
        patch_im = patch_ref[0, 1]
        if transmit_first:
            wave_re = patch_re * wave[0] - patch_im * wave[1]
            wave_im = patch_re * wave[1] + patch_im * wave[0]
        else:
            wave_re = wave[0]
            wave_im = wave[1]
        stacked = jnp.concatenate([wave_re, wave_im], axis=0).astype(jnp.bfloat16)
        first = jnp.dot(fl_ref[...], stacked, preferred_element_type=jnp.float32).astype(jnp.bfloat16)
        rowwise = jnp.concatenate([first[:width], first[width:]], axis=1)
        spectrum = jnp.dot(rowwise, fr_ref[...], preferred_element_type=jnp.float32)
        spec_re = spectrum[:, :width]
        spec_im = spectrum[:, width:]
        chirp_re = chirp_ref[0]
        chirp_im = chirp_ref[1]
        if backward:
            chirp_im = -chirp_im
        filtered = jnp.concatenate(
            [spec_re * chirp_re - spec_im * chirp_im, spec_re * chirp_im + spec_im * chirp_re],
            axis=1,
        ).astype(jnp.bfloat16)
        back = jnp.dot(filtered, gr_ref[...], preferred_element_type=jnp.float32).astype(jnp.bfloat16)
        columnwise = jnp.concatenate([back[:, :width], back[:, width:]], axis=0)
        out = jnp.dot(gl_ref[...], columnwise, preferred_element_type=jnp.float32).astype(jnp.bfloat16)
        values = out.astype(jnp.float32)
        out_re = values[:width]
        out_im = values[width:]
        if residual_after:
            measured = extra_ref[0]
            weight = RESIDUAL_SCALE * (out_re * out_re + out_im * out_im - measured)
            result_ref = refs[0]
            result_ref[0, 0] = (weight * out_re).astype(jnp.bfloat16)
            result_ref[0, 1] = (weight * out_im).astype(jnp.bfloat16)
        elif backward:
            source = extra_ref[0].astype(jnp.float32)
            passed_ref, term_ref = refs[0], refs[1]
            passed_ref[0, 0] = (patch_re * out_re + patch_im * out_im).astype(jnp.bfloat16)
            passed_ref[0, 1] = (patch_re * out_im - patch_im * out_re).astype(jnp.bfloat16)
            term_ref[0, 0] = source[0] * out_re + source[1] * out_im
            term_ref[0, 1] = source[0] * out_im - source[1] * out_re
        else:
            result_ref = refs[0]
            result_ref[0, 0] = out[:width]
            result_ref[0, 1] = out[width:]

    return kernel


def run_waves(waves, patches, chirps, blocks, extra=None, transmit_first=True, residual_after=False, backward=False):
    number, _, width, _ = waves.shape
    wave_spec = pl.BlockSpec((1, 2, width, width), lambda i: (i, 0, 0, 0))
    chirp_spec = pl.BlockSpec((2, width, width), lambda i: (0, 0, 0))
    block_spec = pl.BlockSpec((2 * width, 2 * width), lambda i: (0, 0))
    in_specs = [wave_spec, wave_spec, chirp_spec] + [block_spec] * 4
    args = [waves, patches, chirps] + list(blocks)
    if residual_after:
        in_specs.append(pl.BlockSpec((1, width, width), lambda i: (i, 0, 0)))
        args.append(extra)
    if backward:
        in_specs.append(wave_spec)
        args.append(extra)
        out_shape = (
            jax.ShapeDtypeStruct(waves.shape, jnp.bfloat16),
            jax.ShapeDtypeStruct(waves.shape, jnp.float32),
        )
        out_specs = (wave_spec, wave_spec)
    else:
        out_shape = jax.ShapeDtypeStruct(waves.shape, jnp.bfloat16)
        out_specs = wave_spec
    return pl.pallas_call(
        wave_kernel(transmit_first, residual_after, backward),
        grid=(number,),
        in_specs=in_specs,
        out_specs=out_specs,
        out_shape=out_shape,
    )(*args)


def scatter_kernel(rows_ref, columns_ref, live_ref, terms_ref, out_ref):
    index = pl.program_id(0)

    @pl.when(index == 0)
    def _():
        out_ref[...] = jnp.zeros(out_ref.shape, out_ref.dtype)

    width = terms_ref.shape[2]
    height = out_ref.shape[1]
    columns_all = out_ref.shape[2]
    row = rows_ref[index]
    column = columns_ref[index]
    alive = live_ref[index] > 0
    for part in range(2):
        term = jnp.where(alive, terms_ref[0, part], 0.0)
        wide = jnp.concatenate(
            [term, jnp.zeros((width, columns_all - width), jnp.float32)], axis=1
        )
        wide = pltpu.roll(wide, column, 1)
        tall = jnp.concatenate(
            [wide, jnp.zeros((height - width, columns_all), jnp.float32)], axis=0
        )
        tall = pltpu.roll(tall, row, 0)
        out_ref[part] = out_ref[part] + tall


def scatter_terms(terms, rows, columns, live, height, columns_all):
    number, _, width, _ = terms.shape
    grid_spec = pltpu.PrefetchScalarGridSpec(
        num_scalar_prefetch=3,
        grid=(number,),
        in_specs=[pl.BlockSpec((1, 2, width, width), lambda i, r, c, a: (i, 0, 0, 0))],
        out_specs=pl.BlockSpec((2, height, columns_all), lambda i, r, c, a: (0, 0, 0)),
    )
    return pl.pallas_call(
        scatter_kernel,
        grid_spec=grid_spec,
        out_shape=jax.ShapeDtypeStruct((2, height, columns_all), jnp.float32),
    )(rows, columns, live.astype(jnp.int32), terms)


def cut_kernel(rows_ref, columns_ref, order_ref, tile_ref, mine_ref, partner_ref, out_ref):
    index = pl.program_id(0)
    width = out_ref.shape[2]
    height = tile_ref.shape[2] + mine_ref.shape[2]
    columns_all = tile_ref.shape[3]
    row_shift = (height - rows_ref[index]) % height
    column_shift = (columns_all - columns_ref[index]) % columns_all
    first = order_ref[0] == 0
    for part in range(2):
        mine = mine_ref[0, part]
        partner = partner_ref[0, part]
        rim = jnp.concatenate(
            [jnp.where(first, mine, partner), jnp.where(first, partner, mine)], axis=1
        )
        full = jnp.concatenate([tile_ref[0, part], rim], axis=0)
        full = pltpu.roll(full, row_shift, 0)[:width]
        full = pltpu.roll(full, column_shift, 1)[:, :width]
        out_ref[0, part] = full


def cut_patches(tile, mine, partner, rows, columns, order, width):
    number = rows.shape[0]
    grid_spec = pltpu.PrefetchScalarGridSpec(
        num_scalar_prefetch=3,
        grid=(number,),
        in_specs=[
            pl.BlockSpec(tile.shape, lambda i, r, c, o: (0, 0, 0, 0)),
            pl.BlockSpec(mine.shape, lambda i, r, c, o: (0, 0, 0, 0)),
            pl.BlockSpec(partner.shape, lambda i, r, c, o: (0, 0, 0, 0)),
        ],
        out_specs=pl.BlockSpec((1, 2, width, width), lambda i, r, c, o: (i, 0, 0, 0)),
    )
    return pl.pallas_call(
        cut_kernel,
        grid_spec=grid_spec,
        out_shape=jax.ShapeDtypeStruct((number, 2, width, width), jnp.float32),
    )(rows, columns, order, tile, mine, partner)


def local(object_field, probe, positions, counts, measured):
    width = probe.shape[1]
    tile_rows = object_field.shape[2]
    columns_all = object_field.shape[3]
    tile_index = lax.axis_index("tile")
    tile_count = lax.axis_size("tile")
    segment = lax.axis_index("depth")
    depth_count = lax.axis_size("depth")
    batch_index = lax.axis_index("batch")
    batch_count = lax.axis_size("batch")
    half = columns_all // batch_count
    wanted = lax.dynamic_slice_in_dim(object_field[:, :, :width, :], batch_index * half, half, 3)
    mine = from_behind(wanted, "tile", -1)
    pairs = [(b, (b + 1) % batch_count) for b in range(batch_count)]
    partner = lax.ppermute(mine, "batch", pairs)
    capacity = positions.shape[0]
    live = jnp.arange(capacity, dtype=jnp.int32) < counts[0]
    local_rows = positions[:, 0] - tile_index * tile_rows
    local_columns = positions[:, 1]
    order = jnp.reshape(batch_index, (1,)).astype(jnp.int32)
    patches = cut_patches(object_field, mine, partner, local_rows, local_columns, order, width)
    number = patches.shape[0]
    forward_block = dft_block(width, -1.0)
    inverse_block = dft_block(width, 1.0)
    coef = jnp.where(
        segment == depth_count - 1, jnp.float32(DETECTOR_COEF), jnp.float32(SLICE_COEF)
    )
    chirp_re, chirp_im = chirp_parts(width, coef)
    start = jnp.broadcast_to(probe[None], (number, 2, width, width))

    chirps = jnp.stack([chirp_re, chirp_im])
    blocks = (forward_block, dft_right(width, -1.0), inverse_block, dft_right(width, 1.0))

    def forward_all(waves):
        return run_waves(waves, patches, chirps, blocks)

    def forward_last(waves):
        return run_waves(waves, patches, chirps, blocks, measured, residual_after=True)

    def silent(waves):
        return jnp.zeros_like(waves)

    carry = start
    inputs = start
    for turn in range(depth_count):
        if turn > 0:
            carry = lax.ppermute(carry, "depth", [(turn - 1, turn)])
            inputs = jnp.where(segment == turn, carry, inputs)
        step = forward_last if turn == depth_count - 1 else forward_all
        carry = lax.cond(segment == turn, step, silent, carry)

    def back_pass(incoming):
        return run_waves(
            incoming, patches, chirps, blocks, inputs, transmit_first=False, backward=True
        )

    def back_silent(incoming):
        return (jnp.zeros_like(incoming), jnp.zeros(incoming.shape, jnp.float32))

    terms = jnp.zeros(start.shape, jnp.float32)
    for turn in reversed(range(depth_count)):
        if turn < depth_count - 1:
            carry = lax.ppermute(carry, "depth", [(turn + 1, turn)])
        carry, got = lax.cond(segment == turn, back_pass, back_silent, carry)
        terms = jnp.where(segment == turn, got, terms)

    gradient = scatter_terms(
        terms, local_rows, local_columns, live, tile_rows + width, columns_all
    )
    spill = gradient[:, tile_rows:, :].astype(jnp.bfloat16)
    arrived = lax.ppermute(spill, "tile", [(t, t + 1) for t in range(tile_count - 1)])
    own = gradient[:, :tile_rows, :]
    own = own.at[:, :width, :].add(arrived.astype(jnp.float32)).astype(jnp.bfloat16)
    partner = lax.ppermute(own, "batch", pairs)
    summed = own.astype(jnp.float32) + partner.astype(jnp.float32)
    return summed[None]


def solution(mesh):
    placed = (
        P(("groups", "depth"), None, "tile", None),
        P("groups", None, None),
        P(("groups", "tile", "batch"), None),
        P(("groups", "tile", "batch")),
        P(("groups", "tile", "batch"), None, None),
    )
    return jax.shard_map(
        local,
        mesh=mesh,
        in_specs=placed,
        out_specs=P(("groups", "depth"), None, "tile", None),
        check_vma=False,
    )
```

```python
import math

import jax
import jax.numpy as jnp
from jax import lax
from jax.sharding import PartitionSpec as P
from jax.experimental import pallas as pl
from jax.experimental.pallas import tpu as pltpu

SLICE_COEF = 0.002
DETECTOR_COEF = 0.006
RESIDUAL_SCALE = 0.125


def from_behind(block, axis, distance):
    devices = range(lax.axis_size(axis))
    route = [(i - distance, i) for i in devices if i - distance in devices]
    return lax.ppermute(block, axis, route)


def dft_block(width, sign):
    freq = jnp.arange(width, dtype=jnp.int32)
    product = freq[:, None] * freq[None, :] % width
    angle = 2.0 * math.pi / width * product.astype(jnp.float32)
    scale = 1.0 / math.sqrt(width)
    real_part = (jnp.cos(angle) * scale).astype(jnp.bfloat16)
    imag_part = (sign * jnp.sin(angle) * scale).astype(jnp.bfloat16)
    upper = jnp.concatenate([real_part, -imag_part], axis=1)
    lower = jnp.concatenate([imag_part, real_part], axis=1)
    return jnp.concatenate([upper, lower], axis=0)


def dft_right(width, sign):
    freq = jnp.arange(width, dtype=jnp.int32)
    product = freq[:, None] * freq[None, :] % width
    angle = 2.0 * math.pi / width * product.astype(jnp.float32)
    scale = 1.0 / math.sqrt(width)
    real_part = (jnp.cos(angle) * scale).astype(jnp.bfloat16)
    imag_part = (sign * jnp.sin(angle) * scale).astype(jnp.bfloat16)
    upper = jnp.concatenate([real_part, imag_part], axis=1)
    lower = jnp.concatenate([-imag_part, real_part], axis=1)
    return jnp.concatenate([upper, lower], axis=0)


def chirp_parts(width, coef):
    freq = jnp.arange(width, dtype=jnp.int32)
    shifted = (freq + width // 2) % width - width // 2
    square = shifted * shifted
    total = (square[:, None] + square[None, :]).astype(jnp.float32)
    phase = -coef * total
    return (jnp.cos(phase), jnp.sin(phase))


def left_apply(block, waves):
    number = waves.shape[0]
    width = waves.shape[2]
    stacked = waves.reshape(number, 2 * width, width)
    result = jnp.einsum("ij,gjk->gik", block, stacked, preferred_element_type=jnp.float32)
    return result.reshape(number, 2, width, width)


def propagate(waves, forward_block, inverse_block, chirp_re, chirp_im):
    first = left_apply(forward_block, waves).astype(jnp.bfloat16)
    spectrum = left_apply(forward_block, jnp.swapaxes(first, -1, -2))
    spec_re = spectrum[:, 0]
    spec_im = spectrum[:, 1]
    filtered = jnp.stack(
        [spec_re * chirp_re - spec_im * chirp_im, spec_re * chirp_im + spec_im * chirp_re], axis=1
    ).astype(jnp.bfloat16)
    back = left_apply(inverse_block, filtered).astype(jnp.bfloat16)
    return left_apply(inverse_block, jnp.swapaxes(back, -1, -2)).astype(jnp.bfloat16)


def transmit(waves, patch):
    values = waves.astype(jnp.float32)
    wave_re = values[:, 0]
    wave_im = values[:, 1]
    return jnp.stack(
        [
            patch[:, 0] * wave_re - patch[:, 1] * wave_im,
            patch[:, 0] * wave_im + patch[:, 1] * wave_re,
        ],
        axis=1,
    ).astype(jnp.bfloat16)


def residual_wave(waves, measured):
    values = waves.astype(jnp.float32)
    intensity = values[:, 0] * values[:, 0] + values[:, 1] * values[:, 1]
    weight = RESIDUAL_SCALE * (intensity - measured)
    return jnp.stack([weight * values[:, 0], weight * values[:, 1]], axis=1).astype(jnp.bfloat16)


def adjoint_terms(incoming, forward_block, inverse_block, chirp_re, chirp_im, inputs, patch):
    spread = propagate(incoming, forward_block, inverse_block, chirp_re, -chirp_im).astype(
        jnp.float32
    )
    source = inputs.astype(jnp.float32)
    term = jnp.stack(
        [
            source[:, 0] * spread[:, 0] + source[:, 1] * spread[:, 1],
            source[:, 0] * spread[:, 1] - source[:, 1] * spread[:, 0],
        ],
        axis=1,
    )
    passed = jnp.stack(
        [
            patch[:, 0] * spread[:, 0] + patch[:, 1] * spread[:, 1],
            patch[:, 0] * spread[:, 1] - patch[:, 1] * spread[:, 0],
        ],
        axis=1,
    ).astype(jnp.bfloat16)
    return (passed, term)


def wave_kernel(transmit_first, residual_after, backward):
    def kernel(*refs):
        refs = list(refs)
        wave_ref = refs.pop(0)
        patch_ref = refs.pop(0)
        chirp_ref = refs.pop(0)
        fl_ref, fr_ref, gl_ref, gr_ref = refs[:4]
        refs = refs[4:]
        extra_ref = refs.pop(0) if (residual_after or backward) else None
        width = wave_ref.shape[2]
        wave = wave_ref[0].astype(jnp.float32)
        patch_re = patch_ref[0, 0]
        patch_im = patch_ref[0, 1]
        if transmit_first:
            wave_re = patch_re * wave[0] - patch_im * wave[1]
            wave_im = patch_re * wave[1] + patch_im * wave[0]
        else:
            wave_re = wave[0]
            wave_im = wave[1]
        stacked = jnp.concatenate([wave_re, wave_im], axis=0).astype(jnp.bfloat16)
        first = jnp.dot(fl_ref[...], stacked, preferred_element_type=jnp.float32).astype(jnp.bfloat16)
        rowwise = jnp.concatenate([first[:width], first[width:]], axis=1)
        spectrum = jnp.dot(rowwise, fr_ref[...], preferred_element_type=jnp.float32)
        spec_re = spectrum[:, :width]
        spec_im = spectrum[:, width:]
        chirp_re = chirp_ref[0]
        chirp_im = chirp_ref[1]
        if backward:
            chirp_im = -chirp_im
        filtered = jnp.concatenate(
            [spec_re * chirp_re - spec_im * chirp_im, spec_re * chirp_im + spec_im * chirp_re],
            axis=1,
        ).astype(jnp.bfloat16)
        back = jnp.dot(filtered, gr_ref[...], preferred_element_type=jnp.float32).astype(jnp.bfloat16)
        columnwise = jnp.concatenate([back[:, :width], back[:, width:]], axis=0)
        out = jnp.dot(gl_ref[...], columnwise, preferred_element_type=jnp.float32).astype(jnp.bfloat16)
        values = out.astype(jnp.float32)
        out_re = values[:width]
        out_im = values[width:]
        if residual_after:
            measured = extra_ref[0]
            weight = RESIDUAL_SCALE * (out_re * out_re + out_im * out_im - measured)
            result_ref = refs[0]
            result_ref[0, 0] = (weight * out_re).astype(jnp.bfloat16)
            result_ref[0, 1] = (weight * out_im).astype(jnp.bfloat16)
        elif backward:
            source = extra_ref[0].astype(jnp.float32)
            passed_ref, term_ref = refs[0], refs[1]
            passed_ref[0, 0] = (patch_re * out_re + patch_im * out_im).astype(jnp.bfloat16)
            passed_ref[0, 1] = (patch_re * out_im - patch_im * out_re).astype(jnp.bfloat16)
            term_ref[0, 0] = source[0] * out_re + source[1] * out_im
            term_ref[0, 1] = source[0] * out_im - source[1] * out_re
        else:
            result_ref = refs[0]
            result_ref[0, 0] = out[:width]
            result_ref[0, 1] = out[width:]

    return kernel


def run_waves(waves, patches, chirps, blocks, extra=None, transmit_first=True, residual_after=False, backward=False):
    number, _, width, _ = waves.shape
    wave_spec = pl.BlockSpec((1, 2, width, width), lambda i: (i, 0, 0, 0))
    chirp_spec = pl.BlockSpec((2, width, width), lambda i: (0, 0, 0))
    block_spec = pl.BlockSpec((2 * width, 2 * width), lambda i: (0, 0))
    in_specs = [wave_spec, wave_spec, chirp_spec] + [block_spec] * 4
    args = [waves, patches, chirps] + list(blocks)
    if residual_after:
        in_specs.append(pl.BlockSpec((1, width, width), lambda i: (i, 0, 0)))
        args.append(extra)
    if backward:
        in_specs.append(wave_spec)
        args.append(extra)
        out_shape = (
            jax.ShapeDtypeStruct(waves.shape, jnp.bfloat16),
            jax.ShapeDtypeStruct(waves.shape, jnp.float32),
        )
        out_specs = (wave_spec, wave_spec)
    else:
        out_shape = jax.ShapeDtypeStruct(waves.shape, jnp.bfloat16)
        out_specs = wave_spec
    return pl.pallas_call(
        wave_kernel(transmit_first, residual_after, backward),
        grid=(number,),
        in_specs=in_specs,
        out_specs=out_specs,
        out_shape=out_shape,
    )(*args)


def scatter_kernel(rows_ref, columns_ref, live_ref, terms_ref, out_ref):
    index = pl.program_id(0)

    @pl.when(index == 0)
    def _():
        out_ref[...] = jnp.zeros(out_ref.shape, out_ref.dtype)

    width = terms_ref.shape[2]
    height = out_ref.shape[1]
    columns_all = out_ref.shape[2]
    row = rows_ref[index]
    column = columns_ref[index]
    alive = live_ref[index] > 0
    for part in range(2):
        term = jnp.where(alive, terms_ref[0, part], 0.0)
        wide = jnp.concatenate(
            [term, jnp.zeros((width, columns_all - width), jnp.float32)], axis=1
        )
        wide = pltpu.roll(wide, column, 1)
        tall = jnp.concatenate(
            [wide, jnp.zeros((height - width, columns_all), jnp.float32)], axis=0
        )
        tall = pltpu.roll(tall, row, 0)
        out_ref[part] = out_ref[part] + tall


def scatter_terms(terms, rows, columns, live, height, columns_all):
    number, _, width, _ = terms.shape
    grid_spec = pltpu.PrefetchScalarGridSpec(
        num_scalar_prefetch=3,
        grid=(number,),
        in_specs=[pl.BlockSpec((1, 2, width, width), lambda i, r, c, a: (i, 0, 0, 0))],
        out_specs=pl.BlockSpec((2, height, columns_all), lambda i, r, c, a: (0, 0, 0)),
    )
    return pl.pallas_call(
        scatter_kernel,
        grid_spec=grid_spec,
        out_shape=jax.ShapeDtypeStruct((2, height, columns_all), jnp.float32),
    )(rows, columns, live.astype(jnp.int32), terms)


def cut_kernel(rows_ref, columns_ref, order_ref, tile_ref, mine_ref, partner_ref, out_ref):
    index = pl.program_id(0)
    width = out_ref.shape[2]
    height = tile_ref.shape[2] + mine_ref.shape[2]
    columns_all = tile_ref.shape[3]
    row_shift = (height - rows_ref[index]) % height
    column_shift = (columns_all - columns_ref[index]) % columns_all
    first = order_ref[0] == 0
    for part in range(2):
        mine = mine_ref[0, part]
        partner = partner_ref[0, part]
        rim = jnp.concatenate(
            [jnp.where(first, mine, partner), jnp.where(first, partner, mine)], axis=1
        )
        full = jnp.concatenate([tile_ref[0, part], rim], axis=0)
        full = pltpu.roll(full, row_shift, 0)[:width]
        full = pltpu.roll(full, column_shift, 1)[:, :width]
        out_ref[0, part] = full


def cut_patches(tile, mine, partner, rows, columns, order, width):
    number = rows.shape[0]
    grid_spec = pltpu.PrefetchScalarGridSpec(
        num_scalar_prefetch=3,
        grid=(number,),
        in_specs=[
            pl.BlockSpec(tile.shape, lambda i, r, c, o: (0, 0, 0, 0)),
            pl.BlockSpec(mine.shape, lambda i, r, c, o: (0, 0, 0, 0)),
            pl.BlockSpec(partner.shape, lambda i, r, c, o: (0, 0, 0, 0)),
        ],
        out_specs=pl.BlockSpec((1, 2, width, width), lambda i, r, c, o: (i, 0, 0, 0)),
    )
    return pl.pallas_call(
        cut_kernel,
        grid_spec=grid_spec,
        out_shape=jax.ShapeDtypeStruct((number, 2, width, width), jnp.float32),
    )(rows, columns, order, tile, mine, partner)


def local(object_field, probe, positions, counts, measured):
    width = probe.shape[1]
    tile_rows = object_field.shape[2]
    columns_all = object_field.shape[3]
    tile_index = lax.axis_index("tile")
    tile_count = lax.axis_size("tile")
    segment = lax.axis_index("depth")
    depth_count = lax.axis_size("depth")
    batch_index = lax.axis_index("batch")
    batch_count = lax.axis_size("batch")
    half = columns_all // batch_count
    wanted = lax.dynamic_slice_in_dim(object_field[:, :, :width, :], batch_index * half, half, 3)
    mine = from_behind(wanted, "tile", -1)
    pairs = [(b, (b + 1) % batch_count) for b in range(batch_count)]
    partner = lax.ppermute(mine, "batch", pairs)
    capacity = positions.shape[0]
    share = -(-capacity // batch_count)
    first_core = batch_index == 0
    both_positions = lax.ppermute(positions, "batch", pairs)
    both_counts = lax.ppermute(counts, "batch", pairs)
    both_measured = lax.ppermute(measured, "batch", pairs)
    all_positions = jnp.where(
        first_core,
        jnp.concatenate([positions, both_positions]),
        jnp.concatenate([both_positions, positions]),
    )
    all_counts = jnp.where(
        first_core, jnp.concatenate([counts, both_counts]), jnp.concatenate([both_counts, counts])
    )
    all_measured = jnp.where(
        first_core,
        jnp.concatenate([measured, both_measured]),
        jnp.concatenate([both_measured, measured]),
    )
    entry = batch_index * share + jnp.arange(share, dtype=jnp.int32)
    live = entry < all_counts[0] + all_counts[1]
    later = entry >= all_counts[0]
    slot = jnp.clip(jnp.where(later, entry - all_counts[0], entry), 0, capacity - 1)
    flat = jnp.where(later, capacity, 0) + slot
    chosen = all_positions[flat]
    measured = all_measured[flat]
    local_rows = chosen[:, 0] - tile_index * tile_rows
    local_columns = chosen[:, 1]
    order = jnp.reshape(batch_index, (1,)).astype(jnp.int32)
    patches = cut_patches(object_field, mine, partner, local_rows, local_columns, order, width)
    number = patches.shape[0]
    forward_block = dft_block(width, -1.0)
    inverse_block = dft_block(width, 1.0)
    coef = jnp.where(
        segment == depth_count - 1, jnp.float32(DETECTOR_COEF), jnp.float32(SLICE_COEF)
    )
    chirp_re, chirp_im = chirp_parts(width, coef)
    start = jnp.broadcast_to(probe[None], (number, 2, width, width))

    chirps = jnp.stack([chirp_re, chirp_im])
    blocks = (forward_block, dft_right(width, -1.0), inverse_block, dft_right(width, 1.0))

    def forward_all(waves):
        return run_waves(waves, patches, chirps, blocks)

    def forward_last(waves):
        return run_waves(waves, patches, chirps, blocks, measured, residual_after=True)

    def silent(waves):
        return jnp.zeros_like(waves)

    carry = start
    inputs = start
    for turn in range(depth_count):
        if turn > 0:
            carry = lax.ppermute(carry, "depth", [(turn - 1, turn)])
            inputs = jnp.where(segment == turn, carry, inputs)
        step = forward_last if turn == depth_count - 1 else forward_all
        carry = lax.cond(segment == turn, step, silent, carry)

    def back_pass(incoming):
        return run_waves(
            incoming, patches, chirps, blocks, inputs, transmit_first=False, backward=True
        )

    def back_silent(incoming):
        return (jnp.zeros_like(incoming), jnp.zeros(incoming.shape, jnp.float32))

    terms = jnp.zeros(start.shape, jnp.float32)
    for turn in reversed(range(depth_count)):
        if turn < depth_count - 1:
            carry = lax.ppermute(carry, "depth", [(turn + 1, turn)])
        carry, got = lax.cond(segment == turn, back_pass, back_silent, carry)
        terms = jnp.where(segment == turn, got, terms)

    gradient = scatter_terms(
        terms, local_rows, local_columns, live, tile_rows + width, columns_all
    )
    spill = gradient[:, tile_rows:, :].astype(jnp.bfloat16)
    arrived = lax.ppermute(spill, "tile", [(t, t + 1) for t in range(tile_count - 1)])
    own = gradient[:, :tile_rows, :]
    own = own.at[:, :width, :].add(arrived.astype(jnp.float32)).astype(jnp.bfloat16)
    partner = lax.ppermute(own, "batch", pairs)
    summed = own.astype(jnp.float32) + partner.astype(jnp.float32)
    return summed[None]


def solution(mesh):
    placed = (
        P(("groups", "depth"), None, "tile", None),
        P("groups", None, None),
        P(("groups", "tile", "batch"), None),
        P(("groups", "tile", "batch")),
        P(("groups", "tile", "batch"), None, None),
    )
    return jax.shard_map(
        local,
        mesh=mesh,
        in_specs=placed,
        out_specs=P(("groups", "depth"), None, "tile", None),
        check_vma=False,
    )
```

```python
import math

import jax
import jax.numpy as jnp
from jax import lax
from jax.sharding import PartitionSpec as P
from jax.experimental import pallas as pl
from jax.experimental.pallas import tpu as pltpu

SLICE_COEF = 0.002
DETECTOR_COEF = 0.006
RESIDUAL_SCALE = 0.125


def from_behind(block, axis, distance):
    devices = range(lax.axis_size(axis))
    route = [(i - distance, i) for i in devices if i - distance in devices]
    return lax.ppermute(block, axis, route)


def dft_block(width, sign):
    freq = jnp.arange(width, dtype=jnp.int32)
    product = freq[:, None] * freq[None, :] % width
    angle = 2.0 * math.pi / width * product.astype(jnp.float32)
    scale = 1.0 / math.sqrt(width)
    real_part = (jnp.cos(angle) * scale).astype(jnp.bfloat16)
    imag_part = (sign * jnp.sin(angle) * scale).astype(jnp.bfloat16)
    upper = jnp.concatenate([real_part, -imag_part], axis=1)
    lower = jnp.concatenate([imag_part, real_part], axis=1)
    return jnp.concatenate([upper, lower], axis=0)


def dft_right(width, sign):
    freq = jnp.arange(width, dtype=jnp.int32)
    product = freq[:, None] * freq[None, :] % width
    angle = 2.0 * math.pi / width * product.astype(jnp.float32)
    scale = 1.0 / math.sqrt(width)
    real_part = (jnp.cos(angle) * scale).astype(jnp.bfloat16)
    imag_part = (sign * jnp.sin(angle) * scale).astype(jnp.bfloat16)
    upper = jnp.concatenate([real_part, imag_part], axis=1)
    lower = jnp.concatenate([-imag_part, real_part], axis=1)
    return jnp.concatenate([upper, lower], axis=0)


def chirp_parts(width, coef):
    freq = jnp.arange(width, dtype=jnp.int32)
    shifted = (freq + width // 2) % width - width // 2
    square = shifted * shifted
    total = (square[:, None] + square[None, :]).astype(jnp.float32)
    phase = -coef * total
    return (jnp.cos(phase), jnp.sin(phase))


def left_apply(block, waves):
    number = waves.shape[0]
    width = waves.shape[2]
    stacked = waves.reshape(number, 2 * width, width)
    result = jnp.einsum("ij,gjk->gik", block, stacked, preferred_element_type=jnp.float32)
    return result.reshape(number, 2, width, width)


def propagate(waves, forward_block, inverse_block, chirp_re, chirp_im):
    first = left_apply(forward_block, waves).astype(jnp.bfloat16)
    spectrum = left_apply(forward_block, jnp.swapaxes(first, -1, -2))
    spec_re = spectrum[:, 0]
    spec_im = spectrum[:, 1]
    filtered = jnp.stack(
        [spec_re * chirp_re - spec_im * chirp_im, spec_re * chirp_im + spec_im * chirp_re], axis=1
    ).astype(jnp.bfloat16)
    back = left_apply(inverse_block, filtered).astype(jnp.bfloat16)
    return left_apply(inverse_block, jnp.swapaxes(back, -1, -2)).astype(jnp.bfloat16)


def transmit(waves, patch):
    values = waves.astype(jnp.float32)
    wave_re = values[:, 0]
    wave_im = values[:, 1]
    return jnp.stack(
        [
            patch[:, 0] * wave_re - patch[:, 1] * wave_im,
            patch[:, 0] * wave_im + patch[:, 1] * wave_re,
        ],
        axis=1,
    ).astype(jnp.bfloat16)


def residual_wave(waves, measured):
    values = waves.astype(jnp.float32)
    intensity = values[:, 0] * values[:, 0] + values[:, 1] * values[:, 1]
    weight = RESIDUAL_SCALE * (intensity - measured)
    return jnp.stack([weight * values[:, 0], weight * values[:, 1]], axis=1).astype(jnp.bfloat16)


def adjoint_terms(incoming, forward_block, inverse_block, chirp_re, chirp_im, inputs, patch):
    spread = propagate(incoming, forward_block, inverse_block, chirp_re, -chirp_im).astype(
        jnp.float32
    )
    source = inputs.astype(jnp.float32)
    term = jnp.stack(
        [
            source[:, 0] * spread[:, 0] + source[:, 1] * spread[:, 1],
            source[:, 0] * spread[:, 1] - source[:, 1] * spread[:, 0],
        ],
        axis=1,
    )
    passed = jnp.stack(
        [
            patch[:, 0] * spread[:, 0] + patch[:, 1] * spread[:, 1],
            patch[:, 0] * spread[:, 1] - patch[:, 1] * spread[:, 0],
        ],
        axis=1,
    ).astype(jnp.bfloat16)
    return (passed, term)


def wave_kernel(transmit_first, residual_after, backward):
    def kernel(*refs):
        refs = list(refs)
        wave_ref = refs.pop(0)
        patch_ref = refs.pop(0)
        chirp_ref = refs.pop(0)
        fl_ref, fr_ref, gl_ref, gr_ref = refs[:4]
        refs = refs[4:]
        extra_ref = refs.pop(0) if (residual_after or backward) else None
        width = wave_ref.shape[2]
        wave = wave_ref[0].astype(jnp.float32)
        patch_re = patch_ref[0, 0]
        patch_im = patch_ref[0, 1]
        if transmit_first:
            wave_re = patch_re * wave[0] - patch_im * wave[1]
            wave_im = patch_re * wave[1] + patch_im * wave[0]
        else:
            wave_re = wave[0]
            wave_im = wave[1]
        stacked = jnp.concatenate([wave_re, wave_im], axis=0).astype(jnp.bfloat16)
        first = jnp.dot(fl_ref[...], stacked, preferred_element_type=jnp.float32).astype(jnp.bfloat16)
        rowwise = jnp.concatenate([first[:width], first[width:]], axis=1)
        spectrum = jnp.dot(rowwise, fr_ref[...], preferred_element_type=jnp.float32)
        spec_re = spectrum[:, :width]
        spec_im = spectrum[:, width:]
        chirp_re = chirp_ref[0]
        chirp_im = chirp_ref[1]
        if backward:
            chirp_im = -chirp_im
        filtered = jnp.concatenate(
            [spec_re * chirp_re - spec_im * chirp_im, spec_re * chirp_im + spec_im * chirp_re],
            axis=1,
        ).astype(jnp.bfloat16)
        back = jnp.dot(filtered, gr_ref[...], preferred_element_type=jnp.float32).astype(jnp.bfloat16)
        columnwise = jnp.concatenate([back[:, :width], back[:, width:]], axis=0)
        out = jnp.dot(gl_ref[...], columnwise, preferred_element_type=jnp.float32).astype(jnp.bfloat16)
        values = out.astype(jnp.float32)
        out_re = values[:width]
        out_im = values[width:]
        if residual_after:
            measured = extra_ref[0]
            weight = RESIDUAL_SCALE * (out_re * out_re + out_im * out_im - measured)
            result_ref = refs[0]
            result_ref[0, 0] = (weight * out_re).astype(jnp.bfloat16)
            result_ref[0, 1] = (weight * out_im).astype(jnp.bfloat16)
        elif backward:
            source = extra_ref[0].astype(jnp.float32)
            passed_ref, term_ref = refs[0], refs[1]
            passed_ref[0, 0] = (patch_re * out_re + patch_im * out_im).astype(jnp.bfloat16)
            passed_ref[0, 1] = (patch_re * out_im - patch_im * out_re).astype(jnp.bfloat16)
            term_ref[0, 0] = source[0] * out_re + source[1] * out_im
            term_ref[0, 1] = source[0] * out_im - source[1] * out_re
        else:
            result_ref = refs[0]
            result_ref[0, 0] = out[:width]
            result_ref[0, 1] = out[width:]

    return kernel


def run_waves(waves, patches, chirps, blocks, extra=None, transmit_first=True, residual_after=False, backward=False):
    number, _, width, _ = waves.shape
    wave_spec = pl.BlockSpec((1, 2, width, width), lambda i: (i, 0, 0, 0))
    chirp_spec = pl.BlockSpec((2, width, width), lambda i: (0, 0, 0))
    block_spec = pl.BlockSpec((2 * width, 2 * width), lambda i: (0, 0))
    in_specs = [wave_spec, wave_spec, chirp_spec] + [block_spec] * 4
    args = [waves, patches, chirps] + list(blocks)
    if residual_after:
        in_specs.append(pl.BlockSpec((1, width, width), lambda i: (i, 0, 0)))
        args.append(extra)
    if backward:
        in_specs.append(wave_spec)
        args.append(extra)
        out_shape = (
            jax.ShapeDtypeStruct(waves.shape, jnp.bfloat16),
            jax.ShapeDtypeStruct(waves.shape, jnp.float32),
        )
        out_specs = (wave_spec, wave_spec)
    else:
        out_shape = jax.ShapeDtypeStruct(waves.shape, jnp.bfloat16)
        out_specs = wave_spec
    return pl.pallas_call(
        wave_kernel(transmit_first, residual_after, backward),
        grid=(number,),
        in_specs=in_specs,
        out_specs=out_specs,
        out_shape=out_shape,
    )(*args)


def scatter_kernel(rows_ref, columns_ref, live_ref, terms_ref, out_ref):
    index = pl.program_id(0)

    @pl.when(index == 0)
    def _():
        out_ref[...] = jnp.zeros(out_ref.shape, out_ref.dtype)

    width = terms_ref.shape[2]
    height = out_ref.shape[1]
    columns_all = out_ref.shape[2]
    row = rows_ref[index]
    column = columns_ref[index]
    alive = live_ref[index] > 0
    for part in range(2):
        term = jnp.where(alive, terms_ref[0, part], 0.0)
        wide = jnp.concatenate(
            [term, jnp.zeros((width, columns_all - width), jnp.float32)], axis=1
        )
        wide = pltpu.roll(wide, column, 1)
        tall = jnp.concatenate(
            [wide, jnp.zeros((height - width, columns_all), jnp.float32)], axis=0
        )
        tall = pltpu.roll(tall, row, 0)
        out_ref[part] = out_ref[part] + tall


def scatter_terms(terms, rows, columns, live, height, columns_all):
    number, _, width, _ = terms.shape
    grid_spec = pltpu.PrefetchScalarGridSpec(
        num_scalar_prefetch=3,
        grid=(number,),
        in_specs=[pl.BlockSpec((1, 2, width, width), lambda i, r, c, a: (i, 0, 0, 0))],
        out_specs=pl.BlockSpec((2, height, columns_all), lambda i, r, c, a: (0, 0, 0)),
    )
    return pl.pallas_call(
        scatter_kernel,
        grid_spec=grid_spec,
        out_shape=jax.ShapeDtypeStruct((2, height, columns_all), jnp.float32),
    )(rows, columns, live.astype(jnp.int32), terms)


def cut_kernel(rows_ref, columns_ref, order_ref, tile_ref, mine_ref, partner_ref, out_ref):
    index = pl.program_id(0)
    width = out_ref.shape[2]
    height = tile_ref.shape[2] + mine_ref.shape[2]
    columns_all = tile_ref.shape[3]
    row_shift = (height - rows_ref[index]) % height
    column_shift = (columns_all - columns_ref[index]) % columns_all
    first = order_ref[0] == 0
    for part in range(2):
        mine = mine_ref[0, part]
        partner = partner_ref[0, part]
        rim = jnp.concatenate(
            [jnp.where(first, mine, partner), jnp.where(first, partner, mine)], axis=1
        )
        full = jnp.concatenate([tile_ref[0, part], rim], axis=0)
        full = pltpu.roll(full, row_shift, 0)[:width]
        full = pltpu.roll(full, column_shift, 1)[:, :width]
        out_ref[0, part] = full


def cut_patches(tile, mine, partner, rows, columns, order, width):
    number = rows.shape[0]
    grid_spec = pltpu.PrefetchScalarGridSpec(
        num_scalar_prefetch=3,
        grid=(number,),
        in_specs=[
            pl.BlockSpec(tile.shape, lambda i, r, c, o: (0, 0, 0, 0)),
            pl.BlockSpec(mine.shape, lambda i, r, c, o: (0, 0, 0, 0)),
            pl.BlockSpec(partner.shape, lambda i, r, c, o: (0, 0, 0, 0)),
        ],
        out_specs=pl.BlockSpec((1, 2, width, width), lambda i, r, c, o: (i, 0, 0, 0)),
    )
    return pl.pallas_call(
        cut_kernel,
        grid_spec=grid_spec,
        out_shape=jax.ShapeDtypeStruct((number, 2, width, width), jnp.float32),
    )(rows, columns, order, tile, mine, partner)


def local(object_field, probe, positions, counts, measured):
    width = probe.shape[1]
    tile_rows = object_field.shape[2]
    columns_all = object_field.shape[3]
    tile_index = lax.axis_index("tile")
    tile_count = lax.axis_size("tile")
    segment = lax.axis_index("depth")
    depth_count = lax.axis_size("depth")
    batch_index = lax.axis_index("batch")
    batch_count = lax.axis_size("batch")
    half = columns_all // batch_count
    wanted = lax.dynamic_slice_in_dim(object_field[:, :, :width, :], batch_index * half, half, 3)
    mine = from_behind(wanted, "tile", -1)
    pairs = [(b, (b + 1) % batch_count) for b in range(batch_count)]
    partner = lax.ppermute(mine, "batch", pairs)
    capacity = positions.shape[0]
    share = -(-capacity // batch_count)
    first_core = batch_index == 0
    both_positions = lax.ppermute(positions, "batch", pairs)
    both_counts = lax.ppermute(counts, "batch", pairs)
    both_measured = lax.ppermute(measured, "batch", pairs)
    all_positions = jnp.where(
        first_core,
        jnp.concatenate([positions, both_positions]),
        jnp.concatenate([both_positions, positions]),
    )
    all_counts = jnp.where(
        first_core, jnp.concatenate([counts, both_counts]), jnp.concatenate([both_counts, counts])
    )
    entry = batch_index * share + jnp.arange(share, dtype=jnp.int32)
    live = entry < all_counts[0] + all_counts[1]
    later = entry >= all_counts[0]
    slot = jnp.clip(jnp.where(later, entry - all_counts[0], entry), 0, capacity - 1)
    flat = jnp.where(later, capacity, 0) + slot
    chosen = all_positions[flat]
    measured = jnp.where(
        (later == first_core)[:, None, None], both_measured[slot], measured[slot]
    )
    local_rows = chosen[:, 0] - tile_index * tile_rows
    local_columns = chosen[:, 1]
    order = jnp.reshape(batch_index, (1,)).astype(jnp.int32)
    patches = cut_patches(object_field, mine, partner, local_rows, local_columns, order, width)
    number = patches.shape[0]
    forward_block = dft_block(width, -1.0)
    inverse_block = dft_block(width, 1.0)
    coef = jnp.where(
        segment == depth_count - 1, jnp.float32(DETECTOR_COEF), jnp.float32(SLICE_COEF)
    )
    chirp_re, chirp_im = chirp_parts(width, coef)
    start = jnp.broadcast_to(probe[None], (number, 2, width, width))

    chirps = jnp.stack([chirp_re, chirp_im])
    blocks = (forward_block, dft_right(width, -1.0), inverse_block, dft_right(width, 1.0))

    def forward_all(waves):
        return run_waves(waves, patches, chirps, blocks)

    def forward_last(waves):
        return run_waves(waves, patches, chirps, blocks, measured, residual_after=True)

    def silent(waves):
        return jnp.zeros_like(waves)

    carry = start
    inputs = start
    for turn in range(depth_count):
        if turn > 0:
            carry = lax.ppermute(carry, "depth", [(turn - 1, turn)])
            inputs = jnp.where(segment == turn, carry, inputs)
        step = forward_last if turn == depth_count - 1 else forward_all
        carry = lax.cond(segment == turn, step, silent, carry)

    def back_pass(incoming):
        return run_waves(
            incoming, patches, chirps, blocks, inputs, transmit_first=False, backward=True
        )

    def back_silent(incoming):
        return (jnp.zeros_like(incoming), jnp.zeros(incoming.shape, jnp.float32))

    terms = jnp.zeros(start.shape, jnp.float32)
    for turn in reversed(range(depth_count)):
        if turn < depth_count - 1:
            carry = lax.ppermute(carry, "depth", [(turn + 1, turn)])
        carry, got = lax.cond(segment == turn, back_pass, back_silent, carry)
        terms = jnp.where(segment == turn, got, terms)

    gradient = scatter_terms(
        terms, local_rows, local_columns, live, tile_rows + width, columns_all
    )
    gradient = gradient.astype(jnp.bfloat16)
    other = lax.ppermute(gradient, "batch", pairs)
    total = gradient.astype(jnp.float32) + other.astype(jnp.float32)
    spill = lax.dynamic_slice_in_dim(total[:, tile_rows:, :], batch_index * half, half, 2)
    arrived = lax.ppermute(
        spill.astype(jnp.bfloat16), "tile", [(t, t + 1) for t in range(tile_count - 1)]
    )
    arrived_other = lax.ppermute(arrived, "batch", pairs)
    incoming = jnp.where(
        first_core,
        jnp.concatenate([arrived, arrived_other], axis=2),
        jnp.concatenate([arrived_other, arrived], axis=2),
    )
    summed = total[:, :tile_rows, :].at[:, :width, :].add(incoming.astype(jnp.float32))
    return summed[None]


def solution(mesh):
    placed = (
        P(("groups", "depth"), None, "tile", None),
        P("groups", None, None),
        P(("groups", "tile", "batch"), None),
        P(("groups", "tile", "batch")),
        P(("groups", "tile", "batch"), None, None),
    )
    return jax.shard_map(
        local,
        mesh=mesh,
        in_specs=placed,
        out_specs=P(("groups", "depth"), None, "tile", None),
        check_vma=False,
    )
```

```python
import math

import jax
import jax.numpy as jnp
from jax import lax
from jax.sharding import PartitionSpec as P
from jax.experimental import pallas as pl
from jax.experimental.pallas import tpu as pltpu

SLICE_COEF = 0.002
DETECTOR_COEF = 0.006
RESIDUAL_SCALE = 0.125


def from_behind(block, axis, distance):
    devices = range(lax.axis_size(axis))
    route = [(i - distance, i) for i in devices if i - distance in devices]
    return lax.ppermute(block, axis, route)


def dft_block(width, sign):
    freq = jnp.arange(width, dtype=jnp.int32)
    product = freq[:, None] * freq[None, :] % width
    angle = 2.0 * math.pi / width * product.astype(jnp.float32)
    scale = 1.0 / math.sqrt(width)
    real_part = (jnp.cos(angle) * scale).astype(jnp.bfloat16)
    imag_part = (sign * jnp.sin(angle) * scale).astype(jnp.bfloat16)
    upper = jnp.concatenate([real_part, -imag_part], axis=1)
    lower = jnp.concatenate([imag_part, real_part], axis=1)
    return jnp.concatenate([upper, lower], axis=0)


def dft_right(width, sign):
    freq = jnp.arange(width, dtype=jnp.int32)
    product = freq[:, None] * freq[None, :] % width
    angle = 2.0 * math.pi / width * product.astype(jnp.float32)
    scale = 1.0 / math.sqrt(width)
    real_part = (jnp.cos(angle) * scale).astype(jnp.bfloat16)
    imag_part = (sign * jnp.sin(angle) * scale).astype(jnp.bfloat16)
    upper = jnp.concatenate([real_part, imag_part], axis=1)
    lower = jnp.concatenate([-imag_part, real_part], axis=1)
    return jnp.concatenate([upper, lower], axis=0)


def chirp_parts(width, coef):
    freq = jnp.arange(width, dtype=jnp.int32)
    shifted = (freq + width // 2) % width - width // 2
    square = shifted * shifted
    total = (square[:, None] + square[None, :]).astype(jnp.float32)
    phase = -coef * total
    return (jnp.cos(phase), jnp.sin(phase))


def left_apply(block, waves):
    number = waves.shape[0]
    width = waves.shape[2]
    stacked = waves.reshape(number, 2 * width, width)
    result = jnp.einsum("ij,gjk->gik", block, stacked, preferred_element_type=jnp.float32)
    return result.reshape(number, 2, width, width)


def propagate(waves, forward_block, inverse_block, chirp_re, chirp_im):
    first = left_apply(forward_block, waves).astype(jnp.bfloat16)
    spectrum = left_apply(forward_block, jnp.swapaxes(first, -1, -2))
    spec_re = spectrum[:, 0]
    spec_im = spectrum[:, 1]
    filtered = jnp.stack(
        [spec_re * chirp_re - spec_im * chirp_im, spec_re * chirp_im + spec_im * chirp_re], axis=1
    ).astype(jnp.bfloat16)
    back = left_apply(inverse_block, filtered).astype(jnp.bfloat16)
    return left_apply(inverse_block, jnp.swapaxes(back, -1, -2)).astype(jnp.bfloat16)


def transmit(waves, patch):
    values = waves.astype(jnp.float32)
    wave_re = values[:, 0]
    wave_im = values[:, 1]
    return jnp.stack(
        [
            patch[:, 0] * wave_re - patch[:, 1] * wave_im,
            patch[:, 0] * wave_im + patch[:, 1] * wave_re,
        ],
        axis=1,
    ).astype(jnp.bfloat16)


def residual_wave(waves, measured):
    values = waves.astype(jnp.float32)
    intensity = values[:, 0] * values[:, 0] + values[:, 1] * values[:, 1]
    weight = RESIDUAL_SCALE * (intensity - measured)
    return jnp.stack([weight * values[:, 0], weight * values[:, 1]], axis=1).astype(jnp.bfloat16)


def adjoint_terms(incoming, forward_block, inverse_block, chirp_re, chirp_im, inputs, patch):
    spread = propagate(incoming, forward_block, inverse_block, chirp_re, -chirp_im).astype(
        jnp.float32
    )
    source = inputs.astype(jnp.float32)
    term = jnp.stack(
        [
            source[:, 0] * spread[:, 0] + source[:, 1] * spread[:, 1],
            source[:, 0] * spread[:, 1] - source[:, 1] * spread[:, 0],
        ],
        axis=1,
    )
    passed = jnp.stack(
        [
            patch[:, 0] * spread[:, 0] + patch[:, 1] * spread[:, 1],
            patch[:, 0] * spread[:, 1] - patch[:, 1] * spread[:, 0],
        ],
        axis=1,
    ).astype(jnp.bfloat16)
    return (passed, term)


def wave_kernel(transmit_first, residual_after, backward):
    def kernel(*refs):
        refs = list(refs)
        wave_ref = refs.pop(0)
        patch_ref = refs.pop(0)
        chirp_ref = refs.pop(0)
        fl_ref, fr_ref, gl_ref, gr_ref = refs[:4]
        refs = refs[4:]
        extra_ref = refs.pop(0) if (residual_after or backward) else None
        width = wave_ref.shape[2]
        wave = wave_ref[0].astype(jnp.float32)
        patch_re = patch_ref[0, 0]
        patch_im = patch_ref[0, 1]
        if transmit_first:
            wave_re = patch_re * wave[0] - patch_im * wave[1]
            wave_im = patch_re * wave[1] + patch_im * wave[0]
        else:
            wave_re = wave[0]
            wave_im = wave[1]
        stacked = jnp.concatenate([wave_re, wave_im], axis=0).astype(jnp.bfloat16)
        first = jnp.dot(fl_ref[...], stacked, preferred_element_type=jnp.float32).astype(jnp.bfloat16)
        rowwise = jnp.concatenate([first[:width], first[width:]], axis=1)
        spectrum = jnp.dot(rowwise, fr_ref[...], preferred_element_type=jnp.float32)
        spec_re = spectrum[:, :width]
        spec_im = spectrum[:, width:]
        chirp_re = chirp_ref[0]
        chirp_im = chirp_ref[1]
        if backward:
            chirp_im = -chirp_im
        filtered = jnp.concatenate(
            [spec_re * chirp_re - spec_im * chirp_im, spec_re * chirp_im + spec_im * chirp_re],
            axis=1,
        ).astype(jnp.bfloat16)
        back = jnp.dot(filtered, gr_ref[...], preferred_element_type=jnp.float32).astype(jnp.bfloat16)
        columnwise = jnp.concatenate([back[:, :width], back[:, width:]], axis=0)
        out = jnp.dot(gl_ref[...], columnwise, preferred_element_type=jnp.float32).astype(jnp.bfloat16)
        values = out.astype(jnp.float32)
        out_re = values[:width]
        out_im = values[width:]
        if residual_after:
            measured = extra_ref[0]
            weight = RESIDUAL_SCALE * (out_re * out_re + out_im * out_im - measured)
            result_ref = refs[0]
            result_ref[0, 0] = (weight * out_re).astype(jnp.bfloat16)
            result_ref[0, 1] = (weight * out_im).astype(jnp.bfloat16)
        elif backward:
            source = extra_ref[0].astype(jnp.float32)
            passed_ref, term_ref = refs[0], refs[1]
            passed_ref[0, 0] = (patch_re * out_re + patch_im * out_im).astype(jnp.bfloat16)
            passed_ref[0, 1] = (patch_re * out_im - patch_im * out_re).astype(jnp.bfloat16)
            term_ref[0, 0] = source[0] * out_re + source[1] * out_im
            term_ref[0, 1] = source[0] * out_im - source[1] * out_re
        else:
            result_ref = refs[0]
            result_ref[0, 0] = out[:width]
            result_ref[0, 1] = out[width:]

    return kernel


def run_waves(waves, patches, chirps, blocks, extra=None, transmit_first=True, residual_after=False, backward=False):
    number, _, width, _ = waves.shape
    wave_spec = pl.BlockSpec((1, 2, width, width), lambda i: (i, 0, 0, 0))
    chirp_spec = pl.BlockSpec((2, width, width), lambda i: (0, 0, 0))
    block_spec = pl.BlockSpec((2 * width, 2 * width), lambda i: (0, 0))
    in_specs = [wave_spec, wave_spec, chirp_spec] + [block_spec] * 4
    args = [waves, patches, chirps] + list(blocks)
    if residual_after:
        in_specs.append(pl.BlockSpec((1, width, width), lambda i: (i, 0, 0)))
        args.append(extra)
    if backward:
        in_specs.append(wave_spec)
        args.append(extra)
        out_shape = (
            jax.ShapeDtypeStruct(waves.shape, jnp.bfloat16),
            jax.ShapeDtypeStruct(waves.shape, jnp.float32),
        )
        out_specs = (wave_spec, wave_spec)
    else:
        out_shape = jax.ShapeDtypeStruct(waves.shape, jnp.bfloat16)
        out_specs = wave_spec
    return pl.pallas_call(
        wave_kernel(transmit_first, residual_after, backward),
        grid=(number,),
        in_specs=in_specs,
        out_specs=out_specs,
        out_shape=out_shape,
    )(*args)


def scatter_kernel(rows_ref, columns_ref, live_ref, terms_ref, out_ref):
    index = pl.program_id(0)

    @pl.when(index == 0)
    def _():
        out_ref[...] = jnp.zeros(out_ref.shape, out_ref.dtype)

    width = terms_ref.shape[2]
    height = out_ref.shape[1]
    columns_all = out_ref.shape[2]
    row = rows_ref[index]
    column = columns_ref[index]
    alive = live_ref[index] > 0
    for part in range(2):
        term = jnp.where(alive, terms_ref[0, part], 0.0)
        wide = jnp.concatenate(
            [term, jnp.zeros((width, columns_all - width), jnp.float32)], axis=1
        )
        wide = pltpu.roll(wide, column, 1)
        tall = jnp.concatenate(
            [wide, jnp.zeros((height - width, columns_all), jnp.float32)], axis=0
        )
        tall = pltpu.roll(tall, row, 0)
        out_ref[part] = out_ref[part] + tall


def scatter_terms(terms, rows, columns, live, height, columns_all):
    number, _, width, _ = terms.shape
    grid_spec = pltpu.PrefetchScalarGridSpec(
        num_scalar_prefetch=3,
        grid=(number,),
        in_specs=[pl.BlockSpec((1, 2, width, width), lambda i, r, c, a: (i, 0, 0, 0))],
        out_specs=pl.BlockSpec((2, height, columns_all), lambda i, r, c, a: (0, 0, 0)),
    )
    return pl.pallas_call(
        scatter_kernel,
        grid_spec=grid_spec,
        out_shape=jax.ShapeDtypeStruct((2, height, columns_all), jnp.float32),
    )(rows, columns, live.astype(jnp.int32), terms)


def cut_kernel(rows_ref, columns_ref, order_ref, tile_ref, mine_ref, partner_ref, out_ref):
    index = pl.program_id(0)
    width = out_ref.shape[2]
    height = tile_ref.shape[2] + mine_ref.shape[2]
    columns_all = tile_ref.shape[3]
    row_shift = (height - rows_ref[index]) % height
    column_shift = (columns_all - columns_ref[index]) % columns_all
    first = order_ref[0] == 0
    for part in range(2):
        mine = mine_ref[0, part]
        partner = partner_ref[0, part]
        rim = jnp.concatenate(
            [jnp.where(first, mine, partner), jnp.where(first, partner, mine)], axis=1
        )
        full = jnp.concatenate([tile_ref[0, part], rim], axis=0)
        full = pltpu.roll(full, row_shift, 0)[:width]
        full = pltpu.roll(full, column_shift, 1)[:, :width]
        out_ref[0, part] = full


def cut_patches(tile, mine, partner, rows, columns, order, width):
    number = rows.shape[0]
    grid_spec = pltpu.PrefetchScalarGridSpec(
        num_scalar_prefetch=3,
        grid=(number,),
        in_specs=[
            pl.BlockSpec(tile.shape, lambda i, r, c, o: (0, 0, 0, 0)),
            pl.BlockSpec(mine.shape, lambda i, r, c, o: (0, 0, 0, 0)),
            pl.BlockSpec(partner.shape, lambda i, r, c, o: (0, 0, 0, 0)),
        ],
        out_specs=pl.BlockSpec((1, 2, width, width), lambda i, r, c, o: (i, 0, 0, 0)),
    )
    return pl.pallas_call(
        cut_kernel,
        grid_spec=grid_spec,
        out_shape=jax.ShapeDtypeStruct((number, 2, width, width), jnp.float32),
    )(rows, columns, order, tile, mine, partner)


def propagate_block(wave_re, wave_im, blocks, chirp_re, chirp_im):
    fl_ref, fr_ref, gl_ref, gr_ref = blocks
    width = wave_re.shape[0]
    stacked = jnp.concatenate([wave_re, wave_im], axis=0).astype(jnp.bfloat16)
    first = jnp.dot(fl_ref[...], stacked, preferred_element_type=jnp.float32).astype(jnp.bfloat16)
    rowwise = jnp.concatenate([first[:width], first[width:]], axis=1)
    spectrum = jnp.dot(rowwise, fr_ref[...], preferred_element_type=jnp.float32)
    spec_re = spectrum[:, :width]
    spec_im = spectrum[:, width:]
    filtered = jnp.concatenate(
        [spec_re * chirp_re - spec_im * chirp_im, spec_re * chirp_im + spec_im * chirp_re],
        axis=1,
    ).astype(jnp.bfloat16)
    back = jnp.dot(filtered, gr_ref[...], preferred_element_type=jnp.float32).astype(jnp.bfloat16)
    columnwise = jnp.concatenate([back[:, :width], back[:, width:]], axis=0)
    out = jnp.dot(gl_ref[...], columnwise, preferred_element_type=jnp.float32).astype(jnp.bfloat16)
    values = out.astype(jnp.float32)
    return (values[:width], values[width:])


def place_term(term_re, term_im, row, column, alive, total_ref):
    width = term_re.shape[0]
    height = total_ref.shape[1]
    columns_all = total_ref.shape[2]
    row_shift = row % height
    column_shift = column % columns_all
    for part, term in enumerate((term_re, term_im)):
        term = jnp.where(alive, term, 0.0)
        wide = jnp.concatenate(
            [term, jnp.zeros((width, columns_all - width), jnp.float32)], axis=1
        )
        wide = pltpu.roll(wide, column_shift, 1)
        tall = jnp.concatenate(
            [wide, jnp.zeros((height - width, columns_all), jnp.float32)], axis=0
        )
        total_ref[part] = total_ref[part] + pltpu.roll(tall, row_shift, 0)


def adjoint_kernel(last):
    def kernel(rows_ref, columns_ref, live_ref, slot_ref, other_ref, *refs):
        refs = list(refs)
        wave_ref = refs.pop(0)
        patch_ref = refs.pop(0)
        chirp_ref = refs.pop(0)
        blocks = refs[:4]
        refs = refs[4:]
        if last:
            own_ref = refs.pop(0)
            partner_ref = refs.pop(0)
        else:
            source_ref = refs.pop(0)
        passed_ref, grad_ref, total_ref = refs
        index = pl.program_id(0)

        @pl.when(index == 0)
        def _():
            total_ref[...] = jnp.zeros(total_ref.shape, total_ref.dtype)

        wave = wave_ref[0].astype(jnp.float32)
        patch_re = patch_ref[0, 0]
        patch_im = patch_ref[0, 1]
        chirp_re = chirp_ref[0]
        chirp_im = chirp_ref[1]
        if last:
            source_re = wave[0]
            source_im = wave[1]
            lit_re = patch_re * wave[0] - patch_im * wave[1]
            lit_im = patch_re * wave[1] + patch_im * wave[0]
            out_re, out_im = propagate_block(lit_re, lit_im, blocks, chirp_re, chirp_im)
            measured = jnp.where(other_ref[index] > 0, partner_ref[0], own_ref[0])
            weight = RESIDUAL_SCALE * (out_re * out_re + out_im * out_im - measured)
            in_re = (weight * out_re).astype(jnp.bfloat16).astype(jnp.float32)
            in_im = (weight * out_im).astype(jnp.bfloat16).astype(jnp.float32)
        else:
            source = source_ref[0].astype(jnp.float32)
            source_re = source[0]
            source_im = source[1]
            in_re = wave[0]
            in_im = wave[1]
        spread_re, spread_im = propagate_block(in_re, in_im, blocks, chirp_re, -chirp_im)
        passed_ref[0, 0] = (patch_re * spread_re + patch_im * spread_im).astype(jnp.bfloat16)
        passed_ref[0, 1] = (patch_re * spread_im - patch_im * spread_re).astype(jnp.bfloat16)
        term_re = source_re * spread_re + source_im * spread_im
        term_im = source_re * spread_im - source_im * spread_re
        place_term(
            term_re, term_im, rows_ref[index], columns_ref[index], live_ref[index] > 0, total_ref
        )

        @pl.when(index == pl.num_programs(0) - 1)
        def _():
            grad_ref[...] = total_ref[...].astype(grad_ref.dtype)

    return kernel


def run_adjoint(waves, patches, chirps, blocks, scalars, extra, height, columns_all, last):
    number, _, width, _ = waves.shape
    wave_spec = pl.BlockSpec((1, 2, width, width), lambda i, *s: (i, 0, 0, 0))
    chirp_spec = pl.BlockSpec((2, width, width), lambda i, *s: (0, 0, 0))
    block_spec = pl.BlockSpec((2 * width, 2 * width), lambda i, *s: (0, 0))
    in_specs = [wave_spec, wave_spec, chirp_spec] + [block_spec] * 4
    if last:
        slot_spec = pl.BlockSpec((1, width, width), lambda i, r, c, a, s, o: (s[i], 0, 0))
        in_specs += [slot_spec, slot_spec]
    else:
        in_specs += [wave_spec]
    grid_spec = pltpu.PrefetchScalarGridSpec(
        num_scalar_prefetch=5,
        grid=(number,),
        in_specs=in_specs,
        out_specs=(
            wave_spec,
            pl.BlockSpec((2, height, columns_all), lambda i, *s: (0, 0, 0)),
        ),
        scratch_shapes=[pltpu.VMEM((2, height, columns_all), jnp.float32)],
    )
    return pl.pallas_call(
        adjoint_kernel(last),
        grid_spec=grid_spec,
        out_shape=(
            jax.ShapeDtypeStruct(waves.shape, jnp.bfloat16),
            jax.ShapeDtypeStruct((2, height, columns_all), jnp.bfloat16),
        ),
    )(*scalars, waves, patches, chirps, *blocks, *extra)


def local(object_field, probe, positions, counts, measured):
    width = probe.shape[1]
    tile_rows = object_field.shape[2]
    columns_all = object_field.shape[3]
    tile_index = lax.axis_index("tile")
    tile_count = lax.axis_size("tile")
    segment = lax.axis_index("depth")
    depth_count = lax.axis_size("depth")
    batch_index = lax.axis_index("batch")
    batch_count = lax.axis_size("batch")
    half = columns_all // batch_count
    wanted = lax.dynamic_slice_in_dim(object_field[:, :, :width, :], batch_index * half, half, 3)
    mine = from_behind(wanted, "tile", -1)
    pairs = [(b, (b + 1) % batch_count) for b in range(batch_count)]
    partner = lax.ppermute(mine, "batch", pairs)
    capacity = positions.shape[0]
    share = -(-capacity // batch_count)
    first_core = batch_index == 0
    both_positions = lax.ppermute(positions, "batch", pairs)
    both_counts = lax.ppermute(counts, "batch", pairs)
    both_measured = lax.ppermute(measured, "batch", pairs)
    all_positions = jnp.where(
        first_core,
        jnp.concatenate([positions, both_positions]),
        jnp.concatenate([both_positions, positions]),
    )
    all_counts = jnp.where(
        first_core, jnp.concatenate([counts, both_counts]), jnp.concatenate([both_counts, counts])
    )
    entry = batch_index * share + jnp.arange(share, dtype=jnp.int32)
    live = entry < all_counts[0] + all_counts[1]
    later = entry >= all_counts[0]
    slot = jnp.clip(jnp.where(later, entry - all_counts[0], entry), 0, capacity - 1)
    flat = jnp.where(later, capacity, 0) + slot
    chosen = all_positions[flat]
    other = (later == first_core).astype(jnp.int32)
    local_rows = chosen[:, 0] - tile_index * tile_rows
    local_columns = chosen[:, 1]
    order = jnp.reshape(batch_index, (1,)).astype(jnp.int32)
    patches = cut_patches(object_field, mine, partner, local_rows, local_columns, order, width)
    number = patches.shape[0]
    forward_block = dft_block(width, -1.0)
    inverse_block = dft_block(width, 1.0)
    coef = jnp.where(
        segment == depth_count - 1, jnp.float32(DETECTOR_COEF), jnp.float32(SLICE_COEF)
    )
    chirp_re, chirp_im = chirp_parts(width, coef)
    start = jnp.broadcast_to(probe[None], (number, 2, width, width))

    chirps = jnp.stack([chirp_re, chirp_im])
    blocks = (forward_block, dft_right(width, -1.0), inverse_block, dft_right(width, 1.0))

    def forward_all(waves):
        return run_waves(waves, patches, chirps, blocks)

    def silent(waves):
        return jnp.zeros_like(waves)

    carry = start
    inputs = start
    for turn in range(depth_count - 1):
        if turn > 0:
            carry = lax.ppermute(carry, "depth", [(turn - 1, turn)])
            inputs = jnp.where(segment == turn, carry, inputs)
        carry = lax.cond(segment == turn, forward_all, silent, carry)

    height = tile_rows + width
    scalars = (local_rows, local_columns, live.astype(jnp.int32), slot, other)

    def last_pass(incoming):
        return run_adjoint(
            incoming, patches, chirps, blocks, scalars, (measured, both_measured),
            height, columns_all, True,
        )

    def last_silent(incoming):
        return (jnp.zeros_like(incoming), jnp.zeros((2, height, columns_all), jnp.bfloat16))

    if depth_count > 1:
        carry = lax.ppermute(carry, "depth", [(depth_count - 2, depth_count - 1)])
    carry, gradient = lax.cond(segment == depth_count - 1, last_pass, last_silent, carry)

    def back_pass(incoming, previous):
        return run_adjoint(
            incoming, patches, chirps, blocks, scalars, (inputs,), height, columns_all, False
        )

    def back_silent(incoming, previous):
        return (jnp.zeros_like(incoming), previous)

    for turn in reversed(range(depth_count - 1)):
        carry = lax.ppermute(carry, "depth", [(turn + 1, turn)])
        carry, gradient = lax.cond(segment == turn, back_pass, back_silent, carry, gradient)

    gradient = gradient.astype(jnp.bfloat16)
    other = lax.ppermute(gradient, "batch", pairs)
    total = gradient.astype(jnp.float32) + other.astype(jnp.float32)
    spill = lax.dynamic_slice_in_dim(total[:, tile_rows:, :], batch_index * half, half, 2)
    arrived = lax.ppermute(
        spill.astype(jnp.bfloat16), "tile", [(t, t + 1) for t in range(tile_count - 1)]
    )
    arrived_other = lax.ppermute(arrived, "batch", pairs)
    incoming = jnp.where(
        first_core,
        jnp.concatenate([arrived, arrived_other], axis=2),
        jnp.concatenate([arrived_other, arrived], axis=2),
    )
    summed = total[:, :tile_rows, :].at[:, :width, :].add(incoming.astype(jnp.float32))
    return summed[None]


def solution(mesh):
    placed = (
        P(("groups", "depth"), None, "tile", None),
        P("groups", None, None),
        P(("groups", "tile", "batch"), None),
        P(("groups", "tile", "batch")),
        P(("groups", "tile", "batch"), None, None),
    )
    return jax.shard_map(
        local,
        mesh=mesh,
        in_specs=placed,
        out_specs=P(("groups", "depth"), None, "tile", None),
        check_vma=False,
    )
```

```python
import math

import jax
import jax.numpy as jnp
from jax import lax
from jax.sharding import PartitionSpec as P
from jax.experimental import pallas as pl
from jax.experimental.pallas import tpu as pltpu

SLICE_COEF = 0.002
DETECTOR_COEF = 0.006
RESIDUAL_SCALE = 0.125


def from_behind(block, axis, distance):
    devices = range(lax.axis_size(axis))
    route = [(i - distance, i) for i in devices if i - distance in devices]
    return lax.ppermute(block, axis, route)


def dft_block(width, sign):
    freq = jnp.arange(width, dtype=jnp.int32)
    product = freq[:, None] * freq[None, :] % width
    angle = 2.0 * math.pi / width * product.astype(jnp.float32)
    scale = 1.0 / math.sqrt(width)
    real_part = (jnp.cos(angle) * scale).astype(jnp.bfloat16)
    imag_part = (sign * jnp.sin(angle) * scale).astype(jnp.bfloat16)
    upper = jnp.concatenate([real_part, -imag_part], axis=1)
    lower = jnp.concatenate([imag_part, real_part], axis=1)
    return jnp.concatenate([upper, lower], axis=0)


def dft_right(width, sign):
    freq = jnp.arange(width, dtype=jnp.int32)
    product = freq[:, None] * freq[None, :] % width
    angle = 2.0 * math.pi / width * product.astype(jnp.float32)
    scale = 1.0 / math.sqrt(width)
    real_part = (jnp.cos(angle) * scale).astype(jnp.bfloat16)
    imag_part = (sign * jnp.sin(angle) * scale).astype(jnp.bfloat16)
    upper = jnp.concatenate([real_part, imag_part], axis=1)
    lower = jnp.concatenate([-imag_part, real_part], axis=1)
    return jnp.concatenate([upper, lower], axis=0)


def chirp_parts(width, coef):
    freq = jnp.arange(width, dtype=jnp.int32)
    shifted = (freq + width // 2) % width - width // 2
    square = shifted * shifted
    total = (square[:, None] + square[None, :]).astype(jnp.float32)
    phase = -coef * total
    return (jnp.cos(phase), jnp.sin(phase))


def left_apply(block, waves):
    number = waves.shape[0]
    width = waves.shape[2]
    stacked = waves.reshape(number, 2 * width, width)
    result = jnp.einsum("ij,gjk->gik", block, stacked, preferred_element_type=jnp.float32)
    return result.reshape(number, 2, width, width)


def propagate(waves, forward_block, inverse_block, chirp_re, chirp_im):
    first = left_apply(forward_block, waves).astype(jnp.bfloat16)
    spectrum = left_apply(forward_block, jnp.swapaxes(first, -1, -2))
    spec_re = spectrum[:, 0]
    spec_im = spectrum[:, 1]
    filtered = jnp.stack(
        [spec_re * chirp_re - spec_im * chirp_im, spec_re * chirp_im + spec_im * chirp_re], axis=1
    ).astype(jnp.bfloat16)
    back = left_apply(inverse_block, filtered).astype(jnp.bfloat16)
    return left_apply(inverse_block, jnp.swapaxes(back, -1, -2)).astype(jnp.bfloat16)


def transmit(waves, patch):
    values = waves.astype(jnp.float32)
    wave_re = values[:, 0]
    wave_im = values[:, 1]
    return jnp.stack(
        [
            patch[:, 0] * wave_re - patch[:, 1] * wave_im,
            patch[:, 0] * wave_im + patch[:, 1] * wave_re,
        ],
        axis=1,
    ).astype(jnp.bfloat16)


def residual_wave(waves, measured):
    values = waves.astype(jnp.float32)
    intensity = values[:, 0] * values[:, 0] + values[:, 1] * values[:, 1]
    weight = RESIDUAL_SCALE * (intensity - measured)
    return jnp.stack([weight * values[:, 0], weight * values[:, 1]], axis=1).astype(jnp.bfloat16)


def adjoint_terms(incoming, forward_block, inverse_block, chirp_re, chirp_im, inputs, patch):
    spread = propagate(incoming, forward_block, inverse_block, chirp_re, -chirp_im).astype(
        jnp.float32
    )
    source = inputs.astype(jnp.float32)
    term = jnp.stack(
        [
            source[:, 0] * spread[:, 0] + source[:, 1] * spread[:, 1],
            source[:, 0] * spread[:, 1] - source[:, 1] * spread[:, 0],
        ],
        axis=1,
    )
    passed = jnp.stack(
        [
            patch[:, 0] * spread[:, 0] + patch[:, 1] * spread[:, 1],
            patch[:, 0] * spread[:, 1] - patch[:, 1] * spread[:, 0],
        ],
        axis=1,
    ).astype(jnp.bfloat16)
    return (passed, term)


def wave_kernel(transmit_first, residual_after, backward):
    def kernel(*refs):
        refs = list(refs)
        wave_ref = refs.pop(0)
        patch_ref = refs.pop(0)
        chirp_ref = refs.pop(0)
        fl_ref, fr_ref, gl_ref, gr_ref = refs[:4]
        refs = refs[4:]
        extra_ref = refs.pop(0) if (residual_after or backward) else None
        width = wave_ref.shape[2]
        wave = wave_ref[0].astype(jnp.float32)
        patch_re = patch_ref[0, 0]
        patch_im = patch_ref[0, 1]
        if transmit_first:
            wave_re = patch_re * wave[0] - patch_im * wave[1]
            wave_im = patch_re * wave[1] + patch_im * wave[0]
        else:
            wave_re = wave[0]
            wave_im = wave[1]
        stacked = jnp.concatenate([wave_re, wave_im], axis=0).astype(jnp.bfloat16)
        first = jnp.dot(fl_ref[...], stacked, preferred_element_type=jnp.float32).astype(jnp.bfloat16)
        rowwise = jnp.concatenate([first[:width], first[width:]], axis=1)
        spectrum = jnp.dot(rowwise, fr_ref[...], preferred_element_type=jnp.float32)
        spec_re = spectrum[:, :width]
        spec_im = spectrum[:, width:]
        chirp_re = chirp_ref[0]
        chirp_im = chirp_ref[1]
        if backward:
            chirp_im = -chirp_im
        filtered = jnp.concatenate(
            [spec_re * chirp_re - spec_im * chirp_im, spec_re * chirp_im + spec_im * chirp_re],
            axis=1,
        ).astype(jnp.bfloat16)
        back = jnp.dot(filtered, gr_ref[...], preferred_element_type=jnp.float32).astype(jnp.bfloat16)
        columnwise = jnp.concatenate([back[:, :width], back[:, width:]], axis=0)
        out = jnp.dot(gl_ref[...], columnwise, preferred_element_type=jnp.float32).astype(jnp.bfloat16)
        values = out.astype(jnp.float32)
        out_re = values[:width]
        out_im = values[width:]
        if residual_after:
            measured = extra_ref[0]
            weight = RESIDUAL_SCALE * (out_re * out_re + out_im * out_im - measured)
            result_ref = refs[0]
            result_ref[0, 0] = (weight * out_re).astype(jnp.bfloat16)
            result_ref[0, 1] = (weight * out_im).astype(jnp.bfloat16)
        elif backward:
            source = extra_ref[0].astype(jnp.float32)
            passed_ref, term_ref = refs[0], refs[1]
            passed_ref[0, 0] = (patch_re * out_re + patch_im * out_im).astype(jnp.bfloat16)
            passed_ref[0, 1] = (patch_re * out_im - patch_im * out_re).astype(jnp.bfloat16)
            term_ref[0, 0] = source[0] * out_re + source[1] * out_im
            term_ref[0, 1] = source[0] * out_im - source[1] * out_re
        else:
            result_ref = refs[0]
            result_ref[0, 0] = out[:width]
            result_ref[0, 1] = out[width:]

    return kernel


def run_waves(waves, patches, chirps, blocks, extra=None, transmit_first=True, residual_after=False, backward=False):
    number, _, width, _ = waves.shape
    wave_spec = pl.BlockSpec((1, 2, width, width), lambda i: (i, 0, 0, 0))
    chirp_spec = pl.BlockSpec((2, width, width), lambda i: (0, 0, 0))
    block_spec = pl.BlockSpec((2 * width, 2 * width), lambda i: (0, 0))
    in_specs = [wave_spec, wave_spec, chirp_spec] + [block_spec] * 4
    args = [waves, patches, chirps] + list(blocks)
    if residual_after:
        in_specs.append(pl.BlockSpec((1, width, width), lambda i: (i, 0, 0)))
        args.append(extra)
    if backward:
        in_specs.append(wave_spec)
        args.append(extra)
        out_shape = (
            jax.ShapeDtypeStruct(waves.shape, jnp.bfloat16),
            jax.ShapeDtypeStruct(waves.shape, jnp.float32),
        )
        out_specs = (wave_spec, wave_spec)
    else:
        out_shape = jax.ShapeDtypeStruct(waves.shape, jnp.bfloat16)
        out_specs = wave_spec
    return pl.pallas_call(
        wave_kernel(transmit_first, residual_after, backward),
        grid=(number,),
        in_specs=in_specs,
        out_specs=out_specs,
        out_shape=out_shape,
    )(*args)


def scatter_kernel(rows_ref, columns_ref, live_ref, terms_ref, out_ref):
    index = pl.program_id(0)

    @pl.when(index == 0)
    def _():
        out_ref[...] = jnp.zeros(out_ref.shape, out_ref.dtype)

    width = terms_ref.shape[2]
    height = out_ref.shape[1]
    columns_all = out_ref.shape[2]
    row = rows_ref[index]
    column = columns_ref[index]
    alive = live_ref[index] > 0
    for part in range(2):
        term = jnp.where(alive, terms_ref[0, part], 0.0)
        wide = jnp.concatenate(
            [term, jnp.zeros((width, columns_all - width), jnp.float32)], axis=1
        )
        wide = pltpu.roll(wide, column, 1)
        tall = jnp.concatenate(
            [wide, jnp.zeros((height - width, columns_all), jnp.float32)], axis=0
        )
        tall = pltpu.roll(tall, row, 0)
        out_ref[part] = out_ref[part] + tall


def scatter_terms(terms, rows, columns, live, height, columns_all):
    number, _, width, _ = terms.shape
    grid_spec = pltpu.PrefetchScalarGridSpec(
        num_scalar_prefetch=3,
        grid=(number,),
        in_specs=[pl.BlockSpec((1, 2, width, width), lambda i, r, c, a: (i, 0, 0, 0))],
        out_specs=pl.BlockSpec((2, height, columns_all), lambda i, r, c, a: (0, 0, 0)),
    )
    return pl.pallas_call(
        scatter_kernel,
        grid_spec=grid_spec,
        out_shape=jax.ShapeDtypeStruct((2, height, columns_all), jnp.float32),
    )(rows, columns, live.astype(jnp.int32), terms)


def cut_kernel(rows_ref, columns_ref, order_ref, tile_ref, mine_ref, partner_ref, out_ref):
    index = pl.program_id(0)
    width = out_ref.shape[2]
    height = tile_ref.shape[2] + mine_ref.shape[2]
    columns_all = tile_ref.shape[3]
    row_shift = (height - rows_ref[index]) % height
    column_shift = (columns_all - columns_ref[index]) % columns_all
    first = order_ref[0] == 0
    for part in range(2):
        mine = mine_ref[0, part].astype(jnp.float32)
        partner = partner_ref[0, part].astype(jnp.float32)
        rim = jnp.concatenate(
            [jnp.where(first, mine, partner), jnp.where(first, partner, mine)], axis=1
        )
        full = jnp.concatenate([tile_ref[0, part], rim], axis=0)
        full = pltpu.roll(full, row_shift, 0)[:width]
        full = pltpu.roll(full, column_shift, 1)[:, :width]
        out_ref[0, part] = full


def cut_patches(tile, mine, partner, rows, columns, order, width):
    number = rows.shape[0]
    grid_spec = pltpu.PrefetchScalarGridSpec(
        num_scalar_prefetch=3,
        grid=(number,),
        in_specs=[
            pl.BlockSpec(tile.shape, lambda i, r, c, o: (0, 0, 0, 0)),
            pl.BlockSpec(mine.shape, lambda i, r, c, o: (0, 0, 0, 0)),
            pl.BlockSpec(partner.shape, lambda i, r, c, o: (0, 0, 0, 0)),
        ],
        out_specs=pl.BlockSpec((1, 2, width, width), lambda i, r, c, o: (i, 0, 0, 0)),
    )
    return pl.pallas_call(
        cut_kernel,
        grid_spec=grid_spec,
        out_shape=jax.ShapeDtypeStruct((number, 2, width, width), jnp.float32),
    )(rows, columns, order, tile, mine, partner)


def propagate_block(wave_re, wave_im, blocks, chirp_re, chirp_im):
    fl_ref, fr_ref, gl_ref, gr_ref = blocks
    width = wave_re.shape[0]
    stacked = jnp.concatenate([wave_re, wave_im], axis=0).astype(jnp.bfloat16)
    first = jnp.dot(fl_ref[...], stacked, preferred_element_type=jnp.float32).astype(jnp.bfloat16)
    rowwise = jnp.concatenate([first[:width], first[width:]], axis=1)
    spectrum = jnp.dot(rowwise, fr_ref[...], preferred_element_type=jnp.float32)
    spec_re = spectrum[:, :width]
    spec_im = spectrum[:, width:]
    filtered = jnp.concatenate(
        [spec_re * chirp_re - spec_im * chirp_im, spec_re * chirp_im + spec_im * chirp_re],
        axis=1,
    ).astype(jnp.bfloat16)
    back = jnp.dot(filtered, gr_ref[...], preferred_element_type=jnp.float32).astype(jnp.bfloat16)
    columnwise = jnp.concatenate([back[:, :width], back[:, width:]], axis=0)
    out = jnp.dot(gl_ref[...], columnwise, preferred_element_type=jnp.float32).astype(jnp.bfloat16)
    values = out.astype(jnp.float32)
    return (values[:width], values[width:])


def place_term(term_re, term_im, row, column, alive, total_ref):
    width = term_re.shape[0]
    height = total_ref.shape[1]
    columns_all = total_ref.shape[2]
    row_shift = row % height
    column_shift = column % columns_all
    for part, term in enumerate((term_re, term_im)):
        term = jnp.where(alive, term, 0.0)
        wide = jnp.concatenate(
            [term, jnp.zeros((width, columns_all - width), jnp.float32)], axis=1
        )
        wide = pltpu.roll(wide, column_shift, 1)
        tall = jnp.concatenate(
            [wide, jnp.zeros((height - width, columns_all), jnp.float32)], axis=0
        )
        total_ref[part] = total_ref[part] + pltpu.roll(tall, row_shift, 0)


def adjoint_kernel(last):
    def kernel(rows_ref, columns_ref, live_ref, slot_ref, other_ref, *refs):
        refs = list(refs)
        wave_ref = refs.pop(0)
        patch_ref = refs.pop(0)
        chirp_ref = refs.pop(0)
        blocks = refs[:4]
        refs = refs[4:]
        if last:
            own_ref = refs.pop(0)
            partner_ref = refs.pop(0)
        else:
            source_ref = refs.pop(0)
        passed_ref, grad_ref, total_ref = refs
        index = pl.program_id(0)

        @pl.when(index == 0)
        def _():
            total_ref[...] = jnp.zeros(total_ref.shape, total_ref.dtype)

        wave = wave_ref[0].astype(jnp.float32)
        patch_re = patch_ref[0, 0]
        patch_im = patch_ref[0, 1]
        chirp_re = chirp_ref[0]
        chirp_im = chirp_ref[1]
        if last:
            source_re = wave[0]
            source_im = wave[1]
            lit_re = patch_re * wave[0] - patch_im * wave[1]
            lit_im = patch_re * wave[1] + patch_im * wave[0]
            out_re, out_im = propagate_block(lit_re, lit_im, blocks, chirp_re, chirp_im)
            measured = jnp.where(other_ref[index] > 0, partner_ref[0], own_ref[0])
            weight = RESIDUAL_SCALE * (out_re * out_re + out_im * out_im - measured)
            in_re = (weight * out_re).astype(jnp.bfloat16).astype(jnp.float32)
            in_im = (weight * out_im).astype(jnp.bfloat16).astype(jnp.float32)
        else:
            source = source_ref[0].astype(jnp.float32)
            source_re = source[0]
            source_im = source[1]
            in_re = wave[0]
            in_im = wave[1]
        spread_re, spread_im = propagate_block(in_re, in_im, blocks, chirp_re, -chirp_im)
        passed_ref[0, 0] = (patch_re * spread_re + patch_im * spread_im).astype(jnp.bfloat16)
        passed_ref[0, 1] = (patch_re * spread_im - patch_im * spread_re).astype(jnp.bfloat16)
        term_re = source_re * spread_re + source_im * spread_im
        term_im = source_re * spread_im - source_im * spread_re
        place_term(
            term_re, term_im, rows_ref[index], columns_ref[index], live_ref[index] > 0, total_ref
        )

        @pl.when(index == pl.num_programs(0) - 1)
        def _():
            grad_ref[...] = total_ref[...].astype(grad_ref.dtype)

    return kernel


def run_adjoint(waves, patches, chirps, blocks, scalars, extra, height, columns_all, last):
    number, _, width, _ = waves.shape
    wave_spec = pl.BlockSpec((1, 2, width, width), lambda i, *s: (i, 0, 0, 0))
    chirp_spec = pl.BlockSpec((2, width, width), lambda i, *s: (0, 0, 0))
    block_spec = pl.BlockSpec((2 * width, 2 * width), lambda i, *s: (0, 0))
    in_specs = [wave_spec, wave_spec, chirp_spec] + [block_spec] * 4
    if last:
        slot_spec = pl.BlockSpec((1, width, width), lambda i, r, c, a, s, o: (s[i], 0, 0))
        in_specs += [slot_spec, slot_spec]
    else:
        in_specs += [wave_spec]
    grid_spec = pltpu.PrefetchScalarGridSpec(
        num_scalar_prefetch=5,
        grid=(number,),
        in_specs=in_specs,
        out_specs=(
            wave_spec,
            pl.BlockSpec((2, height, columns_all), lambda i, *s: (0, 0, 0)),
        ),
        scratch_shapes=[pltpu.VMEM((2, height, columns_all), jnp.float32)],
    )
    return pl.pallas_call(
        adjoint_kernel(last),
        grid_spec=grid_spec,
        out_shape=(
            jax.ShapeDtypeStruct(waves.shape, jnp.bfloat16),
            jax.ShapeDtypeStruct((2, height, columns_all), jnp.bfloat16),
        ),
    )(*scalars, waves, patches, chirps, *blocks, *extra)


def local(object_field, probe, positions, counts, measured):
    width = probe.shape[1]
    tile_rows = object_field.shape[2]
    columns_all = object_field.shape[3]
    tile_index = lax.axis_index("tile")
    tile_count = lax.axis_size("tile")
    segment = lax.axis_index("depth")
    depth_count = lax.axis_size("depth")
    batch_index = lax.axis_index("batch")
    batch_count = lax.axis_size("batch")
    half = columns_all // batch_count
    wanted = lax.dynamic_slice_in_dim(object_field[:, :, :width, :], batch_index * half, half, 3)
    mine = from_behind(wanted.astype(jnp.bfloat16), "tile", -1)
    pairs = [(b, (b + 1) % batch_count) for b in range(batch_count)]
    partner = lax.ppermute(mine, "batch", pairs)
    capacity = positions.shape[0]
    share = -(-capacity // batch_count)
    first_core = batch_index == 0
    both_positions = lax.ppermute(positions, "batch", pairs)
    both_counts = lax.ppermute(counts, "batch", pairs)
    both_measured = lax.ppermute(measured, "batch", pairs)
    all_positions = jnp.where(
        first_core,
        jnp.concatenate([positions, both_positions]),
        jnp.concatenate([both_positions, positions]),
    )
    all_counts = jnp.where(
        first_core, jnp.concatenate([counts, both_counts]), jnp.concatenate([both_counts, counts])
    )
    entry = batch_index * share + jnp.arange(share, dtype=jnp.int32)
    live = entry < all_counts[0] + all_counts[1]
    later = entry >= all_counts[0]
    slot = jnp.clip(jnp.where(later, entry - all_counts[0], entry), 0, capacity - 1)
    flat = jnp.where(later, capacity, 0) + slot
    chosen = all_positions[flat]
    other = (later == first_core).astype(jnp.int32)
    local_rows = chosen[:, 0] - tile_index * tile_rows
    local_columns = chosen[:, 1]
    order = jnp.reshape(batch_index, (1,)).astype(jnp.int32)
    patches = cut_patches(object_field, mine, partner, local_rows, local_columns, order, width)
    number = patches.shape[0]
    forward_block = dft_block(width, -1.0)
    inverse_block = dft_block(width, 1.0)
    coef = jnp.where(
        segment == depth_count - 1, jnp.float32(DETECTOR_COEF), jnp.float32(SLICE_COEF)
    )
    chirp_re, chirp_im = chirp_parts(width, coef)
    start = jnp.broadcast_to(probe[None], (number, 2, width, width))

    chirps = jnp.stack([chirp_re, chirp_im])
    blocks = (forward_block, dft_right(width, -1.0), inverse_block, dft_right(width, 1.0))

    def forward_all(waves):
        return run_waves(waves, patches, chirps, blocks)

    def silent(waves):
        return jnp.zeros_like(waves)

    carry = start
    inputs = start
    for turn in range(depth_count - 1):
        if turn > 0:
            carry = lax.ppermute(carry, "depth", [(turn - 1, turn)])
            inputs = jnp.where(segment == turn, carry, inputs)
        carry = lax.cond(segment == turn, forward_all, silent, carry)

    height = tile_rows + width
    scalars = (local_rows, local_columns, live.astype(jnp.int32), slot, other)

    def last_pass(incoming):
        return run_adjoint(
            incoming, patches, chirps, blocks, scalars, (measured, both_measured),
            height, columns_all, True,
        )

    def last_silent(incoming):
        return (jnp.zeros_like(incoming), jnp.zeros((2, height, columns_all), jnp.bfloat16))

    if depth_count > 1:
        carry = lax.ppermute(carry, "depth", [(depth_count - 2, depth_count - 1)])
    carry, gradient = lax.cond(segment == depth_count - 1, last_pass, last_silent, carry)

    def back_pass(incoming, previous):
        return run_adjoint(
            incoming, patches, chirps, blocks, scalars, (inputs,), height, columns_all, False
        )

    def back_silent(incoming, previous):
        return (jnp.zeros_like(incoming), previous)

    for turn in reversed(range(depth_count - 1)):
        carry = lax.ppermute(carry, "depth", [(turn + 1, turn)])
        carry, gradient = lax.cond(segment == turn, back_pass, back_silent, carry, gradient)

    gradient = gradient.astype(jnp.bfloat16)
    other = lax.ppermute(gradient, "batch", pairs)
    total = gradient.astype(jnp.float32) + other.astype(jnp.float32)
    spill = lax.dynamic_slice_in_dim(total[:, tile_rows:, :], batch_index * half, half, 2)
    arrived = lax.ppermute(
        spill.astype(jnp.bfloat16), "tile", [(t, t + 1) for t in range(tile_count - 1)]
    )
    arrived_other = lax.ppermute(arrived, "batch", pairs)
    incoming = jnp.where(
        first_core,
        jnp.concatenate([arrived, arrived_other], axis=2),
        jnp.concatenate([arrived_other, arrived], axis=2),
    )
    summed = total[:, :tile_rows, :].at[:, :width, :].add(incoming.astype(jnp.float32))
    return summed[None]


def solution(mesh):
    placed = (
        P(("groups", "depth"), None, "tile", None),
        P("groups", None, None),
        P(("groups", "tile", "batch"), None),
        P(("groups", "tile", "batch")),
        P(("groups", "tile", "batch"), None, None),
    )
    return jax.shard_map(
        local,
        mesh=mesh,
        in_specs=placed,
        out_specs=P(("groups", "depth"), None, "tile", None),
        check_vma=False,
    )
```

```python
import math

import jax
import jax.numpy as jnp
from jax import lax
from jax.sharding import PartitionSpec as P
from jax.experimental import pallas as pl
from jax.experimental.pallas import tpu as pltpu

SLICE_COEF = 0.002
DETECTOR_COEF = 0.006
RESIDUAL_SCALE = 0.125


def from_behind(block, axis, distance):
    devices = range(lax.axis_size(axis))
    route = [(i - distance, i) for i in devices if i - distance in devices]
    return lax.ppermute(block, axis, route)


def dft_block(width, sign):
    freq = jnp.arange(width, dtype=jnp.int32)
    product = freq[:, None] * freq[None, :] % width
    angle = 2.0 * math.pi / width * product.astype(jnp.float32)
    scale = 1.0 / math.sqrt(width)
    real_part = (jnp.cos(angle) * scale).astype(jnp.bfloat16)
    imag_part = (sign * jnp.sin(angle) * scale).astype(jnp.bfloat16)
    upper = jnp.concatenate([real_part, -imag_part], axis=1)
    lower = jnp.concatenate([imag_part, real_part], axis=1)
    return jnp.concatenate([upper, lower], axis=0)


def dft_right(width, sign):
    freq = jnp.arange(width, dtype=jnp.int32)
    product = freq[:, None] * freq[None, :] % width
    angle = 2.0 * math.pi / width * product.astype(jnp.float32)
    scale = 1.0 / math.sqrt(width)
    real_part = (jnp.cos(angle) * scale).astype(jnp.bfloat16)
    imag_part = (sign * jnp.sin(angle) * scale).astype(jnp.bfloat16)
    upper = jnp.concatenate([real_part, imag_part], axis=1)
    lower = jnp.concatenate([-imag_part, real_part], axis=1)
    return jnp.concatenate([upper, lower], axis=0)


def chirp_parts(width, coef):
    freq = jnp.arange(width, dtype=jnp.int32)
    shifted = (freq + width // 2) % width - width // 2
    square = shifted * shifted
    total = (square[:, None] + square[None, :]).astype(jnp.float32)
    phase = -coef * total
    return (jnp.cos(phase), jnp.sin(phase))


def left_apply(block, waves):
    number = waves.shape[0]
    width = waves.shape[2]
    stacked = waves.reshape(number, 2 * width, width)
    result = jnp.einsum("ij,gjk->gik", block, stacked, preferred_element_type=jnp.float32)
    return result.reshape(number, 2, width, width)


def propagate(waves, forward_block, inverse_block, chirp_re, chirp_im):
    first = left_apply(forward_block, waves).astype(jnp.bfloat16)
    spectrum = left_apply(forward_block, jnp.swapaxes(first, -1, -2))
    spec_re = spectrum[:, 0]
    spec_im = spectrum[:, 1]
    filtered = jnp.stack(
        [spec_re * chirp_re - spec_im * chirp_im, spec_re * chirp_im + spec_im * chirp_re], axis=1
    ).astype(jnp.bfloat16)
    back = left_apply(inverse_block, filtered).astype(jnp.bfloat16)
    return left_apply(inverse_block, jnp.swapaxes(back, -1, -2)).astype(jnp.bfloat16)


def transmit(waves, patch):
    values = waves.astype(jnp.float32)
    wave_re = values[:, 0]
    wave_im = values[:, 1]
    return jnp.stack(
        [
            patch[:, 0] * wave_re - patch[:, 1] * wave_im,
            patch[:, 0] * wave_im + patch[:, 1] * wave_re,
        ],
        axis=1,
    ).astype(jnp.bfloat16)


def residual_wave(waves, measured):
    values = waves.astype(jnp.float32)
    intensity = values[:, 0] * values[:, 0] + values[:, 1] * values[:, 1]
    weight = RESIDUAL_SCALE * (intensity - measured)
    return jnp.stack([weight * values[:, 0], weight * values[:, 1]], axis=1).astype(jnp.bfloat16)


def adjoint_terms(incoming, forward_block, inverse_block, chirp_re, chirp_im, inputs, patch):
    spread = propagate(incoming, forward_block, inverse_block, chirp_re, -chirp_im).astype(
        jnp.float32
    )
    source = inputs.astype(jnp.float32)
    term = jnp.stack(
        [
            source[:, 0] * spread[:, 0] + source[:, 1] * spread[:, 1],
            source[:, 0] * spread[:, 1] - source[:, 1] * spread[:, 0],
        ],
        axis=1,
    )
    passed = jnp.stack(
        [
            patch[:, 0] * spread[:, 0] + patch[:, 1] * spread[:, 1],
            patch[:, 0] * spread[:, 1] - patch[:, 1] * spread[:, 0],
        ],
        axis=1,
    ).astype(jnp.bfloat16)
    return (passed, term)


def wave_kernel(transmit_first, residual_after, backward):
    def kernel(*refs):
        refs = list(refs)
        wave_ref = refs.pop(0)
        patch_ref = refs.pop(0)
        chirp_ref = refs.pop(0)
        fl_ref, fr_ref, gl_ref, gr_ref = refs[:4]
        refs = refs[4:]
        extra_ref = refs.pop(0) if (residual_after or backward) else None
        width = wave_ref.shape[2]
        wave = wave_ref[0].astype(jnp.float32)
        patch_re = patch_ref[0, 0]
        patch_im = patch_ref[0, 1]
        if transmit_first:
            wave_re = patch_re * wave[0] - patch_im * wave[1]
            wave_im = patch_re * wave[1] + patch_im * wave[0]
        else:
            wave_re = wave[0]
            wave_im = wave[1]
        stacked = jnp.concatenate([wave_re, wave_im], axis=0).astype(jnp.bfloat16)
        first = jnp.dot(fl_ref[...], stacked, preferred_element_type=jnp.float32).astype(jnp.bfloat16)
        rowwise = jnp.concatenate([first[:width], first[width:]], axis=1)
        spectrum = jnp.dot(rowwise, fr_ref[...], preferred_element_type=jnp.float32)
        spec_re = spectrum[:, :width]
        spec_im = spectrum[:, width:]
        chirp_re = chirp_ref[0]
        chirp_im = chirp_ref[1]
        if backward:
            chirp_im = -chirp_im
        filtered = jnp.concatenate(
            [spec_re * chirp_re - spec_im * chirp_im, spec_re * chirp_im + spec_im * chirp_re],
            axis=1,
        ).astype(jnp.bfloat16)
        back = jnp.dot(filtered, gr_ref[...], preferred_element_type=jnp.float32).astype(jnp.bfloat16)
        columnwise = jnp.concatenate([back[:, :width], back[:, width:]], axis=0)
        out = jnp.dot(gl_ref[...], columnwise, preferred_element_type=jnp.float32).astype(jnp.bfloat16)
        values = out.astype(jnp.float32)
        out_re = values[:width]
        out_im = values[width:]
        if residual_after:
            measured = extra_ref[0]
            weight = RESIDUAL_SCALE * (out_re * out_re + out_im * out_im - measured)
            result_ref = refs[0]
            result_ref[0, 0] = (weight * out_re).astype(jnp.bfloat16)
            result_ref[0, 1] = (weight * out_im).astype(jnp.bfloat16)
        elif backward:
            source = extra_ref[0].astype(jnp.float32)
            passed_ref, term_ref = refs[0], refs[1]
            passed_ref[0, 0] = (patch_re * out_re + patch_im * out_im).astype(jnp.bfloat16)
            passed_ref[0, 1] = (patch_re * out_im - patch_im * out_re).astype(jnp.bfloat16)
            term_ref[0, 0] = source[0] * out_re + source[1] * out_im
            term_ref[0, 1] = source[0] * out_im - source[1] * out_re
        else:
            result_ref = refs[0]
            result_ref[0, 0] = out[:width]
            result_ref[0, 1] = out[width:]

    return kernel


def run_waves(waves, patches, chirps, blocks, extra=None, transmit_first=True, residual_after=False, backward=False):
    number, _, width, _ = waves.shape
    wave_spec = pl.BlockSpec((1, 2, width, width), lambda i: (i, 0, 0, 0))
    chirp_spec = pl.BlockSpec((2, width, width), lambda i: (0, 0, 0))
    block_spec = pl.BlockSpec((2 * width, 2 * width), lambda i: (0, 0))
    in_specs = [wave_spec, wave_spec, chirp_spec] + [block_spec] * 4
    args = [waves, patches, chirps] + list(blocks)
    if residual_after:
        in_specs.append(pl.BlockSpec((1, width, width), lambda i: (i, 0, 0)))
        args.append(extra)
    if backward:
        in_specs.append(wave_spec)
        args.append(extra)
        out_shape = (
            jax.ShapeDtypeStruct(waves.shape, jnp.bfloat16),
            jax.ShapeDtypeStruct(waves.shape, jnp.float32),
        )
        out_specs = (wave_spec, wave_spec)
    else:
        out_shape = jax.ShapeDtypeStruct(waves.shape, jnp.bfloat16)
        out_specs = wave_spec
    return pl.pallas_call(
        wave_kernel(transmit_first, residual_after, backward),
        grid=(number,),
        in_specs=in_specs,
        out_specs=out_specs,
        out_shape=out_shape,
    )(*args)


def scatter_kernel(rows_ref, columns_ref, live_ref, terms_ref, out_ref):
    index = pl.program_id(0)

    @pl.when(index == 0)
    def _():
        out_ref[...] = jnp.zeros(out_ref.shape, out_ref.dtype)

    width = terms_ref.shape[2]
    height = out_ref.shape[1]
    columns_all = out_ref.shape[2]
    row = rows_ref[index]
    column = columns_ref[index]
    alive = live_ref[index] > 0
    for part in range(2):
        term = jnp.where(alive, terms_ref[0, part], 0.0)
        wide = jnp.concatenate(
            [term, jnp.zeros((width, columns_all - width), jnp.float32)], axis=1
        )
        wide = pltpu.roll(wide, column, 1)
        tall = jnp.concatenate(
            [wide, jnp.zeros((height - width, columns_all), jnp.float32)], axis=0
        )
        tall = pltpu.roll(tall, row, 0)
        out_ref[part] = out_ref[part] + tall


def scatter_terms(terms, rows, columns, live, height, columns_all):
    number, _, width, _ = terms.shape
    grid_spec = pltpu.PrefetchScalarGridSpec(
        num_scalar_prefetch=3,
        grid=(number,),
        in_specs=[pl.BlockSpec((1, 2, width, width), lambda i, r, c, a: (i, 0, 0, 0))],
        out_specs=pl.BlockSpec((2, height, columns_all), lambda i, r, c, a: (0, 0, 0)),
    )
    return pl.pallas_call(
        scatter_kernel,
        grid_spec=grid_spec,
        out_shape=jax.ShapeDtypeStruct((2, height, columns_all), jnp.float32),
    )(rows, columns, live.astype(jnp.int32), terms)


def cut_kernel(rows_ref, columns_ref, order_ref, tile_ref, mine_ref, partner_ref, out_ref):
    index = pl.program_id(0)
    width = out_ref.shape[2]
    height = tile_ref.shape[2] + mine_ref.shape[2]
    columns_all = tile_ref.shape[3]
    row_shift = (height - rows_ref[index]) % height
    column_shift = (columns_all - columns_ref[index]) % columns_all
    first = order_ref[0] == 0
    for part in range(2):
        mine = mine_ref[0, part].astype(jnp.float32)
        partner = partner_ref[0, part].astype(jnp.float32)
        rim = jnp.concatenate(
            [jnp.where(first, mine, partner), jnp.where(first, partner, mine)], axis=1
        )
        full = jnp.concatenate([tile_ref[0, part], rim], axis=0)
        full = pltpu.roll(full, row_shift, 0)[:width]
        full = pltpu.roll(full, column_shift, 1)[:, :width]
        out_ref[0, part] = full


def cut_patches(tile, mine, partner, rows, columns, order, width):
    number = rows.shape[0]
    grid_spec = pltpu.PrefetchScalarGridSpec(
        num_scalar_prefetch=3,
        grid=(number,),
        in_specs=[
            pl.BlockSpec(tile.shape, lambda i, r, c, o: (0, 0, 0, 0)),
            pl.BlockSpec(mine.shape, lambda i, r, c, o: (0, 0, 0, 0)),
            pl.BlockSpec(partner.shape, lambda i, r, c, o: (0, 0, 0, 0)),
        ],
        out_specs=pl.BlockSpec((1, 2, width, width), lambda i, r, c, o: (i, 0, 0, 0)),
    )
    return pl.pallas_call(
        cut_kernel,
        grid_spec=grid_spec,
        out_shape=jax.ShapeDtypeStruct((number, 2, width, width), jnp.float32),
    )(rows, columns, order, tile, mine, partner)


def propagate_block(wave_re, wave_im, blocks, chirp_re, chirp_im):
    fl_ref, fr_ref, gl_ref, gr_ref = blocks
    width = wave_re.shape[0]
    stacked = jnp.concatenate([wave_re, wave_im], axis=0).astype(jnp.bfloat16)
    first = jnp.dot(fl_ref[...], stacked, preferred_element_type=jnp.float32).astype(jnp.bfloat16)
    rowwise = jnp.concatenate([first[:width], first[width:]], axis=1)
    spectrum = jnp.dot(rowwise, fr_ref[...], preferred_element_type=jnp.float32)
    spec_re = spectrum[:, :width]
    spec_im = spectrum[:, width:]
    filtered = jnp.concatenate(
        [spec_re * chirp_re - spec_im * chirp_im, spec_re * chirp_im + spec_im * chirp_re],
        axis=1,
    ).astype(jnp.bfloat16)
    back = jnp.dot(filtered, gr_ref[...], preferred_element_type=jnp.float32).astype(jnp.bfloat16)
    columnwise = jnp.concatenate([back[:, :width], back[:, width:]], axis=0)
    out = jnp.dot(gl_ref[...], columnwise, preferred_element_type=jnp.float32).astype(jnp.bfloat16)
    values = out.astype(jnp.float32)
    return (values[:width], values[width:])


def place_term(term_re, term_im, row, column, alive, total_ref):
    width = term_re.shape[0]
    height = total_ref.shape[1]
    columns_all = total_ref.shape[2]
    row_shift = row % height
    column_shift = column % columns_all
    for part, term in enumerate((term_re, term_im)):
        term = jnp.where(alive, term, 0.0)
        wide = jnp.concatenate(
            [term, jnp.zeros((width, columns_all - width), jnp.float32)], axis=1
        )
        wide = pltpu.roll(wide, column_shift, 1)
        tall = jnp.concatenate(
            [wide, jnp.zeros((height - width, columns_all), jnp.float32)], axis=0
        )
        total_ref[part] = total_ref[part] + pltpu.roll(tall, row_shift, 0)


def adjoint_kernel(last):
    def kernel(rows_ref, columns_ref, live_ref, slot_ref, other_ref, *refs):
        refs = list(refs)
        wave_ref = refs.pop(0)
        patch_ref = refs.pop(0)
        chirp_ref = refs.pop(0)
        blocks = refs[:4]
        refs = refs[4:]
        if last:
            own_ref = refs.pop(0)
            partner_ref = refs.pop(0)
        else:
            source_ref = refs.pop(0)
        passed_ref, grad_ref, total_ref = refs
        index = pl.program_id(0)

        @pl.when(index == 0)
        def _():
            total_ref[...] = jnp.zeros(total_ref.shape, total_ref.dtype)

        wave = wave_ref[0].astype(jnp.float32)
        patch_re = patch_ref[0, 0]
        patch_im = patch_ref[0, 1]
        chirp_re = chirp_ref[0]
        chirp_im = chirp_ref[1]
        if last:
            source_re = wave[0]
            source_im = wave[1]
            lit_re = patch_re * wave[0] - patch_im * wave[1]
            lit_im = patch_re * wave[1] + patch_im * wave[0]
            out_re, out_im = propagate_block(lit_re, lit_im, blocks, chirp_re, chirp_im)
            measured = jnp.where(other_ref[index] > 0, partner_ref[0], own_ref[0])
            weight = RESIDUAL_SCALE * (out_re * out_re + out_im * out_im - measured)
            in_re = (weight * out_re).astype(jnp.bfloat16).astype(jnp.float32)
            in_im = (weight * out_im).astype(jnp.bfloat16).astype(jnp.float32)
        else:
            source = source_ref[0].astype(jnp.float32)
            source_re = source[0]
            source_im = source[1]
            in_re = wave[0]
            in_im = wave[1]
        spread_re, spread_im = propagate_block(in_re, in_im, blocks, chirp_re, -chirp_im)
        passed_ref[0, 0] = (patch_re * spread_re + patch_im * spread_im).astype(jnp.bfloat16)
        passed_ref[0, 1] = (patch_re * spread_im - patch_im * spread_re).astype(jnp.bfloat16)
        term_re = source_re * spread_re + source_im * spread_im
        term_im = source_re * spread_im - source_im * spread_re
        place_term(
            term_re, term_im, rows_ref[index], columns_ref[index], live_ref[index] > 0, total_ref
        )

        @pl.when(index == pl.num_programs(0) - 1)
        def _():
            grad_ref[...] = total_ref[...].astype(grad_ref.dtype)

    return kernel


def run_adjoint(waves, patches, chirps, blocks, scalars, extra, height, columns_all, last):
    number, _, width, _ = waves.shape
    wave_spec = pl.BlockSpec((1, 2, width, width), lambda i, *s: (i, 0, 0, 0))
    chirp_spec = pl.BlockSpec((2, width, width), lambda i, *s: (0, 0, 0))
    block_spec = pl.BlockSpec((2 * width, 2 * width), lambda i, *s: (0, 0))
    in_specs = [wave_spec, wave_spec, chirp_spec] + [block_spec] * 4
    if last:
        slot_spec = pl.BlockSpec((1, width, width), lambda i, r, c, a, s, o: (s[i], 0, 0))
        in_specs += [slot_spec, slot_spec]
    else:
        in_specs += [wave_spec]
    grid_spec = pltpu.PrefetchScalarGridSpec(
        num_scalar_prefetch=5,
        grid=(number,),
        in_specs=in_specs,
        out_specs=(
            wave_spec,
            pl.BlockSpec((2, height, columns_all), lambda i, *s: (0, 0, 0)),
        ),
        scratch_shapes=[pltpu.VMEM((2, height, columns_all), jnp.float32)],
    )
    return pl.pallas_call(
        adjoint_kernel(last),
        grid_spec=grid_spec,
        out_shape=(
            jax.ShapeDtypeStruct(waves.shape, jnp.bfloat16),
            jax.ShapeDtypeStruct((2, height, columns_all), jnp.bfloat16),
        ),
    )(*scalars, waves, patches, chirps, *blocks, *extra)


def local(object_field, probe, positions, counts, measured):
    width = probe.shape[1]
    tile_rows = object_field.shape[2]
    columns_all = object_field.shape[3]
    tile_index = lax.axis_index("tile")
    tile_count = lax.axis_size("tile")
    segment = lax.axis_index("depth")
    depth_count = lax.axis_size("depth")
    batch_index = lax.axis_index("batch")
    batch_count = lax.axis_size("batch")
    half = columns_all // batch_count
    wanted = lax.dynamic_slice_in_dim(object_field[:, :, :width, :], batch_index * half, half, 3)
    mine = from_behind(wanted.astype(jnp.bfloat16), "tile", -1)
    pairs = [(b, (b + 1) % batch_count) for b in range(batch_count)]
    partner = lax.ppermute(mine, "batch", pairs)
    capacity = positions.shape[0]
    share = -(-capacity // batch_count)
    first_core = batch_index == 0
    both_positions = lax.ppermute(positions, "batch", pairs)
    both_counts = lax.ppermute(counts, "batch", pairs)
    both_measured = lax.ppermute(measured, "batch", pairs)
    all_positions = jnp.where(
        first_core,
        jnp.concatenate([positions, both_positions]),
        jnp.concatenate([both_positions, positions]),
    )
    all_counts = jnp.where(
        first_core, jnp.concatenate([counts, both_counts]), jnp.concatenate([both_counts, counts])
    )
    entry = batch_index * share + jnp.arange(share, dtype=jnp.int32)
    live = entry < all_counts[0] + all_counts[1]
    later = entry >= all_counts[0]
    slot = jnp.clip(jnp.where(later, entry - all_counts[0], entry), 0, capacity - 1)
    flat = jnp.where(later, capacity, 0) + slot
    chosen = all_positions[flat]
    other = (later == first_core).astype(jnp.int32)
    local_rows = chosen[:, 0] - tile_index * tile_rows
    local_columns = chosen[:, 1]
    order = jnp.reshape(batch_index, (1,)).astype(jnp.int32)
    patches = cut_patches(object_field, mine, partner, local_rows, local_columns, order, width)
    number = patches.shape[0]
    forward_block = dft_block(width, -1.0)
    inverse_block = dft_block(width, 1.0)
    coef = jnp.where(
        segment == depth_count - 1, jnp.float32(DETECTOR_COEF), jnp.float32(SLICE_COEF)
    )
    chirp_re, chirp_im = chirp_parts(width, coef)
    start = jnp.broadcast_to(probe[None], (number, 2, width, width))

    chirps = jnp.stack([chirp_re, chirp_im])
    blocks = (forward_block, dft_right(width, -1.0), inverse_block, dft_right(width, 1.0))

    def forward_all(waves):
        return run_waves(waves, patches, chirps, blocks)

    def silent(waves):
        return jnp.zeros_like(waves)

    carry = start
    inputs = start
    for turn in range(depth_count - 1):
        if turn > 0:
            carry = lax.ppermute(carry, "depth", [(turn - 1, turn)])
            inputs = jnp.where(segment == turn, carry, inputs)
        carry = lax.cond(segment == turn, forward_all, silent, carry)

    height = tile_rows + width
    scalars = (local_rows, local_columns, live.astype(jnp.int32), slot, other)

    def last_pass(incoming):
        return run_adjoint(
            incoming, patches, chirps, blocks, scalars, (measured, both_measured),
            height, columns_all, True,
        )

    def last_silent(incoming):
        return (jnp.zeros_like(incoming), jnp.zeros((2, height, columns_all), jnp.bfloat16))

    if depth_count > 1:
        carry = lax.ppermute(carry, "depth", [(depth_count - 2, depth_count - 1)])
    carry, gradient = lax.cond(segment == depth_count - 1, last_pass, last_silent, carry)

    def back_pass(incoming, previous):
        return run_adjoint(
            incoming, patches, chirps, blocks, scalars, (inputs,), height, columns_all, False
        )

    def back_silent(incoming, previous):
        return (jnp.zeros_like(incoming), previous)

    for turn in reversed(range(depth_count - 1)):
        carry = lax.ppermute(carry, "depth", [(turn + 1, turn)])
        carry, gradient = lax.cond(segment == turn, back_pass, back_silent, carry, gradient)

    gradient = gradient.astype(jnp.bfloat16)
    spill = gradient[:, tile_rows:, :]
    keep = lax.dynamic_slice_in_dim(spill, batch_index * half, half, 2)
    give = lax.dynamic_slice_in_dim(spill, (1 - batch_index) * half, half, 2)
    got = lax.ppermute(give, "batch", pairs)
    spill_sum = (keep.astype(jnp.float32) + got.astype(jnp.float32)).astype(jnp.bfloat16)
    arrived = lax.ppermute(spill_sum, "tile", [(t, t + 1) for t in range(tile_count - 1)])
    own = gradient[:, :tile_rows, :]
    other = lax.ppermute(own, "batch", pairs)
    arrived_other = lax.ppermute(arrived, "batch", pairs)
    incoming = jnp.where(
        first_core,
        jnp.concatenate([arrived, arrived_other], axis=2),
        jnp.concatenate([arrived_other, arrived], axis=2),
    )
    summed = own.astype(jnp.float32) + other.astype(jnp.float32)
    summed = summed.at[:, :width, :].add(incoming.astype(jnp.float32))
    return summed[None]


def solution(mesh):
    placed = (
        P(("groups", "depth"), None, "tile", None),
        P("groups", None, None),
        P(("groups", "tile", "batch"), None),
        P(("groups", "tile", "batch")),
        P(("groups", "tile", "batch"), None, None),
    )
    return jax.shard_map(
        local,
        mesh=mesh,
        in_specs=placed,
        out_specs=P(("groups", "depth"), None, "tile", None),
        check_vma=False,
    )
```

```python
import math

import jax
import jax.numpy as jnp
from jax import lax
from jax.sharding import PartitionSpec as P
from jax.experimental import pallas as pl
from jax.experimental.pallas import tpu as pltpu

SLICE_COEF = 0.002
DETECTOR_COEF = 0.006
RESIDUAL_SCALE = 0.125


def from_behind(block, axis, distance):
    devices = range(lax.axis_size(axis))
    route = [(i - distance, i) for i in devices if i - distance in devices]
    return lax.ppermute(block, axis, route)


def dft_block(width, sign):
    freq = jnp.arange(width, dtype=jnp.int32)
    product = freq[:, None] * freq[None, :] % width
    angle = 2.0 * math.pi / width * product.astype(jnp.float32)
    scale = 1.0 / math.sqrt(width)
    real_part = (jnp.cos(angle) * scale).astype(jnp.bfloat16)
    imag_part = (sign * jnp.sin(angle) * scale).astype(jnp.bfloat16)
    upper = jnp.concatenate([real_part, -imag_part], axis=1)
    lower = jnp.concatenate([imag_part, real_part], axis=1)
    return jnp.concatenate([upper, lower], axis=0)


def dft_right(width, sign):
    freq = jnp.arange(width, dtype=jnp.int32)
    product = freq[:, None] * freq[None, :] % width
    angle = 2.0 * math.pi / width * product.astype(jnp.float32)
    scale = 1.0 / math.sqrt(width)
    real_part = (jnp.cos(angle) * scale).astype(jnp.bfloat16)
    imag_part = (sign * jnp.sin(angle) * scale).astype(jnp.bfloat16)
    upper = jnp.concatenate([real_part, imag_part], axis=1)
    lower = jnp.concatenate([-imag_part, real_part], axis=1)
    return jnp.concatenate([upper, lower], axis=0)


def chirp_parts(width, coef):
    freq = jnp.arange(width, dtype=jnp.int32)
    shifted = (freq + width // 2) % width - width // 2
    square = shifted * shifted
    total = (square[:, None] + square[None, :]).astype(jnp.float32)
    phase = -coef * total
    return (jnp.cos(phase), jnp.sin(phase))


def left_apply(block, waves):
    number = waves.shape[0]
    width = waves.shape[2]
    stacked = waves.reshape(number, 2 * width, width)
    result = jnp.einsum("ij,gjk->gik", block, stacked, preferred_element_type=jnp.float32)
    return result.reshape(number, 2, width, width)


def propagate(waves, forward_block, inverse_block, chirp_re, chirp_im):
    first = left_apply(forward_block, waves).astype(jnp.bfloat16)
    spectrum = left_apply(forward_block, jnp.swapaxes(first, -1, -2))
    spec_re = spectrum[:, 0]
    spec_im = spectrum[:, 1]
    filtered = jnp.stack(
        [spec_re * chirp_re - spec_im * chirp_im, spec_re * chirp_im + spec_im * chirp_re], axis=1
    ).astype(jnp.bfloat16)
    back = left_apply(inverse_block, filtered).astype(jnp.bfloat16)
    return left_apply(inverse_block, jnp.swapaxes(back, -1, -2)).astype(jnp.bfloat16)


def transmit(waves, patch):
    values = waves.astype(jnp.float32)
    wave_re = values[:, 0]
    wave_im = values[:, 1]
    return jnp.stack(
        [
            patch[:, 0] * wave_re - patch[:, 1] * wave_im,
            patch[:, 0] * wave_im + patch[:, 1] * wave_re,
        ],
        axis=1,
    ).astype(jnp.bfloat16)


def residual_wave(waves, measured):
    values = waves.astype(jnp.float32)
    intensity = values[:, 0] * values[:, 0] + values[:, 1] * values[:, 1]
    weight = RESIDUAL_SCALE * (intensity - measured)
    return jnp.stack([weight * values[:, 0], weight * values[:, 1]], axis=1).astype(jnp.bfloat16)


def adjoint_terms(incoming, forward_block, inverse_block, chirp_re, chirp_im, inputs, patch):
    spread = propagate(incoming, forward_block, inverse_block, chirp_re, -chirp_im).astype(
        jnp.float32
    )
    source = inputs.astype(jnp.float32)
    term = jnp.stack(
        [
            source[:, 0] * spread[:, 0] + source[:, 1] * spread[:, 1],
            source[:, 0] * spread[:, 1] - source[:, 1] * spread[:, 0],
        ],
        axis=1,
    )
    passed = jnp.stack(
        [
            patch[:, 0] * spread[:, 0] + patch[:, 1] * spread[:, 1],
            patch[:, 0] * spread[:, 1] - patch[:, 1] * spread[:, 0],
        ],
        axis=1,
    ).astype(jnp.bfloat16)
    return (passed, term)


def wave_kernel(transmit_first, residual_after, backward):
    def kernel(*refs):
        refs = list(refs)
        wave_ref = refs.pop(0)
        patch_ref = refs.pop(0)
        chirp_ref = refs.pop(0)
        fl_ref, fr_ref, gl_ref, gr_ref = refs[:4]
        refs = refs[4:]
        extra_ref = refs.pop(0) if (residual_after or backward) else None
        width = wave_ref.shape[2]
        wave = wave_ref[0].astype(jnp.float32)
        patch_re = patch_ref[0, 0]
        patch_im = patch_ref[0, 1]
        if transmit_first:
            wave_re = patch_re * wave[0] - patch_im * wave[1]
            wave_im = patch_re * wave[1] + patch_im * wave[0]
        else:
            wave_re = wave[0]
            wave_im = wave[1]
        stacked = jnp.concatenate([wave_re, wave_im], axis=0).astype(jnp.bfloat16)
        first = jnp.dot(fl_ref[...], stacked, preferred_element_type=jnp.float32).astype(jnp.bfloat16)
        rowwise = jnp.concatenate([first[:width], first[width:]], axis=1)
        spectrum = jnp.dot(rowwise, fr_ref[...], preferred_element_type=jnp.float32)
        spec_re = spectrum[:, :width]
        spec_im = spectrum[:, width:]
        chirp_re = chirp_ref[0]
        chirp_im = chirp_ref[1]
        if backward:
            chirp_im = -chirp_im
        filtered = jnp.concatenate(
            [spec_re * chirp_re - spec_im * chirp_im, spec_re * chirp_im + spec_im * chirp_re],
            axis=1,
        ).astype(jnp.bfloat16)
        back = jnp.dot(filtered, gr_ref[...], preferred_element_type=jnp.float32).astype(jnp.bfloat16)
        columnwise = jnp.concatenate([back[:, :width], back[:, width:]], axis=0)
        out = jnp.dot(gl_ref[...], columnwise, preferred_element_type=jnp.float32).astype(jnp.bfloat16)
        values = out.astype(jnp.float32)
        out_re = values[:width]
        out_im = values[width:]
        if residual_after:
            measured = extra_ref[0]
            weight = RESIDUAL_SCALE * (out_re * out_re + out_im * out_im - measured)
            result_ref = refs[0]
            result_ref[0, 0] = (weight * out_re).astype(jnp.bfloat16)
            result_ref[0, 1] = (weight * out_im).astype(jnp.bfloat16)
        elif backward:
            source = extra_ref[0].astype(jnp.float32)
            passed_ref, term_ref = refs[0], refs[1]
            passed_ref[0, 0] = (patch_re * out_re + patch_im * out_im).astype(jnp.bfloat16)
            passed_ref[0, 1] = (patch_re * out_im - patch_im * out_re).astype(jnp.bfloat16)
            term_ref[0, 0] = source[0] * out_re + source[1] * out_im
            term_ref[0, 1] = source[0] * out_im - source[1] * out_re
        else:
            result_ref = refs[0]
            result_ref[0, 0] = out[:width]
            result_ref[0, 1] = out[width:]

    return kernel


def run_waves(waves, patches, chirps, blocks, extra=None, transmit_first=True, residual_after=False, backward=False):
    number, _, width, _ = waves.shape
    wave_spec = pl.BlockSpec((1, 2, width, width), lambda i: (i, 0, 0, 0))
    chirp_spec = pl.BlockSpec((2, width, width), lambda i: (0, 0, 0))
    block_spec = pl.BlockSpec((2 * width, 2 * width), lambda i: (0, 0))
    in_specs = [wave_spec, wave_spec, chirp_spec] + [block_spec] * 4
    args = [waves, patches, chirps] + list(blocks)
    if residual_after:
        in_specs.append(pl.BlockSpec((1, width, width), lambda i: (i, 0, 0)))
        args.append(extra)
    if backward:
        in_specs.append(wave_spec)
        args.append(extra)
        out_shape = (
            jax.ShapeDtypeStruct(waves.shape, jnp.bfloat16),
            jax.ShapeDtypeStruct(waves.shape, jnp.float32),
        )
        out_specs = (wave_spec, wave_spec)
    else:
        out_shape = jax.ShapeDtypeStruct(waves.shape, jnp.bfloat16)
        out_specs = wave_spec
    return pl.pallas_call(
        wave_kernel(transmit_first, residual_after, backward),
        grid=(number,),
        in_specs=in_specs,
        out_specs=out_specs,
        out_shape=out_shape,
    )(*args)


def scatter_kernel(rows_ref, columns_ref, live_ref, terms_ref, out_ref):
    index = pl.program_id(0)

    @pl.when(index == 0)
    def _():
        out_ref[...] = jnp.zeros(out_ref.shape, out_ref.dtype)

    width = terms_ref.shape[2]
    height = out_ref.shape[1]
    columns_all = out_ref.shape[2]
    row = rows_ref[index]
    column = columns_ref[index]
    alive = live_ref[index] > 0
    for part in range(2):
        term = jnp.where(alive, terms_ref[0, part], 0.0)
        wide = jnp.concatenate(
            [term, jnp.zeros((width, columns_all - width), jnp.float32)], axis=1
        )
        wide = pltpu.roll(wide, column, 1)
        tall = jnp.concatenate(
            [wide, jnp.zeros((height - width, columns_all), jnp.float32)], axis=0
        )
        tall = pltpu.roll(tall, row, 0)
        out_ref[part] = out_ref[part] + tall


def scatter_terms(terms, rows, columns, live, height, columns_all):
    number, _, width, _ = terms.shape
    grid_spec = pltpu.PrefetchScalarGridSpec(
        num_scalar_prefetch=3,
        grid=(number,),
        in_specs=[pl.BlockSpec((1, 2, width, width), lambda i, r, c, a: (i, 0, 0, 0))],
        out_specs=pl.BlockSpec((2, height, columns_all), lambda i, r, c, a: (0, 0, 0)),
    )
    return pl.pallas_call(
        scatter_kernel,
        grid_spec=grid_spec,
        out_shape=jax.ShapeDtypeStruct((2, height, columns_all), jnp.float32),
    )(rows, columns, live.astype(jnp.int32), terms)


def cut_kernel(rows_ref, columns_ref, order_ref, tile_ref, mine_ref, partner_ref, out_ref):
    index = pl.program_id(0)
    width = out_ref.shape[2]
    height = tile_ref.shape[2] + mine_ref.shape[2]
    columns_all = tile_ref.shape[3]
    row_shift = (height - rows_ref[index]) % height
    column_shift = (columns_all - columns_ref[index]) % columns_all
    first = order_ref[0] == 0
    for part in range(2):
        mine = mine_ref[0, part].astype(jnp.float32)
        partner = partner_ref[0, part].astype(jnp.float32)
        rim = jnp.concatenate(
            [jnp.where(first, mine, partner), jnp.where(first, partner, mine)], axis=1
        )
        full = jnp.concatenate([tile_ref[0, part], rim], axis=0)
        full = pltpu.roll(full, row_shift, 0)[:width]
        full = pltpu.roll(full, column_shift, 1)[:, :width]
        out_ref[0, part] = full


def cut_patches(tile, mine, partner, rows, columns, order, width):
    number = rows.shape[0]
    grid_spec = pltpu.PrefetchScalarGridSpec(
        num_scalar_prefetch=3,
        grid=(number,),
        in_specs=[
            pl.BlockSpec(tile.shape, lambda i, r, c, o: (0, 0, 0, 0)),
            pl.BlockSpec(mine.shape, lambda i, r, c, o: (0, 0, 0, 0)),
            pl.BlockSpec(partner.shape, lambda i, r, c, o: (0, 0, 0, 0)),
        ],
        out_specs=pl.BlockSpec((1, 2, width, width), lambda i, r, c, o: (i, 0, 0, 0)),
    )
    return pl.pallas_call(
        cut_kernel,
        grid_spec=grid_spec,
        out_shape=jax.ShapeDtypeStruct((number, 2, width, width), jnp.float32),
    )(rows, columns, order, tile, mine, partner)


def propagate_block(wave_re, wave_im, blocks, chirp_re, chirp_im):
    fl_ref, fr_ref, gl_ref, gr_ref = blocks
    width = wave_re.shape[0]
    stacked = jnp.concatenate([wave_re, wave_im], axis=0).astype(jnp.bfloat16)
    first = jnp.dot(fl_ref[...], stacked, preferred_element_type=jnp.float32).astype(jnp.bfloat16)
    rowwise = jnp.concatenate([first[:width], first[width:]], axis=1)
    spectrum = jnp.dot(rowwise, fr_ref[...], preferred_element_type=jnp.float32)
    spec_re = spectrum[:, :width]
    spec_im = spectrum[:, width:]
    filtered = jnp.concatenate(
        [spec_re * chirp_re - spec_im * chirp_im, spec_re * chirp_im + spec_im * chirp_re],
        axis=1,
    ).astype(jnp.bfloat16)
    back = jnp.dot(filtered, gr_ref[...], preferred_element_type=jnp.float32).astype(jnp.bfloat16)
    columnwise = jnp.concatenate([back[:, :width], back[:, width:]], axis=0)
    out = jnp.dot(gl_ref[...], columnwise, preferred_element_type=jnp.float32).astype(jnp.bfloat16)
    values = out.astype(jnp.float32)
    return (values[:width], values[width:])


def place_term(term_re, term_im, row, column, alive, total_ref):
    width = term_re.shape[0]
    height = total_ref.shape[1]
    columns_all = total_ref.shape[2]
    row_shift = row % height
    column_shift = column % columns_all
    for part, term in enumerate((term_re, term_im)):
        term = jnp.where(alive, term, 0.0)
        wide = jnp.concatenate(
            [term, jnp.zeros((width, columns_all - width), jnp.float32)], axis=1
        )
        wide = pltpu.roll(wide, column_shift, 1)
        tall = jnp.concatenate(
            [wide, jnp.zeros((height - width, columns_all), jnp.float32)], axis=0
        )
        total_ref[part] = total_ref[part] + pltpu.roll(tall, row_shift, 0)


def adjoint_kernel(last):
    def kernel(rows_ref, columns_ref, live_ref, slot_ref, other_ref, *refs):
        refs = list(refs)
        wave_ref = refs.pop(0)
        patch_ref = refs.pop(0)
        chirp_ref = refs.pop(0)
        blocks = refs[:4]
        refs = refs[4:]
        if last:
            own_ref = refs.pop(0)
            partner_ref = refs.pop(0)
        else:
            source_ref = refs.pop(0)
        passed_ref, grad_ref, total_ref = refs
        index = pl.program_id(0)

        @pl.when(index == 0)
        def _():
            total_ref[...] = jnp.zeros(total_ref.shape, total_ref.dtype)

        wave = wave_ref[0].astype(jnp.float32)
        patch_re = patch_ref[0, 0]
        patch_im = patch_ref[0, 1]
        chirp_re = chirp_ref[0]
        chirp_im = chirp_ref[1]
        if last:
            source_re = wave[0]
            source_im = wave[1]
            lit_re = patch_re * wave[0] - patch_im * wave[1]
            lit_im = patch_re * wave[1] + patch_im * wave[0]
            out_re, out_im = propagate_block(lit_re, lit_im, blocks, chirp_re, chirp_im)
            measured = jnp.where(other_ref[index] > 0, partner_ref[0], own_ref[0])
            weight = RESIDUAL_SCALE * (out_re * out_re + out_im * out_im - measured)
            in_re = (weight * out_re).astype(jnp.bfloat16).astype(jnp.float32)
            in_im = (weight * out_im).astype(jnp.bfloat16).astype(jnp.float32)
        else:
            source = source_ref[0].astype(jnp.float32)
            source_re = source[0]
            source_im = source[1]
            in_re = wave[0]
            in_im = wave[1]
        spread_re, spread_im = propagate_block(in_re, in_im, blocks, chirp_re, -chirp_im)
        passed_ref[0, 0] = (patch_re * spread_re + patch_im * spread_im).astype(jnp.bfloat16)
        passed_ref[0, 1] = (patch_re * spread_im - patch_im * spread_re).astype(jnp.bfloat16)
        term_re = source_re * spread_re + source_im * spread_im
        term_im = source_re * spread_im - source_im * spread_re
        place_term(
            term_re, term_im, rows_ref[index], columns_ref[index], live_ref[index] > 0, total_ref
        )

        @pl.when(index == pl.num_programs(0) - 1)
        def _():
            grad_ref[...] = total_ref[...].astype(grad_ref.dtype)

    return kernel


def run_adjoint(waves, patches, chirps, blocks, scalars, extra, height, columns_all, last):
    number, _, width, _ = waves.shape
    wave_spec = pl.BlockSpec((1, 2, width, width), lambda i, *s: (i, 0, 0, 0))
    chirp_spec = pl.BlockSpec((2, width, width), lambda i, *s: (0, 0, 0))
    block_spec = pl.BlockSpec((2 * width, 2 * width), lambda i, *s: (0, 0))
    in_specs = [wave_spec, wave_spec, chirp_spec] + [block_spec] * 4
    if last:
        slot_spec = pl.BlockSpec((1, width, width), lambda i, r, c, a, s, o: (s[i], 0, 0))
        in_specs += [slot_spec, slot_spec]
    else:
        in_specs += [wave_spec]
    grid_spec = pltpu.PrefetchScalarGridSpec(
        num_scalar_prefetch=5,
        grid=(number,),
        in_specs=in_specs,
        out_specs=(
            wave_spec,
            pl.BlockSpec((2, height, columns_all), lambda i, *s: (0, 0, 0)),
        ),
        scratch_shapes=[pltpu.VMEM((2, height, columns_all), jnp.float32)],
    )
    return pl.pallas_call(
        adjoint_kernel(last),
        grid_spec=grid_spec,
        out_shape=(
            jax.ShapeDtypeStruct(waves.shape, jnp.bfloat16),
            jax.ShapeDtypeStruct((2, height, columns_all), jnp.bfloat16),
        ),
    )(*scalars, waves, patches, chirps, *blocks, *extra)


def local(object_field, probe, positions, counts, measured):
    width = probe.shape[1]
    tile_rows = object_field.shape[2]
    columns_all = object_field.shape[3]
    tile_index = lax.axis_index("tile")
    tile_count = lax.axis_size("tile")
    segment = lax.axis_index("depth")
    depth_count = lax.axis_size("depth")
    batch_index = lax.axis_index("batch")
    batch_count = lax.axis_size("batch")
    half = columns_all // batch_count
    wanted = lax.dynamic_slice_in_dim(object_field[:, :, :width, :], batch_index * half, half, 3)
    mine = from_behind(wanted.astype(jnp.bfloat16), "tile", -1)
    pairs = [(b, (b + 1) % batch_count) for b in range(batch_count)]
    partner = lax.ppermute(mine, "batch", pairs)
    capacity = positions.shape[0]
    share = -(-capacity // batch_count)
    first_core = batch_index == 0
    both_positions = lax.ppermute(positions, "batch", pairs)
    both_counts = lax.ppermute(counts, "batch", pairs)
    both_measured = lax.ppermute(measured, "batch", pairs)
    all_positions = jnp.where(
        first_core,
        jnp.concatenate([positions, both_positions]),
        jnp.concatenate([both_positions, positions]),
    )
    all_counts = jnp.where(
        first_core, jnp.concatenate([counts, both_counts]), jnp.concatenate([both_counts, counts])
    )
    entry = batch_index * share + jnp.arange(share, dtype=jnp.int32)
    live = entry < all_counts[0] + all_counts[1]
    later = entry >= all_counts[0]
    slot = jnp.clip(jnp.where(later, entry - all_counts[0], entry), 0, capacity - 1)
    flat = jnp.where(later, capacity, 0) + slot
    chosen = all_positions[flat]
    other = (later == first_core).astype(jnp.int32)
    local_rows = chosen[:, 0] - tile_index * tile_rows
    local_columns = chosen[:, 1]
    order = jnp.reshape(batch_index, (1,)).astype(jnp.int32)
    patches = cut_patches(object_field, mine, partner, local_rows, local_columns, order, width)
    columns_half = lax.dynamic_slice_in_dim(object_field, batch_index * half, half, 3)
    prior_tile = lax.ppermute(columns_half.astype(jnp.bfloat16), "depth", [(0, 1)])
    prior_rim = lax.ppermute(
        wanted.astype(jnp.bfloat16),
        ("tile", "depth"),
        [((t + 1) * depth_count, t * depth_count + 1) for t in range(tile_count - 1)],
    )
    prior_tile_other = lax.ppermute(prior_tile, "batch", pairs)
    prior_rim_other = lax.ppermute(prior_rim, "batch", pairs)
    prior_full = jnp.where(
        first_core,
        jnp.concatenate([prior_tile, prior_tile_other], axis=3),
        jnp.concatenate([prior_tile_other, prior_tile], axis=3),
    ).astype(jnp.float32)
    prior_patches = cut_patches(
        prior_full, prior_rim, prior_rim_other, local_rows, local_columns, order, width
    )
    number = patches.shape[0]
    forward_block = dft_block(width, -1.0)
    inverse_block = dft_block(width, 1.0)
    coef = jnp.where(
        segment == depth_count - 1, jnp.float32(DETECTOR_COEF), jnp.float32(SLICE_COEF)
    )
    chirp_re, chirp_im = chirp_parts(width, coef)
    start = jnp.broadcast_to(probe[None], (number, 2, width, width))

    chirps = jnp.stack([chirp_re, chirp_im])
    blocks = (forward_block, dft_right(width, -1.0), inverse_block, dft_right(width, 1.0))

    def forward_all(waves):
        return run_waves(waves, patches, chirps, blocks)

    def silent(waves):
        return jnp.zeros_like(waves)

    first_re, first_im = chirp_parts(width, jnp.float32(SLICE_COEF))
    first_chirps = jnp.stack([first_re, first_im])

    def forward_first(waves):
        return run_waves(waves, prior_patches, first_chirps, blocks)

    carry = lax.cond(segment == 1, forward_first, silent, start)
    inputs = jnp.where(segment == 1, carry, start)
    for turn in range(1, depth_count - 1):
        if turn > 1:
            carry = lax.ppermute(carry, "depth", [(turn - 1, turn)])
            inputs = jnp.where(segment == turn, carry, inputs)
        carry = lax.cond(segment == turn, forward_all, silent, carry)

    height = tile_rows + width
    scalars = (local_rows, local_columns, live.astype(jnp.int32), slot, other)

    def last_pass(incoming):
        return run_adjoint(
            incoming, patches, chirps, blocks, scalars, (measured, both_measured),
            height, columns_all, True,
        )

    def last_silent(incoming):
        return (jnp.zeros_like(incoming), jnp.zeros((2, height, columns_all), jnp.bfloat16))

    if depth_count > 2:
        carry = lax.ppermute(carry, "depth", [(depth_count - 2, depth_count - 1)])
    carry, gradient = lax.cond(segment == depth_count - 1, last_pass, last_silent, carry)

    def back_pass(incoming, previous):
        return run_adjoint(
            incoming, patches, chirps, blocks, scalars, (inputs,), height, columns_all, False
        )

    def back_silent(incoming, previous):
        return (jnp.zeros_like(incoming), previous)

    for turn in reversed(range(depth_count - 1)):
        carry = lax.ppermute(carry, "depth", [(turn + 1, turn)])
        carry, gradient = lax.cond(segment == turn, back_pass, back_silent, carry, gradient)

    gradient = gradient.astype(jnp.bfloat16)
    spill = gradient[:, tile_rows:, :]
    keep = lax.dynamic_slice_in_dim(spill, batch_index * half, half, 2)
    give = lax.dynamic_slice_in_dim(spill, (1 - batch_index) * half, half, 2)
    got = lax.ppermute(give, "batch", pairs)
    spill_sum = (keep.astype(jnp.float32) + got.astype(jnp.float32)).astype(jnp.bfloat16)
    arrived = lax.ppermute(spill_sum, "tile", [(t, t + 1) for t in range(tile_count - 1)])
    own = gradient[:, :tile_rows, :]
    other = lax.ppermute(own, "batch", pairs)
    arrived_other = lax.ppermute(arrived, "batch", pairs)
    incoming = jnp.where(
        first_core,
        jnp.concatenate([arrived, arrived_other], axis=2),
        jnp.concatenate([arrived_other, arrived], axis=2),
    )
    summed = own.astype(jnp.float32) + other.astype(jnp.float32)
    summed = summed.at[:, :width, :].add(incoming.astype(jnp.float32))
    return summed[None]


def solution(mesh):
    placed = (
        P(("groups", "depth"), None, "tile", None),
        P("groups", None, None),
        P(("groups", "tile", "batch"), None),
        P(("groups", "tile", "batch")),
        P(("groups", "tile", "batch"), None, None),
    )
    return jax.shard_map(
        local,
        mesh=mesh,
        in_specs=placed,
        out_specs=P(("groups", "depth"), None, "tile", None),
        check_vma=False,
    )
```

```python
import math

import jax
import jax.numpy as jnp
from jax import lax
from jax.sharding import PartitionSpec as P
from jax.experimental import pallas as pl
from jax.experimental.pallas import tpu as pltpu

SLICE_COEF = 0.002
DETECTOR_COEF = 0.006
RESIDUAL_SCALE = 0.125


def from_behind(block, axis, distance):
    devices = range(lax.axis_size(axis))
    route = [(i - distance, i) for i in devices if i - distance in devices]
    return lax.ppermute(block, axis, route)


def dft_block(width, sign):
    freq = jnp.arange(width, dtype=jnp.int32)
    product = freq[:, None] * freq[None, :] % width
    angle = 2.0 * math.pi / width * product.astype(jnp.float32)
    scale = 1.0 / math.sqrt(width)
    real_part = (jnp.cos(angle) * scale).astype(jnp.bfloat16)
    imag_part = (sign * jnp.sin(angle) * scale).astype(jnp.bfloat16)
    upper = jnp.concatenate([real_part, -imag_part], axis=1)
    lower = jnp.concatenate([imag_part, real_part], axis=1)
    return jnp.concatenate([upper, lower], axis=0)


def dft_right(width, sign):
    freq = jnp.arange(width, dtype=jnp.int32)
    product = freq[:, None] * freq[None, :] % width
    angle = 2.0 * math.pi / width * product.astype(jnp.float32)
    scale = 1.0 / math.sqrt(width)
    real_part = (jnp.cos(angle) * scale).astype(jnp.bfloat16)
    imag_part = (sign * jnp.sin(angle) * scale).astype(jnp.bfloat16)
    upper = jnp.concatenate([real_part, imag_part], axis=1)
    lower = jnp.concatenate([-imag_part, real_part], axis=1)
    return jnp.concatenate([upper, lower], axis=0)


def chirp_parts(width, coef):
    freq = jnp.arange(width, dtype=jnp.int32)
    shifted = (freq + width // 2) % width - width // 2
    square = shifted * shifted
    total = (square[:, None] + square[None, :]).astype(jnp.float32)
    phase = -coef * total
    return (jnp.cos(phase), jnp.sin(phase))


def left_apply(block, waves):
    number = waves.shape[0]
    width = waves.shape[2]
    stacked = waves.reshape(number, 2 * width, width)
    result = jnp.einsum("ij,gjk->gik", block, stacked, preferred_element_type=jnp.float32)
    return result.reshape(number, 2, width, width)


def propagate(waves, forward_block, inverse_block, chirp_re, chirp_im):
    first = left_apply(forward_block, waves).astype(jnp.bfloat16)
    spectrum = left_apply(forward_block, jnp.swapaxes(first, -1, -2))
    spec_re = spectrum[:, 0]
    spec_im = spectrum[:, 1]
    filtered = jnp.stack(
        [spec_re * chirp_re - spec_im * chirp_im, spec_re * chirp_im + spec_im * chirp_re], axis=1
    ).astype(jnp.bfloat16)
    back = left_apply(inverse_block, filtered).astype(jnp.bfloat16)
    return left_apply(inverse_block, jnp.swapaxes(back, -1, -2)).astype(jnp.bfloat16)


def transmit(waves, patch):
    values = waves.astype(jnp.float32)
    wave_re = values[:, 0]
    wave_im = values[:, 1]
    return jnp.stack(
        [
            patch[:, 0] * wave_re - patch[:, 1] * wave_im,
            patch[:, 0] * wave_im + patch[:, 1] * wave_re,
        ],
        axis=1,
    ).astype(jnp.bfloat16)


def residual_wave(waves, measured):
    values = waves.astype(jnp.float32)
    intensity = values[:, 0] * values[:, 0] + values[:, 1] * values[:, 1]
    weight = RESIDUAL_SCALE * (intensity - measured)
    return jnp.stack([weight * values[:, 0], weight * values[:, 1]], axis=1).astype(jnp.bfloat16)


def adjoint_terms(incoming, forward_block, inverse_block, chirp_re, chirp_im, inputs, patch):
    spread = propagate(incoming, forward_block, inverse_block, chirp_re, -chirp_im).astype(
        jnp.float32
    )
    source = inputs.astype(jnp.float32)
    term = jnp.stack(
        [
            source[:, 0] * spread[:, 0] + source[:, 1] * spread[:, 1],
            source[:, 0] * spread[:, 1] - source[:, 1] * spread[:, 0],
        ],
        axis=1,
    )
    passed = jnp.stack(
        [
            patch[:, 0] * spread[:, 0] + patch[:, 1] * spread[:, 1],
            patch[:, 0] * spread[:, 1] - patch[:, 1] * spread[:, 0],
        ],
        axis=1,
    ).astype(jnp.bfloat16)
    return (passed, term)


def wave_kernel(transmit_first, residual_after, backward):
    def kernel(*refs):
        refs = list(refs)
        wave_ref = refs.pop(0)
        patch_ref = refs.pop(0)
        chirp_ref = refs.pop(0)
        fl_ref, fr_ref, gl_ref, gr_ref = refs[:4]
        refs = refs[4:]
        extra_ref = refs.pop(0) if (residual_after or backward) else None
        width = wave_ref.shape[2]
        wave = wave_ref[0].astype(jnp.float32)
        patch_re = patch_ref[0, 0]
        patch_im = patch_ref[0, 1]
        if transmit_first:
            wave_re = patch_re * wave[0] - patch_im * wave[1]
            wave_im = patch_re * wave[1] + patch_im * wave[0]
        else:
            wave_re = wave[0]
            wave_im = wave[1]
        stacked = jnp.concatenate([wave_re, wave_im], axis=0).astype(jnp.bfloat16)
        first = jnp.dot(fl_ref[...], stacked, preferred_element_type=jnp.float32).astype(jnp.bfloat16)
        rowwise = jnp.concatenate([first[:width], first[width:]], axis=1)
        spectrum = jnp.dot(rowwise, fr_ref[...], preferred_element_type=jnp.float32)
        spec_re = spectrum[:, :width]
        spec_im = spectrum[:, width:]
        chirp_re = chirp_ref[0]
        chirp_im = chirp_ref[1]
        if backward:
            chirp_im = -chirp_im
        filtered = jnp.concatenate(
            [spec_re * chirp_re - spec_im * chirp_im, spec_re * chirp_im + spec_im * chirp_re],
            axis=1,
        ).astype(jnp.bfloat16)
        back = jnp.dot(filtered, gr_ref[...], preferred_element_type=jnp.float32).astype(jnp.bfloat16)
        columnwise = jnp.concatenate([back[:, :width], back[:, width:]], axis=0)
        out = jnp.dot(gl_ref[...], columnwise, preferred_element_type=jnp.float32).astype(jnp.bfloat16)
        values = out.astype(jnp.float32)
        out_re = values[:width]
        out_im = values[width:]
        if residual_after:
            measured = extra_ref[0]
            weight = RESIDUAL_SCALE * (out_re * out_re + out_im * out_im - measured)
            result_ref = refs[0]
            result_ref[0, 0] = (weight * out_re).astype(jnp.bfloat16)
            result_ref[0, 1] = (weight * out_im).astype(jnp.bfloat16)
        elif backward:
            source = extra_ref[0].astype(jnp.float32)
            passed_ref, term_ref = refs[0], refs[1]
            passed_ref[0, 0] = (patch_re * out_re + patch_im * out_im).astype(jnp.bfloat16)
            passed_ref[0, 1] = (patch_re * out_im - patch_im * out_re).astype(jnp.bfloat16)
            term_ref[0, 0] = source[0] * out_re + source[1] * out_im
            term_ref[0, 1] = source[0] * out_im - source[1] * out_re
        else:
            result_ref = refs[0]
            result_ref[0, 0] = out[:width]
            result_ref[0, 1] = out[width:]

    return kernel


def run_waves(waves, patches, chirps, blocks, extra=None, transmit_first=True, residual_after=False, backward=False):
    number, _, width, _ = waves.shape
    wave_spec = pl.BlockSpec((1, 2, width, width), lambda i: (i, 0, 0, 0))
    chirp_spec = pl.BlockSpec((2, width, width), lambda i: (0, 0, 0))
    block_spec = pl.BlockSpec((2 * width, 2 * width), lambda i: (0, 0))
    in_specs = [wave_spec, wave_spec, chirp_spec] + [block_spec] * 4
    args = [waves, patches, chirps] + list(blocks)
    if residual_after:
        in_specs.append(pl.BlockSpec((1, width, width), lambda i: (i, 0, 0)))
        args.append(extra)
    if backward:
        in_specs.append(wave_spec)
        args.append(extra)
        out_shape = (
            jax.ShapeDtypeStruct(waves.shape, jnp.bfloat16),
            jax.ShapeDtypeStruct(waves.shape, jnp.float32),
        )
        out_specs = (wave_spec, wave_spec)
    else:
        out_shape = jax.ShapeDtypeStruct(waves.shape, jnp.bfloat16)
        out_specs = wave_spec
    return pl.pallas_call(
        wave_kernel(transmit_first, residual_after, backward),
        grid=(number,),
        in_specs=in_specs,
        out_specs=out_specs,
        out_shape=out_shape,
    )(*args)


def scatter_kernel(rows_ref, columns_ref, live_ref, terms_ref, out_ref):
    index = pl.program_id(0)

    @pl.when(index == 0)
    def _():
        out_ref[...] = jnp.zeros(out_ref.shape, out_ref.dtype)

    width = terms_ref.shape[2]
    height = out_ref.shape[1]
    columns_all = out_ref.shape[2]
    row = rows_ref[index]
    column = columns_ref[index]
    alive = live_ref[index] > 0
    for part in range(2):
        term = jnp.where(alive, terms_ref[0, part], 0.0)
        wide = jnp.concatenate(
            [term, jnp.zeros((width, columns_all - width), jnp.float32)], axis=1
        )
        wide = pltpu.roll(wide, column, 1)
        tall = jnp.concatenate(
            [wide, jnp.zeros((height - width, columns_all), jnp.float32)], axis=0
        )
        tall = pltpu.roll(tall, row, 0)
        out_ref[part] = out_ref[part] + tall


def scatter_terms(terms, rows, columns, live, height, columns_all):
    number, _, width, _ = terms.shape
    grid_spec = pltpu.PrefetchScalarGridSpec(
        num_scalar_prefetch=3,
        grid=(number,),
        in_specs=[pl.BlockSpec((1, 2, width, width), lambda i, r, c, a: (i, 0, 0, 0))],
        out_specs=pl.BlockSpec((2, height, columns_all), lambda i, r, c, a: (0, 0, 0)),
    )
    return pl.pallas_call(
        scatter_kernel,
        grid_spec=grid_spec,
        out_shape=jax.ShapeDtypeStruct((2, height, columns_all), jnp.float32),
    )(rows, columns, live.astype(jnp.int32), terms)


def cut_kernel(rows_ref, columns_ref, order_ref, tile_ref, mine_ref, partner_ref, out_ref):
    index = pl.program_id(0)
    width = out_ref.shape[2]
    height = tile_ref.shape[2] + mine_ref.shape[2]
    columns_all = tile_ref.shape[3]
    row_shift = (height - rows_ref[index]) % height
    column_shift = (columns_all - columns_ref[index]) % columns_all
    first = order_ref[0] == 0
    for part in range(2):
        mine = mine_ref[0, part].astype(jnp.float32)
        partner = partner_ref[0, part].astype(jnp.float32)
        rim = jnp.concatenate(
            [jnp.where(first, mine, partner), jnp.where(first, partner, mine)], axis=1
        )
        full = jnp.concatenate([tile_ref[0, part], rim], axis=0)
        full = pltpu.roll(full, row_shift, 0)[:width]
        full = pltpu.roll(full, column_shift, 1)[:, :width]
        out_ref[0, part] = full


def cut_patches(tile, mine, partner, rows, columns, order, width):
    number = rows.shape[0]
    grid_spec = pltpu.PrefetchScalarGridSpec(
        num_scalar_prefetch=3,
        grid=(number,),
        in_specs=[
            pl.BlockSpec(tile.shape, lambda i, r, c, o: (0, 0, 0, 0)),
            pl.BlockSpec(mine.shape, lambda i, r, c, o: (0, 0, 0, 0)),
            pl.BlockSpec(partner.shape, lambda i, r, c, o: (0, 0, 0, 0)),
        ],
        out_specs=pl.BlockSpec((1, 2, width, width), lambda i, r, c, o: (i, 0, 0, 0)),
    )
    return pl.pallas_call(
        cut_kernel,
        grid_spec=grid_spec,
        out_shape=jax.ShapeDtypeStruct((number, 2, width, width), jnp.float32),
    )(rows, columns, order, tile, mine, partner)


def propagate_block(wave_re, wave_im, blocks, chirp_re, chirp_im):
    fl_ref, fr_ref, gl_ref, gr_ref = blocks
    width = wave_re.shape[0]
    stacked = jnp.concatenate([wave_re, wave_im], axis=0).astype(jnp.bfloat16)
    first = jnp.dot(fl_ref[...], stacked, preferred_element_type=jnp.float32).astype(jnp.bfloat16)
    rowwise = jnp.concatenate([first[:width], first[width:]], axis=1)
    spectrum = jnp.dot(rowwise, fr_ref[...], preferred_element_type=jnp.float32)
    spec_re = spectrum[:, :width]
    spec_im = spectrum[:, width:]
    filtered = jnp.concatenate(
        [spec_re * chirp_re - spec_im * chirp_im, spec_re * chirp_im + spec_im * chirp_re],
        axis=1,
    ).astype(jnp.bfloat16)
    back = jnp.dot(filtered, gr_ref[...], preferred_element_type=jnp.float32).astype(jnp.bfloat16)
    columnwise = jnp.concatenate([back[:, :width], back[:, width:]], axis=0)
    out = jnp.dot(gl_ref[...], columnwise, preferred_element_type=jnp.float32).astype(jnp.bfloat16)
    values = out.astype(jnp.float32)
    return (values[:width], values[width:])


def place_term(term_re, term_im, row, column, alive, total_ref, direct_ref=None):
    width = term_re.shape[0]
    height = total_ref.shape[1]
    columns_all = total_ref.shape[2]
    row_shift = row % height
    column_shift = column % columns_all
    for part, term in enumerate((term_re, term_im)):
        term = jnp.where(alive, term, 0.0)
        wide = jnp.concatenate(
            [term, jnp.zeros((width, columns_all - width), jnp.float32)], axis=1
        )
        wide = pltpu.roll(wide, column_shift, 1)
        tall = jnp.concatenate(
            [wide, jnp.zeros((height - width, columns_all), jnp.float32)], axis=0
        )
        if direct_ref is None:
            total_ref[part] = total_ref[part] + pltpu.roll(tall, row_shift, 0)
        else:
            direct_ref[part] = pltpu.roll(tall, row_shift, 0).astype(direct_ref.dtype)


def adjoint_kernel(last, single):
    def kernel(rows_ref, columns_ref, live_ref, slot_ref, other_ref, *refs):
        refs = list(refs)
        wave_ref = refs.pop(0)
        patch_ref = refs.pop(0)
        chirp_ref = refs.pop(0)
        blocks = refs[:4]
        refs = refs[4:]
        if last:
            own_ref = refs.pop(0)
            partner_ref = refs.pop(0)
        else:
            source_ref = refs.pop(0)
        passed_ref, grad_ref, total_ref = refs
        index = pl.program_id(0)

        if not single:
            @pl.when(index == 0)
            def _():
                total_ref[...] = jnp.zeros(total_ref.shape, total_ref.dtype)

        wave = wave_ref[0].astype(jnp.float32)
        patch_re = patch_ref[0, 0]
        patch_im = patch_ref[0, 1]
        chirp_re = chirp_ref[0]
        chirp_im = chirp_ref[1]
        if last:
            source_re = wave[0]
            source_im = wave[1]
            lit_re = patch_re * wave[0] - patch_im * wave[1]
            lit_im = patch_re * wave[1] + patch_im * wave[0]
            out_re, out_im = propagate_block(lit_re, lit_im, blocks, chirp_re, chirp_im)
            measured = jnp.where(other_ref[index] > 0, partner_ref[0], own_ref[0])
            weight = RESIDUAL_SCALE * (out_re * out_re + out_im * out_im - measured)
            in_re = (weight * out_re).astype(jnp.bfloat16).astype(jnp.float32)
            in_im = (weight * out_im).astype(jnp.bfloat16).astype(jnp.float32)
        else:
            source = source_ref[0].astype(jnp.float32)
            source_re = source[0]
            source_im = source[1]
            in_re = wave[0]
            in_im = wave[1]
        spread_re, spread_im = propagate_block(in_re, in_im, blocks, chirp_re, -chirp_im)
        passed_ref[0, 0] = (patch_re * spread_re + patch_im * spread_im).astype(jnp.bfloat16)
        passed_ref[0, 1] = (patch_re * spread_im - patch_im * spread_re).astype(jnp.bfloat16)
        term_re = source_re * spread_re + source_im * spread_im
        term_im = source_re * spread_im - source_im * spread_re
        place_term(
            term_re, term_im, rows_ref[index], columns_ref[index], live_ref[index] > 0,
            total_ref, grad_ref if single else None,
        )

        if not single:
            @pl.when(index == pl.num_programs(0) - 1)
            def _():
                grad_ref[...] = total_ref[...].astype(grad_ref.dtype)

    return kernel


def run_adjoint(waves, patches, chirps, blocks, scalars, extra, height, columns_all, last):
    number, _, width, _ = waves.shape
    wave_spec = pl.BlockSpec((1, 2, width, width), lambda i, *s: (i, 0, 0, 0))
    chirp_spec = pl.BlockSpec((2, width, width), lambda i, *s: (0, 0, 0))
    block_spec = pl.BlockSpec((2 * width, 2 * width), lambda i, *s: (0, 0))
    in_specs = [wave_spec, wave_spec, chirp_spec] + [block_spec] * 4
    if last:
        slot_spec = pl.BlockSpec((1, width, width), lambda i, r, c, a, s, o: (s[i], 0, 0))
        in_specs += [slot_spec, slot_spec]
    else:
        in_specs += [wave_spec]
    grid_spec = pltpu.PrefetchScalarGridSpec(
        num_scalar_prefetch=5,
        grid=(number,),
        in_specs=in_specs,
        out_specs=(
            wave_spec,
            pl.BlockSpec((2, height, columns_all), lambda i, *s: (0, 0, 0)),
        ),
        scratch_shapes=[pltpu.VMEM((2, height, columns_all), jnp.float32)],
    )
    return pl.pallas_call(
        adjoint_kernel(last, number == 1),
        grid_spec=grid_spec,
        out_shape=(
            jax.ShapeDtypeStruct(waves.shape, jnp.bfloat16),
            jax.ShapeDtypeStruct((2, height, columns_all), jnp.bfloat16),
        ),
    )(*scalars, waves, patches, chirps, *blocks, *extra)


def local(object_field, probe, positions, counts, measured):
    width = probe.shape[1]
    tile_rows = object_field.shape[2]
    columns_all = object_field.shape[3]
    tile_index = lax.axis_index("tile")
    tile_count = lax.axis_size("tile")
    segment = lax.axis_index("depth")
    depth_count = lax.axis_size("depth")
    batch_index = lax.axis_index("batch")
    batch_count = lax.axis_size("batch")
    half = columns_all // batch_count
    wanted = lax.dynamic_slice_in_dim(object_field[:, :, :width, :], batch_index * half, half, 3)
    mine = from_behind(wanted.astype(jnp.bfloat16), "tile", -1)
    pairs = [(b, (b + 1) % batch_count) for b in range(batch_count)]
    partner = lax.ppermute(mine, "batch", pairs)
    capacity = positions.shape[0]
    share = -(-capacity // batch_count)
    first_core = batch_index == 0
    both_positions = lax.ppermute(positions, "batch", pairs)
    both_counts = lax.ppermute(counts, "batch", pairs)
    both_measured = lax.ppermute(measured, "batch", pairs)
    all_positions = jnp.where(
        first_core,
        jnp.concatenate([positions, both_positions]),
        jnp.concatenate([both_positions, positions]),
    )
    all_counts = jnp.where(
        first_core, jnp.concatenate([counts, both_counts]), jnp.concatenate([both_counts, counts])
    )
    entry = batch_index * share + jnp.arange(share, dtype=jnp.int32)
    live = entry < all_counts[0] + all_counts[1]
    later = entry >= all_counts[0]
    slot = jnp.clip(jnp.where(later, entry - all_counts[0], entry), 0, capacity - 1)
    flat = jnp.where(later, capacity, 0) + slot
    chosen = all_positions[flat]
    other = (later == first_core).astype(jnp.int32)
    local_rows = chosen[:, 0] - tile_index * tile_rows
    local_columns = chosen[:, 1]
    order = jnp.reshape(batch_index, (1,)).astype(jnp.int32)
    patches = cut_patches(object_field, mine, partner, local_rows, local_columns, order, width)
    number = patches.shape[0]
    forward_block = dft_block(width, -1.0)
    inverse_block = dft_block(width, 1.0)
    coef = jnp.where(
        segment == depth_count - 1, jnp.float32(DETECTOR_COEF), jnp.float32(SLICE_COEF)
    )
    chirp_re, chirp_im = chirp_parts(width, coef)
    start = jnp.broadcast_to(probe[None], (number, 2, width, width))

    chirps = jnp.stack([chirp_re, chirp_im])
    blocks = (forward_block, dft_right(width, -1.0), inverse_block, dft_right(width, 1.0))

    def forward_all(waves):
        return run_waves(waves, patches, chirps, blocks)

    def silent(waves):
        return jnp.zeros_like(waves)

    carry = start
    inputs = start
    for turn in range(depth_count - 1):
        if turn > 0:
            carry = lax.ppermute(carry, "depth", [(turn - 1, turn)])
            inputs = jnp.where(segment == turn, carry, inputs)
        carry = lax.cond(segment == turn, forward_all, silent, carry)

    height = tile_rows + width
    scalars = (local_rows, local_columns, live.astype(jnp.int32), slot, other)

    def last_pass(incoming):
        return run_adjoint(
            incoming, patches, chirps, blocks, scalars, (measured, both_measured),
            height, columns_all, True,
        )

    def last_silent(incoming):
        return (jnp.zeros_like(incoming), jnp.zeros((2, height, columns_all), jnp.bfloat16))

    if depth_count > 1:
        carry = lax.ppermute(carry, "depth", [(depth_count - 2, depth_count - 1)])
    carry, gradient = lax.cond(segment == depth_count - 1, last_pass, last_silent, carry)

    def back_pass(incoming, previous):
        return run_adjoint(
            incoming, patches, chirps, blocks, scalars, (inputs,), height, columns_all, False
        )

    def back_silent(incoming, previous):
        return (jnp.zeros_like(incoming), previous)

    for turn in reversed(range(depth_count - 1)):
        carry = lax.ppermute(carry, "depth", [(turn + 1, turn)])
        carry, gradient = lax.cond(segment == turn, back_pass, back_silent, carry, gradient)

    gradient = gradient.astype(jnp.bfloat16)
    spill = gradient[:, tile_rows:, :]
    keep = lax.dynamic_slice_in_dim(spill, batch_index * half, half, 2)
    give = lax.dynamic_slice_in_dim(spill, (1 - batch_index) * half, half, 2)
    got = lax.ppermute(give, "batch", pairs)
    spill_sum = (keep.astype(jnp.float32) + got.astype(jnp.float32)).astype(jnp.bfloat16)
    arrived = lax.ppermute(spill_sum, "tile", [(t, t + 1) for t in range(tile_count - 1)])
    own = gradient[:, :tile_rows, :]
    other = lax.ppermute(own, "batch", pairs)
    arrived_other = lax.ppermute(arrived, "batch", pairs)
    incoming = jnp.where(
        first_core,
        jnp.concatenate([arrived, arrived_other], axis=2),
        jnp.concatenate([arrived_other, arrived], axis=2),
    )
    summed = own.astype(jnp.float32) + other.astype(jnp.float32)
    summed = summed.at[:, :width, :].add(incoming.astype(jnp.float32))
    return summed[None]


def solution(mesh):
    placed = (
        P(("groups", "depth"), None, "tile", None),
        P("groups", None, None),
        P(("groups", "tile", "batch"), None),
        P(("groups", "tile", "batch")),
        P(("groups", "tile", "batch"), None, None),
    )
    return jax.shard_map(
        local,
        mesh=mesh,
        in_specs=placed,
        out_specs=P(("groups", "depth"), None, "tile", None),
        check_vma=False,
    )
```

```python
import math

import jax
import jax.numpy as jnp
from jax import lax
from jax.sharding import PartitionSpec as P
from jax.experimental import pallas as pl
from jax.experimental.pallas import tpu as pltpu

SLICE_COEF = 0.002
DETECTOR_COEF = 0.006
RESIDUAL_SCALE = 0.125


def from_behind(block, axis, distance):
    devices = range(lax.axis_size(axis))
    route = [(i - distance, i) for i in devices if i - distance in devices]
    return lax.ppermute(block, axis, route)


def dft_block(width, sign):
    freq = jnp.arange(width, dtype=jnp.int32)
    product = freq[:, None] * freq[None, :] % width
    angle = 2.0 * math.pi / width * product.astype(jnp.float32)
    scale = 1.0 / math.sqrt(width)
    real_part = (jnp.cos(angle) * scale).astype(jnp.bfloat16)
    imag_part = (sign * jnp.sin(angle) * scale).astype(jnp.bfloat16)
    upper = jnp.concatenate([real_part, -imag_part], axis=1)
    lower = jnp.concatenate([imag_part, real_part], axis=1)
    return jnp.concatenate([upper, lower], axis=0)


def dft_right(width, sign):
    freq = jnp.arange(width, dtype=jnp.int32)
    product = freq[:, None] * freq[None, :] % width
    angle = 2.0 * math.pi / width * product.astype(jnp.float32)
    scale = 1.0 / math.sqrt(width)
    real_part = (jnp.cos(angle) * scale).astype(jnp.bfloat16)
    imag_part = (sign * jnp.sin(angle) * scale).astype(jnp.bfloat16)
    upper = jnp.concatenate([real_part, imag_part], axis=1)
    lower = jnp.concatenate([-imag_part, real_part], axis=1)
    return jnp.concatenate([upper, lower], axis=0)


def dft_parts(width):
    freq = jnp.arange(width, dtype=jnp.int32)
    product = freq[:, None] * freq[None, :] % width
    angle = 2.0 * math.pi / width * product.astype(jnp.float32)
    scale = 1.0 / math.sqrt(width)
    real_part = (jnp.cos(angle) * scale).astype(jnp.bfloat16)
    imag_part = (-jnp.sin(angle) * scale).astype(jnp.bfloat16)
    return (real_part, imag_part)


def chirp_parts(width, coef):
    freq = jnp.arange(width, dtype=jnp.int32)
    shifted = (freq + width // 2) % width - width // 2
    square = shifted * shifted
    total = (square[:, None] + square[None, :]).astype(jnp.float32)
    phase = -coef * total
    return (jnp.cos(phase), jnp.sin(phase))


def left_apply(block, waves):
    number = waves.shape[0]
    width = waves.shape[2]
    stacked = waves.reshape(number, 2 * width, width)
    result = jnp.einsum("ij,gjk->gik", block, stacked, preferred_element_type=jnp.float32)
    return result.reshape(number, 2, width, width)


def propagate(waves, forward_block, inverse_block, chirp_re, chirp_im):
    first = left_apply(forward_block, waves).astype(jnp.bfloat16)
    spectrum = left_apply(forward_block, jnp.swapaxes(first, -1, -2))
    spec_re = spectrum[:, 0]
    spec_im = spectrum[:, 1]
    filtered = jnp.stack(
        [spec_re * chirp_re - spec_im * chirp_im, spec_re * chirp_im + spec_im * chirp_re], axis=1
    ).astype(jnp.bfloat16)
    back = left_apply(inverse_block, filtered).astype(jnp.bfloat16)
    return left_apply(inverse_block, jnp.swapaxes(back, -1, -2)).astype(jnp.bfloat16)


def transmit(waves, patch):
    values = waves.astype(jnp.float32)
    wave_re = values[:, 0]
    wave_im = values[:, 1]
    return jnp.stack(
        [
            patch[:, 0] * wave_re - patch[:, 1] * wave_im,
            patch[:, 0] * wave_im + patch[:, 1] * wave_re,
        ],
        axis=1,
    ).astype(jnp.bfloat16)


def residual_wave(waves, measured):
    values = waves.astype(jnp.float32)
    intensity = values[:, 0] * values[:, 0] + values[:, 1] * values[:, 1]
    weight = RESIDUAL_SCALE * (intensity - measured)
    return jnp.stack([weight * values[:, 0], weight * values[:, 1]], axis=1).astype(jnp.bfloat16)


def adjoint_terms(incoming, forward_block, inverse_block, chirp_re, chirp_im, inputs, patch):
    spread = propagate(incoming, forward_block, inverse_block, chirp_re, -chirp_im).astype(
        jnp.float32
    )
    source = inputs.astype(jnp.float32)
    term = jnp.stack(
        [
            source[:, 0] * spread[:, 0] + source[:, 1] * spread[:, 1],
            source[:, 0] * spread[:, 1] - source[:, 1] * spread[:, 0],
        ],
        axis=1,
    )
    passed = jnp.stack(
        [
            patch[:, 0] * spread[:, 0] + patch[:, 1] * spread[:, 1],
            patch[:, 0] * spread[:, 1] - patch[:, 1] * spread[:, 0],
        ],
        axis=1,
    ).astype(jnp.bfloat16)
    return (passed, term)


def wave_kernel(transmit_first, residual_after, backward):
    def kernel(*refs):
        refs = list(refs)
        wave_ref = refs.pop(0)
        patch_ref = refs.pop(0)
        chirp_ref = refs.pop(0)
        blocks = refs[:2]
        refs = refs[2:]
        extra_ref = refs.pop(0) if (residual_after or backward) else None
        wave = wave_ref[0].astype(jnp.float32)
        patch_re = patch_ref[0, 0]
        patch_im = patch_ref[0, 1]
        if transmit_first:
            wave_re = patch_re * wave[0] - patch_im * wave[1]
            wave_im = patch_re * wave[1] + patch_im * wave[0]
        else:
            wave_re = wave[0]
            wave_im = wave[1]
        chirp_re = chirp_ref[0]
        chirp_im = chirp_ref[1]
        if backward:
            chirp_im = -chirp_im
        out_re, out_im = propagate_block(wave_re, wave_im, blocks, chirp_re, chirp_im)
        if residual_after:
            measured = extra_ref[0]
            weight = RESIDUAL_SCALE * (out_re * out_re + out_im * out_im - measured)
            result_ref = refs[0]
            result_ref[0, 0] = (weight * out_re).astype(jnp.bfloat16)
            result_ref[0, 1] = (weight * out_im).astype(jnp.bfloat16)
        elif backward:
            source = extra_ref[0].astype(jnp.float32)
            passed_ref, term_ref = refs[0], refs[1]
            passed_ref[0, 0] = (patch_re * out_re + patch_im * out_im).astype(jnp.bfloat16)
            passed_ref[0, 1] = (patch_re * out_im - patch_im * out_re).astype(jnp.bfloat16)
            term_ref[0, 0] = source[0] * out_re + source[1] * out_im
            term_ref[0, 1] = source[0] * out_im - source[1] * out_re
        else:
            result_ref = refs[0]
            result_ref[0, 0] = out_re.astype(jnp.bfloat16)
            result_ref[0, 1] = out_im.astype(jnp.bfloat16)

    return kernel


def run_waves(waves, patches, chirps, blocks, extra=None, transmit_first=True, residual_after=False, backward=False):
    number, _, width, _ = waves.shape
    wave_spec = pl.BlockSpec((1, 2, width, width), lambda i: (i, 0, 0, 0))
    chirp_spec = pl.BlockSpec((2, width, width), lambda i: (0, 0, 0))
    in_specs = [wave_spec, wave_spec, chirp_spec] + [
        pl.BlockSpec((2 * width, width), lambda i: (0, 0)),
        pl.BlockSpec((width, 2 * width), lambda i: (0, 0)),
    ]
    args = [waves, patches, chirps] + list(blocks)
    if residual_after:
        in_specs.append(pl.BlockSpec((1, width, width), lambda i: (i, 0, 0)))
        args.append(extra)
    if backward:
        in_specs.append(wave_spec)
        args.append(extra)
        out_shape = (
            jax.ShapeDtypeStruct(waves.shape, jnp.bfloat16),
            jax.ShapeDtypeStruct(waves.shape, jnp.float32),
        )
        out_specs = (wave_spec, wave_spec)
    else:
        out_shape = jax.ShapeDtypeStruct(waves.shape, jnp.bfloat16)
        out_specs = wave_spec
    return pl.pallas_call(
        wave_kernel(transmit_first, residual_after, backward),
        grid=(number,),
        in_specs=in_specs,
        out_specs=out_specs,
        out_shape=out_shape,
    )(*args)


def scatter_kernel(rows_ref, columns_ref, live_ref, terms_ref, out_ref):
    index = pl.program_id(0)

    @pl.when(index == 0)
    def _():
        out_ref[...] = jnp.zeros(out_ref.shape, out_ref.dtype)

    width = terms_ref.shape[2]
    height = out_ref.shape[1]
    columns_all = out_ref.shape[2]
    row = rows_ref[index]
    column = columns_ref[index]
    alive = live_ref[index] > 0
    for part in range(2):
        term = jnp.where(alive, terms_ref[0, part], 0.0)
        wide = jnp.concatenate(
            [term, jnp.zeros((width, columns_all - width), jnp.float32)], axis=1
        )
        wide = pltpu.roll(wide, column, 1)
        tall = jnp.concatenate(
            [wide, jnp.zeros((height - width, columns_all), jnp.float32)], axis=0
        )
        tall = pltpu.roll(tall, row, 0)
        out_ref[part] = out_ref[part] + tall


def scatter_terms(terms, rows, columns, live, height, columns_all):
    number, _, width, _ = terms.shape
    grid_spec = pltpu.PrefetchScalarGridSpec(
        num_scalar_prefetch=3,
        grid=(number,),
        in_specs=[pl.BlockSpec((1, 2, width, width), lambda i, r, c, a: (i, 0, 0, 0))],
        out_specs=pl.BlockSpec((2, height, columns_all), lambda i, r, c, a: (0, 0, 0)),
    )
    return pl.pallas_call(
        scatter_kernel,
        grid_spec=grid_spec,
        out_shape=jax.ShapeDtypeStruct((2, height, columns_all), jnp.float32),
    )(rows, columns, live.astype(jnp.int32), terms)


def cut_kernel(rows_ref, columns_ref, order_ref, tile_ref, mine_ref, partner_ref, out_ref):
    index = pl.program_id(0)
    width = out_ref.shape[2]
    height = tile_ref.shape[2] + mine_ref.shape[2]
    columns_all = tile_ref.shape[3]
    row_shift = (height - rows_ref[index]) % height
    column_shift = (columns_all - columns_ref[index]) % columns_all
    first = order_ref[0] == 0
    for part in range(2):
        mine = mine_ref[0, part].astype(jnp.float32)
        partner = partner_ref[0, part].astype(jnp.float32)
        rim = jnp.concatenate(
            [jnp.where(first, mine, partner), jnp.where(first, partner, mine)], axis=1
        )
        full = jnp.concatenate([tile_ref[0, part], rim], axis=0)
        full = pltpu.roll(full, row_shift, 0)[:width]
        full = pltpu.roll(full, column_shift, 1)[:, :width]
        out_ref[0, part] = full


def cut_patches(tile, mine, partner, rows, columns, order, width):
    number = rows.shape[0]
    grid_spec = pltpu.PrefetchScalarGridSpec(
        num_scalar_prefetch=3,
        grid=(number,),
        in_specs=[
            pl.BlockSpec(tile.shape, lambda i, r, c, o: (0, 0, 0, 0)),
            pl.BlockSpec(mine.shape, lambda i, r, c, o: (0, 0, 0, 0)),
            pl.BlockSpec(partner.shape, lambda i, r, c, o: (0, 0, 0, 0)),
        ],
        out_specs=pl.BlockSpec((1, 2, width, width), lambda i, r, c, o: (i, 0, 0, 0)),
    )
    return pl.pallas_call(
        cut_kernel,
        grid_spec=grid_spec,
        out_shape=jax.ShapeDtypeStruct((number, 2, width, width), jnp.float32),
    )(rows, columns, order, tile, mine, partner)


def propagate_block(wave_re, wave_im, blocks, chirp_re, chirp_im):
    rows_ref, cols_ref = blocks
    width = wave_re.shape[0]
    dft_rows = rows_ref[...]
    dft_cols = cols_ref[...]

    def left(part_re, part_im):
        lanes = jnp.concatenate([part_re, part_im], axis=1).astype(jnp.bfloat16)
        return jnp.dot(dft_rows, lanes, preferred_element_type=jnp.float32)

    def right(part_re, part_im):
        rows = jnp.concatenate([part_re, part_im], axis=0).astype(jnp.bfloat16)
        return jnp.dot(rows, dft_cols, preferred_element_type=jnp.float32)

    first = left(wave_re, wave_im)
    z_re = (first[:width, :width] - first[width:, width:]).astype(jnp.bfloat16)
    z_im = (first[:width, width:] + first[width:, :width]).astype(jnp.bfloat16)
    second = right(z_re, z_im)
    spec_re = second[:width, :width] - second[width:, width:]
    spec_im = second[:width, width:] + second[width:, :width]
    w_re = spec_re * chirp_re - spec_im * chirp_im
    w_im = spec_re * chirp_im + spec_im * chirp_re
    third = right(w_re.astype(jnp.bfloat16), w_im.astype(jnp.bfloat16))
    v_re = (third[:width, :width] + third[width:, width:]).astype(jnp.bfloat16)
    v_im = (third[width:, :width] - third[:width, width:]).astype(jnp.bfloat16)
    fourth = left(v_re, v_im)
    out_re = (fourth[:width, :width] + fourth[width:, width:]).astype(jnp.bfloat16)
    out_im = (fourth[:width, width:] - fourth[width:, :width]).astype(jnp.bfloat16)
    return (out_re.astype(jnp.float32), out_im.astype(jnp.float32))


def place_term(term_re, term_im, row, column, alive, total_ref, direct_ref=None):
    width = term_re.shape[0]
    height = total_ref.shape[1]
    columns_all = total_ref.shape[2]
    row_shift = row % height
    column_shift = column % columns_all
    for part, term in enumerate((term_re, term_im)):
        term = jnp.where(alive, term, 0.0)
        wide = jnp.concatenate(
            [term, jnp.zeros((width, columns_all - width), jnp.float32)], axis=1
        )
        wide = pltpu.roll(wide, column_shift, 1)
        tall = jnp.concatenate(
            [wide, jnp.zeros((height - width, columns_all), jnp.float32)], axis=0
        )
        if direct_ref is None:
            total_ref[part] = total_ref[part] + pltpu.roll(tall, row_shift, 0)
        else:
            direct_ref[part] = pltpu.roll(tall, row_shift, 0).astype(direct_ref.dtype)


def adjoint_kernel(last, single):
    def kernel(rows_ref, columns_ref, live_ref, slot_ref, other_ref, *refs):
        refs = list(refs)
        wave_ref = refs.pop(0)
        patch_ref = refs.pop(0)
        chirp_ref = refs.pop(0)
        blocks = refs[:2]
        refs = refs[2:]
        if last:
            own_ref = refs.pop(0)
            partner_ref = refs.pop(0)
        else:
            source_ref = refs.pop(0)
        passed_ref, grad_ref, total_ref = refs
        index = pl.program_id(0)

        if not single:
            @pl.when(index == 0)
            def _():
                total_ref[...] = jnp.zeros(total_ref.shape, total_ref.dtype)

        wave = wave_ref[0].astype(jnp.float32)
        patch_re = patch_ref[0, 0]
        patch_im = patch_ref[0, 1]
        chirp_re = chirp_ref[0]
        chirp_im = chirp_ref[1]
        if last:
            source_re = wave[0]
            source_im = wave[1]
            lit_re = patch_re * wave[0] - patch_im * wave[1]
            lit_im = patch_re * wave[1] + patch_im * wave[0]
            out_re, out_im = propagate_block(lit_re, lit_im, blocks, chirp_re, chirp_im)
            measured = jnp.where(other_ref[index] > 0, partner_ref[0], own_ref[0])
            weight = RESIDUAL_SCALE * (out_re * out_re + out_im * out_im - measured)
            in_re = (weight * out_re).astype(jnp.bfloat16).astype(jnp.float32)
            in_im = (weight * out_im).astype(jnp.bfloat16).astype(jnp.float32)
        else:
            source = source_ref[0].astype(jnp.float32)
            source_re = source[0]
            source_im = source[1]
            in_re = wave[0]
            in_im = wave[1]
        spread_re, spread_im = propagate_block(in_re, in_im, blocks, chirp_re, -chirp_im)
        passed_ref[0, 0] = (patch_re * spread_re + patch_im * spread_im).astype(jnp.bfloat16)
        passed_ref[0, 1] = (patch_re * spread_im - patch_im * spread_re).astype(jnp.bfloat16)
        term_re = source_re * spread_re + source_im * spread_im
        term_im = source_re * spread_im - source_im * spread_re
        place_term(
            term_re, term_im, rows_ref[index], columns_ref[index], live_ref[index] > 0,
            total_ref, grad_ref if single else None,
        )

        if not single:
            @pl.when(index == pl.num_programs(0) - 1)
            def _():
                grad_ref[...] = total_ref[...].astype(grad_ref.dtype)

    return kernel


def run_adjoint(waves, patches, chirps, blocks, scalars, extra, height, columns_all, last):
    number, _, width, _ = waves.shape
    wave_spec = pl.BlockSpec((1, 2, width, width), lambda i, *s: (i, 0, 0, 0))
    chirp_spec = pl.BlockSpec((2, width, width), lambda i, *s: (0, 0, 0))
    in_specs = [wave_spec, wave_spec, chirp_spec] + [
        pl.BlockSpec((2 * width, width), lambda i, *s: (0, 0)),
        pl.BlockSpec((width, 2 * width), lambda i, *s: (0, 0)),
    ]
    if last:
        slot_spec = pl.BlockSpec((1, width, width), lambda i, r, c, a, s, o: (s[i], 0, 0))
        in_specs += [slot_spec, slot_spec]
    else:
        in_specs += [wave_spec]
    grid_spec = pltpu.PrefetchScalarGridSpec(
        num_scalar_prefetch=5,
        grid=(number,),
        in_specs=in_specs,
        out_specs=(
            wave_spec,
            pl.BlockSpec((2, height, columns_all), lambda i, *s: (0, 0, 0)),
        ),
        scratch_shapes=[pltpu.VMEM((2, height, columns_all), jnp.float32)],
    )
    return pl.pallas_call(
        adjoint_kernel(last, number == 1),
        grid_spec=grid_spec,
        out_shape=(
            jax.ShapeDtypeStruct(waves.shape, jnp.bfloat16),
            jax.ShapeDtypeStruct((2, height, columns_all), jnp.bfloat16),
        ),
    )(*scalars, waves, patches, chirps, *blocks, *extra)


def local(object_field, probe, positions, counts, measured):
    width = probe.shape[1]
    tile_rows = object_field.shape[2]
    columns_all = object_field.shape[3]
    tile_index = lax.axis_index("tile")
    tile_count = lax.axis_size("tile")
    segment = lax.axis_index("depth")
    depth_count = lax.axis_size("depth")
    batch_index = lax.axis_index("batch")
    batch_count = lax.axis_size("batch")
    half = columns_all // batch_count
    wanted = lax.dynamic_slice_in_dim(object_field[:, :, :width, :], batch_index * half, half, 3)
    mine = from_behind(wanted.astype(jnp.bfloat16), "tile", -1)
    pairs = [(b, (b + 1) % batch_count) for b in range(batch_count)]
    partner = lax.ppermute(mine, "batch", pairs)
    capacity = positions.shape[0]
    share = -(-capacity // batch_count)
    first_core = batch_index == 0
    both_positions = lax.ppermute(positions, "batch", pairs)
    both_counts = lax.ppermute(counts, "batch", pairs)
    both_measured = lax.ppermute(measured, "batch", pairs)
    all_positions = jnp.where(
        first_core,
        jnp.concatenate([positions, both_positions]),
        jnp.concatenate([both_positions, positions]),
    )
    all_counts = jnp.where(
        first_core, jnp.concatenate([counts, both_counts]), jnp.concatenate([both_counts, counts])
    )
    entry = batch_index * share + jnp.arange(share, dtype=jnp.int32)
    live = entry < all_counts[0] + all_counts[1]
    later = entry >= all_counts[0]
    slot = jnp.clip(jnp.where(later, entry - all_counts[0], entry), 0, capacity - 1)
    flat = jnp.where(later, capacity, 0) + slot
    chosen = all_positions[flat]
    other = (later == first_core).astype(jnp.int32)
    local_rows = chosen[:, 0] - tile_index * tile_rows
    local_columns = chosen[:, 1]
    order = jnp.reshape(batch_index, (1,)).astype(jnp.int32)
    patches = cut_patches(object_field, mine, partner, local_rows, local_columns, order, width)
    number = patches.shape[0]
    coef = jnp.where(
        segment == depth_count - 1, jnp.float32(DETECTOR_COEF), jnp.float32(SLICE_COEF)
    )
    chirp_re, chirp_im = chirp_parts(width, coef)
    start = jnp.broadcast_to(probe[None], (number, 2, width, width))

    chirps = jnp.stack([chirp_re, chirp_im])
    dft_re, dft_im = dft_parts(width)
    blocks = (
        jnp.concatenate([dft_re, dft_im], axis=0),
        jnp.concatenate([dft_re, dft_im], axis=1),
    )

    def forward_all(waves):
        return run_waves(waves, patches, chirps, blocks)

    def silent(waves):
        return jnp.zeros_like(waves)

    carry = start
    inputs = start
    for turn in range(depth_count - 1):
        if turn > 0:
            carry = lax.ppermute(carry, "depth", [(turn - 1, turn)])
            inputs = jnp.where(segment == turn, carry, inputs)
        carry = lax.cond(segment == turn, forward_all, silent, carry)

    height = tile_rows + width
    scalars = (local_rows, local_columns, live.astype(jnp.int32), slot, other)

    def last_pass(incoming):
        return run_adjoint(
            incoming, patches, chirps, blocks, scalars, (measured, both_measured),
            height, columns_all, True,
        )

    def last_silent(incoming):
        return (jnp.zeros_like(incoming), jnp.zeros((2, height, columns_all), jnp.bfloat16))

    if depth_count > 1:
        carry = lax.ppermute(carry, "depth", [(depth_count - 2, depth_count - 1)])
    carry, gradient = lax.cond(segment == depth_count - 1, last_pass, last_silent, carry)

    def back_pass(incoming, previous):
        return run_adjoint(
            incoming, patches, chirps, blocks, scalars, (inputs,), height, columns_all, False
        )

    def back_silent(incoming, previous):
        return (jnp.zeros_like(incoming), previous)

    for turn in reversed(range(depth_count - 1)):
        carry = lax.ppermute(carry, "depth", [(turn + 1, turn)])
        carry, gradient = lax.cond(segment == turn, back_pass, back_silent, carry, gradient)

    gradient = gradient.astype(jnp.bfloat16)
    spill = gradient[:, tile_rows:, :]
    keep = lax.dynamic_slice_in_dim(spill, batch_index * half, half, 2)
    give = lax.dynamic_slice_in_dim(spill, (1 - batch_index) * half, half, 2)
    got = lax.ppermute(give, "batch", pairs)
    spill_sum = (keep.astype(jnp.float32) + got.astype(jnp.float32)).astype(jnp.bfloat16)
    arrived = lax.ppermute(spill_sum, "tile", [(t, t + 1) for t in range(tile_count - 1)])
    own = gradient[:, :tile_rows, :]
    other = lax.ppermute(own, "batch", pairs)
    arrived_other = lax.ppermute(arrived, "batch", pairs)
    incoming = jnp.where(
        first_core,
        jnp.concatenate([arrived, arrived_other], axis=2),
        jnp.concatenate([arrived_other, arrived], axis=2),
    )
    summed = own.astype(jnp.float32) + other.astype(jnp.float32)
    summed = summed.at[:, :width, :].add(incoming.astype(jnp.float32))
    return summed[None]


def solution(mesh):
    placed = (
        P(("groups", "depth"), None, "tile", None),
        P("groups", None, None),
        P(("groups", "tile", "batch"), None),
        P(("groups", "tile", "batch")),
        P(("groups", "tile", "batch"), None, None),
    )
    return jax.shard_map(
        local,
        mesh=mesh,
        in_specs=placed,
        out_specs=P(("groups", "depth"), None, "tile", None),
        check_vma=False,
    )
```

```python
import math

import jax
import jax.numpy as jnp
from jax import lax
from jax.sharding import PartitionSpec as P
from jax.experimental import pallas as pl
from jax.experimental.pallas import tpu as pltpu

SLICE_COEF = 0.002
DETECTOR_COEF = 0.006
RESIDUAL_SCALE = 0.125


def from_behind(block, axis, distance):
    devices = range(lax.axis_size(axis))
    route = [(i - distance, i) for i in devices if i - distance in devices]
    return lax.ppermute(block, axis, route)


def dft_block(width, sign):
    freq = jnp.arange(width, dtype=jnp.int32)
    product = freq[:, None] * freq[None, :] % width
    angle = 2.0 * math.pi / width * product.astype(jnp.float32)
    scale = 1.0 / math.sqrt(width)
    real_part = (jnp.cos(angle) * scale).astype(jnp.bfloat16)
    imag_part = (sign * jnp.sin(angle) * scale).astype(jnp.bfloat16)
    upper = jnp.concatenate([real_part, -imag_part], axis=1)
    lower = jnp.concatenate([imag_part, real_part], axis=1)
    return jnp.concatenate([upper, lower], axis=0)


def dft_right(width, sign):
    freq = jnp.arange(width, dtype=jnp.int32)
    product = freq[:, None] * freq[None, :] % width
    angle = 2.0 * math.pi / width * product.astype(jnp.float32)
    scale = 1.0 / math.sqrt(width)
    real_part = (jnp.cos(angle) * scale).astype(jnp.bfloat16)
    imag_part = (sign * jnp.sin(angle) * scale).astype(jnp.bfloat16)
    upper = jnp.concatenate([real_part, imag_part], axis=1)
    lower = jnp.concatenate([-imag_part, real_part], axis=1)
    return jnp.concatenate([upper, lower], axis=0)


def dft_parts(width):
    freq = jnp.arange(width, dtype=jnp.int32)
    product = freq[:, None] * freq[None, :] % width
    angle = 2.0 * math.pi / width * product.astype(jnp.float32)
    scale = 1.0 / math.sqrt(width)
    real_part = (jnp.cos(angle) * scale).astype(jnp.bfloat16)
    imag_part = (-jnp.sin(angle) * scale).astype(jnp.bfloat16)
    return (real_part, imag_part)


def chirp_parts(width, coef):
    freq = jnp.arange(width, dtype=jnp.int32)
    shifted = (freq + width // 2) % width - width // 2
    square = shifted * shifted
    total = (square[:, None] + square[None, :]).astype(jnp.float32)
    phase = -coef * total
    return (jnp.cos(phase), jnp.sin(phase))


def left_apply(block, waves):
    number = waves.shape[0]
    width = waves.shape[2]
    stacked = waves.reshape(number, 2 * width, width)
    result = jnp.einsum("ij,gjk->gik", block, stacked, preferred_element_type=jnp.float32)
    return result.reshape(number, 2, width, width)


def propagate(waves, forward_block, inverse_block, chirp_re, chirp_im):
    first = left_apply(forward_block, waves).astype(jnp.bfloat16)
    spectrum = left_apply(forward_block, jnp.swapaxes(first, -1, -2))
    spec_re = spectrum[:, 0]
    spec_im = spectrum[:, 1]
    filtered = jnp.stack(
        [spec_re * chirp_re - spec_im * chirp_im, spec_re * chirp_im + spec_im * chirp_re], axis=1
    ).astype(jnp.bfloat16)
    back = left_apply(inverse_block, filtered).astype(jnp.bfloat16)
    return left_apply(inverse_block, jnp.swapaxes(back, -1, -2)).astype(jnp.bfloat16)


def transmit(waves, patch):
    values = waves.astype(jnp.float32)
    wave_re = values[:, 0]
    wave_im = values[:, 1]
    return jnp.stack(
        [
            patch[:, 0] * wave_re - patch[:, 1] * wave_im,
            patch[:, 0] * wave_im + patch[:, 1] * wave_re,
        ],
        axis=1,
    ).astype(jnp.bfloat16)


def residual_wave(waves, measured):
    values = waves.astype(jnp.float32)
    intensity = values[:, 0] * values[:, 0] + values[:, 1] * values[:, 1]
    weight = RESIDUAL_SCALE * (intensity - measured)
    return jnp.stack([weight * values[:, 0], weight * values[:, 1]], axis=1).astype(jnp.bfloat16)


def adjoint_terms(incoming, forward_block, inverse_block, chirp_re, chirp_im, inputs, patch):
    spread = propagate(incoming, forward_block, inverse_block, chirp_re, -chirp_im).astype(
        jnp.float32
    )
    source = inputs.astype(jnp.float32)
    term = jnp.stack(
        [
            source[:, 0] * spread[:, 0] + source[:, 1] * spread[:, 1],
            source[:, 0] * spread[:, 1] - source[:, 1] * spread[:, 0],
        ],
        axis=1,
    )
    passed = jnp.stack(
        [
            patch[:, 0] * spread[:, 0] + patch[:, 1] * spread[:, 1],
            patch[:, 0] * spread[:, 1] - patch[:, 1] * spread[:, 0],
        ],
        axis=1,
    ).astype(jnp.bfloat16)
    return (passed, term)


def wave_kernel(transmit_first, residual_after, backward):
    def kernel(*refs):
        refs = list(refs)
        wave_ref = refs.pop(0)
        patch_ref = refs.pop(0)
        chirp_ref = refs.pop(0)
        blocks = refs[:2]
        refs = refs[2:]
        extra_ref = refs.pop(0) if (residual_after or backward) else None
        wave = wave_ref[0].astype(jnp.float32)
        patch_re = patch_ref[0, 0]
        patch_im = patch_ref[0, 1]
        if transmit_first:
            wave_re = patch_re * wave[0] - patch_im * wave[1]
            wave_im = patch_re * wave[1] + patch_im * wave[0]
        else:
            wave_re = wave[0]
            wave_im = wave[1]
        chirp_re = chirp_ref[0]
        chirp_im = chirp_ref[1]
        if backward:
            chirp_im = -chirp_im
        out_re, out_im = propagate_block(wave_re, wave_im, blocks, chirp_re, chirp_im)
        if residual_after:
            measured = extra_ref[0]
            weight = RESIDUAL_SCALE * (out_re * out_re + out_im * out_im - measured)
            result_ref = refs[0]
            result_ref[0, 0] = (weight * out_re).astype(jnp.bfloat16)
            result_ref[0, 1] = (weight * out_im).astype(jnp.bfloat16)
        elif backward:
            source = extra_ref[0].astype(jnp.float32)
            passed_ref, term_ref = refs[0], refs[1]
            passed_ref[0, 0] = (patch_re * out_re + patch_im * out_im).astype(jnp.bfloat16)
            passed_ref[0, 1] = (patch_re * out_im - patch_im * out_re).astype(jnp.bfloat16)
            term_ref[0, 0] = source[0] * out_re + source[1] * out_im
            term_ref[0, 1] = source[0] * out_im - source[1] * out_re
        else:
            result_ref = refs[0]
            result_ref[0, 0] = out_re.astype(jnp.bfloat16)
            result_ref[0, 1] = out_im.astype(jnp.bfloat16)

    return kernel


def run_waves(waves, patches, chirps, blocks, extra=None, transmit_first=True, residual_after=False, backward=False):
    number, _, width, _ = waves.shape
    wave_spec = pl.BlockSpec((1, 2, width, width), lambda i: (i, 0, 0, 0))
    chirp_spec = pl.BlockSpec((2, width, width), lambda i: (0, 0, 0))
    in_specs = [wave_spec, wave_spec, chirp_spec] + [
        pl.BlockSpec((2 * width, width), lambda i: (0, 0)),
        pl.BlockSpec((width, 2 * width), lambda i: (0, 0)),
    ]
    args = [waves, patches, chirps] + list(blocks)
    if residual_after:
        in_specs.append(pl.BlockSpec((1, width, width), lambda i: (i, 0, 0)))
        args.append(extra)
    if backward:
        in_specs.append(wave_spec)
        args.append(extra)
        out_shape = (
            jax.ShapeDtypeStruct(waves.shape, jnp.bfloat16),
            jax.ShapeDtypeStruct(waves.shape, jnp.float32),
        )
        out_specs = (wave_spec, wave_spec)
    else:
        out_shape = jax.ShapeDtypeStruct(waves.shape, jnp.bfloat16)
        out_specs = wave_spec
    return pl.pallas_call(
        wave_kernel(transmit_first, residual_after, backward),
        grid=(number,),
        in_specs=in_specs,
        out_specs=out_specs,
        out_shape=out_shape,
    )(*args)


def scatter_kernel(rows_ref, columns_ref, live_ref, terms_ref, out_ref):
    index = pl.program_id(0)

    @pl.when(index == 0)
    def _():
        out_ref[...] = jnp.zeros(out_ref.shape, out_ref.dtype)

    width = terms_ref.shape[2]
    height = out_ref.shape[1]
    columns_all = out_ref.shape[2]
    row = rows_ref[index]
    column = columns_ref[index]
    alive = live_ref[index] > 0
    for part in range(2):
        term = jnp.where(alive, terms_ref[0, part], 0.0)
        wide = jnp.concatenate(
            [term, jnp.zeros((width, columns_all - width), jnp.float32)], axis=1
        )
        wide = pltpu.roll(wide, column, 1)
        tall = jnp.concatenate(
            [wide, jnp.zeros((height - width, columns_all), jnp.float32)], axis=0
        )
        tall = pltpu.roll(tall, row, 0)
        out_ref[part] = out_ref[part] + tall


def scatter_terms(terms, rows, columns, live, height, columns_all):
    number, _, width, _ = terms.shape
    grid_spec = pltpu.PrefetchScalarGridSpec(
        num_scalar_prefetch=3,
        grid=(number,),
        in_specs=[pl.BlockSpec((1, 2, width, width), lambda i, r, c, a: (i, 0, 0, 0))],
        out_specs=pl.BlockSpec((2, height, columns_all), lambda i, r, c, a: (0, 0, 0)),
    )
    return pl.pallas_call(
        scatter_kernel,
        grid_spec=grid_spec,
        out_shape=jax.ShapeDtypeStruct((2, height, columns_all), jnp.float32),
    )(rows, columns, live.astype(jnp.int32), terms)


def cut_kernel(rows_ref, columns_ref, order_ref, tile_ref, mine_ref, partner_ref, out_ref):
    index = pl.program_id(0)
    width = out_ref.shape[2]
    height = tile_ref.shape[2] + mine_ref.shape[2]
    columns_all = tile_ref.shape[3]
    row_shift = (height - rows_ref[index]) % height
    column_shift = (columns_all - columns_ref[index]) % columns_all
    first = order_ref[0] == 0
    for part in range(2):
        mine = mine_ref[0, part].astype(jnp.float32)
        partner = partner_ref[0, part].astype(jnp.float32)
        rim = jnp.concatenate(
            [jnp.where(first, mine, partner), jnp.where(first, partner, mine)], axis=1
        )
        full = jnp.concatenate([tile_ref[0, part], rim], axis=0)
        full = pltpu.roll(full, row_shift, 0)[:width]
        full = pltpu.roll(full, column_shift, 1)[:, :width]
        out_ref[0, part] = full


def cut_patches(tile, mine, partner, rows, columns, order, width):
    number = rows.shape[0]
    grid_spec = pltpu.PrefetchScalarGridSpec(
        num_scalar_prefetch=3,
        grid=(number,),
        in_specs=[
            pl.BlockSpec(tile.shape, lambda i, r, c, o: (0, 0, 0, 0)),
            pl.BlockSpec(mine.shape, lambda i, r, c, o: (0, 0, 0, 0)),
            pl.BlockSpec(partner.shape, lambda i, r, c, o: (0, 0, 0, 0)),
        ],
        out_specs=pl.BlockSpec((1, 2, width, width), lambda i, r, c, o: (i, 0, 0, 0)),
    )
    return pl.pallas_call(
        cut_kernel,
        grid_spec=grid_spec,
        out_shape=jax.ShapeDtypeStruct((number, 2, width, width), jnp.float32),
    )(rows, columns, order, tile, mine, partner)


def propagate_block(wave_re, wave_im, blocks, chirp_re, chirp_im):
    rows_ref, cols_ref = blocks
    width = wave_re.shape[0]
    dft_rows = rows_ref[...]
    dft_cols = cols_ref[...]

    def left(part_re, part_im):
        lanes = jnp.concatenate([part_re, part_im], axis=1).astype(jnp.bfloat16)
        return jnp.dot(dft_rows, lanes, preferred_element_type=jnp.float32)

    def right(part_re, part_im):
        rows = jnp.concatenate([part_re, part_im], axis=0).astype(jnp.bfloat16)
        return jnp.dot(rows, dft_cols, preferred_element_type=jnp.float32)

    first = left(wave_re, wave_im)
    z_re = (first[:width, :width] - first[width:, width:]).astype(jnp.bfloat16)
    z_im = (first[:width, width:] + first[width:, :width]).astype(jnp.bfloat16)
    second = right(z_re, z_im)
    spec_re = second[:width, :width] - second[width:, width:]
    spec_im = second[:width, width:] + second[width:, :width]
    w_re = spec_re * chirp_re - spec_im * chirp_im
    w_im = spec_re * chirp_im + spec_im * chirp_re
    third = right(w_re.astype(jnp.bfloat16), w_im.astype(jnp.bfloat16))
    v_re = (third[:width, :width] + third[width:, width:]).astype(jnp.bfloat16)
    v_im = (third[width:, :width] - third[:width, width:]).astype(jnp.bfloat16)
    fourth = left(v_re, v_im)
    out_re = (fourth[:width, :width] + fourth[width:, width:]).astype(jnp.bfloat16)
    out_im = (fourth[:width, width:] - fourth[width:, :width]).astype(jnp.bfloat16)
    return (out_re.astype(jnp.float32), out_im.astype(jnp.float32))


def place_term(term_re, term_im, row, column, alive, total_ref, direct_ref=None):
    width = term_re.shape[0]
    height = total_ref.shape[1]
    columns_all = total_ref.shape[2]
    row_shift = row % height
    column_shift = column % columns_all
    for part, term in enumerate((term_re, term_im)):
        term = jnp.where(alive, term, 0.0)
        wide = jnp.concatenate(
            [term, jnp.zeros((width, columns_all - width), jnp.float32)], axis=1
        )
        wide = pltpu.roll(wide, column_shift, 1)
        tall = jnp.concatenate(
            [wide, jnp.zeros((height - width, columns_all), jnp.float32)], axis=0
        )
        if direct_ref is None:
            total_ref[part] = total_ref[part] + pltpu.roll(tall, row_shift, 0)
        else:
            direct_ref[part] = pltpu.roll(tall, row_shift, 0).astype(direct_ref.dtype)


def adjoint_kernel(last, single):
    def kernel(rows_ref, columns_ref, live_ref, slot_ref, other_ref, *refs):
        refs = list(refs)
        wave_ref = refs.pop(0)
        patch_ref = refs.pop(0)
        chirp_ref = refs.pop(0)
        blocks = refs[:2]
        refs = refs[2:]
        if last:
            own_ref = refs.pop(0)
            partner_ref = refs.pop(0)
        else:
            source_ref = refs.pop(0)
        passed_ref, grad_ref, total_ref = refs
        index = pl.program_id(0)

        if not single:
            @pl.when(index == 0)
            def _():
                total_ref[...] = jnp.zeros(total_ref.shape, total_ref.dtype)

        wave = wave_ref[0].astype(jnp.float32)
        patch_re = patch_ref[0, 0]
        patch_im = patch_ref[0, 1]
        chirp_re = chirp_ref[0]
        chirp_im = chirp_ref[1]
        if last:
            source_re = wave[0]
            source_im = wave[1]
            lit_re = patch_re * wave[0] - patch_im * wave[1]
            lit_im = patch_re * wave[1] + patch_im * wave[0]
            out_re, out_im = propagate_block(lit_re, lit_im, blocks, chirp_re, chirp_im)
            measured = jnp.where(other_ref[index] > 0, partner_ref[0], own_ref[0])
            weight = RESIDUAL_SCALE * (out_re * out_re + out_im * out_im - measured)
            in_re = (weight * out_re).astype(jnp.bfloat16).astype(jnp.float32)
            in_im = (weight * out_im).astype(jnp.bfloat16).astype(jnp.float32)
        else:
            source = source_ref[0].astype(jnp.float32)
            source_re = source[0]
            source_im = source[1]
            in_re = wave[0]
            in_im = wave[1]
        spread_re, spread_im = propagate_block(in_re, in_im, blocks, chirp_re, -chirp_im)
        passed_ref[0, 0] = (patch_re * spread_re + patch_im * spread_im).astype(jnp.bfloat16)
        passed_ref[0, 1] = (patch_re * spread_im - patch_im * spread_re).astype(jnp.bfloat16)
        term_re = source_re * spread_re + source_im * spread_im
        term_im = source_re * spread_im - source_im * spread_re
        place_term(
            term_re, term_im, rows_ref[index], columns_ref[index], live_ref[index] > 0,
            total_ref, grad_ref if single else None,
        )

        if not single:
            @pl.when(index == pl.num_programs(0) - 1)
            def _():
                grad_ref[...] = total_ref[...].astype(grad_ref.dtype)

    return kernel


def run_adjoint(waves, patches, chirps, blocks, scalars, extra, height, columns_all, last):
    number, _, width, _ = waves.shape
    wave_spec = pl.BlockSpec((1, 2, width, width), lambda i, *s: (i, 0, 0, 0))
    chirp_spec = pl.BlockSpec((2, width, width), lambda i, *s: (0, 0, 0))
    in_specs = [wave_spec, wave_spec, chirp_spec] + [
        pl.BlockSpec((2 * width, width), lambda i, *s: (0, 0)),
        pl.BlockSpec((width, 2 * width), lambda i, *s: (0, 0)),
    ]
    if last:
        slot_spec = pl.BlockSpec((1, width, width), lambda i, r, c, a, s, o: (s[i], 0, 0))
        in_specs += [slot_spec, slot_spec]
    else:
        in_specs += [wave_spec]
    grid_spec = pltpu.PrefetchScalarGridSpec(
        num_scalar_prefetch=5,
        grid=(number,),
        in_specs=in_specs,
        out_specs=(
            wave_spec,
            pl.BlockSpec((2, height, columns_all), lambda i, *s: (0, 0, 0)),
        ),
        scratch_shapes=[pltpu.VMEM((2, height, columns_all), jnp.float32)],
    )
    return pl.pallas_call(
        adjoint_kernel(last, number == 1),
        grid_spec=grid_spec,
        out_shape=(
            jax.ShapeDtypeStruct(waves.shape, jnp.bfloat16),
            jax.ShapeDtypeStruct((2, height, columns_all), jnp.bfloat16),
        ),
    )(*scalars, waves, patches, chirps, *blocks, *extra)


def first_kernel(rows_ref, columns_ref, order_ref, wave_ref, tile_ref, mine_ref, partner_ref,
                 chirp_ref, dft_rows_ref, dft_cols_ref, result_ref):
    index = pl.program_id(0)
    width = wave_ref.shape[2]
    height = tile_ref.shape[2] + mine_ref.shape[2]
    columns_all = tile_ref.shape[3]
    row_shift = (height - rows_ref[index]) % height
    column_shift = (columns_all - columns_ref[index]) % columns_all
    first = order_ref[0] == 0
    patch = []
    for part in range(2):
        mine = mine_ref[0, part].astype(jnp.float32)
        partner = partner_ref[0, part].astype(jnp.float32)
        rim = jnp.concatenate(
            [jnp.where(first, mine, partner), jnp.where(first, partner, mine)], axis=1
        )
        full = jnp.concatenate([tile_ref[0, part], rim], axis=0)
        full = pltpu.roll(full, row_shift, 0)[:width]
        patch.append(pltpu.roll(full, column_shift, 1)[:, :width])
    wave = wave_ref[0].astype(jnp.float32)
    wave_re = patch[0] * wave[0] - patch[1] * wave[1]
    wave_im = patch[0] * wave[1] + patch[1] * wave[0]
    out_re, out_im = propagate_block(
        wave_re, wave_im, (dft_rows_ref, dft_cols_ref), chirp_ref[0], chirp_ref[1]
    )
    result_ref[0, 0] = out_re.astype(jnp.bfloat16)
    result_ref[0, 1] = out_im.astype(jnp.bfloat16)


def run_first(waves, tile, mine, partner, rows, columns, order, chirps, blocks):
    number, _, width, _ = waves.shape
    wave_spec = pl.BlockSpec((1, 2, width, width), lambda i, r, c, o: (i, 0, 0, 0))
    whole = lambda shape: pl.BlockSpec(shape, lambda i, r, c, o: (0,) * len(shape))
    grid_spec = pltpu.PrefetchScalarGridSpec(
        num_scalar_prefetch=3,
        grid=(number,),
        in_specs=[
            wave_spec,
            whole(tile.shape),
            whole(mine.shape),
            whole(partner.shape),
            whole(chirps.shape),
            whole(blocks[0].shape),
            whole(blocks[1].shape),
        ],
        out_specs=wave_spec,
    )
    return pl.pallas_call(
        first_kernel,
        grid_spec=grid_spec,
        out_shape=jax.ShapeDtypeStruct(waves.shape, jnp.bfloat16),
    )(rows, columns, order, waves, tile, mine, partner, chirps, *blocks)


def local(object_field, probe, positions, counts, measured):
    width = probe.shape[1]
    tile_rows = object_field.shape[2]
    columns_all = object_field.shape[3]
    tile_index = lax.axis_index("tile")
    tile_count = lax.axis_size("tile")
    segment = lax.axis_index("depth")
    depth_count = lax.axis_size("depth")
    batch_index = lax.axis_index("batch")
    batch_count = lax.axis_size("batch")
    half = columns_all // batch_count
    wanted = lax.dynamic_slice_in_dim(object_field[:, :, :width, :], batch_index * half, half, 3)
    mine = from_behind(wanted.astype(jnp.bfloat16), "tile", -1)
    pairs = [(b, (b + 1) % batch_count) for b in range(batch_count)]
    partner = lax.ppermute(mine, "batch", pairs)
    capacity = positions.shape[0]
    share = -(-capacity // batch_count)
    first_core = batch_index == 0
    both_positions = lax.ppermute(positions, "batch", pairs)
    both_counts = lax.ppermute(counts, "batch", pairs)
    both_measured = lax.ppermute(measured, "batch", pairs)
    all_positions = jnp.where(
        first_core,
        jnp.concatenate([positions, both_positions]),
        jnp.concatenate([both_positions, positions]),
    )
    all_counts = jnp.where(
        first_core, jnp.concatenate([counts, both_counts]), jnp.concatenate([both_counts, counts])
    )
    entry = batch_index * share + jnp.arange(share, dtype=jnp.int32)
    live = entry < all_counts[0] + all_counts[1]
    later = entry >= all_counts[0]
    slot = jnp.clip(jnp.where(later, entry - all_counts[0], entry), 0, capacity - 1)
    flat = jnp.where(later, capacity, 0) + slot
    chosen = all_positions[flat]
    other = (later == first_core).astype(jnp.int32)
    local_rows = chosen[:, 0] - tile_index * tile_rows
    local_columns = chosen[:, 1]
    order = jnp.reshape(batch_index, (1,)).astype(jnp.int32)
    patches = cut_patches(object_field, mine, partner, local_rows, local_columns, order, width)
    number = patches.shape[0]
    coef = jnp.where(
        segment == depth_count - 1, jnp.float32(DETECTOR_COEF), jnp.float32(SLICE_COEF)
    )
    chirp_re, chirp_im = chirp_parts(width, coef)
    start = jnp.broadcast_to(probe[None], (number, 2, width, width))

    chirps = jnp.stack([chirp_re, chirp_im])
    dft_re, dft_im = dft_parts(width)
    blocks = (
        jnp.concatenate([dft_re, dft_im], axis=0),
        jnp.concatenate([dft_re, dft_im], axis=1),
    )

    def forward_all(waves):
        return run_first(
            waves, object_field, mine, partner, local_rows, local_columns, order, chirps, blocks
        )

    def silent(waves):
        return jnp.zeros_like(waves)

    carry = start
    inputs = start
    for turn in range(depth_count - 1):
        if turn > 0:
            carry = lax.ppermute(carry, "depth", [(turn - 1, turn)])
            inputs = jnp.where(segment == turn, carry, inputs)
        carry = lax.cond(segment == turn, forward_all, silent, carry)

    height = tile_rows + width
    scalars = (local_rows, local_columns, live.astype(jnp.int32), slot, other)

    def last_pass(incoming):
        return run_adjoint(
            incoming, patches, chirps, blocks, scalars, (measured, both_measured),
            height, columns_all, True,
        )

    def last_silent(incoming):
        return (jnp.zeros_like(incoming), jnp.zeros((2, height, columns_all), jnp.bfloat16))

    if depth_count > 1:
        carry = lax.ppermute(carry, "depth", [(depth_count - 2, depth_count - 1)])
    carry, gradient = lax.cond(segment == depth_count - 1, last_pass, last_silent, carry)

    def back_pass(incoming, previous):
        return run_adjoint(
            incoming, patches, chirps, blocks, scalars, (inputs,), height, columns_all, False
        )

    def back_silent(incoming, previous):
        return (jnp.zeros_like(incoming), previous)

    for turn in reversed(range(depth_count - 1)):
        carry = lax.ppermute(carry, "depth", [(turn + 1, turn)])
        carry, gradient = lax.cond(segment == turn, back_pass, back_silent, carry, gradient)

    gradient = gradient.astype(jnp.bfloat16)
    spill = gradient[:, tile_rows:, :]
    keep = lax.dynamic_slice_in_dim(spill, batch_index * half, half, 2)
    give = lax.dynamic_slice_in_dim(spill, (1 - batch_index) * half, half, 2)
    got = lax.ppermute(give, "batch", pairs)
    spill_sum = (keep.astype(jnp.float32) + got.astype(jnp.float32)).astype(jnp.bfloat16)
    arrived = lax.ppermute(spill_sum, "tile", [(t, t + 1) for t in range(tile_count - 1)])
    own = gradient[:, :tile_rows, :]
    other = lax.ppermute(own, "batch", pairs)
    arrived_other = lax.ppermute(arrived, "batch", pairs)
    incoming = jnp.where(
        first_core,
        jnp.concatenate([arrived, arrived_other], axis=2),
        jnp.concatenate([arrived_other, arrived], axis=2),
    )
    summed = own.astype(jnp.float32) + other.astype(jnp.float32)
    summed = summed.at[:, :width, :].add(incoming.astype(jnp.float32))
    return summed[None]


def solution(mesh):
    placed = (
        P(("groups", "depth"), None, "tile", None),
        P("groups", None, None),
        P(("groups", "tile", "batch"), None),
        P(("groups", "tile", "batch")),
        P(("groups", "tile", "batch"), None, None),
    )
    return jax.shard_map(
        local,
        mesh=mesh,
        in_specs=placed,
        out_specs=P(("groups", "depth"), None, "tile", None),
        check_vma=False,
    )
```

```python
import math

import jax
import jax.numpy as jnp
from jax import lax
from jax.sharding import PartitionSpec as P
from jax.experimental import pallas as pl
from jax.experimental.pallas import tpu as pltpu

SLICE_COEF = 0.002
DETECTOR_COEF = 0.006
RESIDUAL_SCALE = 0.125


def from_behind(block, axis, distance):
    devices = range(lax.axis_size(axis))
    route = [(i - distance, i) for i in devices if i - distance in devices]
    return lax.ppermute(block, axis, route)


def dft_block(width, sign):
    freq = jnp.arange(width, dtype=jnp.int32)
    product = freq[:, None] * freq[None, :] % width
    angle = 2.0 * math.pi / width * product.astype(jnp.float32)
    scale = 1.0 / math.sqrt(width)
    real_part = (jnp.cos(angle) * scale).astype(jnp.bfloat16)
    imag_part = (sign * jnp.sin(angle) * scale).astype(jnp.bfloat16)
    upper = jnp.concatenate([real_part, -imag_part], axis=1)
    lower = jnp.concatenate([imag_part, real_part], axis=1)
    return jnp.concatenate([upper, lower], axis=0)


def dft_right(width, sign):
    freq = jnp.arange(width, dtype=jnp.int32)
    product = freq[:, None] * freq[None, :] % width
    angle = 2.0 * math.pi / width * product.astype(jnp.float32)
    scale = 1.0 / math.sqrt(width)
    real_part = (jnp.cos(angle) * scale).astype(jnp.bfloat16)
    imag_part = (sign * jnp.sin(angle) * scale).astype(jnp.bfloat16)
    upper = jnp.concatenate([real_part, imag_part], axis=1)
    lower = jnp.concatenate([-imag_part, real_part], axis=1)
    return jnp.concatenate([upper, lower], axis=0)


def dft_parts(width):
    freq = jnp.arange(width, dtype=jnp.int32)
    product = freq[:, None] * freq[None, :] % width
    angle = 2.0 * math.pi / width * product.astype(jnp.float32)
    scale = 1.0 / math.sqrt(width)
    real_part = (jnp.cos(angle) * scale).astype(jnp.bfloat16)
    imag_part = (-jnp.sin(angle) * scale).astype(jnp.bfloat16)
    return (real_part, imag_part)


def chirp_parts(width, coef):
    freq = jnp.arange(width, dtype=jnp.int32)
    shifted = (freq + width // 2) % width - width // 2
    square = shifted * shifted
    total = (square[:, None] + square[None, :]).astype(jnp.float32)
    phase = -coef * total
    return (jnp.cos(phase), jnp.sin(phase))


def left_apply(block, waves):
    number = waves.shape[0]
    width = waves.shape[2]
    stacked = waves.reshape(number, 2 * width, width)
    result = jnp.einsum("ij,gjk->gik", block, stacked, preferred_element_type=jnp.float32)
    return result.reshape(number, 2, width, width)


def propagate(waves, forward_block, inverse_block, chirp_re, chirp_im):
    first = left_apply(forward_block, waves).astype(jnp.bfloat16)
    spectrum = left_apply(forward_block, jnp.swapaxes(first, -1, -2))
    spec_re = spectrum[:, 0]
    spec_im = spectrum[:, 1]
    filtered = jnp.stack(
        [spec_re * chirp_re - spec_im * chirp_im, spec_re * chirp_im + spec_im * chirp_re], axis=1
    ).astype(jnp.bfloat16)
    back = left_apply(inverse_block, filtered).astype(jnp.bfloat16)
    return left_apply(inverse_block, jnp.swapaxes(back, -1, -2)).astype(jnp.bfloat16)


def transmit(waves, patch):
    values = waves.astype(jnp.float32)
    wave_re = values[:, 0]
    wave_im = values[:, 1]
    return jnp.stack(
        [
            patch[:, 0] * wave_re - patch[:, 1] * wave_im,
            patch[:, 0] * wave_im + patch[:, 1] * wave_re,
        ],
        axis=1,
    ).astype(jnp.bfloat16)


def residual_wave(waves, measured):
    values = waves.astype(jnp.float32)
    intensity = values[:, 0] * values[:, 0] + values[:, 1] * values[:, 1]
    weight = RESIDUAL_SCALE * (intensity - measured)
    return jnp.stack([weight * values[:, 0], weight * values[:, 1]], axis=1).astype(jnp.bfloat16)


def adjoint_terms(incoming, forward_block, inverse_block, chirp_re, chirp_im, inputs, patch):
    spread = propagate(incoming, forward_block, inverse_block, chirp_re, -chirp_im).astype(
        jnp.float32
    )
    source = inputs.astype(jnp.float32)
    term = jnp.stack(
        [
            source[:, 0] * spread[:, 0] + source[:, 1] * spread[:, 1],
            source[:, 0] * spread[:, 1] - source[:, 1] * spread[:, 0],
        ],
        axis=1,
    )
    passed = jnp.stack(
        [
            patch[:, 0] * spread[:, 0] + patch[:, 1] * spread[:, 1],
            patch[:, 0] * spread[:, 1] - patch[:, 1] * spread[:, 0],
        ],
        axis=1,
    ).astype(jnp.bfloat16)
    return (passed, term)


def wave_kernel(transmit_first, residual_after, backward):
    def kernel(*refs):
        refs = list(refs)
        wave_ref = refs.pop(0)
        patch_ref = refs.pop(0)
        chirp_ref = refs.pop(0)
        blocks = refs[:2]
        refs = refs[2:]
        extra_ref = refs.pop(0) if (residual_after or backward) else None
        wave = wave_ref[0].astype(jnp.float32)
        patch_re = patch_ref[0, 0]
        patch_im = patch_ref[0, 1]
        if transmit_first:
            wave_re = patch_re * wave[0] - patch_im * wave[1]
            wave_im = patch_re * wave[1] + patch_im * wave[0]
        else:
            wave_re = wave[0]
            wave_im = wave[1]
        chirp_re = chirp_ref[0]
        chirp_im = chirp_ref[1]
        if backward:
            chirp_im = -chirp_im
        out_re, out_im = propagate_block(wave_re, wave_im, blocks, chirp_re, chirp_im)
        if residual_after:
            measured = extra_ref[0]
            weight = RESIDUAL_SCALE * (out_re * out_re + out_im * out_im - measured)
            result_ref = refs[0]
            result_ref[0, 0] = (weight * out_re).astype(jnp.bfloat16)
            result_ref[0, 1] = (weight * out_im).astype(jnp.bfloat16)
        elif backward:
            source = extra_ref[0].astype(jnp.float32)
            passed_ref, term_ref = refs[0], refs[1]
            passed_ref[0, 0] = (patch_re * out_re + patch_im * out_im).astype(jnp.bfloat16)
            passed_ref[0, 1] = (patch_re * out_im - patch_im * out_re).astype(jnp.bfloat16)
            term_ref[0, 0] = source[0] * out_re + source[1] * out_im
            term_ref[0, 1] = source[0] * out_im - source[1] * out_re
        else:
            result_ref = refs[0]
            result_ref[0, 0] = out_re.astype(jnp.bfloat16)
            result_ref[0, 1] = out_im.astype(jnp.bfloat16)

    return kernel


def run_waves(waves, patches, chirps, blocks, extra=None, transmit_first=True, residual_after=False, backward=False):
    number, _, width, _ = waves.shape
    wave_spec = pl.BlockSpec((1, 2, width, width), lambda i: (i, 0, 0, 0))
    chirp_spec = pl.BlockSpec((2, width, width), lambda i: (0, 0, 0))
    in_specs = [wave_spec, wave_spec, chirp_spec] + [
        pl.BlockSpec((2 * width, width), lambda i: (0, 0)),
        pl.BlockSpec((width, 2 * width), lambda i: (0, 0)),
    ]
    args = [waves, patches, chirps] + list(blocks)
    if residual_after:
        in_specs.append(pl.BlockSpec((1, width, width), lambda i: (i, 0, 0)))
        args.append(extra)
    if backward:
        in_specs.append(wave_spec)
        args.append(extra)
        out_shape = (
            jax.ShapeDtypeStruct(waves.shape, jnp.bfloat16),
            jax.ShapeDtypeStruct(waves.shape, jnp.float32),
        )
        out_specs = (wave_spec, wave_spec)
    else:
        out_shape = jax.ShapeDtypeStruct(waves.shape, jnp.bfloat16)
        out_specs = wave_spec
    return pl.pallas_call(
        wave_kernel(transmit_first, residual_after, backward),
        grid=(number,),
        in_specs=in_specs,
        out_specs=out_specs,
        out_shape=out_shape,
    )(*args)


def scatter_kernel(rows_ref, columns_ref, live_ref, terms_ref, out_ref):
    index = pl.program_id(0)

    @pl.when(index == 0)
    def _():
        out_ref[...] = jnp.zeros(out_ref.shape, out_ref.dtype)

    width = terms_ref.shape[2]
    height = out_ref.shape[1]
    columns_all = out_ref.shape[2]
    row = rows_ref[index]
    column = columns_ref[index]
    alive = live_ref[index] > 0
    for part in range(2):
        term = jnp.where(alive, terms_ref[0, part], 0.0)
        wide = jnp.concatenate(
            [term, jnp.zeros((width, columns_all - width), jnp.float32)], axis=1
        )
        wide = pltpu.roll(wide, column, 1)
        tall = jnp.concatenate(
            [wide, jnp.zeros((height - width, columns_all), jnp.float32)], axis=0
        )
        tall = pltpu.roll(tall, row, 0)
        out_ref[part] = out_ref[part] + tall


def scatter_terms(terms, rows, columns, live, height, columns_all):
    number, _, width, _ = terms.shape
    grid_spec = pltpu.PrefetchScalarGridSpec(
        num_scalar_prefetch=3,
        grid=(number,),
        in_specs=[pl.BlockSpec((1, 2, width, width), lambda i, r, c, a: (i, 0, 0, 0))],
        out_specs=pl.BlockSpec((2, height, columns_all), lambda i, r, c, a: (0, 0, 0)),
    )
    return pl.pallas_call(
        scatter_kernel,
        grid_spec=grid_spec,
        out_shape=jax.ShapeDtypeStruct((2, height, columns_all), jnp.float32),
    )(rows, columns, live.astype(jnp.int32), terms)


def cut_kernel(rows_ref, columns_ref, order_ref, tile_ref, mine_ref, partner_ref, out_ref):
    index = pl.program_id(0)
    width = out_ref.shape[2]
    height = tile_ref.shape[2] + mine_ref.shape[2]
    columns_all = tile_ref.shape[3]
    row_shift = (height - rows_ref[index]) % height
    column_shift = (columns_all - columns_ref[index]) % columns_all
    first = order_ref[0] == 0
    for part in range(2):
        mine = mine_ref[0, part].astype(jnp.float32)
        partner = partner_ref[0, part].astype(jnp.float32)
        rim = jnp.concatenate(
            [jnp.where(first, mine, partner), jnp.where(first, partner, mine)], axis=1
        )
        full = jnp.concatenate([tile_ref[0, part], rim], axis=0)
        full = pltpu.roll(full, row_shift, 0)[:width]
        full = pltpu.roll(full, column_shift, 1)[:, :width]
        out_ref[0, part] = full


def cut_patches(tile, mine, partner, rows, columns, order, width):
    number = rows.shape[0]
    grid_spec = pltpu.PrefetchScalarGridSpec(
        num_scalar_prefetch=3,
        grid=(number,),
        in_specs=[
            pl.BlockSpec(tile.shape, lambda i, r, c, o: (0, 0, 0, 0)),
            pl.BlockSpec(mine.shape, lambda i, r, c, o: (0, 0, 0, 0)),
            pl.BlockSpec(partner.shape, lambda i, r, c, o: (0, 0, 0, 0)),
        ],
        out_specs=pl.BlockSpec((1, 2, width, width), lambda i, r, c, o: (i, 0, 0, 0)),
    )
    return pl.pallas_call(
        cut_kernel,
        grid_spec=grid_spec,
        out_shape=jax.ShapeDtypeStruct((number, 2, width, width), jnp.float32),
    )(rows, columns, order, tile, mine, partner)


def propagate_block(wave_re, wave_im, blocks, chirp_re, chirp_im):
    rows_ref, cols_ref = blocks
    width = wave_re.shape[0]
    dft_rows = rows_ref[...]
    dft_cols = cols_ref[...]

    def left(part_re, part_im):
        lanes = jnp.concatenate([part_re, part_im], axis=1).astype(jnp.bfloat16)
        return jnp.dot(dft_rows, lanes, preferred_element_type=jnp.float32)

    def right(part_re, part_im):
        rows = jnp.concatenate([part_re, part_im], axis=0).astype(jnp.bfloat16)
        return jnp.dot(rows, dft_cols, preferred_element_type=jnp.float32)

    first = left(wave_re, wave_im)
    z_re = (first[:width, :width] - first[width:, width:]).astype(jnp.bfloat16)
    z_im = (first[:width, width:] + first[width:, :width]).astype(jnp.bfloat16)
    second = right(z_re, z_im)
    spec_re = second[:width, :width] - second[width:, width:]
    spec_im = second[:width, width:] + second[width:, :width]
    w_re = spec_re * chirp_re - spec_im * chirp_im
    w_im = spec_re * chirp_im + spec_im * chirp_re
    third = right(w_re.astype(jnp.bfloat16), w_im.astype(jnp.bfloat16))
    v_re = (third[:width, :width] + third[width:, width:]).astype(jnp.bfloat16)
    v_im = (third[width:, :width] - third[:width, width:]).astype(jnp.bfloat16)
    fourth = left(v_re, v_im)
    out_re = (fourth[:width, :width] + fourth[width:, width:]).astype(jnp.bfloat16)
    out_im = (fourth[:width, width:] - fourth[width:, :width]).astype(jnp.bfloat16)
    return (out_re.astype(jnp.float32), out_im.astype(jnp.float32))


def place_term(term_re, term_im, row, column, alive, total_ref, direct_ref=None):
    width = term_re.shape[0]
    height = total_ref.shape[1]
    columns_all = total_ref.shape[2]
    row_shift = row % height
    column_shift = column % columns_all
    for part, term in enumerate((term_re, term_im)):
        term = jnp.where(alive, term, 0.0)
        wide = jnp.concatenate(
            [term, jnp.zeros((width, columns_all - width), jnp.float32)], axis=1
        )
        wide = pltpu.roll(wide, column_shift, 1)
        if height == 2 * width:
            rolled = pltpu.roll(wide, row % width, 0)
            below = lax.broadcasted_iota(jnp.int32, rolled.shape, 0) < row
            upper = jnp.where(below, 0.0, rolled)
            lower = jnp.where(below, rolled, 0.0)
            if direct_ref is None:
                total_ref[part, :width] = total_ref[part, :width] + upper
                total_ref[part, width:] = total_ref[part, width:] + lower
            else:
                direct_ref[part, :width] = upper.astype(direct_ref.dtype)
                direct_ref[part, width:] = lower.astype(direct_ref.dtype)
            continue
        tall = jnp.concatenate(
            [wide, jnp.zeros((height - width, columns_all), jnp.float32)], axis=0
        )
        if direct_ref is None:
            total_ref[part] = total_ref[part] + pltpu.roll(tall, row_shift, 0)
        else:
            direct_ref[part] = pltpu.roll(tall, row_shift, 0).astype(direct_ref.dtype)


def adjoint_kernel(last, single):
    def kernel(rows_ref, columns_ref, live_ref, slot_ref, other_ref, *refs):
        refs = list(refs)
        wave_ref = refs.pop(0)
        patch_ref = refs.pop(0)
        chirp_ref = refs.pop(0)
        blocks = refs[:2]
        refs = refs[2:]
        if last:
            own_ref = refs.pop(0)
            partner_ref = refs.pop(0)
        else:
            source_ref = refs.pop(0)
        passed_ref, grad_ref, total_ref = refs
        index = pl.program_id(0)

        if not single:
            @pl.when(index == 0)
            def _():
                total_ref[...] = jnp.zeros(total_ref.shape, total_ref.dtype)

        wave = wave_ref[0].astype(jnp.float32)
        patch_re = patch_ref[0, 0]
        patch_im = patch_ref[0, 1]
        chirp_re = chirp_ref[0]
        chirp_im = chirp_ref[1]
        if last:
            source_re = wave[0]
            source_im = wave[1]
            lit_re = patch_re * wave[0] - patch_im * wave[1]
            lit_im = patch_re * wave[1] + patch_im * wave[0]
            out_re, out_im = propagate_block(lit_re, lit_im, blocks, chirp_re, chirp_im)
            measured = jnp.where(other_ref[index] > 0, partner_ref[0], own_ref[0])
            weight = RESIDUAL_SCALE * (out_re * out_re + out_im * out_im - measured)
            in_re = (weight * out_re).astype(jnp.bfloat16).astype(jnp.float32)
            in_im = (weight * out_im).astype(jnp.bfloat16).astype(jnp.float32)
        else:
            source = source_ref[0].astype(jnp.float32)
            source_re = source[0]
            source_im = source[1]
            in_re = wave[0]
            in_im = wave[1]
        spread_re, spread_im = propagate_block(in_re, in_im, blocks, chirp_re, -chirp_im)
        passed_ref[0, 0] = (patch_re * spread_re + patch_im * spread_im).astype(jnp.bfloat16)
        passed_ref[0, 1] = (patch_re * spread_im - patch_im * spread_re).astype(jnp.bfloat16)
        term_re = source_re * spread_re + source_im * spread_im
        term_im = source_re * spread_im - source_im * spread_re
        place_term(
            term_re, term_im, rows_ref[index], columns_ref[index], live_ref[index] > 0,
            total_ref, grad_ref if single else None,
        )

        if not single:
            @pl.when(index == pl.num_programs(0) - 1)
            def _():
                grad_ref[...] = total_ref[...].astype(grad_ref.dtype)

    return kernel


def run_adjoint(waves, patches, chirps, blocks, scalars, extra, height, columns_all, last):
    number, _, width, _ = waves.shape
    wave_spec = pl.BlockSpec((1, 2, width, width), lambda i, *s: (i, 0, 0, 0))
    chirp_spec = pl.BlockSpec((2, width, width), lambda i, *s: (0, 0, 0))
    in_specs = [wave_spec, wave_spec, chirp_spec] + [
        pl.BlockSpec((2 * width, width), lambda i, *s: (0, 0)),
        pl.BlockSpec((width, 2 * width), lambda i, *s: (0, 0)),
    ]
    if last:
        slot_spec = pl.BlockSpec((1, width, width), lambda i, r, c, a, s, o: (s[i], 0, 0))
        in_specs += [slot_spec, slot_spec]
    else:
        in_specs += [wave_spec]
    grid_spec = pltpu.PrefetchScalarGridSpec(
        num_scalar_prefetch=5,
        grid=(number,),
        in_specs=in_specs,
        out_specs=(
            wave_spec,
            pl.BlockSpec((2, height, columns_all), lambda i, *s: (0, 0, 0)),
        ),
        scratch_shapes=[pltpu.VMEM((2, height, columns_all), jnp.float32)],
    )
    return pl.pallas_call(
        adjoint_kernel(last, number == 1),
        grid_spec=grid_spec,
        out_shape=(
            jax.ShapeDtypeStruct(waves.shape, jnp.bfloat16),
            jax.ShapeDtypeStruct((2, height, columns_all), jnp.bfloat16),
        ),
    )(*scalars, waves, patches, chirps, *blocks, *extra)


def first_kernel(rows_ref, columns_ref, order_ref, wave_ref, tile_ref, mine_ref, partner_ref,
                 chirp_ref, dft_rows_ref, dft_cols_ref, result_ref):
    index = pl.program_id(0)
    width = wave_ref.shape[2]
    height = tile_ref.shape[2] + mine_ref.shape[2]
    columns_all = tile_ref.shape[3]
    row_shift = (height - rows_ref[index]) % height
    column_shift = (columns_all - columns_ref[index]) % columns_all
    first = order_ref[0] == 0
    patch = []
    for part in range(2):
        mine = mine_ref[0, part].astype(jnp.float32)
        partner = partner_ref[0, part].astype(jnp.float32)
        rim = jnp.concatenate(
            [jnp.where(first, mine, partner), jnp.where(first, partner, mine)], axis=1
        )
        full = jnp.concatenate([tile_ref[0, part], rim], axis=0)
        full = pltpu.roll(full, row_shift, 0)[:width]
        patch.append(pltpu.roll(full, column_shift, 1)[:, :width])
    wave = wave_ref[0].astype(jnp.float32)
    wave_re = patch[0] * wave[0] - patch[1] * wave[1]
    wave_im = patch[0] * wave[1] + patch[1] * wave[0]
    out_re, out_im = propagate_block(
        wave_re, wave_im, (dft_rows_ref, dft_cols_ref), chirp_ref[0], chirp_ref[1]
    )
    result_ref[0, 0] = out_re.astype(jnp.bfloat16)
    result_ref[0, 1] = out_im.astype(jnp.bfloat16)


def run_first(waves, tile, mine, partner, rows, columns, order, chirps, blocks):
    number, _, width, _ = waves.shape
    wave_spec = pl.BlockSpec((1, 2, width, width), lambda i, r, c, o: (i, 0, 0, 0))
    whole = lambda shape: pl.BlockSpec(shape, lambda i, r, c, o: (0,) * len(shape))
    grid_spec = pltpu.PrefetchScalarGridSpec(
        num_scalar_prefetch=3,
        grid=(number,),
        in_specs=[
            wave_spec,
            whole(tile.shape),
            whole(mine.shape),
            whole(partner.shape),
            whole(chirps.shape),
            whole(blocks[0].shape),
            whole(blocks[1].shape),
        ],
        out_specs=wave_spec,
    )
    return pl.pallas_call(
        first_kernel,
        grid_spec=grid_spec,
        out_shape=jax.ShapeDtypeStruct(waves.shape, jnp.bfloat16),
    )(rows, columns, order, waves, tile, mine, partner, chirps, *blocks)


def local(object_field, probe, positions, counts, measured):
    width = probe.shape[1]
    tile_rows = object_field.shape[2]
    columns_all = object_field.shape[3]
    tile_index = lax.axis_index("tile")
    tile_count = lax.axis_size("tile")
    segment = lax.axis_index("depth")
    depth_count = lax.axis_size("depth")
    batch_index = lax.axis_index("batch")
    batch_count = lax.axis_size("batch")
    half = columns_all // batch_count
    wanted = lax.dynamic_slice_in_dim(object_field[:, :, :width, :], batch_index * half, half, 3)
    mine = from_behind(wanted.astype(jnp.bfloat16), "tile", -1)
    pairs = [(b, (b + 1) % batch_count) for b in range(batch_count)]
    partner = lax.ppermute(mine, "batch", pairs)
    capacity = positions.shape[0]
    share = -(-capacity // batch_count)
    first_core = batch_index == 0
    both_positions = lax.ppermute(positions, "batch", pairs)
    both_counts = lax.ppermute(counts, "batch", pairs)
    both_measured = lax.ppermute(measured, "batch", pairs)
    all_positions = jnp.where(
        first_core,
        jnp.concatenate([positions, both_positions]),
        jnp.concatenate([both_positions, positions]),
    )
    all_counts = jnp.where(
        first_core, jnp.concatenate([counts, both_counts]), jnp.concatenate([both_counts, counts])
    )
    entry = batch_index * share + jnp.arange(share, dtype=jnp.int32)
    live = entry < all_counts[0] + all_counts[1]
    later = entry >= all_counts[0]
    slot = jnp.clip(jnp.where(later, entry - all_counts[0], entry), 0, capacity - 1)
    flat = jnp.where(later, capacity, 0) + slot
    chosen = all_positions[flat]
    other = (later == first_core).astype(jnp.int32)
    local_rows = chosen[:, 0] - tile_index * tile_rows
    local_columns = chosen[:, 1]
    order = jnp.reshape(batch_index, (1,)).astype(jnp.int32)
    patches = cut_patches(object_field, mine, partner, local_rows, local_columns, order, width)
    number = patches.shape[0]
    coef = jnp.where(
        segment == depth_count - 1, jnp.float32(DETECTOR_COEF), jnp.float32(SLICE_COEF)
    )
    chirp_re, chirp_im = chirp_parts(width, coef)
    start = jnp.broadcast_to(probe[None], (number, 2, width, width))

    chirps = jnp.stack([chirp_re, chirp_im])
    dft_re, dft_im = dft_parts(width)
    blocks = (
        jnp.concatenate([dft_re, dft_im], axis=0),
        jnp.concatenate([dft_re, dft_im], axis=1),
    )

    def forward_all(waves):
        return run_first(
            waves, object_field, mine, partner, local_rows, local_columns, order, chirps, blocks
        )

    def silent(waves):
        return jnp.zeros_like(waves)

    carry = start
    inputs = start
    for turn in range(depth_count - 1):
        if turn > 0:
            carry = lax.ppermute(carry, "depth", [(turn - 1, turn)])
            inputs = jnp.where(segment == turn, carry, inputs)
        carry = lax.cond(segment == turn, forward_all, silent, carry)

    height = tile_rows + width
    scalars = (local_rows, local_columns, live.astype(jnp.int32), slot, other)

    def last_pass(incoming):
        return run_adjoint(
            incoming, patches, chirps, blocks, scalars, (measured, both_measured),
            height, columns_all, True,
        )

    def last_silent(incoming):
        return (jnp.zeros_like(incoming), jnp.zeros((2, height, columns_all), jnp.bfloat16))

    if depth_count > 1:
        carry = lax.ppermute(carry, "depth", [(depth_count - 2, depth_count - 1)])
    carry, gradient = lax.cond(segment == depth_count - 1, last_pass, last_silent, carry)

    def back_pass(incoming, previous):
        return run_adjoint(
            incoming, patches, chirps, blocks, scalars, (inputs,), height, columns_all, False
        )

    def back_silent(incoming, previous):
        return (jnp.zeros_like(incoming), previous)

    for turn in reversed(range(depth_count - 1)):
        carry = lax.ppermute(carry, "depth", [(turn + 1, turn)])
        carry, gradient = lax.cond(segment == turn, back_pass, back_silent, carry, gradient)

    gradient = gradient.astype(jnp.bfloat16)
    spill = gradient[:, tile_rows:, :]
    keep = lax.dynamic_slice_in_dim(spill, batch_index * half, half, 2)
    give = lax.dynamic_slice_in_dim(spill, (1 - batch_index) * half, half, 2)
    got = lax.ppermute(give, "batch", pairs)
    spill_sum = (keep.astype(jnp.float32) + got.astype(jnp.float32)).astype(jnp.bfloat16)
    arrived = lax.ppermute(spill_sum, "tile", [(t, t + 1) for t in range(tile_count - 1)])
    own = gradient[:, :tile_rows, :]
    other = lax.ppermute(own, "batch", pairs)
    arrived_other = lax.ppermute(arrived, "batch", pairs)
    incoming = jnp.where(
        first_core,
        jnp.concatenate([arrived, arrived_other], axis=2),
        jnp.concatenate([arrived_other, arrived], axis=2),
    )
    summed = own.astype(jnp.float32) + other.astype(jnp.float32)
    summed = summed.at[:, :width, :].add(incoming.astype(jnp.float32))
    return summed[None]


def solution(mesh):
    placed = (
        P(("groups", "depth"), None, "tile", None),
        P("groups", None, None),
        P(("groups", "tile", "batch"), None),
        P(("groups", "tile", "batch")),
        P(("groups", "tile", "batch"), None, None),
    )
    return jax.shard_map(
        local,
        mesh=mesh,
        in_specs=placed,
        out_specs=P(("groups", "depth"), None, "tile", None),
        check_vma=False,
    )
```

```python
import math

import jax
import jax.numpy as jnp
from jax import lax
from jax.sharding import PartitionSpec as P
from jax.experimental import pallas as pl
from jax.experimental.pallas import tpu as pltpu

SLICE_COEF = 0.002
DETECTOR_COEF = 0.006
RESIDUAL_SCALE = 0.125


def from_behind(block, axis, distance):
    devices = range(lax.axis_size(axis))
    route = [(i - distance, i) for i in devices if i - distance in devices]
    return lax.ppermute(block, axis, route)


def dft_block(width, sign):
    freq = jnp.arange(width, dtype=jnp.int32)
    product = freq[:, None] * freq[None, :] % width
    angle = 2.0 * math.pi / width * product.astype(jnp.float32)
    scale = 1.0 / math.sqrt(width)
    real_part = (jnp.cos(angle) * scale).astype(jnp.bfloat16)
    imag_part = (sign * jnp.sin(angle) * scale).astype(jnp.bfloat16)
    upper = jnp.concatenate([real_part, -imag_part], axis=1)
    lower = jnp.concatenate([imag_part, real_part], axis=1)
    return jnp.concatenate([upper, lower], axis=0)


def dft_right(width, sign):
    freq = jnp.arange(width, dtype=jnp.int32)
    product = freq[:, None] * freq[None, :] % width
    angle = 2.0 * math.pi / width * product.astype(jnp.float32)
    scale = 1.0 / math.sqrt(width)
    real_part = (jnp.cos(angle) * scale).astype(jnp.bfloat16)
    imag_part = (sign * jnp.sin(angle) * scale).astype(jnp.bfloat16)
    upper = jnp.concatenate([real_part, imag_part], axis=1)
    lower = jnp.concatenate([-imag_part, real_part], axis=1)
    return jnp.concatenate([upper, lower], axis=0)


def dft_parts(width):
    freq = jnp.arange(width, dtype=jnp.int32)
    product = freq[:, None] * freq[None, :] % width
    angle = 2.0 * math.pi / width * product.astype(jnp.float32)
    scale = 1.0 / math.sqrt(width)
    real_part = (jnp.cos(angle) * scale).astype(jnp.bfloat16)
    imag_part = (-jnp.sin(angle) * scale).astype(jnp.bfloat16)
    return (real_part, imag_part)


def chirp_parts(width, coef):
    freq = jnp.arange(width, dtype=jnp.int32)
    shifted = (freq + width // 2) % width - width // 2
    square = shifted * shifted
    total = (square[:, None] + square[None, :]).astype(jnp.float32)
    phase = -coef * total
    return (jnp.cos(phase), jnp.sin(phase))


def left_apply(block, waves):
    number = waves.shape[0]
    width = waves.shape[2]
    stacked = waves.reshape(number, 2 * width, width)
    result = jnp.einsum("ij,gjk->gik", block, stacked, preferred_element_type=jnp.float32)
    return result.reshape(number, 2, width, width)


def propagate(waves, forward_block, inverse_block, chirp_re, chirp_im):
    first = left_apply(forward_block, waves).astype(jnp.bfloat16)
    spectrum = left_apply(forward_block, jnp.swapaxes(first, -1, -2))
    spec_re = spectrum[:, 0]
    spec_im = spectrum[:, 1]
    filtered = jnp.stack(
        [spec_re * chirp_re - spec_im * chirp_im, spec_re * chirp_im + spec_im * chirp_re], axis=1
    ).astype(jnp.bfloat16)
    back = left_apply(inverse_block, filtered).astype(jnp.bfloat16)
    return left_apply(inverse_block, jnp.swapaxes(back, -1, -2)).astype(jnp.bfloat16)


def transmit(waves, patch):
    values = waves.astype(jnp.float32)
    wave_re = values[:, 0]
    wave_im = values[:, 1]
    return jnp.stack(
        [
            patch[:, 0] * wave_re - patch[:, 1] * wave_im,
            patch[:, 0] * wave_im + patch[:, 1] * wave_re,
        ],
        axis=1,
    ).astype(jnp.bfloat16)


def residual_wave(waves, measured):
    values = waves.astype(jnp.float32)
    intensity = values[:, 0] * values[:, 0] + values[:, 1] * values[:, 1]
    weight = RESIDUAL_SCALE * (intensity - measured)
    return jnp.stack([weight * values[:, 0], weight * values[:, 1]], axis=1).astype(jnp.bfloat16)


def adjoint_terms(incoming, forward_block, inverse_block, chirp_re, chirp_im, inputs, patch):
    spread = propagate(incoming, forward_block, inverse_block, chirp_re, -chirp_im).astype(
        jnp.float32
    )
    source = inputs.astype(jnp.float32)
    term = jnp.stack(
        [
            source[:, 0] * spread[:, 0] + source[:, 1] * spread[:, 1],
            source[:, 0] * spread[:, 1] - source[:, 1] * spread[:, 0],
        ],
        axis=1,
    )
    passed = jnp.stack(
        [
            patch[:, 0] * spread[:, 0] + patch[:, 1] * spread[:, 1],
            patch[:, 0] * spread[:, 1] - patch[:, 1] * spread[:, 0],
        ],
        axis=1,
    ).astype(jnp.bfloat16)
    return (passed, term)


def wave_kernel(transmit_first, residual_after, backward):
    def kernel(*refs):
        refs = list(refs)
        wave_ref = refs.pop(0)
        patch_ref = refs.pop(0)
        chirp_ref = refs.pop(0)
        blocks = refs[:2]
        refs = refs[2:]
        extra_ref = refs.pop(0) if (residual_after or backward) else None
        wave = wave_ref[0].astype(jnp.float32)
        patch_re = patch_ref[0, 0]
        patch_im = patch_ref[0, 1]
        if transmit_first:
            wave_re = patch_re * wave[0] - patch_im * wave[1]
            wave_im = patch_re * wave[1] + patch_im * wave[0]
        else:
            wave_re = wave[0]
            wave_im = wave[1]
        chirp_re = chirp_ref[0]
        chirp_im = chirp_ref[1]
        if backward:
            chirp_im = -chirp_im
        out_re, out_im = propagate_block(wave_re, wave_im, blocks, chirp_re, chirp_im)
        if residual_after:
            measured = extra_ref[0]
            weight = RESIDUAL_SCALE * (out_re * out_re + out_im * out_im - measured)
            result_ref = refs[0]
            result_ref[0, 0] = (weight * out_re).astype(jnp.bfloat16)
            result_ref[0, 1] = (weight * out_im).astype(jnp.bfloat16)
        elif backward:
            source = extra_ref[0].astype(jnp.float32)
            passed_ref, term_ref = refs[0], refs[1]
            passed_ref[0, 0] = (patch_re * out_re + patch_im * out_im).astype(jnp.bfloat16)
            passed_ref[0, 1] = (patch_re * out_im - patch_im * out_re).astype(jnp.bfloat16)
            term_ref[0, 0] = source[0] * out_re + source[1] * out_im
            term_ref[0, 1] = source[0] * out_im - source[1] * out_re
        else:
            result_ref = refs[0]
            result_ref[0, 0] = out_re.astype(jnp.bfloat16)
            result_ref[0, 1] = out_im.astype(jnp.bfloat16)

    return kernel


def run_waves(waves, patches, chirps, blocks, extra=None, transmit_first=True, residual_after=False, backward=False):
    number, _, width, _ = waves.shape
    wave_spec = pl.BlockSpec((1, 2, width, width), lambda i: (i, 0, 0, 0))
    chirp_spec = pl.BlockSpec((2, width, width), lambda i: (0, 0, 0))
    in_specs = [wave_spec, wave_spec, chirp_spec] + [
        pl.BlockSpec((2 * width, width), lambda i: (0, 0)),
        pl.BlockSpec((width, 2 * width), lambda i: (0, 0)),
    ]
    args = [waves, patches, chirps] + list(blocks)
    if residual_after:
        in_specs.append(pl.BlockSpec((1, width, width), lambda i: (i, 0, 0)))
        args.append(extra)
    if backward:
        in_specs.append(wave_spec)
        args.append(extra)
        out_shape = (
            jax.ShapeDtypeStruct(waves.shape, jnp.bfloat16),
            jax.ShapeDtypeStruct(waves.shape, jnp.float32),
        )
        out_specs = (wave_spec, wave_spec)
    else:
        out_shape = jax.ShapeDtypeStruct(waves.shape, jnp.bfloat16)
        out_specs = wave_spec
    return pl.pallas_call(
        wave_kernel(transmit_first, residual_after, backward),
        grid=(number,),
        in_specs=in_specs,
        out_specs=out_specs,
        out_shape=out_shape,
    )(*args)


def scatter_kernel(rows_ref, columns_ref, live_ref, terms_ref, out_ref):
    index = pl.program_id(0)

    @pl.when(index == 0)
    def _():
        out_ref[...] = jnp.zeros(out_ref.shape, out_ref.dtype)

    width = terms_ref.shape[2]
    height = out_ref.shape[1]
    columns_all = out_ref.shape[2]
    row = rows_ref[index]
    column = columns_ref[index]
    alive = live_ref[index] > 0
    for part in range(2):
        term = jnp.where(alive, terms_ref[0, part], 0.0)
        wide = jnp.concatenate(
            [term, jnp.zeros((width, columns_all - width), jnp.float32)], axis=1
        )
        wide = pltpu.roll(wide, column, 1)
        tall = jnp.concatenate(
            [wide, jnp.zeros((height - width, columns_all), jnp.float32)], axis=0
        )
        tall = pltpu.roll(tall, row, 0)
        out_ref[part] = out_ref[part] + tall


def scatter_terms(terms, rows, columns, live, height, columns_all):
    number, _, width, _ = terms.shape
    grid_spec = pltpu.PrefetchScalarGridSpec(
        num_scalar_prefetch=3,
        grid=(number,),
        in_specs=[pl.BlockSpec((1, 2, width, width), lambda i, r, c, a: (i, 0, 0, 0))],
        out_specs=pl.BlockSpec((2, height, columns_all), lambda i, r, c, a: (0, 0, 0)),
    )
    return pl.pallas_call(
        scatter_kernel,
        grid_spec=grid_spec,
        out_shape=jax.ShapeDtypeStruct((2, height, columns_all), jnp.float32),
    )(rows, columns, live.astype(jnp.int32), terms)


def cut_kernel(rows_ref, columns_ref, order_ref, tile_ref, mine_ref, partner_ref, out_ref):
    index = pl.program_id(0)
    width = out_ref.shape[2]
    height = tile_ref.shape[2] + mine_ref.shape[2]
    columns_all = tile_ref.shape[3]
    row_shift = (height - rows_ref[index]) % height
    column_shift = (columns_all - columns_ref[index]) % columns_all
    first = order_ref[0] == 0
    for part in range(2):
        mine = mine_ref[0, part].astype(jnp.float32)
        partner = partner_ref[0, part].astype(jnp.float32)
        rim = jnp.concatenate(
            [jnp.where(first, mine, partner), jnp.where(first, partner, mine)], axis=1
        )
        full = jnp.concatenate([tile_ref[0, part], rim], axis=0)
        full = pltpu.roll(full, row_shift, 0)[:width]
        full = pltpu.roll(full, column_shift, 1)[:, :width]
        out_ref[0, part] = full


def cut_patches(tile, mine, partner, rows, columns, order, width):
    number = rows.shape[0]
    grid_spec = pltpu.PrefetchScalarGridSpec(
        num_scalar_prefetch=3,
        grid=(number,),
        in_specs=[
            pl.BlockSpec(tile.shape, lambda i, r, c, o: (0, 0, 0, 0)),
            pl.BlockSpec(mine.shape, lambda i, r, c, o: (0, 0, 0, 0)),
            pl.BlockSpec(partner.shape, lambda i, r, c, o: (0, 0, 0, 0)),
        ],
        out_specs=pl.BlockSpec((1, 2, width, width), lambda i, r, c, o: (i, 0, 0, 0)),
    )
    return pl.pallas_call(
        cut_kernel,
        grid_spec=grid_spec,
        out_shape=jax.ShapeDtypeStruct((number, 2, width, width), jnp.float32),
    )(rows, columns, order, tile, mine, partner)


def propagate_block(wave_re, wave_im, blocks, chirp_re, chirp_im):
    rows_ref, cols_ref = blocks
    width = wave_re.shape[0]
    dft_rows = rows_ref[...]
    dft_cols = cols_ref[...]

    def left(part_re, part_im):
        lanes = jnp.concatenate([part_re, part_im], axis=1).astype(jnp.bfloat16)
        return jnp.dot(dft_rows, lanes, preferred_element_type=jnp.float32)

    def right(part_re, part_im):
        rows = jnp.concatenate([part_re, part_im], axis=0).astype(jnp.bfloat16)
        return jnp.dot(rows, dft_cols, preferred_element_type=jnp.float32)

    first = left(wave_re, wave_im)
    z_re = (first[:width, :width] - first[width:, width:]).astype(jnp.bfloat16)
    z_im = (first[:width, width:] + first[width:, :width]).astype(jnp.bfloat16)
    second = right(z_re, z_im)
    spec_re = second[:width, :width] - second[width:, width:]
    spec_im = second[:width, width:] + second[width:, :width]
    w_re = spec_re * chirp_re - spec_im * chirp_im
    w_im = spec_re * chirp_im + spec_im * chirp_re
    third = right(w_re.astype(jnp.bfloat16), w_im.astype(jnp.bfloat16))
    v_re = (third[:width, :width] + third[width:, width:]).astype(jnp.bfloat16)
    v_im = (third[width:, :width] - third[:width, width:]).astype(jnp.bfloat16)
    fourth = left(v_re, v_im)
    out_re = (fourth[:width, :width] + fourth[width:, width:]).astype(jnp.bfloat16)
    out_im = (fourth[:width, width:] - fourth[width:, :width]).astype(jnp.bfloat16)
    return (out_re.astype(jnp.float32), out_im.astype(jnp.float32))


def place_term(term_re, term_im, row, column, alive, total_ref, direct_ref=None):
    width = term_re.shape[0]
    height = total_ref.shape[1]
    columns_all = total_ref.shape[2]
    row_shift = row % height
    column_shift = column % columns_all
    for part, term in enumerate((term_re, term_im)):
        term = jnp.where(alive, term, 0.0)
        wide = jnp.concatenate(
            [term, jnp.zeros((width, columns_all - width), jnp.float32)], axis=1
        )
        wide = pltpu.roll(wide, column_shift, 1)
        if height == 2 * width:
            rolled = pltpu.roll(wide, row % width, 0)
            below = lax.broadcasted_iota(jnp.int32, rolled.shape, 0) < row
            upper = jnp.where(below, 0.0, rolled)
            lower = jnp.where(below, rolled, 0.0)
            if direct_ref is None:
                total_ref[part, :width] = total_ref[part, :width] + upper
                total_ref[part, width:] = total_ref[part, width:] + lower
            else:
                direct_ref[part, :width] = upper.astype(direct_ref.dtype)
                direct_ref[part, width:] = lower.astype(direct_ref.dtype)
            continue
        tall = jnp.concatenate(
            [wide, jnp.zeros((height - width, columns_all), jnp.float32)], axis=0
        )
        if direct_ref is None:
            total_ref[part] = total_ref[part] + pltpu.roll(tall, row_shift, 0)
        else:
            direct_ref[part] = pltpu.roll(tall, row_shift, 0).astype(direct_ref.dtype)


def adjoint_kernel(last, single):
    def kernel(rows_ref, columns_ref, live_ref, slot_ref, other_ref, *refs):
        refs = list(refs)
        wave_ref = refs.pop(0)
        patch_ref = refs.pop(0)
        chirp_ref = refs.pop(0)
        blocks = refs[:2]
        refs = refs[2:]
        if last:
            own_ref = refs.pop(0)
            partner_ref = refs.pop(0)
        else:
            source_ref = refs.pop(0)
        passed_ref, grad_ref, total_ref = refs
        index = pl.program_id(0)

        if not single:
            @pl.when(index == 0)
            def _():
                total_ref[...] = jnp.zeros(total_ref.shape, total_ref.dtype)

        wave = wave_ref[0].astype(jnp.float32)
        patch_re = patch_ref[0, 0]
        patch_im = patch_ref[0, 1]
        chirp_re = chirp_ref[0]
        chirp_im = chirp_ref[1]
        if last:
            source_re = wave[0]
            source_im = wave[1]
            lit_re = patch_re * wave[0] - patch_im * wave[1]
            lit_im = patch_re * wave[1] + patch_im * wave[0]
            out_re, out_im = propagate_block(lit_re, lit_im, blocks, chirp_re, chirp_im)
            measured = jnp.where(other_ref[index] > 0, partner_ref[0], own_ref[0])
            weight = RESIDUAL_SCALE * (out_re * out_re + out_im * out_im - measured)
            in_re = (weight * out_re).astype(jnp.bfloat16).astype(jnp.float32)
            in_im = (weight * out_im).astype(jnp.bfloat16).astype(jnp.float32)
        else:
            source = source_ref[0].astype(jnp.float32)
            source_re = source[0]
            source_im = source[1]
            in_re = wave[0]
            in_im = wave[1]
        spread_re, spread_im = propagate_block(in_re, in_im, blocks, chirp_re, -chirp_im)
        passed_ref[0, 0] = (patch_re * spread_re + patch_im * spread_im).astype(jnp.bfloat16)
        passed_ref[0, 1] = (patch_re * spread_im - patch_im * spread_re).astype(jnp.bfloat16)
        if last:
            grad_ref[0, 0] = spread_re.astype(jnp.bfloat16)
            grad_ref[0, 1] = spread_im.astype(jnp.bfloat16)
            return
        term_re = source_re * spread_re + source_im * spread_im
        term_im = source_re * spread_im - source_im * spread_re
        place_term(
            term_re, term_im, rows_ref[index], columns_ref[index], live_ref[index] > 0,
            total_ref, grad_ref if single else None,
        )

        if not single:
            @pl.when(index == pl.num_programs(0) - 1)
            def _():
                grad_ref[...] = total_ref[...].astype(grad_ref.dtype)

    return kernel


def run_adjoint(waves, patches, chirps, blocks, scalars, extra, height, columns_all, last):
    number, _, width, _ = waves.shape
    wave_spec = pl.BlockSpec((1, 2, width, width), lambda i, *s: (i, 0, 0, 0))
    chirp_spec = pl.BlockSpec((2, width, width), lambda i, *s: (0, 0, 0))
    in_specs = [wave_spec, wave_spec, chirp_spec] + [
        pl.BlockSpec((2 * width, width), lambda i, *s: (0, 0)),
        pl.BlockSpec((width, 2 * width), lambda i, *s: (0, 0)),
    ]
    if last:
        slot_spec = pl.BlockSpec((1, width, width), lambda i, r, c, a, s, o: (s[i], 0, 0))
        in_specs += [slot_spec, slot_spec]
    else:
        in_specs += [wave_spec]
    if last:
        second_spec = wave_spec
        second_shape = jax.ShapeDtypeStruct(waves.shape, jnp.bfloat16)
    else:
        second_spec = pl.BlockSpec((2, height, columns_all), lambda i, *s: (0, 0, 0))
        second_shape = jax.ShapeDtypeStruct((2, height, columns_all), jnp.bfloat16)
    grid_spec = pltpu.PrefetchScalarGridSpec(
        num_scalar_prefetch=5,
        grid=(number,),
        in_specs=in_specs,
        out_specs=(wave_spec, second_spec),
        scratch_shapes=[pltpu.VMEM((2, height, columns_all), jnp.float32)],
    )
    return pl.pallas_call(
        adjoint_kernel(last, number == 1),
        grid_spec=grid_spec,
        out_shape=(jax.ShapeDtypeStruct(waves.shape, jnp.bfloat16), second_shape),
    )(*scalars, waves, patches, chirps, *blocks, *extra)


def place_kernel(rows_ref, columns_ref, live_ref, spread_ref, source_ref, grad_ref, total_ref):
    index = pl.program_id(0)

    @pl.when(index == 0)
    def _():
        total_ref[...] = jnp.zeros(total_ref.shape, total_ref.dtype)

    spread = spread_ref[0].astype(jnp.float32)
    source = source_ref[0].astype(jnp.float32)
    term_re = source[0] * spread[0] + source[1] * spread[1]
    term_im = source[0] * spread[1] - source[1] * spread[0]
    place_term(
        term_re, term_im, rows_ref[index], columns_ref[index], live_ref[index] > 0, total_ref
    )

    @pl.when(index == pl.num_programs(0) - 1)
    def _():
        grad_ref[...] = total_ref[...].astype(grad_ref.dtype)


def run_place(spread, source, scalars, height, columns_all):
    number, _, width, _ = spread.shape
    wave_spec = pl.BlockSpec((1, 2, width, width), lambda i, *s: (i, 0, 0, 0))
    grid_spec = pltpu.PrefetchScalarGridSpec(
        num_scalar_prefetch=3,
        grid=(number,),
        in_specs=[wave_spec, wave_spec],
        out_specs=pl.BlockSpec((2, height, columns_all), lambda i, *s: (0, 0, 0)),
        scratch_shapes=[pltpu.VMEM((2, height, columns_all), jnp.float32)],
    )
    return pl.pallas_call(
        place_kernel,
        grid_spec=grid_spec,
        out_shape=jax.ShapeDtypeStruct((2, height, columns_all), jnp.bfloat16),
    )(*scalars[:3], spread, source)


def first_kernel(rows_ref, columns_ref, order_ref, wave_ref, tile_ref, mine_ref, partner_ref,
                 chirp_ref, dft_rows_ref, dft_cols_ref, result_ref):
    index = pl.program_id(0)
    width = wave_ref.shape[2]
    height = tile_ref.shape[2] + mine_ref.shape[2]
    columns_all = tile_ref.shape[3]
    row_shift = (height - rows_ref[index]) % height
    column_shift = (columns_all - columns_ref[index]) % columns_all
    first = order_ref[0] == 0
    patch = []
    for part in range(2):
        mine = mine_ref[0, part].astype(jnp.float32)
        partner = partner_ref[0, part].astype(jnp.float32)
        rim = jnp.concatenate(
            [jnp.where(first, mine, partner), jnp.where(first, partner, mine)], axis=1
        )
        full = jnp.concatenate([tile_ref[0, part], rim], axis=0)
        full = pltpu.roll(full, row_shift, 0)[:width]
        patch.append(pltpu.roll(full, column_shift, 1)[:, :width])
    wave = wave_ref[0].astype(jnp.float32)
    wave_re = patch[0] * wave[0] - patch[1] * wave[1]
    wave_im = patch[0] * wave[1] + patch[1] * wave[0]
    out_re, out_im = propagate_block(
        wave_re, wave_im, (dft_rows_ref, dft_cols_ref), chirp_ref[0], chirp_ref[1]
    )
    result_ref[0, 0] = out_re.astype(jnp.bfloat16)
    result_ref[0, 1] = out_im.astype(jnp.bfloat16)


def run_first(waves, tile, mine, partner, rows, columns, order, chirps, blocks):
    number, _, width, _ = waves.shape
    wave_spec = pl.BlockSpec((1, 2, width, width), lambda i, r, c, o: (i, 0, 0, 0))
    whole = lambda shape: pl.BlockSpec(shape, lambda i, r, c, o: (0,) * len(shape))
    grid_spec = pltpu.PrefetchScalarGridSpec(
        num_scalar_prefetch=3,
        grid=(number,),
        in_specs=[
            wave_spec,
            whole(tile.shape),
            whole(mine.shape),
            whole(partner.shape),
            whole(chirps.shape),
            whole(blocks[0].shape),
            whole(blocks[1].shape),
        ],
        out_specs=wave_spec,
    )
    return pl.pallas_call(
        first_kernel,
        grid_spec=grid_spec,
        out_shape=jax.ShapeDtypeStruct(waves.shape, jnp.bfloat16),
    )(rows, columns, order, waves, tile, mine, partner, chirps, *blocks)


def local(object_field, probe, positions, counts, measured):
    width = probe.shape[1]
    tile_rows = object_field.shape[2]
    columns_all = object_field.shape[3]
    tile_index = lax.axis_index("tile")
    tile_count = lax.axis_size("tile")
    segment = lax.axis_index("depth")
    depth_count = lax.axis_size("depth")
    batch_index = lax.axis_index("batch")
    batch_count = lax.axis_size("batch")
    half = columns_all // batch_count
    wanted = lax.dynamic_slice_in_dim(object_field[:, :, :width, :], batch_index * half, half, 3)
    mine = from_behind(wanted.astype(jnp.bfloat16), "tile", -1)
    pairs = [(b, (b + 1) % batch_count) for b in range(batch_count)]
    partner = lax.ppermute(mine, "batch", pairs)
    capacity = positions.shape[0]
    share = -(-capacity // batch_count)
    first_core = batch_index == 0
    both_positions = lax.ppermute(positions, "batch", pairs)
    both_counts = lax.ppermute(counts, "batch", pairs)
    both_measured = lax.ppermute(measured, "batch", pairs)
    all_positions = jnp.where(
        first_core,
        jnp.concatenate([positions, both_positions]),
        jnp.concatenate([both_positions, positions]),
    )
    all_counts = jnp.where(
        first_core, jnp.concatenate([counts, both_counts]), jnp.concatenate([both_counts, counts])
    )
    entry = batch_index * share + jnp.arange(share, dtype=jnp.int32)
    live = entry < all_counts[0] + all_counts[1]
    later = entry >= all_counts[0]
    slot = jnp.clip(jnp.where(later, entry - all_counts[0], entry), 0, capacity - 1)
    flat = jnp.where(later, capacity, 0) + slot
    chosen = all_positions[flat]
    other = (later == first_core).astype(jnp.int32)
    local_rows = chosen[:, 0] - tile_index * tile_rows
    local_columns = chosen[:, 1]
    order = jnp.reshape(batch_index, (1,)).astype(jnp.int32)
    patches = cut_patches(object_field, mine, partner, local_rows, local_columns, order, width)
    number = patches.shape[0]
    coef = jnp.where(
        segment == depth_count - 1, jnp.float32(DETECTOR_COEF), jnp.float32(SLICE_COEF)
    )
    chirp_re, chirp_im = chirp_parts(width, coef)
    start = jnp.broadcast_to(probe[None], (number, 2, width, width))

    chirps = jnp.stack([chirp_re, chirp_im])
    dft_re, dft_im = dft_parts(width)
    blocks = (
        jnp.concatenate([dft_re, dft_im], axis=0),
        jnp.concatenate([dft_re, dft_im], axis=1),
    )

    def forward_all(waves):
        return run_first(
            waves, object_field, mine, partner, local_rows, local_columns, order, chirps, blocks
        )

    def silent(waves):
        return jnp.zeros_like(waves)

    carry = start
    inputs = start
    for turn in range(depth_count - 1):
        if turn > 0:
            carry = lax.ppermute(carry, "depth", [(turn - 1, turn)])
            inputs = jnp.where(segment == turn, carry, inputs)
        carry = lax.cond(segment == turn, forward_all, silent, carry)

    height = tile_rows + width
    scalars = (local_rows, local_columns, live.astype(jnp.int32), slot, other)

    def last_pass(incoming):
        return run_adjoint(
            incoming, patches, chirps, blocks, scalars, (measured, both_measured),
            height, columns_all, True,
        )

    def last_silent(incoming):
        return (jnp.zeros_like(incoming), jnp.zeros_like(incoming))

    if depth_count > 1:
        carry = lax.ppermute(carry, "depth", [(depth_count - 2, depth_count - 1)])
    arrived_last = carry
    carry, spread_last = lax.cond(segment == depth_count - 1, last_pass, last_silent, carry)
    gradient = run_place(spread_last, arrived_last, scalars, height, columns_all)

    def back_pass(incoming, previous):
        return run_adjoint(
            incoming, patches, chirps, blocks, scalars, (inputs,), height, columns_all, False
        )

    def back_silent(incoming, previous):
        return (jnp.zeros_like(incoming), previous)

    for turn in reversed(range(depth_count - 1)):
        carry = lax.ppermute(carry, "depth", [(turn + 1, turn)])
        carry, gradient = lax.cond(segment == turn, back_pass, back_silent, carry, gradient)

    gradient = gradient.astype(jnp.bfloat16)
    spill = gradient[:, tile_rows:, :]
    keep = lax.dynamic_slice_in_dim(spill, batch_index * half, half, 2)
    give = lax.dynamic_slice_in_dim(spill, (1 - batch_index) * half, half, 2)
    got = lax.ppermute(give, "batch", pairs)
    spill_sum = (keep.astype(jnp.float32) + got.astype(jnp.float32)).astype(jnp.bfloat16)
    arrived = lax.ppermute(spill_sum, "tile", [(t, t + 1) for t in range(tile_count - 1)])
    own = gradient[:, :tile_rows, :]
    other = lax.ppermute(own, "batch", pairs)
    arrived_other = lax.ppermute(arrived, "batch", pairs)
    incoming = jnp.where(
        first_core,
        jnp.concatenate([arrived, arrived_other], axis=2),
        jnp.concatenate([arrived_other, arrived], axis=2),
    )
    summed = own.astype(jnp.float32) + other.astype(jnp.float32)
    summed = summed.at[:, :width, :].add(incoming.astype(jnp.float32))
    return summed[None]


def solution(mesh):
    placed = (
        P(("groups", "depth"), None, "tile", None),
        P("groups", None, None),
        P(("groups", "tile", "batch"), None),
        P(("groups", "tile", "batch")),
        P(("groups", "tile", "batch"), None, None),
    )
    return jax.shard_map(
        local,
        mesh=mesh,
        in_specs=placed,
        out_specs=P(("groups", "depth"), None, "tile", None),
        check_vma=False,
    )
```

```python
import math

import jax
import jax.numpy as jnp
from jax import lax
from jax.sharding import PartitionSpec as P
from jax.experimental import pallas as pl
from jax.experimental.pallas import tpu as pltpu

SLICE_COEF = 0.002
DETECTOR_COEF = 0.006
RESIDUAL_SCALE = 0.125


def from_behind(block, axis, distance):
    devices = range(lax.axis_size(axis))
    route = [(i - distance, i) for i in devices if i - distance in devices]
    return lax.ppermute(block, axis, route)


def dft_block(width, sign):
    freq = jnp.arange(width, dtype=jnp.int32)
    product = freq[:, None] * freq[None, :] % width
    angle = 2.0 * math.pi / width * product.astype(jnp.float32)
    scale = 1.0 / math.sqrt(width)
    real_part = (jnp.cos(angle) * scale).astype(jnp.bfloat16)
    imag_part = (sign * jnp.sin(angle) * scale).astype(jnp.bfloat16)
    upper = jnp.concatenate([real_part, -imag_part], axis=1)
    lower = jnp.concatenate([imag_part, real_part], axis=1)
    return jnp.concatenate([upper, lower], axis=0)


def dft_right(width, sign):
    freq = jnp.arange(width, dtype=jnp.int32)
    product = freq[:, None] * freq[None, :] % width
    angle = 2.0 * math.pi / width * product.astype(jnp.float32)
    scale = 1.0 / math.sqrt(width)
    real_part = (jnp.cos(angle) * scale).astype(jnp.bfloat16)
    imag_part = (sign * jnp.sin(angle) * scale).astype(jnp.bfloat16)
    upper = jnp.concatenate([real_part, imag_part], axis=1)
    lower = jnp.concatenate([-imag_part, real_part], axis=1)
    return jnp.concatenate([upper, lower], axis=0)


def dft_parts(width):
    freq = jnp.arange(width, dtype=jnp.int32)
    product = freq[:, None] * freq[None, :] % width
    angle = 2.0 * math.pi / width * product.astype(jnp.float32)
    scale = 1.0 / math.sqrt(width)
    real_part = (jnp.cos(angle) * scale).astype(jnp.bfloat16)
    imag_part = (-jnp.sin(angle) * scale).astype(jnp.bfloat16)
    return (real_part, imag_part)


def chirp_parts(width, coef):
    freq = jnp.arange(width, dtype=jnp.int32)
    shifted = (freq + width // 2) % width - width // 2
    square = shifted * shifted
    total = (square[:, None] + square[None, :]).astype(jnp.float32)
    phase = -coef * total
    return (jnp.cos(phase), jnp.sin(phase))


def left_apply(block, waves):
    number = waves.shape[0]
    width = waves.shape[2]
    stacked = waves.reshape(number, 2 * width, width)
    result = jnp.einsum("ij,gjk->gik", block, stacked, preferred_element_type=jnp.float32)
    return result.reshape(number, 2, width, width)


def propagate(waves, forward_block, inverse_block, chirp_re, chirp_im):
    first = left_apply(forward_block, waves).astype(jnp.bfloat16)
    spectrum = left_apply(forward_block, jnp.swapaxes(first, -1, -2))
    spec_re = spectrum[:, 0]
    spec_im = spectrum[:, 1]
    filtered = jnp.stack(
        [spec_re * chirp_re - spec_im * chirp_im, spec_re * chirp_im + spec_im * chirp_re], axis=1
    ).astype(jnp.bfloat16)
    back = left_apply(inverse_block, filtered).astype(jnp.bfloat16)
    return left_apply(inverse_block, jnp.swapaxes(back, -1, -2)).astype(jnp.bfloat16)


def transmit(waves, patch):
    values = waves.astype(jnp.float32)
    wave_re = values[:, 0]
    wave_im = values[:, 1]
    return jnp.stack(
        [
            patch[:, 0] * wave_re - patch[:, 1] * wave_im,
            patch[:, 0] * wave_im + patch[:, 1] * wave_re,
        ],
        axis=1,
    ).astype(jnp.bfloat16)


def residual_wave(waves, measured):
    values = waves.astype(jnp.float32)
    intensity = values[:, 0] * values[:, 0] + values[:, 1] * values[:, 1]
    weight = RESIDUAL_SCALE * (intensity - measured)
    return jnp.stack([weight * values[:, 0], weight * values[:, 1]], axis=1).astype(jnp.bfloat16)


def adjoint_terms(incoming, forward_block, inverse_block, chirp_re, chirp_im, inputs, patch):
    spread = propagate(incoming, forward_block, inverse_block, chirp_re, -chirp_im).astype(
        jnp.float32
    )
    source = inputs.astype(jnp.float32)
    term = jnp.stack(
        [
            source[:, 0] * spread[:, 0] + source[:, 1] * spread[:, 1],
            source[:, 0] * spread[:, 1] - source[:, 1] * spread[:, 0],
        ],
        axis=1,
    )
    passed = jnp.stack(
        [
            patch[:, 0] * spread[:, 0] + patch[:, 1] * spread[:, 1],
            patch[:, 0] * spread[:, 1] - patch[:, 1] * spread[:, 0],
        ],
        axis=1,
    ).astype(jnp.bfloat16)
    return (passed, term)


def wave_kernel(transmit_first, residual_after, backward):
    def kernel(*refs):
        refs = list(refs)
        wave_ref = refs.pop(0)
        patch_ref = refs.pop(0)
        chirp_ref = refs.pop(0)
        blocks = refs[:2]
        refs = refs[2:]
        extra_ref = refs.pop(0) if (residual_after or backward) else None
        wave = wave_ref[0].astype(jnp.float32)
        patch_re = patch_ref[0, 0]
        patch_im = patch_ref[0, 1]
        if transmit_first:
            wave_re = patch_re * wave[0] - patch_im * wave[1]
            wave_im = patch_re * wave[1] + patch_im * wave[0]
        else:
            wave_re = wave[0]
            wave_im = wave[1]
        chirp_re = chirp_ref[0]
        chirp_im = chirp_ref[1]
        if backward:
            chirp_im = -chirp_im
        out_re, out_im = propagate_block(wave_re, wave_im, blocks, chirp_re, chirp_im)
        if residual_after:
            measured = extra_ref[0]
            weight = RESIDUAL_SCALE * (out_re * out_re + out_im * out_im - measured)
            result_ref = refs[0]
            result_ref[0, 0] = (weight * out_re).astype(jnp.bfloat16)
            result_ref[0, 1] = (weight * out_im).astype(jnp.bfloat16)
        elif backward:
            source = extra_ref[0].astype(jnp.float32)
            passed_ref, term_ref = refs[0], refs[1]
            passed_ref[0, 0] = (patch_re * out_re + patch_im * out_im).astype(jnp.bfloat16)
            passed_ref[0, 1] = (patch_re * out_im - patch_im * out_re).astype(jnp.bfloat16)
            term_ref[0, 0] = source[0] * out_re + source[1] * out_im
            term_ref[0, 1] = source[0] * out_im - source[1] * out_re
        else:
            result_ref = refs[0]
            result_ref[0, 0] = out_re.astype(jnp.bfloat16)
            result_ref[0, 1] = out_im.astype(jnp.bfloat16)

    return kernel


def run_waves(waves, patches, chirps, blocks, extra=None, transmit_first=True, residual_after=False, backward=False):
    number, _, width, _ = waves.shape
    wave_spec = pl.BlockSpec((1, 2, width, width), lambda i: (i, 0, 0, 0))
    chirp_spec = pl.BlockSpec((2, width, width), lambda i: (0, 0, 0))
    in_specs = [wave_spec, wave_spec, chirp_spec] + [
        pl.BlockSpec((2 * width, width), lambda i: (0, 0)),
        pl.BlockSpec((width, 2 * width), lambda i: (0, 0)),
    ]
    args = [waves, patches, chirps] + list(blocks)
    if residual_after:
        in_specs.append(pl.BlockSpec((1, width, width), lambda i: (i, 0, 0)))
        args.append(extra)
    if backward:
        in_specs.append(wave_spec)
        args.append(extra)
        out_shape = (
            jax.ShapeDtypeStruct(waves.shape, jnp.bfloat16),
            jax.ShapeDtypeStruct(waves.shape, jnp.float32),
        )
        out_specs = (wave_spec, wave_spec)
    else:
        out_shape = jax.ShapeDtypeStruct(waves.shape, jnp.bfloat16)
        out_specs = wave_spec
    return pl.pallas_call(
        wave_kernel(transmit_first, residual_after, backward),
        grid=(number,),
        in_specs=in_specs,
        out_specs=out_specs,
        out_shape=out_shape,
    )(*args)


def scatter_kernel(rows_ref, columns_ref, live_ref, terms_ref, out_ref):
    index = pl.program_id(0)

    @pl.when(index == 0)
    def _():
        out_ref[...] = jnp.zeros(out_ref.shape, out_ref.dtype)

    width = terms_ref.shape[2]
    height = out_ref.shape[1]
    columns_all = out_ref.shape[2]
    row = rows_ref[index]
    column = columns_ref[index]
    alive = live_ref[index] > 0
    for part in range(2):
        term = jnp.where(alive, terms_ref[0, part], 0.0)
        wide = jnp.concatenate(
            [term, jnp.zeros((width, columns_all - width), jnp.float32)], axis=1
        )
        wide = pltpu.roll(wide, column, 1)
        tall = jnp.concatenate(
            [wide, jnp.zeros((height - width, columns_all), jnp.float32)], axis=0
        )
        tall = pltpu.roll(tall, row, 0)
        out_ref[part] = out_ref[part] + tall


def scatter_terms(terms, rows, columns, live, height, columns_all):
    number, _, width, _ = terms.shape
    grid_spec = pltpu.PrefetchScalarGridSpec(
        num_scalar_prefetch=3,
        grid=(number,),
        in_specs=[pl.BlockSpec((1, 2, width, width), lambda i, r, c, a: (i, 0, 0, 0))],
        out_specs=pl.BlockSpec((2, height, columns_all), lambda i, r, c, a: (0, 0, 0)),
    )
    return pl.pallas_call(
        scatter_kernel,
        grid_spec=grid_spec,
        out_shape=jax.ShapeDtypeStruct((2, height, columns_all), jnp.float32),
    )(rows, columns, live.astype(jnp.int32), terms)


def cut_kernel(rows_ref, columns_ref, order_ref, tile_ref, mine_ref, partner_ref, out_ref):
    index = pl.program_id(0)
    width = out_ref.shape[2]
    height = tile_ref.shape[2] + mine_ref.shape[2]
    columns_all = tile_ref.shape[3]
    row_shift = (height - rows_ref[index]) % height
    column_shift = (columns_all - columns_ref[index]) % columns_all
    first = order_ref[0] == 0
    for part in range(2):
        mine = mine_ref[0, part].astype(jnp.float32)
        partner = partner_ref[0, part].astype(jnp.float32)
        rim = jnp.concatenate(
            [jnp.where(first, mine, partner), jnp.where(first, partner, mine)], axis=1
        )
        full = jnp.concatenate([tile_ref[0, part], rim], axis=0)
        full = pltpu.roll(full, row_shift, 0)[:width]
        full = pltpu.roll(full, column_shift, 1)[:, :width]
        out_ref[0, part] = full


def cut_patches(tile, mine, partner, rows, columns, order, width):
    number = rows.shape[0]
    grid_spec = pltpu.PrefetchScalarGridSpec(
        num_scalar_prefetch=3,
        grid=(number,),
        in_specs=[
            pl.BlockSpec(tile.shape, lambda i, r, c, o: (0, 0, 0, 0)),
            pl.BlockSpec(mine.shape, lambda i, r, c, o: (0, 0, 0, 0)),
            pl.BlockSpec(partner.shape, lambda i, r, c, o: (0, 0, 0, 0)),
        ],
        out_specs=pl.BlockSpec((1, 2, width, width), lambda i, r, c, o: (i, 0, 0, 0)),
    )
    return pl.pallas_call(
        cut_kernel,
        grid_spec=grid_spec,
        out_shape=jax.ShapeDtypeStruct((number, 2, width, width), jnp.float32),
    )(rows, columns, order, tile, mine, partner)


def propagate_block(wave_re, wave_im, blocks, chirp_re, chirp_im):
    rows_ref, cols_ref = blocks
    width = wave_re.shape[0]
    dft_rows = rows_ref[...]
    dft_cols = cols_ref[...]

    def left(part_re, part_im):
        lanes = jnp.concatenate([part_re, part_im], axis=1).astype(jnp.bfloat16)
        return jnp.dot(dft_rows, lanes, preferred_element_type=jnp.float32)

    def right(part_re, part_im):
        rows = jnp.concatenate([part_re, part_im], axis=0).astype(jnp.bfloat16)
        return jnp.dot(rows, dft_cols, preferred_element_type=jnp.float32)

    first = left(wave_re, wave_im)
    z_re = (first[:width, :width] - first[width:, width:]).astype(jnp.bfloat16)
    z_im = (first[:width, width:] + first[width:, :width]).astype(jnp.bfloat16)
    second = right(z_re, z_im)
    spec_re = second[:width, :width] - second[width:, width:]
    spec_im = second[:width, width:] + second[width:, :width]
    w_re = spec_re * chirp_re - spec_im * chirp_im
    w_im = spec_re * chirp_im + spec_im * chirp_re
    third = right(w_re.astype(jnp.bfloat16), w_im.astype(jnp.bfloat16))
    v_re = (third[:width, :width] + third[width:, width:]).astype(jnp.bfloat16)
    v_im = (third[width:, :width] - third[:width, width:]).astype(jnp.bfloat16)
    fourth = left(v_re, v_im)
    out_re = (fourth[:width, :width] + fourth[width:, width:]).astype(jnp.bfloat16)
    out_im = (fourth[:width, width:] - fourth[width:, :width]).astype(jnp.bfloat16)
    return (out_re.astype(jnp.float32), out_im.astype(jnp.float32))


def place_term(term_re, term_im, row, column, alive, total_ref, direct_ref=None):
    width = term_re.shape[0]
    height = total_ref.shape[1]
    columns_all = total_ref.shape[2]
    row_shift = row % height
    column_shift = column % columns_all
    for part, term in enumerate((term_re, term_im)):
        term = jnp.where(alive, term, 0.0)
        wide = jnp.concatenate(
            [term, jnp.zeros((width, columns_all - width), jnp.float32)], axis=1
        )
        wide = pltpu.roll(wide, column_shift, 1)
        if height == 2 * width:
            rolled = pltpu.roll(wide, row % width, 0)
            below = lax.broadcasted_iota(jnp.int32, rolled.shape, 0) < row
            upper = jnp.where(below, 0.0, rolled)
            lower = jnp.where(below, rolled, 0.0)
            if direct_ref is None:
                total_ref[part, :width] = total_ref[part, :width] + upper
                total_ref[part, width:] = total_ref[part, width:] + lower
            else:
                direct_ref[part, :width] = upper.astype(direct_ref.dtype)
                direct_ref[part, width:] = lower.astype(direct_ref.dtype)
            continue
        tall = jnp.concatenate(
            [wide, jnp.zeros((height - width, columns_all), jnp.float32)], axis=0
        )
        if direct_ref is None:
            total_ref[part] = total_ref[part] + pltpu.roll(tall, row_shift, 0)
        else:
            direct_ref[part] = pltpu.roll(tall, row_shift, 0).astype(direct_ref.dtype)


def adjoint_kernel(last, single):
    def kernel(rows_ref, columns_ref, live_ref, slot_ref, other_ref, *refs):
        refs = list(refs)
        wave_ref = refs.pop(0)
        patch_ref = refs.pop(0)
        chirp_ref = refs.pop(0)
        blocks = refs[:2]
        refs = refs[2:]
        if last:
            own_ref = refs.pop(0)
            partner_ref = refs.pop(0)
        else:
            source_ref = refs.pop(0)
        passed_ref, grad_ref, total_ref = refs
        index = pl.program_id(0)

        if not single:
            @pl.when(index == 0)
            def _():
                total_ref[...] = jnp.zeros(total_ref.shape, total_ref.dtype)

        wave = wave_ref[0].astype(jnp.float32)
        patch_re = patch_ref[0, 0]
        patch_im = patch_ref[0, 1]
        chirp_re = chirp_ref[0]
        chirp_im = chirp_ref[1]
        if last:
            source_re = wave[0]
            source_im = wave[1]
            lit_re = patch_re * wave[0] - patch_im * wave[1]
            lit_im = patch_re * wave[1] + patch_im * wave[0]
            out_re, out_im = propagate_block(lit_re, lit_im, blocks, chirp_re, chirp_im)
            measured = jnp.where(other_ref[index] > 0, partner_ref[0], own_ref[0])
            weight = RESIDUAL_SCALE * (out_re * out_re + out_im * out_im - measured)
            in_re = (weight * out_re).astype(jnp.bfloat16).astype(jnp.float32)
            in_im = (weight * out_im).astype(jnp.bfloat16).astype(jnp.float32)
        else:
            source = source_ref[0].astype(jnp.float32)
            source_re = source[0]
            source_im = source[1]
            in_re = wave[0]
            in_im = wave[1]
        spread_re, spread_im = propagate_block(in_re, in_im, blocks, chirp_re, -chirp_im)
        passed_ref[0, 0] = (patch_re * spread_re + patch_im * spread_im).astype(jnp.bfloat16)
        passed_ref[0, 1] = (patch_re * spread_im - patch_im * spread_re).astype(jnp.bfloat16)
        term_re = source_re * spread_re + source_im * spread_im
        term_im = source_re * spread_im - source_im * spread_re
        place_term(
            term_re, term_im, rows_ref[index], columns_ref[index], live_ref[index] > 0,
            total_ref, grad_ref if single else None,
        )

        if not single:
            @pl.when(index == pl.num_programs(0) - 1)
            def _():
                grad_ref[...] = total_ref[...].astype(grad_ref.dtype)

    return kernel


def run_adjoint(waves, patches, chirps, blocks, scalars, extra, height, columns_all, last):
    number, _, width, _ = waves.shape
    wave_spec = pl.BlockSpec((1, 2, width, width), lambda i, *s: (i, 0, 0, 0))
    chirp_spec = pl.BlockSpec((2, width, width), lambda i, *s: (0, 0, 0))
    in_specs = [wave_spec, wave_spec, chirp_spec] + [
        pl.BlockSpec((2 * width, width), lambda i, *s: (0, 0)),
        pl.BlockSpec((width, 2 * width), lambda i, *s: (0, 0)),
    ]
    if last:
        slot_spec = pl.BlockSpec((1, width, width), lambda i, r, c, a, s, o: (s[i], 0, 0))
        in_specs += [slot_spec, slot_spec]
    else:
        in_specs += [wave_spec]
    grid_spec = pltpu.PrefetchScalarGridSpec(
        num_scalar_prefetch=5,
        grid=(number,),
        in_specs=in_specs,
        out_specs=(
            wave_spec,
            pl.BlockSpec((2, height, columns_all), lambda i, *s: (0, 0, 0)),
        ),
        scratch_shapes=[pltpu.VMEM((2, height, columns_all), jnp.float32)],
    )
    return pl.pallas_call(
        adjoint_kernel(last, number == 1),
        grid_spec=grid_spec,
        out_shape=(
            jax.ShapeDtypeStruct(waves.shape, jnp.bfloat16),
            jax.ShapeDtypeStruct((2, height, columns_all), jnp.bfloat16),
        ),
    )(*scalars, waves, patches, chirps, *blocks, *extra)


def first_kernel(rows_ref, columns_ref, order_ref, wave_ref, tile_ref, mine_ref, partner_ref,
                 chirp_ref, dft_rows_ref, dft_cols_ref, result_ref):
    index = pl.program_id(0)
    width = wave_ref.shape[2]
    height = tile_ref.shape[2] + mine_ref.shape[2]
    columns_all = tile_ref.shape[3]
    row_shift = (height - rows_ref[index]) % height
    column_shift = (columns_all - columns_ref[index]) % columns_all
    first = order_ref[0] == 0
    patch = []
    for part in range(2):
        mine = mine_ref[0, part].astype(jnp.float32)
        partner = partner_ref[0, part].astype(jnp.float32)
        rim = jnp.concatenate(
            [jnp.where(first, mine, partner), jnp.where(first, partner, mine)], axis=1
        )
        full = jnp.concatenate([tile_ref[0, part], rim], axis=0)
        full = pltpu.roll(full, row_shift, 0)[:width]
        patch.append(pltpu.roll(full, column_shift, 1)[:, :width])
    wave = wave_ref[0].astype(jnp.float32)
    wave_re = patch[0] * wave[0] - patch[1] * wave[1]
    wave_im = patch[0] * wave[1] + patch[1] * wave[0]
    out_re, out_im = propagate_block(
        wave_re, wave_im, (dft_rows_ref, dft_cols_ref), chirp_ref[0], chirp_ref[1]
    )
    result_ref[0, 0] = out_re.astype(jnp.bfloat16)
    result_ref[0, 1] = out_im.astype(jnp.bfloat16)


def run_first(waves, tile, mine, partner, rows, columns, order, chirps, blocks):
    number, _, width, _ = waves.shape
    wave_spec = pl.BlockSpec((1, 2, width, width), lambda i, r, c, o: (i, 0, 0, 0))
    whole = lambda shape: pl.BlockSpec(shape, lambda i, r, c, o: (0,) * len(shape))
    grid_spec = pltpu.PrefetchScalarGridSpec(
        num_scalar_prefetch=3,
        grid=(number,),
        in_specs=[
            wave_spec,
            whole(tile.shape),
            whole(mine.shape),
            whole(partner.shape),
            whole(chirps.shape),
            whole(blocks[0].shape),
            whole(blocks[1].shape),
        ],
        out_specs=wave_spec,
    )
    return pl.pallas_call(
        first_kernel,
        grid_spec=grid_spec,
        out_shape=jax.ShapeDtypeStruct(waves.shape, jnp.bfloat16),
    )(rows, columns, order, waves, tile, mine, partner, chirps, *blocks)


def local(object_field, probe, positions, counts, measured):
    width = probe.shape[1]
    tile_rows = object_field.shape[2]
    columns_all = object_field.shape[3]
    tile_index = lax.axis_index("tile")
    tile_count = lax.axis_size("tile")
    segment = lax.axis_index("depth")
    depth_count = lax.axis_size("depth")
    batch_index = lax.axis_index("batch")
    batch_count = lax.axis_size("batch")
    half = columns_all // batch_count
    wanted = lax.dynamic_slice_in_dim(object_field[:, :, :width, :], batch_index * half, half, 3)
    mine = from_behind(wanted.astype(jnp.bfloat16), "tile", -1)
    pairs = [(b, (b + 1) % batch_count) for b in range(batch_count)]
    partner = lax.ppermute(mine, "batch", pairs)
    capacity = positions.shape[0]
    share = -(-capacity // batch_count)
    first_core = batch_index == 0
    both_positions = lax.ppermute(positions, "batch", pairs)
    both_counts = lax.ppermute(counts, "batch", pairs)
    all_positions = jnp.where(
        first_core,
        jnp.concatenate([positions, both_positions]),
        jnp.concatenate([both_positions, positions]),
    )
    all_counts = jnp.where(
        first_core, jnp.concatenate([counts, both_counts]), jnp.concatenate([both_counts, counts])
    )
    entry = batch_index * share + jnp.arange(share, dtype=jnp.int32)
    live = entry < all_counts[0] + all_counts[1]
    later = entry >= all_counts[0]
    slot = jnp.clip(jnp.where(later, entry - all_counts[0], entry), 0, capacity - 1)
    flat = jnp.where(later, capacity, 0) + slot
    chosen = all_positions[flat]
    other = (later == first_core).astype(jnp.int32)
    local_rows = chosen[:, 0] - tile_index * tile_rows
    local_columns = chosen[:, 1]
    order = jnp.reshape(batch_index, (1,)).astype(jnp.int32)
    patches = cut_patches(object_field, mine, partner, local_rows, local_columns, order, width)
    number = patches.shape[0]
    coef = jnp.where(
        segment == depth_count - 1, jnp.float32(DETECTOR_COEF), jnp.float32(SLICE_COEF)
    )
    chirp_re, chirp_im = chirp_parts(width, coef)
    start = jnp.broadcast_to(probe[None], (number, 2, width, width))

    chirps = jnp.stack([chirp_re, chirp_im])
    dft_re, dft_im = dft_parts(width)
    blocks = (
        jnp.concatenate([dft_re, dft_im], axis=0),
        jnp.concatenate([dft_re, dft_im], axis=1),
    )

    def forward_all(waves):
        return run_first(
            waves, object_field, mine, partner, local_rows, local_columns, order, chirps, blocks
        )

    def silent(waves):
        return jnp.zeros_like(waves)

    carry = start
    inputs = start
    for turn in range(depth_count - 1):
        if turn > 0:
            carry = lax.ppermute(carry, "depth", [(turn - 1, turn)])
            inputs = jnp.where(segment == turn, carry, inputs)
        carry = lax.cond(segment == turn, forward_all, silent, carry)

    measured, carry = lax.optimization_barrier((measured, carry))
    both_measured = lax.ppermute(measured, "batch", pairs)
    height = tile_rows + width
    scalars = (local_rows, local_columns, live.astype(jnp.int32), slot, other)

    def last_pass(incoming):
        return run_adjoint(
            incoming, patches, chirps, blocks, scalars, (measured, both_measured),
            height, columns_all, True,
        )

    def last_silent(incoming):
        return (jnp.zeros_like(incoming), jnp.zeros((2, height, columns_all), jnp.bfloat16))

    if depth_count > 1:
        carry = lax.ppermute(carry, "depth", [(depth_count - 2, depth_count - 1)])
    carry, gradient = lax.cond(segment == depth_count - 1, last_pass, last_silent, carry)

    def back_pass(incoming, previous):
        return run_adjoint(
            incoming, patches, chirps, blocks, scalars, (inputs,), height, columns_all, False
        )

    def back_silent(incoming, previous):
        return (jnp.zeros_like(incoming), previous)

    for turn in reversed(range(depth_count - 1)):
        carry = lax.ppermute(carry, "depth", [(turn + 1, turn)])
        carry, gradient = lax.cond(segment == turn, back_pass, back_silent, carry, gradient)

    gradient = gradient.astype(jnp.bfloat16)
    spill = gradient[:, tile_rows:, :]
    keep = lax.dynamic_slice_in_dim(spill, batch_index * half, half, 2)
    give = lax.dynamic_slice_in_dim(spill, (1 - batch_index) * half, half, 2)
    got = lax.ppermute(give, "batch", pairs)
    spill_sum = (keep.astype(jnp.float32) + got.astype(jnp.float32)).astype(jnp.bfloat16)
    arrived = lax.ppermute(spill_sum, "tile", [(t, t + 1) for t in range(tile_count - 1)])
    own = gradient[:, :tile_rows, :]
    other = lax.ppermute(own, "batch", pairs)
    arrived_other = lax.ppermute(arrived, "batch", pairs)
    incoming = jnp.where(
        first_core,
        jnp.concatenate([arrived, arrived_other], axis=2),
        jnp.concatenate([arrived_other, arrived], axis=2),
    )
    summed = own.astype(jnp.float32) + other.astype(jnp.float32)
    summed = summed.at[:, :width, :].add(incoming.astype(jnp.float32))
    return summed[None]


def solution(mesh):
    placed = (
        P(("groups", "depth"), None, "tile", None),
        P("groups", None, None),
        P(("groups", "tile", "batch"), None),
        P(("groups", "tile", "batch")),
        P(("groups", "tile", "batch"), None, None),
    )
    return jax.shard_map(
        local,
        mesh=mesh,
        in_specs=placed,
        out_specs=P(("groups", "depth"), None, "tile", None),
        check_vma=False,
    )
```

```python
import math

import jax
import jax.numpy as jnp
from jax import lax
from jax.sharding import PartitionSpec as P
from jax.experimental import pallas as pl
from jax.experimental.pallas import tpu as pltpu

SLICE_COEF = 0.002
DETECTOR_COEF = 0.006
RESIDUAL_SCALE = 0.125


def from_behind(block, axis, distance):
    devices = range(lax.axis_size(axis))
    route = [(i - distance, i) for i in devices if i - distance in devices]
    return lax.ppermute(block, axis, route)


def dft_block(width, sign):
    freq = jnp.arange(width, dtype=jnp.int32)
    product = freq[:, None] * freq[None, :] % width
    angle = 2.0 * math.pi / width * product.astype(jnp.float32)
    scale = 1.0 / math.sqrt(width)
    real_part = (jnp.cos(angle) * scale).astype(jnp.bfloat16)
    imag_part = (sign * jnp.sin(angle) * scale).astype(jnp.bfloat16)
    upper = jnp.concatenate([real_part, -imag_part], axis=1)
    lower = jnp.concatenate([imag_part, real_part], axis=1)
    return jnp.concatenate([upper, lower], axis=0)


def dft_right(width, sign):
    freq = jnp.arange(width, dtype=jnp.int32)
    product = freq[:, None] * freq[None, :] % width
    angle = 2.0 * math.pi / width * product.astype(jnp.float32)
    scale = 1.0 / math.sqrt(width)
    real_part = (jnp.cos(angle) * scale).astype(jnp.bfloat16)
    imag_part = (sign * jnp.sin(angle) * scale).astype(jnp.bfloat16)
    upper = jnp.concatenate([real_part, imag_part], axis=1)
    lower = jnp.concatenate([-imag_part, real_part], axis=1)
    return jnp.concatenate([upper, lower], axis=0)


def dft_parts(width):
    freq = jnp.arange(width, dtype=jnp.int32)
    product = freq[:, None] * freq[None, :] % width
    angle = 2.0 * math.pi / width * product.astype(jnp.float32)
    scale = 1.0 / math.sqrt(width)
    real_part = (jnp.cos(angle) * scale).astype(jnp.bfloat16)
    imag_part = (-jnp.sin(angle) * scale).astype(jnp.bfloat16)
    return (real_part, imag_part)


def chirp_parts(width, coef):
    freq = jnp.arange(width, dtype=jnp.int32)
    shifted = (freq + width // 2) % width - width // 2
    square = shifted * shifted
    total = (square[:, None] + square[None, :]).astype(jnp.float32)
    phase = -coef * total
    return (jnp.cos(phase), jnp.sin(phase))


def left_apply(block, waves):
    number = waves.shape[0]
    width = waves.shape[2]
    stacked = waves.reshape(number, 2 * width, width)
    result = jnp.einsum("ij,gjk->gik", block, stacked, preferred_element_type=jnp.float32)
    return result.reshape(number, 2, width, width)


def propagate(waves, forward_block, inverse_block, chirp_re, chirp_im):
    first = left_apply(forward_block, waves).astype(jnp.bfloat16)
    spectrum = left_apply(forward_block, jnp.swapaxes(first, -1, -2))
    spec_re = spectrum[:, 0]
    spec_im = spectrum[:, 1]
    filtered = jnp.stack(
        [spec_re * chirp_re - spec_im * chirp_im, spec_re * chirp_im + spec_im * chirp_re], axis=1
    ).astype(jnp.bfloat16)
    back = left_apply(inverse_block, filtered).astype(jnp.bfloat16)
    return left_apply(inverse_block, jnp.swapaxes(back, -1, -2)).astype(jnp.bfloat16)


def transmit(waves, patch):
    values = waves.astype(jnp.float32)
    wave_re = values[:, 0]
    wave_im = values[:, 1]
    return jnp.stack(
        [
            patch[:, 0] * wave_re - patch[:, 1] * wave_im,
            patch[:, 0] * wave_im + patch[:, 1] * wave_re,
        ],
        axis=1,
    ).astype(jnp.bfloat16)


def residual_wave(waves, measured):
    values = waves.astype(jnp.float32)
    intensity = values[:, 0] * values[:, 0] + values[:, 1] * values[:, 1]
    weight = RESIDUAL_SCALE * (intensity - measured)
    return jnp.stack([weight * values[:, 0], weight * values[:, 1]], axis=1).astype(jnp.bfloat16)


def adjoint_terms(incoming, forward_block, inverse_block, chirp_re, chirp_im, inputs, patch):
    spread = propagate(incoming, forward_block, inverse_block, chirp_re, -chirp_im).astype(
        jnp.float32
    )
    source = inputs.astype(jnp.float32)
    term = jnp.stack(
        [
            source[:, 0] * spread[:, 0] + source[:, 1] * spread[:, 1],
            source[:, 0] * spread[:, 1] - source[:, 1] * spread[:, 0],
        ],
        axis=1,
    )
    passed = jnp.stack(
        [
            patch[:, 0] * spread[:, 0] + patch[:, 1] * spread[:, 1],
            patch[:, 0] * spread[:, 1] - patch[:, 1] * spread[:, 0],
        ],
        axis=1,
    ).astype(jnp.bfloat16)
    return (passed, term)


def wave_kernel(transmit_first, residual_after, backward):
    def kernel(*refs):
        refs = list(refs)
        wave_ref = refs.pop(0)
        patch_ref = refs.pop(0)
        chirp_ref = refs.pop(0)
        blocks = refs[:2]
        refs = refs[2:]
        extra_ref = refs.pop(0) if (residual_after or backward) else None
        wave = wave_ref[0].astype(jnp.float32)
        patch_re = patch_ref[0, 0]
        patch_im = patch_ref[0, 1]
        if transmit_first:
            wave_re = patch_re * wave[0] - patch_im * wave[1]
            wave_im = patch_re * wave[1] + patch_im * wave[0]
        else:
            wave_re = wave[0]
            wave_im = wave[1]
        chirp_re = chirp_ref[0]
        chirp_im = chirp_ref[1]
        if backward:
            chirp_im = -chirp_im
        out_re, out_im = propagate_block(wave_re, wave_im, blocks, chirp_re, chirp_im)
        if residual_after:
            measured = extra_ref[0]
            weight = RESIDUAL_SCALE * (out_re * out_re + out_im * out_im - measured)
            result_ref = refs[0]
            result_ref[0, 0] = (weight * out_re).astype(jnp.bfloat16)
            result_ref[0, 1] = (weight * out_im).astype(jnp.bfloat16)
        elif backward:
            source = extra_ref[0].astype(jnp.float32)
            passed_ref, term_ref = refs[0], refs[1]
            passed_ref[0, 0] = (patch_re * out_re + patch_im * out_im).astype(jnp.bfloat16)
            passed_ref[0, 1] = (patch_re * out_im - patch_im * out_re).astype(jnp.bfloat16)
            term_ref[0, 0] = source[0] * out_re + source[1] * out_im
            term_ref[0, 1] = source[0] * out_im - source[1] * out_re
        else:
            result_ref = refs[0]
            result_ref[0, 0] = out_re.astype(jnp.bfloat16)
            result_ref[0, 1] = out_im.astype(jnp.bfloat16)

    return kernel


def run_waves(waves, patches, chirps, blocks, extra=None, transmit_first=True, residual_after=False, backward=False):
    number, _, width, _ = waves.shape
    wave_spec = pl.BlockSpec((1, 2, width, width), lambda i: (i, 0, 0, 0))
    chirp_spec = pl.BlockSpec((2, width, width), lambda i: (0, 0, 0))
    in_specs = [wave_spec, wave_spec, chirp_spec] + [
        pl.BlockSpec((2 * width, width), lambda i: (0, 0)),
        pl.BlockSpec((width, 2 * width), lambda i: (0, 0)),
    ]
    args = [waves, patches, chirps] + list(blocks)
    if residual_after:
        in_specs.append(pl.BlockSpec((1, width, width), lambda i: (i, 0, 0)))
        args.append(extra)
    if backward:
        in_specs.append(wave_spec)
        args.append(extra)
        out_shape = (
            jax.ShapeDtypeStruct(waves.shape, jnp.bfloat16),
            jax.ShapeDtypeStruct(waves.shape, jnp.float32),
        )
        out_specs = (wave_spec, wave_spec)
    else:
        out_shape = jax.ShapeDtypeStruct(waves.shape, jnp.bfloat16)
        out_specs = wave_spec
    return pl.pallas_call(
        wave_kernel(transmit_first, residual_after, backward),
        grid=(number,),
        in_specs=in_specs,
        out_specs=out_specs,
        out_shape=out_shape,
    )(*args)


def scatter_kernel(rows_ref, columns_ref, live_ref, terms_ref, out_ref):
    index = pl.program_id(0)

    @pl.when(index == 0)
    def _():
        out_ref[...] = jnp.zeros(out_ref.shape, out_ref.dtype)

    width = terms_ref.shape[2]
    height = out_ref.shape[1]
    columns_all = out_ref.shape[2]
    row = rows_ref[index]
    column = columns_ref[index]
    alive = live_ref[index] > 0
    for part in range(2):
        term = jnp.where(alive, terms_ref[0, part], 0.0)
        wide = jnp.concatenate(
            [term, jnp.zeros((width, columns_all - width), jnp.float32)], axis=1
        )
        wide = pltpu.roll(wide, column, 1)
        tall = jnp.concatenate(
            [wide, jnp.zeros((height - width, columns_all), jnp.float32)], axis=0
        )
        tall = pltpu.roll(tall, row, 0)
        out_ref[part] = out_ref[part] + tall


def scatter_terms(terms, rows, columns, live, height, columns_all):
    number, _, width, _ = terms.shape
    grid_spec = pltpu.PrefetchScalarGridSpec(
        num_scalar_prefetch=3,
        grid=(number,),
        in_specs=[pl.BlockSpec((1, 2, width, width), lambda i, r, c, a: (i, 0, 0, 0))],
        out_specs=pl.BlockSpec((2, height, columns_all), lambda i, r, c, a: (0, 0, 0)),
    )
    return pl.pallas_call(
        scatter_kernel,
        grid_spec=grid_spec,
        out_shape=jax.ShapeDtypeStruct((2, height, columns_all), jnp.float32),
    )(rows, columns, live.astype(jnp.int32), terms)


def cut_kernel(rows_ref, columns_ref, order_ref, tile_ref, mine_ref, partner_ref, out_ref):
    index = pl.program_id(0)
    width = out_ref.shape[2]
    height = tile_ref.shape[2] + mine_ref.shape[2]
    columns_all = tile_ref.shape[3]
    row_shift = (height - rows_ref[index]) % height
    column_shift = (columns_all - columns_ref[index]) % columns_all
    first = order_ref[0] == 0
    for part in range(2):
        mine = mine_ref[0, part].astype(jnp.float32)
        partner = partner_ref[0, part].astype(jnp.float32)
        rim = jnp.concatenate(
            [jnp.where(first, mine, partner), jnp.where(first, partner, mine)], axis=1
        )
        full = jnp.concatenate([tile_ref[0, part], rim], axis=0)
        full = pltpu.roll(full, row_shift, 0)[:width]
        full = pltpu.roll(full, column_shift, 1)[:, :width]
        out_ref[0, part] = full


def cut_patches(tile, mine, partner, rows, columns, order, width):
    number = rows.shape[0]
    grid_spec = pltpu.PrefetchScalarGridSpec(
        num_scalar_prefetch=3,
        grid=(number,),
        in_specs=[
            pl.BlockSpec(tile.shape, lambda i, r, c, o: (0, 0, 0, 0)),
            pl.BlockSpec(mine.shape, lambda i, r, c, o: (0, 0, 0, 0)),
            pl.BlockSpec(partner.shape, lambda i, r, c, o: (0, 0, 0, 0)),
        ],
        out_specs=pl.BlockSpec((1, 2, width, width), lambda i, r, c, o: (i, 0, 0, 0)),
    )
    return pl.pallas_call(
        cut_kernel,
        grid_spec=grid_spec,
        out_shape=jax.ShapeDtypeStruct((number, 2, width, width), jnp.float32),
    )(rows, columns, order, tile, mine, partner)


def propagate_block(wave_re, wave_im, blocks, chirp_re, chirp_im):
    rows_ref, cols_ref = blocks
    width = wave_re.shape[0]
    dft_rows = rows_ref[...]
    dft_cols = cols_ref[...]

    def left(part_re, part_im):
        lanes = jnp.concatenate([part_re, part_im], axis=1).astype(jnp.bfloat16)
        return jnp.dot(dft_rows, lanes, preferred_element_type=jnp.float32)

    def right(part_re, part_im):
        rows = jnp.concatenate([part_re, part_im], axis=0).astype(jnp.bfloat16)
        return jnp.dot(rows, dft_cols, preferred_element_type=jnp.float32)

    first = left(wave_re, wave_im)
    z_re = (first[:width, :width] - first[width:, width:]).astype(jnp.bfloat16)
    z_im = (first[:width, width:] + first[width:, :width]).astype(jnp.bfloat16)
    second = right(z_re, z_im)
    spec_re = second[:width, :width] - second[width:, width:]
    spec_im = second[:width, width:] + second[width:, :width]
    w_re = spec_re * chirp_re - spec_im * chirp_im
    w_im = spec_re * chirp_im + spec_im * chirp_re
    third = right(w_re.astype(jnp.bfloat16), w_im.astype(jnp.bfloat16))
    v_re = (third[:width, :width] + third[width:, width:]).astype(jnp.bfloat16)
    v_im = (third[width:, :width] - third[:width, width:]).astype(jnp.bfloat16)
    fourth = left(v_re, v_im)
    out_re = (fourth[:width, :width] + fourth[width:, width:]).astype(jnp.bfloat16)
    out_im = (fourth[:width, width:] - fourth[width:, :width]).astype(jnp.bfloat16)
    return (out_re.astype(jnp.float32), out_im.astype(jnp.float32))


def place_term(term_re, term_im, row, column, alive, total_ref, direct_ref=None):
    width = term_re.shape[0]
    height = total_ref.shape[1]
    columns_all = total_ref.shape[2]
    row_shift = row % height
    column_shift = column % columns_all
    for part, term in enumerate((term_re, term_im)):
        term = jnp.where(alive, term, 0.0)
        wide = jnp.concatenate(
            [term, jnp.zeros((width, columns_all - width), jnp.float32)], axis=1
        )
        wide = pltpu.roll(wide, column_shift, 1)
        if height == 2 * width:
            rolled = pltpu.roll(wide, row % width, 0)
            below = lax.broadcasted_iota(jnp.int32, rolled.shape, 0) < row
            upper = jnp.where(below, 0.0, rolled)
            lower = jnp.where(below, rolled, 0.0)
            if direct_ref is None:
                total_ref[part, :width] = total_ref[part, :width] + upper
                total_ref[part, width:] = total_ref[part, width:] + lower
            else:
                direct_ref[part, :width] = upper.astype(direct_ref.dtype)
                direct_ref[part, width:] = lower.astype(direct_ref.dtype)
            continue
        tall = jnp.concatenate(
            [wide, jnp.zeros((height - width, columns_all), jnp.float32)], axis=0
        )
        if direct_ref is None:
            total_ref[part] = total_ref[part] + pltpu.roll(tall, row_shift, 0)
        else:
            direct_ref[part] = pltpu.roll(tall, row_shift, 0).astype(direct_ref.dtype)


def adjoint_kernel(last, single):
    def kernel(rows_ref, columns_ref, live_ref, slot_ref, other_ref, *refs):
        refs = list(refs)
        wave_ref = refs.pop(0)
        patch_ref = refs.pop(0)
        chirp_ref = refs.pop(0)
        blocks = refs[:2]
        refs = refs[2:]
        if last:
            own_ref = refs.pop(0)
            partner_ref = refs.pop(0)
        else:
            source_ref = refs.pop(0)
        passed_ref, grad_ref, total_ref = refs
        index = pl.program_id(0)

        if not single:
            @pl.when(index == 0)
            def _():
                total_ref[...] = jnp.zeros(total_ref.shape, total_ref.dtype)

        wave = wave_ref[0].astype(jnp.float32)
        patch_re = patch_ref[0, 0]
        patch_im = patch_ref[0, 1]
        chirp_re = chirp_ref[0]
        chirp_im = chirp_ref[1]
        if last:
            source_re = wave[0]
            source_im = wave[1]
            lit_re = patch_re * wave[0] - patch_im * wave[1]
            lit_im = patch_re * wave[1] + patch_im * wave[0]
            out_re, out_im = propagate_block(lit_re, lit_im, blocks, chirp_re, chirp_im)
            measured = jnp.where(other_ref[index] > 0, partner_ref[0], own_ref[0])
            weight = RESIDUAL_SCALE * (out_re * out_re + out_im * out_im - measured)
            in_re = (weight * out_re).astype(jnp.bfloat16).astype(jnp.float32)
            in_im = (weight * out_im).astype(jnp.bfloat16).astype(jnp.float32)
        else:
            source = source_ref[0].astype(jnp.float32)
            source_re = source[0]
            source_im = source[1]
            in_re = wave[0]
            in_im = wave[1]
        spread_re, spread_im = propagate_block(in_re, in_im, blocks, chirp_re, -chirp_im)
        passed_ref[0, 0] = (patch_re * spread_re + patch_im * spread_im).astype(jnp.bfloat16)
        passed_ref[0, 1] = (patch_re * spread_im - patch_im * spread_re).astype(jnp.bfloat16)
        term_re = source_re * spread_re + source_im * spread_im
        term_im = source_re * spread_im - source_im * spread_re
        place_term(
            term_re, term_im, rows_ref[index], columns_ref[index], live_ref[index] > 0,
            total_ref, grad_ref if single else None,
        )

        if not single:
            @pl.when(index == pl.num_programs(0) - 1)
            def _():
                grad_ref[...] = total_ref[...].astype(grad_ref.dtype)

    return kernel


def run_adjoint(waves, patches, chirps, blocks, scalars, extra, height, columns_all, last):
    number, _, width, _ = waves.shape
    wave_spec = pl.BlockSpec((1, 2, width, width), lambda i, *s: (i, 0, 0, 0))
    chirp_spec = pl.BlockSpec((2, width, width), lambda i, *s: (0, 0, 0))
    in_specs = [wave_spec, wave_spec, chirp_spec] + [
        pl.BlockSpec((2 * width, width), lambda i, *s: (0, 0)),
        pl.BlockSpec((width, 2 * width), lambda i, *s: (0, 0)),
    ]
    if last:
        slot_spec = pl.BlockSpec((1, width, width), lambda i, r, c, a, s, o: (s[i], 0, 0))
        in_specs += [slot_spec, slot_spec]
    else:
        in_specs += [wave_spec]
    grid_spec = pltpu.PrefetchScalarGridSpec(
        num_scalar_prefetch=5,
        grid=(number,),
        in_specs=in_specs,
        out_specs=(
            wave_spec,
            pl.BlockSpec((2, height, columns_all), lambda i, *s: (0, 0, 0)),
        ),
        scratch_shapes=[pltpu.VMEM((2, height, columns_all), jnp.float32)],
    )
    return pl.pallas_call(
        adjoint_kernel(last, number == 1),
        grid_spec=grid_spec,
        out_shape=(
            jax.ShapeDtypeStruct(waves.shape, jnp.bfloat16),
            jax.ShapeDtypeStruct((2, height, columns_all), jnp.bfloat16),
        ),
    )(*scalars, waves, patches, chirps, *blocks, *extra)


def tile_cut_kernel(rows_ref, columns_ref, tile_ref, out_ref):
    index = pl.program_id(0)
    width = out_ref.shape[2]
    rows_all = tile_ref.shape[2]
    columns_all = tile_ref.shape[3]
    row_shift = (rows_all - rows_ref[index]) % rows_all
    column_shift = (columns_all - columns_ref[index]) % columns_all
    for part in range(2):
        rolled = pltpu.roll(tile_ref[0, part], row_shift, 0)
        out_ref[0, part] = pltpu.roll(rolled, column_shift, 1)[:, :width]


def cut_tile(tile, rows, columns, width):
    number = rows.shape[0]
    grid_spec = pltpu.PrefetchScalarGridSpec(
        num_scalar_prefetch=2,
        grid=(number,),
        in_specs=[pl.BlockSpec(tile.shape, lambda i, r, c: (0, 0, 0, 0))],
        out_specs=pl.BlockSpec((1, 2, width, width), lambda i, r, c: (i, 0, 0, 0)),
    )
    return pl.pallas_call(
        tile_cut_kernel,
        grid_spec=grid_spec,
        out_shape=jax.ShapeDtypeStruct((number, 2, width, width), jnp.float32),
    )(rows, columns, tile)


def first_kernel(rows_ref, columns_ref, order_ref, wave_ref, top_ref, mine_ref, partner_ref,
                 chirp_ref, dft_rows_ref, dft_cols_ref, result_ref):
    index = pl.program_id(0)
    width = wave_ref.shape[2]
    rim_rows = mine_ref.shape[2]
    columns_all = 2 * mine_ref.shape[3]
    row = rows_ref[index]
    row_shift = (rim_rows - row) % rim_rows
    column_shift = (columns_all - columns_ref[index]) % columns_all
    first = order_ref[0] == 0
    from_tile = lax.broadcasted_iota(jnp.int32, (width, width), 0) < width - row
    patch = []
    for part in range(2):
        mine = mine_ref[0, part].astype(jnp.float32)
        partner = partner_ref[0, part].astype(jnp.float32)
        rim = jnp.concatenate(
            [jnp.where(first, mine, partner), jnp.where(first, partner, mine)], axis=1
        )
        rim = pltpu.roll(pltpu.roll(rim, row_shift, 0), column_shift, 1)[:width, :width]
        patch.append(jnp.where(from_tile, top_ref[0, part], rim))
    wave = wave_ref[0].astype(jnp.float32)
    wave_re = patch[0] * wave[0] - patch[1] * wave[1]
    wave_im = patch[0] * wave[1] + patch[1] * wave[0]
    out_re, out_im = propagate_block(
        wave_re, wave_im, (dft_rows_ref, dft_cols_ref), chirp_ref[0], chirp_ref[1]
    )
    result_ref[0, 0] = out_re.astype(jnp.bfloat16)
    result_ref[0, 1] = out_im.astype(jnp.bfloat16)


def run_first(waves, top, mine, partner, rows, columns, order, chirps, blocks):
    number, _, width, _ = waves.shape
    wave_spec = pl.BlockSpec((1, 2, width, width), lambda i, r, c, o: (i, 0, 0, 0))
    whole = lambda shape: pl.BlockSpec(shape, lambda i, r, c, o: (0,) * len(shape))
    grid_spec = pltpu.PrefetchScalarGridSpec(
        num_scalar_prefetch=3,
        grid=(number,),
        in_specs=[
            wave_spec,
            wave_spec,
            whole(mine.shape),
            whole(partner.shape),
            whole(chirps.shape),
            whole(blocks[0].shape),
            whole(blocks[1].shape),
        ],
        out_specs=wave_spec,
    )
    return pl.pallas_call(
        first_kernel,
        grid_spec=grid_spec,
        out_shape=jax.ShapeDtypeStruct(waves.shape, jnp.bfloat16),
    )(rows, columns, order, waves, top, mine, partner, chirps, *blocks)


def local(object_field, probe, positions, counts, measured):
    width = probe.shape[1]
    tile_rows = object_field.shape[2]
    columns_all = object_field.shape[3]
    tile_index = lax.axis_index("tile")
    tile_count = lax.axis_size("tile")
    segment = lax.axis_index("depth")
    depth_count = lax.axis_size("depth")
    batch_index = lax.axis_index("batch")
    batch_count = lax.axis_size("batch")
    half = columns_all // batch_count
    wanted = lax.dynamic_slice_in_dim(object_field[:, :, :width, :], batch_index * half, half, 3)
    mine = from_behind(wanted.astype(jnp.bfloat16), "tile", -1)
    pairs = [(b, (b + 1) % batch_count) for b in range(batch_count)]
    partner = lax.ppermute(mine, "batch", pairs)
    capacity = positions.shape[0]
    share = -(-capacity // batch_count)
    first_core = batch_index == 0
    both_positions = lax.ppermute(positions, "batch", pairs)
    both_counts = lax.ppermute(counts, "batch", pairs)
    all_positions = jnp.where(
        first_core,
        jnp.concatenate([positions, both_positions]),
        jnp.concatenate([both_positions, positions]),
    )
    all_counts = jnp.where(
        first_core, jnp.concatenate([counts, both_counts]), jnp.concatenate([both_counts, counts])
    )
    entry = batch_index * share + jnp.arange(share, dtype=jnp.int32)
    live = entry < all_counts[0] + all_counts[1]
    later = entry >= all_counts[0]
    slot = jnp.clip(jnp.where(later, entry - all_counts[0], entry), 0, capacity - 1)
    flat = jnp.where(later, capacity, 0) + slot
    chosen = all_positions[flat]
    other = (later == first_core).astype(jnp.int32)
    local_rows = chosen[:, 0] - tile_index * tile_rows
    local_columns = chosen[:, 1]
    order = jnp.reshape(batch_index, (1,)).astype(jnp.int32)
    top = cut_tile(object_field, local_rows, local_columns, width)
    patches = cut_patches(object_field, mine, partner, local_rows, local_columns, order, width)
    number = patches.shape[0]
    coef = jnp.where(
        segment == depth_count - 1, jnp.float32(DETECTOR_COEF), jnp.float32(SLICE_COEF)
    )
    chirp_re, chirp_im = chirp_parts(width, coef)
    start = jnp.broadcast_to(probe[None], (number, 2, width, width))

    chirps = jnp.stack([chirp_re, chirp_im])
    dft_re, dft_im = dft_parts(width)
    blocks = (
        jnp.concatenate([dft_re, dft_im], axis=0),
        jnp.concatenate([dft_re, dft_im], axis=1),
    )

    def forward_all(waves):
        return run_first(
            waves, top, mine, partner, local_rows, local_columns, order, chirps, blocks
        )

    def silent(waves):
        return jnp.zeros_like(waves)

    carry = start
    inputs = start
    for turn in range(depth_count - 1):
        if turn > 0:
            carry = lax.ppermute(carry, "depth", [(turn - 1, turn)])
            inputs = jnp.where(segment == turn, carry, inputs)
        carry = lax.cond(segment == turn, forward_all, silent, carry)

    measured, carry = lax.optimization_barrier((measured, carry))
    both_measured = lax.ppermute(measured, "batch", pairs)
    height = tile_rows + width
    scalars = (local_rows, local_columns, live.astype(jnp.int32), slot, other)

    def last_pass(incoming):
        return run_adjoint(
            incoming, patches, chirps, blocks, scalars, (measured, both_measured),
            height, columns_all, True,
        )

    def last_silent(incoming):
        return (jnp.zeros_like(incoming), jnp.zeros((2, height, columns_all), jnp.bfloat16))

    if depth_count > 1:
        carry = lax.ppermute(carry, "depth", [(depth_count - 2, depth_count - 1)])
    carry, gradient = lax.cond(segment == depth_count - 1, last_pass, last_silent, carry)

    def back_pass(incoming, previous):
        return run_adjoint(
            incoming, patches, chirps, blocks, scalars, (inputs,), height, columns_all, False
        )

    def back_silent(incoming, previous):
        return (jnp.zeros_like(incoming), previous)

    for turn in reversed(range(depth_count - 1)):
        carry = lax.ppermute(carry, "depth", [(turn + 1, turn)])
        carry, gradient = lax.cond(segment == turn, back_pass, back_silent, carry, gradient)

    gradient = gradient.astype(jnp.bfloat16)
    spill = gradient[:, tile_rows:, :]
    keep = lax.dynamic_slice_in_dim(spill, batch_index * half, half, 2)
    give = lax.dynamic_slice_in_dim(spill, (1 - batch_index) * half, half, 2)
    got = lax.ppermute(give, "batch", pairs)
    spill_sum = (keep.astype(jnp.float32) + got.astype(jnp.float32)).astype(jnp.bfloat16)
    arrived = lax.ppermute(spill_sum, "tile", [(t, t + 1) for t in range(tile_count - 1)])
    own = gradient[:, :tile_rows, :]
    other = lax.ppermute(own, "batch", pairs)
    arrived_other = lax.ppermute(arrived, "batch", pairs)
    incoming = jnp.where(
        first_core,
        jnp.concatenate([arrived, arrived_other], axis=2),
        jnp.concatenate([arrived_other, arrived], axis=2),
    )
    summed = own.astype(jnp.float32) + other.astype(jnp.float32)
    summed = summed.at[:, :width, :].add(incoming.astype(jnp.float32))
    return summed[None]


def solution(mesh):
    placed = (
        P(("groups", "depth"), None, "tile", None),
        P("groups", None, None),
        P(("groups", "tile", "batch"), None),
        P(("groups", "tile", "batch")),
        P(("groups", "tile", "batch"), None, None),
    )
    return jax.shard_map(
        local,
        mesh=mesh,
        in_specs=placed,
        out_specs=P(("groups", "depth"), None, "tile", None),
        check_vma=False,
    )
```

```python
import math

import jax
import jax.numpy as jnp
from jax import lax
from jax.sharding import PartitionSpec as P
from jax.experimental import pallas as pl
from jax.experimental.pallas import tpu as pltpu

SLICE_COEF = 0.002
DETECTOR_COEF = 0.006
RESIDUAL_SCALE = 0.125


def from_behind(block, axis, distance):
    devices = range(lax.axis_size(axis))
    route = [(i - distance, i) for i in devices if i - distance in devices]
    return lax.ppermute(block, axis, route)


def dft_block(width, sign):
    freq = jnp.arange(width, dtype=jnp.int32)
    product = freq[:, None] * freq[None, :] % width
    angle = 2.0 * math.pi / width * product.astype(jnp.float32)
    scale = 1.0 / math.sqrt(width)
    real_part = (jnp.cos(angle) * scale).astype(jnp.bfloat16)
    imag_part = (sign * jnp.sin(angle) * scale).astype(jnp.bfloat16)
    upper = jnp.concatenate([real_part, -imag_part], axis=1)
    lower = jnp.concatenate([imag_part, real_part], axis=1)
    return jnp.concatenate([upper, lower], axis=0)


def dft_right(width, sign):
    freq = jnp.arange(width, dtype=jnp.int32)
    product = freq[:, None] * freq[None, :] % width
    angle = 2.0 * math.pi / width * product.astype(jnp.float32)
    scale = 1.0 / math.sqrt(width)
    real_part = (jnp.cos(angle) * scale).astype(jnp.bfloat16)
    imag_part = (sign * jnp.sin(angle) * scale).astype(jnp.bfloat16)
    upper = jnp.concatenate([real_part, imag_part], axis=1)
    lower = jnp.concatenate([-imag_part, real_part], axis=1)
    return jnp.concatenate([upper, lower], axis=0)


def dft_parts(width):
    freq = jnp.arange(width, dtype=jnp.int32)
    product = freq[:, None] * freq[None, :] % width
    angle = 2.0 * math.pi / width * product.astype(jnp.float32)
    scale = 1.0 / math.sqrt(width)
    real_part = (jnp.cos(angle) * scale).astype(jnp.bfloat16)
    imag_part = (-jnp.sin(angle) * scale).astype(jnp.bfloat16)
    return (real_part, imag_part)


def chirp_parts(width, coef):
    freq = jnp.arange(width, dtype=jnp.int32)
    shifted = (freq + width // 2) % width - width // 2
    square = shifted * shifted
    total = (square[:, None] + square[None, :]).astype(jnp.float32)
    phase = -coef * total
    return (jnp.cos(phase), jnp.sin(phase))


def left_apply(block, waves):
    number = waves.shape[0]
    width = waves.shape[2]
    stacked = waves.reshape(number, 2 * width, width)
    result = jnp.einsum("ij,gjk->gik", block, stacked, preferred_element_type=jnp.float32)
    return result.reshape(number, 2, width, width)


def propagate(waves, forward_block, inverse_block, chirp_re, chirp_im):
    first = left_apply(forward_block, waves).astype(jnp.bfloat16)
    spectrum = left_apply(forward_block, jnp.swapaxes(first, -1, -2))
    spec_re = spectrum[:, 0]
    spec_im = spectrum[:, 1]
    filtered = jnp.stack(
        [spec_re * chirp_re - spec_im * chirp_im, spec_re * chirp_im + spec_im * chirp_re], axis=1
    ).astype(jnp.bfloat16)
    back = left_apply(inverse_block, filtered).astype(jnp.bfloat16)
    return left_apply(inverse_block, jnp.swapaxes(back, -1, -2)).astype(jnp.bfloat16)


def transmit(waves, patch):
    values = waves.astype(jnp.float32)
    wave_re = values[:, 0]
    wave_im = values[:, 1]
    return jnp.stack(
        [
            patch[:, 0] * wave_re - patch[:, 1] * wave_im,
            patch[:, 0] * wave_im + patch[:, 1] * wave_re,
        ],
        axis=1,
    ).astype(jnp.bfloat16)


def residual_wave(waves, measured):
    values = waves.astype(jnp.float32)
    intensity = values[:, 0] * values[:, 0] + values[:, 1] * values[:, 1]
    weight = RESIDUAL_SCALE * (intensity - measured)
    return jnp.stack([weight * values[:, 0], weight * values[:, 1]], axis=1).astype(jnp.bfloat16)


def adjoint_terms(incoming, forward_block, inverse_block, chirp_re, chirp_im, inputs, patch):
    spread = propagate(incoming, forward_block, inverse_block, chirp_re, -chirp_im).astype(
        jnp.float32
    )
    source = inputs.astype(jnp.float32)
    term = jnp.stack(
        [
            source[:, 0] * spread[:, 0] + source[:, 1] * spread[:, 1],
            source[:, 0] * spread[:, 1] - source[:, 1] * spread[:, 0],
        ],
        axis=1,
    )
    passed = jnp.stack(
        [
            patch[:, 0] * spread[:, 0] + patch[:, 1] * spread[:, 1],
            patch[:, 0] * spread[:, 1] - patch[:, 1] * spread[:, 0],
        ],
        axis=1,
    ).astype(jnp.bfloat16)
    return (passed, term)


def wave_kernel(transmit_first, residual_after, backward):
    def kernel(*refs):
        refs = list(refs)
        wave_ref = refs.pop(0)
        patch_ref = refs.pop(0)
        chirp_ref = refs.pop(0)
        blocks = refs[:2]
        refs = refs[2:]
        extra_ref = refs.pop(0) if (residual_after or backward) else None
        wave = wave_ref[0].astype(jnp.float32)
        patch_re = patch_ref[0, 0]
        patch_im = patch_ref[0, 1]
        if transmit_first:
            wave_re = patch_re * wave[0] - patch_im * wave[1]
            wave_im = patch_re * wave[1] + patch_im * wave[0]
        else:
            wave_re = wave[0]
            wave_im = wave[1]
        chirp_re = chirp_ref[0]
        chirp_im = chirp_ref[1]
        if backward:
            chirp_im = -chirp_im
        out_re, out_im = propagate_block(wave_re, wave_im, blocks, chirp_re, chirp_im)
        if residual_after:
            measured = extra_ref[0]
            weight = RESIDUAL_SCALE * (out_re * out_re + out_im * out_im - measured)
            result_ref = refs[0]
            result_ref[0, 0] = (weight * out_re).astype(jnp.bfloat16)
            result_ref[0, 1] = (weight * out_im).astype(jnp.bfloat16)
        elif backward:
            source = extra_ref[0].astype(jnp.float32)
            passed_ref, term_ref = refs[0], refs[1]
            passed_ref[0, 0] = (patch_re * out_re + patch_im * out_im).astype(jnp.bfloat16)
            passed_ref[0, 1] = (patch_re * out_im - patch_im * out_re).astype(jnp.bfloat16)
            term_ref[0, 0] = source[0] * out_re + source[1] * out_im
            term_ref[0, 1] = source[0] * out_im - source[1] * out_re
        else:
            result_ref = refs[0]
            result_ref[0, 0] = out_re.astype(jnp.bfloat16)
            result_ref[0, 1] = out_im.astype(jnp.bfloat16)

    return kernel


def run_waves(waves, patches, chirps, blocks, extra=None, transmit_first=True, residual_after=False, backward=False):
    number, _, width, _ = waves.shape
    wave_spec = pl.BlockSpec((1, 2, width, width), lambda i: (i, 0, 0, 0))
    chirp_spec = pl.BlockSpec((2, width, width), lambda i: (0, 0, 0))
    in_specs = [wave_spec, wave_spec, chirp_spec] + [
        pl.BlockSpec((2 * width, width), lambda i: (0, 0)),
        pl.BlockSpec((width, 2 * width), lambda i: (0, 0)),
    ]
    args = [waves, patches, chirps] + list(blocks)
    if residual_after:
        in_specs.append(pl.BlockSpec((1, width, width), lambda i: (i, 0, 0)))
        args.append(extra)
    if backward:
        in_specs.append(wave_spec)
        args.append(extra)
        out_shape = (
            jax.ShapeDtypeStruct(waves.shape, jnp.bfloat16),
            jax.ShapeDtypeStruct(waves.shape, jnp.float32),
        )
        out_specs = (wave_spec, wave_spec)
    else:
        out_shape = jax.ShapeDtypeStruct(waves.shape, jnp.bfloat16)
        out_specs = wave_spec
    return pl.pallas_call(
        wave_kernel(transmit_first, residual_after, backward),
        grid=(number,),
        in_specs=in_specs,
        out_specs=out_specs,
        out_shape=out_shape,
    )(*args)


def scatter_kernel(rows_ref, columns_ref, live_ref, terms_ref, out_ref):
    index = pl.program_id(0)

    @pl.when(index == 0)
    def _():
        out_ref[...] = jnp.zeros(out_ref.shape, out_ref.dtype)

    width = terms_ref.shape[2]
    height = out_ref.shape[1]
    columns_all = out_ref.shape[2]
    row = rows_ref[index]
    column = columns_ref[index]
    alive = live_ref[index] > 0
    for part in range(2):
        term = jnp.where(alive, terms_ref[0, part], 0.0)
        wide = jnp.concatenate(
            [term, jnp.zeros((width, columns_all - width), jnp.float32)], axis=1
        )
        wide = pltpu.roll(wide, column, 1)
        tall = jnp.concatenate(
            [wide, jnp.zeros((height - width, columns_all), jnp.float32)], axis=0
        )
        tall = pltpu.roll(tall, row, 0)
        out_ref[part] = out_ref[part] + tall


def scatter_terms(terms, rows, columns, live, height, columns_all):
    number, _, width, _ = terms.shape
    grid_spec = pltpu.PrefetchScalarGridSpec(
        num_scalar_prefetch=3,
        grid=(number,),
        in_specs=[pl.BlockSpec((1, 2, width, width), lambda i, r, c, a: (i, 0, 0, 0))],
        out_specs=pl.BlockSpec((2, height, columns_all), lambda i, r, c, a: (0, 0, 0)),
    )
    return pl.pallas_call(
        scatter_kernel,
        grid_spec=grid_spec,
        out_shape=jax.ShapeDtypeStruct((2, height, columns_all), jnp.float32),
    )(rows, columns, live.astype(jnp.int32), terms)


def cut_kernel(rows_ref, columns_ref, order_ref, tile_ref, mine_ref, partner_ref, out_ref):
    index = pl.program_id(0)
    width = out_ref.shape[2]
    height = tile_ref.shape[2] + mine_ref.shape[2]
    columns_all = tile_ref.shape[3]
    row_shift = (height - rows_ref[index]) % height
    column_shift = (columns_all - columns_ref[index]) % columns_all
    first = order_ref[0] == 0
    for part in range(2):
        mine = mine_ref[0, part].astype(jnp.float32)
        partner = partner_ref[0, part].astype(jnp.float32)
        rim = jnp.concatenate(
            [jnp.where(first, mine, partner), jnp.where(first, partner, mine)], axis=1
        )
        full = jnp.concatenate([tile_ref[0, part], rim], axis=0)
        full = pltpu.roll(full, row_shift, 0)[:width]
        full = pltpu.roll(full, column_shift, 1)[:, :width]
        out_ref[0, part] = full


def cut_patches(tile, mine, partner, rows, columns, order, width):
    number = rows.shape[0]
    grid_spec = pltpu.PrefetchScalarGridSpec(
        num_scalar_prefetch=3,
        grid=(number,),
        in_specs=[
            pl.BlockSpec(tile.shape, lambda i, r, c, o: (0, 0, 0, 0)),
            pl.BlockSpec(mine.shape, lambda i, r, c, o: (0, 0, 0, 0)),
            pl.BlockSpec(partner.shape, lambda i, r, c, o: (0, 0, 0, 0)),
        ],
        out_specs=pl.BlockSpec((1, 2, width, width), lambda i, r, c, o: (i, 0, 0, 0)),
    )
    return pl.pallas_call(
        cut_kernel,
        grid_spec=grid_spec,
        out_shape=jax.ShapeDtypeStruct((number, 2, width, width), jnp.float32),
    )(rows, columns, order, tile, mine, partner)


def propagate_block(wave_re, wave_im, blocks, chirp_re, chirp_im):
    rows_ref, cols_ref = blocks
    width = wave_re.shape[0]
    dft_rows = rows_ref[...]
    dft_cols = cols_ref[...]

    def left(part_re, part_im):
        lanes = jnp.concatenate([part_re, part_im], axis=1).astype(jnp.bfloat16)
        return jnp.dot(dft_rows, lanes, preferred_element_type=jnp.float32)

    def right(part_re, part_im):
        rows = jnp.concatenate([part_re, part_im], axis=0).astype(jnp.bfloat16)
        return jnp.dot(rows, dft_cols, preferred_element_type=jnp.float32)

    first = left(wave_re, wave_im)
    z_re = (first[:width, :width] - first[width:, width:]).astype(jnp.bfloat16)
    z_im = (first[:width, width:] + first[width:, :width]).astype(jnp.bfloat16)
    second = right(z_re, z_im)
    spec_re = second[:width, :width] - second[width:, width:]
    spec_im = second[:width, width:] + second[width:, :width]
    w_re = spec_re * chirp_re - spec_im * chirp_im
    w_im = spec_re * chirp_im + spec_im * chirp_re
    third = right(w_re.astype(jnp.bfloat16), w_im.astype(jnp.bfloat16))
    v_re = (third[:width, :width] + third[width:, width:]).astype(jnp.bfloat16)
    v_im = (third[width:, :width] - third[:width, width:]).astype(jnp.bfloat16)
    fourth = left(v_re, v_im)
    out_re = (fourth[:width, :width] + fourth[width:, width:]).astype(jnp.bfloat16)
    out_im = (fourth[:width, width:] - fourth[width:, :width]).astype(jnp.bfloat16)
    return (out_re.astype(jnp.float32), out_im.astype(jnp.float32))


def place_term(term_re, term_im, row, column, alive, total_ref, direct_ref=None):
    width = term_re.shape[0]
    height = total_ref.shape[1]
    columns_all = total_ref.shape[2]
    row_shift = row % height
    column_shift = column % columns_all
    for part, term in enumerate((term_re, term_im)):
        term = jnp.where(alive, term, 0.0)
        wide = jnp.concatenate(
            [term, jnp.zeros((width, columns_all - width), jnp.float32)], axis=1
        )
        wide = pltpu.roll(wide, column_shift, 1)
        if height == 2 * width:
            rolled = pltpu.roll(wide, row % width, 0)
            below = lax.broadcasted_iota(jnp.int32, rolled.shape, 0) < row
            upper = jnp.where(below, 0.0, rolled)
            lower = jnp.where(below, rolled, 0.0)
            if direct_ref is None:
                total_ref[part, :width] = total_ref[part, :width] + upper
                total_ref[part, width:] = total_ref[part, width:] + lower
            else:
                direct_ref[part, :width] = upper.astype(direct_ref.dtype)
                direct_ref[part, width:] = lower.astype(direct_ref.dtype)
            continue
        tall = jnp.concatenate(
            [wide, jnp.zeros((height - width, columns_all), jnp.float32)], axis=0
        )
        if direct_ref is None:
            total_ref[part] = total_ref[part] + pltpu.roll(tall, row_shift, 0)
        else:
            direct_ref[part] = pltpu.roll(tall, row_shift, 0).astype(direct_ref.dtype)


def adjoint_kernel(last, single):
    def kernel(rows_ref, columns_ref, live_ref, slot_ref, other_ref, *refs):
        refs = list(refs)
        wave_ref = refs.pop(0)
        patch_ref = refs.pop(0)
        chirp_ref = refs.pop(0)
        blocks = refs[:2]
        refs = refs[2:]
        if last:
            own_ref = refs.pop(0)
            partner_ref = refs.pop(0)
        else:
            source_ref = refs.pop(0)
        passed_ref, grad_ref, total_ref = refs
        index = pl.program_id(0)

        if not single:
            @pl.when(index == 0)
            def _():
                total_ref[...] = jnp.zeros(total_ref.shape, total_ref.dtype)

        wave = wave_ref[0].astype(jnp.float32)
        patch_re = patch_ref[0, 0]
        patch_im = patch_ref[0, 1]
        chirp_re = chirp_ref[0]
        chirp_im = chirp_ref[1]
        if last:
            source_re = wave[0]
            source_im = wave[1]
            lit_re = patch_re * wave[0] - patch_im * wave[1]
            lit_im = patch_re * wave[1] + patch_im * wave[0]
            out_re, out_im = propagate_block(lit_re, lit_im, blocks, chirp_re, chirp_im)
            measured = jnp.where(other_ref[index] > 0, partner_ref[0], own_ref[0])
            weight = RESIDUAL_SCALE * (out_re * out_re + out_im * out_im - measured)
            in_re = (weight * out_re).astype(jnp.bfloat16).astype(jnp.float32)
            in_im = (weight * out_im).astype(jnp.bfloat16).astype(jnp.float32)
        else:
            source = source_ref[0].astype(jnp.float32)
            source_re = source[0]
            source_im = source[1]
            in_re = wave[0]
            in_im = wave[1]
        spread_re, spread_im = propagate_block(in_re, in_im, blocks, chirp_re, -chirp_im)
        passed_ref[0, 0] = (patch_re * spread_re + patch_im * spread_im).astype(jnp.bfloat16)
        passed_ref[0, 1] = (patch_re * spread_im - patch_im * spread_re).astype(jnp.bfloat16)
        term_re = source_re * spread_re + source_im * spread_im
        term_im = source_re * spread_im - source_im * spread_re
        place_term(
            term_re, term_im, rows_ref[index], columns_ref[index], live_ref[index] > 0,
            total_ref, grad_ref if single else None,
        )

        if not single:
            @pl.when(index == pl.num_programs(0) - 1)
            def _():
                grad_ref[...] = total_ref[...].astype(grad_ref.dtype)

    return kernel


def run_adjoint(waves, patches, chirps, blocks, scalars, extra, height, columns_all, last):
    number, _, width, _ = waves.shape
    wave_spec = pl.BlockSpec((1, 2, width, width), lambda i, *s: (i, 0, 0, 0))
    chirp_spec = pl.BlockSpec((2, width, width), lambda i, *s: (0, 0, 0))
    in_specs = [wave_spec, wave_spec, chirp_spec] + [
        pl.BlockSpec((2 * width, width), lambda i, *s: (0, 0)),
        pl.BlockSpec((width, 2 * width), lambda i, *s: (0, 0)),
    ]
    if last:
        slot_spec = pl.BlockSpec((1, width, width), lambda i, r, c, a, s, o: (s[i], 0, 0))
        in_specs += [slot_spec, slot_spec]
    else:
        in_specs += [wave_spec]
    grid_spec = pltpu.PrefetchScalarGridSpec(
        num_scalar_prefetch=5,
        grid=(number,),
        in_specs=in_specs,
        out_specs=(
            wave_spec,
            pl.BlockSpec((2, height, columns_all), lambda i, *s: (0, 0, 0)),
        ),
        scratch_shapes=[pltpu.VMEM((2, height, columns_all), jnp.float32)],
    )
    return pl.pallas_call(
        adjoint_kernel(last, number == 1),
        grid_spec=grid_spec,
        out_shape=(
            jax.ShapeDtypeStruct(waves.shape, jnp.bfloat16),
            jax.ShapeDtypeStruct((2, height, columns_all), jnp.bfloat16),
        ),
    )(*scalars, waves, patches, chirps, *blocks, *extra)


def first_kernel(rows_ref, columns_ref, order_ref, wave_ref, tile_ref, mine_ref, partner_ref,
                 chirp_ref, dft_rows_ref, dft_cols_ref, result_ref):
    index = pl.program_id(0)
    width = wave_ref.shape[2]
    height = tile_ref.shape[2] + mine_ref.shape[2]
    columns_all = tile_ref.shape[3]
    row_shift = (height - rows_ref[index]) % height
    column_shift = (columns_all - columns_ref[index]) % columns_all
    first = order_ref[0] == 0
    patch = []
    for part in range(2):
        mine = mine_ref[0, part].astype(jnp.float32)
        partner = partner_ref[0, part].astype(jnp.float32)
        rim = jnp.concatenate(
            [jnp.where(first, mine, partner), jnp.where(first, partner, mine)], axis=1
        )
        full = jnp.concatenate([tile_ref[0, part], rim], axis=0)
        full = pltpu.roll(full, row_shift, 0)[:width]
        patch.append(pltpu.roll(full, column_shift, 1)[:, :width])
    wave = wave_ref[0].astype(jnp.float32)
    wave_re = patch[0] * wave[0] - patch[1] * wave[1]
    wave_im = patch[0] * wave[1] + patch[1] * wave[0]
    out_re, out_im = propagate_block(
        wave_re, wave_im, (dft_rows_ref, dft_cols_ref), chirp_ref[0], chirp_ref[1]
    )
    result_ref[0, 0] = out_re.astype(jnp.bfloat16)
    result_ref[0, 1] = out_im.astype(jnp.bfloat16)


def run_first(waves, tile, mine, partner, rows, columns, order, chirps, blocks):
    number, _, width, _ = waves.shape
    wave_spec = pl.BlockSpec((1, 2, width, width), lambda i, r, c, o: (i, 0, 0, 0))
    whole = lambda shape: pl.BlockSpec(shape, lambda i, r, c, o: (0,) * len(shape))
    grid_spec = pltpu.PrefetchScalarGridSpec(
        num_scalar_prefetch=3,
        grid=(number,),
        in_specs=[
            wave_spec,
            whole(tile.shape),
            whole(mine.shape),
            whole(partner.shape),
            whole(chirps.shape),
            whole(blocks[0].shape),
            whole(blocks[1].shape),
        ],
        out_specs=wave_spec,
    )
    return pl.pallas_call(
        first_kernel,
        grid_spec=grid_spec,
        out_shape=jax.ShapeDtypeStruct(waves.shape, jnp.bfloat16),
    )(rows, columns, order, waves, tile, mine, partner, chirps, *blocks)


def local(object_field, probe, positions, counts, measured):
    width = probe.shape[1]
    tile_rows = object_field.shape[2]
    columns_all = object_field.shape[3]
    tile_index = lax.axis_index("tile")
    tile_count = lax.axis_size("tile")
    segment = lax.axis_index("depth")
    depth_count = lax.axis_size("depth")
    batch_index = lax.axis_index("batch")
    batch_count = lax.axis_size("batch")
    half = columns_all // batch_count
    wanted = lax.dynamic_slice_in_dim(object_field[:, :, :width, :], batch_index * half, half, 3)
    mine = from_behind(wanted.astype(jnp.bfloat16), "tile", -1)
    pairs = [(b, (b + 1) % batch_count) for b in range(batch_count)]
    partner = lax.ppermute(mine, "batch", pairs)
    capacity = positions.shape[0]
    share = -(-capacity // batch_count)
    first_core = batch_index == 0
    both_positions = lax.ppermute(positions, "batch", pairs)
    both_counts = lax.ppermute(counts, "batch", pairs)
    all_positions = jnp.where(
        first_core,
        jnp.concatenate([positions, both_positions]),
        jnp.concatenate([both_positions, positions]),
    )
    all_counts = jnp.where(
        first_core, jnp.concatenate([counts, both_counts]), jnp.concatenate([both_counts, counts])
    )
    entry = batch_index * share + jnp.arange(share, dtype=jnp.int32)
    live = entry < all_counts[0] + all_counts[1]
    later = entry >= all_counts[0]
    slot = jnp.clip(jnp.where(later, entry - all_counts[0], entry), 0, capacity - 1)
    flat = jnp.where(later, capacity, 0) + slot
    chosen = all_positions[flat]
    other = (later == first_core).astype(jnp.int32)
    local_rows = chosen[:, 0] - tile_index * tile_rows
    local_columns = chosen[:, 1]
    order = jnp.reshape(batch_index, (1,)).astype(jnp.int32)
    patches = cut_patches(object_field, mine, partner, local_rows, local_columns, order, width)
    number = patches.shape[0]
    coef = jnp.where(
        segment == depth_count - 1, jnp.float32(DETECTOR_COEF), jnp.float32(SLICE_COEF)
    )
    chirp_re, chirp_im = chirp_parts(width, coef)
    start = jnp.broadcast_to(probe[None], (number, 2, width, width))

    chirps = jnp.stack([chirp_re, chirp_im])
    dft_re, dft_im = dft_parts(width)
    blocks = (
        jnp.concatenate([dft_re, dft_im], axis=0),
        jnp.concatenate([dft_re, dft_im], axis=1),
    )

    def forward_all(waves):
        return run_first(
            waves, object_field, mine, partner, local_rows, local_columns, order, chirps, blocks
        )

    def silent(waves):
        return jnp.zeros_like(waves)

    carry = start
    inputs = start
    for turn in range(depth_count - 1):
        if turn > 0:
            carry = lax.ppermute(carry, "depth", [(turn - 1, turn)])
            inputs = jnp.where(segment == turn, carry, inputs)
        carry = forward_all(carry)

    measured, carry = lax.optimization_barrier((measured, carry))
    both_measured = lax.ppermute(measured, "batch", pairs)
    height = tile_rows + width
    scalars = (local_rows, local_columns, live.astype(jnp.int32), slot, other)

    def last_pass(incoming):
        return run_adjoint(
            incoming, patches, chirps, blocks, scalars, (measured, both_measured),
            height, columns_all, True,
        )

    def last_silent(incoming):
        return (jnp.zeros_like(incoming), jnp.zeros((2, height, columns_all), jnp.bfloat16))

    if depth_count > 1:
        carry = lax.ppermute(carry, "depth", [(depth_count - 2, depth_count - 1)])
    carry, gradient = last_pass(carry)

    def back_pass(incoming, previous):
        return run_adjoint(
            incoming, patches, chirps, blocks, scalars, (inputs,), height, columns_all, False
        )

    def back_silent(incoming, previous):
        return (jnp.zeros_like(incoming), previous)

    for turn in reversed(range(depth_count - 1)):
        carry = lax.ppermute(carry, "depth", [(turn + 1, turn)])
        carry, gradient = lax.cond(segment == turn, back_pass, back_silent, carry, gradient)

    gradient = gradient.astype(jnp.bfloat16)
    spill = gradient[:, tile_rows:, :]
    keep = lax.dynamic_slice_in_dim(spill, batch_index * half, half, 2)
    give = lax.dynamic_slice_in_dim(spill, (1 - batch_index) * half, half, 2)
    got = lax.ppermute(give, "batch", pairs)
    spill_sum = (keep.astype(jnp.float32) + got.astype(jnp.float32)).astype(jnp.bfloat16)
    arrived = lax.ppermute(spill_sum, "tile", [(t, t + 1) for t in range(tile_count - 1)])
    own = gradient[:, :tile_rows, :]
    other = lax.ppermute(own, "batch", pairs)
    arrived_other = lax.ppermute(arrived, "batch", pairs)
    incoming = jnp.where(
        first_core,
        jnp.concatenate([arrived, arrived_other], axis=2),
        jnp.concatenate([arrived_other, arrived], axis=2),
    )
    summed = own.astype(jnp.float32) + other.astype(jnp.float32)
    summed = summed.at[:, :width, :].add(incoming.astype(jnp.float32))
    return summed[None]


def solution(mesh):
    placed = (
        P(("groups", "depth"), None, "tile", None),
        P("groups", None, None),
        P(("groups", "tile", "batch"), None),
        P(("groups", "tile", "batch")),
        P(("groups", "tile", "batch"), None, None),
    )
    return jax.shard_map(
        local,
        mesh=mesh,
        in_specs=placed,
        out_specs=P(("groups", "depth"), None, "tile", None),
        check_vma=False,
    )
```

```python
import math

import jax
import jax.numpy as jnp
from jax import lax
from jax.sharding import PartitionSpec as P
from jax.experimental import pallas as pl
from jax.experimental.pallas import tpu as pltpu

SLICE_COEF = 0.002
DETECTOR_COEF = 0.006
RESIDUAL_SCALE = 0.125


def from_behind(block, axis, distance):
    devices = range(lax.axis_size(axis))
    route = [(i - distance, i) for i in devices if i - distance in devices]
    return lax.ppermute(block, axis, route)


def dft_block(width, sign):
    freq = jnp.arange(width, dtype=jnp.int32)
    product = freq[:, None] * freq[None, :] % width
    angle = 2.0 * math.pi / width * product.astype(jnp.float32)
    scale = 1.0 / math.sqrt(width)
    real_part = (jnp.cos(angle) * scale).astype(jnp.bfloat16)
    imag_part = (sign * jnp.sin(angle) * scale).astype(jnp.bfloat16)
    upper = jnp.concatenate([real_part, -imag_part], axis=1)
    lower = jnp.concatenate([imag_part, real_part], axis=1)
    return jnp.concatenate([upper, lower], axis=0)


def dft_right(width, sign):
    freq = jnp.arange(width, dtype=jnp.int32)
    product = freq[:, None] * freq[None, :] % width
    angle = 2.0 * math.pi / width * product.astype(jnp.float32)
    scale = 1.0 / math.sqrt(width)
    real_part = (jnp.cos(angle) * scale).astype(jnp.bfloat16)
    imag_part = (sign * jnp.sin(angle) * scale).astype(jnp.bfloat16)
    upper = jnp.concatenate([real_part, imag_part], axis=1)
    lower = jnp.concatenate([-imag_part, real_part], axis=1)
    return jnp.concatenate([upper, lower], axis=0)


def dft_parts(width):
    freq = jnp.arange(width, dtype=jnp.int32)
    product = freq[:, None] * freq[None, :] % width
    angle = 2.0 * math.pi / width * product.astype(jnp.float32)
    scale = 1.0 / math.sqrt(width)
    real_part = (jnp.cos(angle) * scale).astype(jnp.bfloat16)
    imag_part = (-jnp.sin(angle) * scale).astype(jnp.bfloat16)
    return (real_part, imag_part)


def chirp_parts(width, coef):
    freq = jnp.arange(width, dtype=jnp.int32)
    shifted = (freq + width // 2) % width - width // 2
    square = shifted * shifted
    total = (square[:, None] + square[None, :]).astype(jnp.float32)
    phase = -coef * total
    return (jnp.cos(phase), jnp.sin(phase))


def left_apply(block, waves):
    number = waves.shape[0]
    width = waves.shape[2]
    stacked = waves.reshape(number, 2 * width, width)
    result = jnp.einsum("ij,gjk->gik", block, stacked, preferred_element_type=jnp.float32)
    return result.reshape(number, 2, width, width)


def propagate(waves, forward_block, inverse_block, chirp_re, chirp_im):
    first = left_apply(forward_block, waves).astype(jnp.bfloat16)
    spectrum = left_apply(forward_block, jnp.swapaxes(first, -1, -2))
    spec_re = spectrum[:, 0]
    spec_im = spectrum[:, 1]
    filtered = jnp.stack(
        [spec_re * chirp_re - spec_im * chirp_im, spec_re * chirp_im + spec_im * chirp_re], axis=1
    ).astype(jnp.bfloat16)
    back = left_apply(inverse_block, filtered).astype(jnp.bfloat16)
    return left_apply(inverse_block, jnp.swapaxes(back, -1, -2)).astype(jnp.bfloat16)


def transmit(waves, patch):
    values = waves.astype(jnp.float32)
    wave_re = values[:, 0]
    wave_im = values[:, 1]
    return jnp.stack(
        [
            patch[:, 0] * wave_re - patch[:, 1] * wave_im,
            patch[:, 0] * wave_im + patch[:, 1] * wave_re,
        ],
        axis=1,
    ).astype(jnp.bfloat16)


def residual_wave(waves, measured):
    values = waves.astype(jnp.float32)
    intensity = values[:, 0] * values[:, 0] + values[:, 1] * values[:, 1]
    weight = RESIDUAL_SCALE * (intensity - measured)
    return jnp.stack([weight * values[:, 0], weight * values[:, 1]], axis=1).astype(jnp.bfloat16)


def adjoint_terms(incoming, forward_block, inverse_block, chirp_re, chirp_im, inputs, patch):
    spread = propagate(incoming, forward_block, inverse_block, chirp_re, -chirp_im).astype(
        jnp.float32
    )
    source = inputs.astype(jnp.float32)
    term = jnp.stack(
        [
            source[:, 0] * spread[:, 0] + source[:, 1] * spread[:, 1],
            source[:, 0] * spread[:, 1] - source[:, 1] * spread[:, 0],
        ],
        axis=1,
    )
    passed = jnp.stack(
        [
            patch[:, 0] * spread[:, 0] + patch[:, 1] * spread[:, 1],
            patch[:, 0] * spread[:, 1] - patch[:, 1] * spread[:, 0],
        ],
        axis=1,
    ).astype(jnp.bfloat16)
    return (passed, term)


def wave_kernel(transmit_first, residual_after, backward):
    def kernel(*refs):
        refs = list(refs)
        wave_ref = refs.pop(0)
        patch_ref = refs.pop(0)
        chirp_ref = refs.pop(0)
        blocks = refs[:2]
        refs = refs[2:]
        extra_ref = refs.pop(0) if (residual_after or backward) else None
        wave = wave_ref[0].astype(jnp.float32)
        patch_re = patch_ref[0, 0]
        patch_im = patch_ref[0, 1]
        if transmit_first:
            wave_re = patch_re * wave[0] - patch_im * wave[1]
            wave_im = patch_re * wave[1] + patch_im * wave[0]
        else:
            wave_re = wave[0]
            wave_im = wave[1]
        chirp_re = chirp_ref[0]
        chirp_im = chirp_ref[1]
        if backward:
            chirp_im = -chirp_im
        out_re, out_im = propagate_block(wave_re, wave_im, blocks, chirp_re, chirp_im)
        if residual_after:
            measured = extra_ref[0]
            weight = RESIDUAL_SCALE * (out_re * out_re + out_im * out_im - measured)
            result_ref = refs[0]
            result_ref[0, 0] = (weight * out_re).astype(jnp.bfloat16)
            result_ref[0, 1] = (weight * out_im).astype(jnp.bfloat16)
        elif backward:
            source = extra_ref[0].astype(jnp.float32)
            passed_ref, term_ref = refs[0], refs[1]
            passed_ref[0, 0] = (patch_re * out_re + patch_im * out_im).astype(jnp.bfloat16)
            passed_ref[0, 1] = (patch_re * out_im - patch_im * out_re).astype(jnp.bfloat16)
            term_ref[0, 0] = source[0] * out_re + source[1] * out_im
            term_ref[0, 1] = source[0] * out_im - source[1] * out_re
        else:
            result_ref = refs[0]
            result_ref[0, 0] = out_re.astype(jnp.bfloat16)
            result_ref[0, 1] = out_im.astype(jnp.bfloat16)

    return kernel


def run_waves(waves, patches, chirps, blocks, extra=None, transmit_first=True, residual_after=False, backward=False):
    number, _, width, _ = waves.shape
    wave_spec = pl.BlockSpec((1, 2, width, width), lambda i: (i, 0, 0, 0))
    chirp_spec = pl.BlockSpec((2, width, width), lambda i: (0, 0, 0))
    in_specs = [wave_spec, wave_spec, chirp_spec] + [
        pl.BlockSpec((2 * width, width), lambda i: (0, 0)),
        pl.BlockSpec((width, 2 * width), lambda i: (0, 0)),
    ]
    args = [waves, patches, chirps] + list(blocks)
    if residual_after:
        in_specs.append(pl.BlockSpec((1, width, width), lambda i: (i, 0, 0)))
        args.append(extra)
    if backward:
        in_specs.append(wave_spec)
        args.append(extra)
        out_shape = (
            jax.ShapeDtypeStruct(waves.shape, jnp.bfloat16),
            jax.ShapeDtypeStruct(waves.shape, jnp.float32),
        )
        out_specs = (wave_spec, wave_spec)
    else:
        out_shape = jax.ShapeDtypeStruct(waves.shape, jnp.bfloat16)
        out_specs = wave_spec
    return pl.pallas_call(
        wave_kernel(transmit_first, residual_after, backward),
        grid=(number,),
        in_specs=in_specs,
        out_specs=out_specs,
        out_shape=out_shape,
    )(*args)


def scatter_kernel(rows_ref, columns_ref, live_ref, terms_ref, out_ref):
    index = pl.program_id(0)

    @pl.when(index == 0)
    def _():
        out_ref[...] = jnp.zeros(out_ref.shape, out_ref.dtype)

    width = terms_ref.shape[2]
    height = out_ref.shape[1]
    columns_all = out_ref.shape[2]
    row = rows_ref[index]
    column = columns_ref[index]
    alive = live_ref[index] > 0
    for part in range(2):
        term = jnp.where(alive, terms_ref[0, part], 0.0)
        wide = jnp.concatenate(
            [term, jnp.zeros((width, columns_all - width), jnp.float32)], axis=1
        )
        wide = pltpu.roll(wide, column, 1)
        tall = jnp.concatenate(
            [wide, jnp.zeros((height - width, columns_all), jnp.float32)], axis=0
        )
        tall = pltpu.roll(tall, row, 0)
        out_ref[part] = out_ref[part] + tall


def scatter_terms(terms, rows, columns, live, height, columns_all):
    number, _, width, _ = terms.shape
    grid_spec = pltpu.PrefetchScalarGridSpec(
        num_scalar_prefetch=3,
        grid=(number,),
        in_specs=[pl.BlockSpec((1, 2, width, width), lambda i, r, c, a: (i, 0, 0, 0))],
        out_specs=pl.BlockSpec((2, height, columns_all), lambda i, r, c, a: (0, 0, 0)),
    )
    return pl.pallas_call(
        scatter_kernel,
        grid_spec=grid_spec,
        out_shape=jax.ShapeDtypeStruct((2, height, columns_all), jnp.float32),
    )(rows, columns, live.astype(jnp.int32), terms)


def cut_kernel(rows_ref, columns_ref, order_ref, tile_ref, mine_ref, partner_ref, out_ref):
    index = pl.program_id(0)
    width = out_ref.shape[2]
    height = tile_ref.shape[2] + mine_ref.shape[2]
    columns_all = tile_ref.shape[3]
    row_shift = (height - rows_ref[index]) % height
    column_shift = (columns_all - columns_ref[index]) % columns_all
    first = order_ref[0] == 0
    for part in range(2):
        mine = mine_ref[0, part].astype(jnp.float32)
        partner = partner_ref[0, part].astype(jnp.float32)
        rim = jnp.concatenate(
            [jnp.where(first, mine, partner), jnp.where(first, partner, mine)], axis=1
        )
        full = jnp.concatenate([tile_ref[0, part], rim], axis=0)
        full = pltpu.roll(full, row_shift, 0)[:width]
        full = pltpu.roll(full, column_shift, 1)[:, :width]
        out_ref[0, part] = full


def cut_patches(tile, mine, partner, rows, columns, order, width):
    number = rows.shape[0]
    grid_spec = pltpu.PrefetchScalarGridSpec(
        num_scalar_prefetch=3,
        grid=(number,),
        in_specs=[
            pl.BlockSpec(tile.shape, lambda i, r, c, o: (0, 0, 0, 0)),
            pl.BlockSpec(mine.shape, lambda i, r, c, o: (0, 0, 0, 0)),
            pl.BlockSpec(partner.shape, lambda i, r, c, o: (0, 0, 0, 0)),
        ],
        out_specs=pl.BlockSpec((1, 2, width, width), lambda i, r, c, o: (i, 0, 0, 0)),
    )
    return pl.pallas_call(
        cut_kernel,
        grid_spec=grid_spec,
        out_shape=jax.ShapeDtypeStruct((number, 2, width, width), jnp.float32),
    )(rows, columns, order, tile, mine, partner)


def propagate_block(wave_re, wave_im, blocks, chirp_re, chirp_im):
    rows_ref, cols_ref = blocks
    width = wave_re.shape[0]
    dft_rows = rows_ref[...]
    dft_cols = cols_ref[...]

    def left(part_re, part_im):
        lanes = jnp.concatenate([part_re, part_im], axis=1).astype(jnp.bfloat16)
        return jnp.dot(dft_rows, lanes, preferred_element_type=jnp.float32)

    def right(part_re, part_im):
        rows = jnp.concatenate([part_re, part_im], axis=0).astype(jnp.bfloat16)
        return jnp.dot(rows, dft_cols, preferred_element_type=jnp.float32)

    first = left(wave_re, wave_im)
    z_re = (first[:width, :width] - first[width:, width:]).astype(jnp.bfloat16)
    z_im = (first[:width, width:] + first[width:, :width]).astype(jnp.bfloat16)
    second = right(z_re, z_im)
    spec_re = second[:width, :width] - second[width:, width:]
    spec_im = second[:width, width:] + second[width:, :width]
    w_re = spec_re * chirp_re - spec_im * chirp_im
    w_im = spec_re * chirp_im + spec_im * chirp_re
    third = right(w_re.astype(jnp.bfloat16), w_im.astype(jnp.bfloat16))
    v_re = (third[:width, :width] + third[width:, width:]).astype(jnp.bfloat16)
    v_im = (third[width:, :width] - third[:width, width:]).astype(jnp.bfloat16)
    fourth = left(v_re, v_im)
    out_re = (fourth[:width, :width] + fourth[width:, width:]).astype(jnp.bfloat16)
    out_im = (fourth[:width, width:] - fourth[width:, :width]).astype(jnp.bfloat16)
    return (out_re.astype(jnp.float32), out_im.astype(jnp.float32))


def place_term(term_re, term_im, row, column, alive, total_ref, direct_ref=None):
    width = term_re.shape[0]
    height = total_ref.shape[1]
    columns_all = total_ref.shape[2]
    row_shift = row % height
    column_shift = column % columns_all
    for part, term in enumerate((term_re, term_im)):
        term = jnp.where(alive, term, 0.0)
        wide = jnp.concatenate(
            [term, jnp.zeros((width, columns_all - width), jnp.float32)], axis=1
        )
        wide = pltpu.roll(wide, column_shift, 1)
        if height == 2 * width:
            rolled = pltpu.roll(wide, row % width, 0)
            below = lax.broadcasted_iota(jnp.int32, rolled.shape, 0) < row
            upper = jnp.where(below, 0.0, rolled)
            lower = jnp.where(below, rolled, 0.0)
            if direct_ref is None:
                total_ref[part, :width] = total_ref[part, :width] + upper
                total_ref[part, width:] = total_ref[part, width:] + lower
            else:
                direct_ref[part, :width] = upper.astype(direct_ref.dtype)
                direct_ref[part, width:] = lower.astype(direct_ref.dtype)
            continue
        tall = jnp.concatenate(
            [wide, jnp.zeros((height - width, columns_all), jnp.float32)], axis=0
        )
        if direct_ref is None:
            total_ref[part] = total_ref[part] + pltpu.roll(tall, row_shift, 0)
        else:
            direct_ref[part] = pltpu.roll(tall, row_shift, 0).astype(direct_ref.dtype)


def adjoint_kernel(last, single):
    def kernel(rows_ref, columns_ref, live_ref, slot_ref, other_ref, *refs):
        refs = list(refs)
        wave_ref = refs.pop(0)
        patch_ref = refs.pop(0)
        chirp_ref = refs.pop(0)
        blocks = refs[:2]
        refs = refs[2:]
        if last:
            own_ref = refs.pop(0)
            partner_ref = refs.pop(0)
        else:
            source_ref = refs.pop(0)
        passed_ref, grad_ref, total_ref = refs
        index = pl.program_id(0)

        if not single:
            @pl.when(index == 0)
            def _():
                total_ref[...] = jnp.zeros(total_ref.shape, total_ref.dtype)

        wave = wave_ref[0].astype(jnp.float32)
        patch_re = patch_ref[0, 0]
        patch_im = patch_ref[0, 1]
        chirp_re = chirp_ref[0]
        chirp_im = chirp_ref[1]
        if last:
            source_re = wave[0]
            source_im = wave[1]
            lit_re = patch_re * wave[0] - patch_im * wave[1]
            lit_im = patch_re * wave[1] + patch_im * wave[0]
            out_re, out_im = propagate_block(lit_re, lit_im, blocks, chirp_re, chirp_im)
            measured = jnp.where(other_ref[index] > 0, partner_ref[0], own_ref[0])
            weight = RESIDUAL_SCALE * (out_re * out_re + out_im * out_im - measured)
            in_re = (weight * out_re).astype(jnp.bfloat16).astype(jnp.float32)
            in_im = (weight * out_im).astype(jnp.bfloat16).astype(jnp.float32)
        else:
            source = source_ref[0].astype(jnp.float32)
            source_re = source[0]
            source_im = source[1]
            in_re = wave[0]
            in_im = wave[1]
        spread_re, spread_im = propagate_block(in_re, in_im, blocks, chirp_re, -chirp_im)
        passed_ref[0, 0] = (patch_re * spread_re + patch_im * spread_im).astype(jnp.bfloat16)
        passed_ref[0, 1] = (patch_re * spread_im - patch_im * spread_re).astype(jnp.bfloat16)
        if last:
            grad_ref[0, 0] = spread_re.astype(jnp.bfloat16)
            grad_ref[0, 1] = spread_im.astype(jnp.bfloat16)
            return
        term_re = source_re * spread_re + source_im * spread_im
        term_im = source_re * spread_im - source_im * spread_re
        place_term(
            term_re, term_im, rows_ref[index], columns_ref[index], live_ref[index] > 0,
            total_ref, grad_ref if single else None,
        )

        if not single:
            @pl.when(index == pl.num_programs(0) - 1)
            def _():
                grad_ref[...] = total_ref[...].astype(grad_ref.dtype)

    return kernel


def run_adjoint(waves, patches, chirps, blocks, scalars, extra, height, columns_all, last):
    number, _, width, _ = waves.shape
    wave_spec = pl.BlockSpec((1, 2, width, width), lambda i, *s: (i, 0, 0, 0))
    chirp_spec = pl.BlockSpec((2, width, width), lambda i, *s: (0, 0, 0))
    in_specs = [wave_spec, wave_spec, chirp_spec] + [
        pl.BlockSpec((2 * width, width), lambda i, *s: (0, 0)),
        pl.BlockSpec((width, 2 * width), lambda i, *s: (0, 0)),
    ]
    if last:
        slot_spec = pl.BlockSpec((1, width, width), lambda i, r, c, a, s, o: (s[i], 0, 0))
        in_specs += [slot_spec, slot_spec]
    else:
        in_specs += [wave_spec]
    if last:
        second_spec = wave_spec
        second_shape = jax.ShapeDtypeStruct(waves.shape, jnp.bfloat16)
    else:
        second_spec = pl.BlockSpec((2, height, columns_all), lambda i, *s: (0, 0, 0))
        second_shape = jax.ShapeDtypeStruct((2, height, columns_all), jnp.bfloat16)
    grid_spec = pltpu.PrefetchScalarGridSpec(
        num_scalar_prefetch=5,
        grid=(number,),
        in_specs=in_specs,
        out_specs=(wave_spec, second_spec),
        scratch_shapes=[pltpu.VMEM((2, height, columns_all), jnp.float32)],
    )
    return pl.pallas_call(
        adjoint_kernel(last, number == 1),
        grid_spec=grid_spec,
        out_shape=(jax.ShapeDtypeStruct(waves.shape, jnp.bfloat16), second_shape),
    )(*scalars, waves, patches, chirps, *blocks, *extra)


def place_kernel(rows_ref, columns_ref, live_ref, spread_ref, source_ref, grad_ref, total_ref):
    index = pl.program_id(0)

    @pl.when(index == 0)
    def _():
        total_ref[...] = jnp.zeros(total_ref.shape, total_ref.dtype)

    spread = spread_ref[0].astype(jnp.float32)
    source = source_ref[0].astype(jnp.float32)
    term_re = source[0] * spread[0] + source[1] * spread[1]
    term_im = source[0] * spread[1] - source[1] * spread[0]
    place_term(
        term_re, term_im, rows_ref[index], columns_ref[index], live_ref[index] > 0, total_ref
    )

    @pl.when(index == pl.num_programs(0) - 1)
    def _():
        grad_ref[...] = total_ref[...].astype(grad_ref.dtype)


def run_place(spread, source, scalars, height, columns_all):
    number, _, width, _ = spread.shape
    wave_spec = pl.BlockSpec((1, 2, width, width), lambda i, *s: (i, 0, 0, 0))
    grid_spec = pltpu.PrefetchScalarGridSpec(
        num_scalar_prefetch=3,
        grid=(number,),
        in_specs=[wave_spec, wave_spec],
        out_specs=pl.BlockSpec((2, height, columns_all), lambda i, *s: (0, 0, 0)),
        scratch_shapes=[pltpu.VMEM((2, height, columns_all), jnp.float32)],
    )
    return pl.pallas_call(
        place_kernel,
        grid_spec=grid_spec,
        out_shape=jax.ShapeDtypeStruct((2, height, columns_all), jnp.bfloat16),
    )(*scalars[:3], spread, source)


def first_kernel(rows_ref, columns_ref, order_ref, wave_ref, tile_ref, mine_ref, partner_ref,
                 chirp_ref, dft_rows_ref, dft_cols_ref, result_ref):
    index = pl.program_id(0)
    width = wave_ref.shape[2]
    height = tile_ref.shape[2] + mine_ref.shape[2]
    columns_all = tile_ref.shape[3]
    row_shift = (height - rows_ref[index]) % height
    column_shift = (columns_all - columns_ref[index]) % columns_all
    first = order_ref[0] == 0
    patch = []
    for part in range(2):
        mine = mine_ref[0, part].astype(jnp.float32)
        partner = partner_ref[0, part].astype(jnp.float32)
        rim = jnp.concatenate(
            [jnp.where(first, mine, partner), jnp.where(first, partner, mine)], axis=1
        )
        full = jnp.concatenate([tile_ref[0, part], rim], axis=0)
        full = pltpu.roll(full, row_shift, 0)[:width]
        patch.append(pltpu.roll(full, column_shift, 1)[:, :width])
    wave = wave_ref[0].astype(jnp.float32)
    wave_re = patch[0] * wave[0] - patch[1] * wave[1]
    wave_im = patch[0] * wave[1] + patch[1] * wave[0]
    out_re, out_im = propagate_block(
        wave_re, wave_im, (dft_rows_ref, dft_cols_ref), chirp_ref[0], chirp_ref[1]
    )
    result_ref[0, 0] = out_re.astype(jnp.bfloat16)
    result_ref[0, 1] = out_im.astype(jnp.bfloat16)


def run_first(waves, tile, mine, partner, rows, columns, order, chirps, blocks):
    number, _, width, _ = waves.shape
    wave_spec = pl.BlockSpec((1, 2, width, width), lambda i, r, c, o: (i, 0, 0, 0))
    whole = lambda shape: pl.BlockSpec(shape, lambda i, r, c, o: (0,) * len(shape))
    grid_spec = pltpu.PrefetchScalarGridSpec(
        num_scalar_prefetch=3,
        grid=(number,),
        in_specs=[
            wave_spec,
            whole(tile.shape),
            whole(mine.shape),
            whole(partner.shape),
            whole(chirps.shape),
            whole(blocks[0].shape),
            whole(blocks[1].shape),
        ],
        out_specs=wave_spec,
    )
    return pl.pallas_call(
        first_kernel,
        grid_spec=grid_spec,
        out_shape=jax.ShapeDtypeStruct(waves.shape, jnp.bfloat16),
    )(rows, columns, order, waves, tile, mine, partner, chirps, *blocks)


def local(object_field, probe, positions, counts, measured):
    width = probe.shape[1]
    tile_rows = object_field.shape[2]
    columns_all = object_field.shape[3]
    tile_index = lax.axis_index("tile")
    tile_count = lax.axis_size("tile")
    segment = lax.axis_index("depth")
    depth_count = lax.axis_size("depth")
    batch_index = lax.axis_index("batch")
    batch_count = lax.axis_size("batch")
    half = columns_all // batch_count
    wanted = lax.dynamic_slice_in_dim(object_field[:, :, :width, :], batch_index * half, half, 3)
    mine = from_behind(wanted.astype(jnp.bfloat16), "tile", -1)
    pairs = [(b, (b + 1) % batch_count) for b in range(batch_count)]
    partner = lax.ppermute(mine, "batch", pairs)
    capacity = positions.shape[0]
    share = -(-capacity // batch_count)
    first_core = batch_index == 0
    both_positions = lax.ppermute(positions, "batch", pairs)
    both_counts = lax.ppermute(counts, "batch", pairs)
    all_positions = jnp.where(
        first_core,
        jnp.concatenate([positions, both_positions]),
        jnp.concatenate([both_positions, positions]),
    )
    all_counts = jnp.where(
        first_core, jnp.concatenate([counts, both_counts]), jnp.concatenate([both_counts, counts])
    )
    entry = batch_index * share + jnp.arange(share, dtype=jnp.int32)
    live = entry < all_counts[0] + all_counts[1]
    later = entry >= all_counts[0]
    slot = jnp.clip(jnp.where(later, entry - all_counts[0], entry), 0, capacity - 1)
    flat = jnp.where(later, capacity, 0) + slot
    chosen = all_positions[flat]
    other = (later == first_core).astype(jnp.int32)
    local_rows = chosen[:, 0] - tile_index * tile_rows
    local_columns = chosen[:, 1]
    order = jnp.reshape(batch_index, (1,)).astype(jnp.int32)
    patches = cut_patches(object_field, mine, partner, local_rows, local_columns, order, width)
    number = patches.shape[0]
    coef = jnp.where(
        segment == depth_count - 1, jnp.float32(DETECTOR_COEF), jnp.float32(SLICE_COEF)
    )
    chirp_re, chirp_im = chirp_parts(width, coef)
    start = jnp.broadcast_to(probe[None], (number, 2, width, width))

    chirps = jnp.stack([chirp_re, chirp_im])
    dft_re, dft_im = dft_parts(width)
    blocks = (
        jnp.concatenate([dft_re, dft_im], axis=0),
        jnp.concatenate([dft_re, dft_im], axis=1),
    )

    def forward_all(waves):
        return run_first(
            waves, object_field, mine, partner, local_rows, local_columns, order, chirps, blocks
        )

    def silent(waves):
        return jnp.zeros_like(waves)

    carry = start
    inputs = start
    for turn in range(depth_count - 1):
        if turn > 0:
            carry = lax.ppermute(carry, "depth", [(turn - 1, turn)])
            inputs = jnp.where(segment == turn, carry, inputs)
        carry = lax.cond(segment == turn, forward_all, silent, carry)

    measured, carry = lax.optimization_barrier((measured, carry))
    both_measured = lax.ppermute(measured, "batch", pairs)
    height = tile_rows + width
    scalars = (local_rows, local_columns, live.astype(jnp.int32), slot, other)

    def last_pass(incoming):
        return run_adjoint(
            incoming, patches, chirps, blocks, scalars, (measured, both_measured),
            height, columns_all, True,
        )

    def last_silent(incoming):
        return (jnp.zeros_like(incoming), jnp.zeros_like(incoming))

    if depth_count > 1:
        carry = lax.ppermute(carry, "depth", [(depth_count - 2, depth_count - 1)])
    arrived_last = carry
    carry, spread_last = lax.cond(segment == depth_count - 1, last_pass, last_silent, carry)
    gradient = lax.cond(
        segment == depth_count - 1,
        lambda s, a: run_place(s, a, scalars, height, columns_all),
        lambda s, a: jnp.zeros((2, height, columns_all), jnp.bfloat16),
        spread_last,
        arrived_last,
    )

    def back_pass(incoming, previous):
        return run_adjoint(
            incoming, patches, chirps, blocks, scalars, (inputs,), height, columns_all, False
        )

    def back_silent(incoming, previous):
        return (jnp.zeros_like(incoming), previous)

    for turn in reversed(range(depth_count - 1)):
        carry = lax.ppermute(carry, "depth", [(turn + 1, turn)])
        carry, gradient = lax.cond(segment == turn, back_pass, back_silent, carry, gradient)

    gradient = gradient.astype(jnp.bfloat16)
    spill = gradient[:, tile_rows:, :]
    keep = lax.dynamic_slice_in_dim(spill, batch_index * half, half, 2)
    give = lax.dynamic_slice_in_dim(spill, (1 - batch_index) * half, half, 2)
    got = lax.ppermute(give, "batch", pairs)
    spill_sum = (keep.astype(jnp.float32) + got.astype(jnp.float32)).astype(jnp.bfloat16)
    arrived = lax.ppermute(spill_sum, "tile", [(t, t + 1) for t in range(tile_count - 1)])
    own = gradient[:, :tile_rows, :]
    other = lax.ppermute(own, "batch", pairs)
    arrived_other = lax.ppermute(arrived, "batch", pairs)
    incoming = jnp.where(
        first_core,
        jnp.concatenate([arrived, arrived_other], axis=2),
        jnp.concatenate([arrived_other, arrived], axis=2),
    )
    summed = own.astype(jnp.float32) + other.astype(jnp.float32)
    summed = summed.at[:, :width, :].add(incoming.astype(jnp.float32))
    return summed[None]


def solution(mesh):
    placed = (
        P(("groups", "depth"), None, "tile", None),
        P("groups", None, None),
        P(("groups", "tile", "batch"), None),
        P(("groups", "tile", "batch")),
        P(("groups", "tile", "batch"), None, None),
    )
    return jax.shard_map(
        local,
        mesh=mesh,
        in_specs=placed,
        out_specs=P(("groups", "depth"), None, "tile", None),
        check_vma=False,
    )
```

```python
import math

import jax
import jax.numpy as jnp
from jax import lax
from jax.sharding import PartitionSpec as P
from jax.experimental import pallas as pl
from jax.experimental.pallas import tpu as pltpu

SLICE_COEF = 0.002
DETECTOR_COEF = 0.006
RESIDUAL_SCALE = 0.125


def from_behind(block, axis, distance):
    devices = range(lax.axis_size(axis))
    route = [(i - distance, i) for i in devices if i - distance in devices]
    return lax.ppermute(block, axis, route)


def dft_block(width, sign):
    freq = jnp.arange(width, dtype=jnp.int32)
    product = freq[:, None] * freq[None, :] % width
    angle = 2.0 * math.pi / width * product.astype(jnp.float32)
    scale = 1.0 / math.sqrt(width)
    real_part = (jnp.cos(angle) * scale).astype(jnp.bfloat16)
    imag_part = (sign * jnp.sin(angle) * scale).astype(jnp.bfloat16)
    upper = jnp.concatenate([real_part, -imag_part], axis=1)
    lower = jnp.concatenate([imag_part, real_part], axis=1)
    return jnp.concatenate([upper, lower], axis=0)


def dft_right(width, sign):
    freq = jnp.arange(width, dtype=jnp.int32)
    product = freq[:, None] * freq[None, :] % width
    angle = 2.0 * math.pi / width * product.astype(jnp.float32)
    scale = 1.0 / math.sqrt(width)
    real_part = (jnp.cos(angle) * scale).astype(jnp.bfloat16)
    imag_part = (sign * jnp.sin(angle) * scale).astype(jnp.bfloat16)
    upper = jnp.concatenate([real_part, imag_part], axis=1)
    lower = jnp.concatenate([-imag_part, real_part], axis=1)
    return jnp.concatenate([upper, lower], axis=0)


def dft_parts(width):
    freq = jnp.arange(width, dtype=jnp.int32)
    product = freq[:, None] * freq[None, :] % width
    angle = 2.0 * math.pi / width * product.astype(jnp.float32)
    scale = 1.0 / math.sqrt(width)
    real_part = (jnp.cos(angle) * scale).astype(jnp.bfloat16)
    imag_part = (-jnp.sin(angle) * scale).astype(jnp.bfloat16)
    return (real_part, imag_part)


def chirp_parts(width, coef):
    freq = jnp.arange(width, dtype=jnp.int32)
    shifted = (freq + width // 2) % width - width // 2
    square = shifted * shifted
    total = (square[:, None] + square[None, :]).astype(jnp.float32)
    phase = -coef * total
    return (jnp.cos(phase), jnp.sin(phase))


def left_apply(block, waves):
    number = waves.shape[0]
    width = waves.shape[2]
    stacked = waves.reshape(number, 2 * width, width)
    result = jnp.einsum("ij,gjk->gik", block, stacked, preferred_element_type=jnp.float32)
    return result.reshape(number, 2, width, width)


def propagate(waves, forward_block, inverse_block, chirp_re, chirp_im):
    first = left_apply(forward_block, waves).astype(jnp.bfloat16)
    spectrum = left_apply(forward_block, jnp.swapaxes(first, -1, -2))
    spec_re = spectrum[:, 0]
    spec_im = spectrum[:, 1]
    filtered = jnp.stack(
        [spec_re * chirp_re - spec_im * chirp_im, spec_re * chirp_im + spec_im * chirp_re], axis=1
    ).astype(jnp.bfloat16)
    back = left_apply(inverse_block, filtered).astype(jnp.bfloat16)
    return left_apply(inverse_block, jnp.swapaxes(back, -1, -2)).astype(jnp.bfloat16)


def transmit(waves, patch):
    values = waves.astype(jnp.float32)
    wave_re = values[:, 0]
    wave_im = values[:, 1]
    return jnp.stack(
        [
            patch[:, 0] * wave_re - patch[:, 1] * wave_im,
            patch[:, 0] * wave_im + patch[:, 1] * wave_re,
        ],
        axis=1,
    ).astype(jnp.bfloat16)


def residual_wave(waves, measured):
    values = waves.astype(jnp.float32)
    intensity = values[:, 0] * values[:, 0] + values[:, 1] * values[:, 1]
    weight = RESIDUAL_SCALE * (intensity - measured)
    return jnp.stack([weight * values[:, 0], weight * values[:, 1]], axis=1).astype(jnp.bfloat16)


def adjoint_terms(incoming, forward_block, inverse_block, chirp_re, chirp_im, inputs, patch):
    spread = propagate(incoming, forward_block, inverse_block, chirp_re, -chirp_im).astype(
        jnp.float32
    )
    source = inputs.astype(jnp.float32)
    term = jnp.stack(
        [
            source[:, 0] * spread[:, 0] + source[:, 1] * spread[:, 1],
            source[:, 0] * spread[:, 1] - source[:, 1] * spread[:, 0],
        ],
        axis=1,
    )
    passed = jnp.stack(
        [
            patch[:, 0] * spread[:, 0] + patch[:, 1] * spread[:, 1],
            patch[:, 0] * spread[:, 1] - patch[:, 1] * spread[:, 0],
        ],
        axis=1,
    ).astype(jnp.bfloat16)
    return (passed, term)


def wave_kernel(transmit_first, residual_after, backward):
    def kernel(*refs):
        refs = list(refs)
        wave_ref = refs.pop(0)
        patch_ref = refs.pop(0)
        chirp_ref = refs.pop(0)
        blocks = refs[:2]
        refs = refs[2:]
        extra_ref = refs.pop(0) if (residual_after or backward) else None
        wave = wave_ref[0].astype(jnp.float32)
        patch_re = patch_ref[0, 0]
        patch_im = patch_ref[0, 1]
        if transmit_first:
            wave_re = patch_re * wave[0] - patch_im * wave[1]
            wave_im = patch_re * wave[1] + patch_im * wave[0]
        else:
            wave_re = wave[0]
            wave_im = wave[1]
        chirp_re = chirp_ref[0]
        chirp_im = chirp_ref[1]
        if backward:
            chirp_im = -chirp_im
        out_re, out_im = propagate_block(wave_re, wave_im, blocks, chirp_re, chirp_im)
        if residual_after:
            measured = extra_ref[0]
            weight = RESIDUAL_SCALE * (out_re * out_re + out_im * out_im - measured)
            result_ref = refs[0]
            result_ref[0, 0] = (weight * out_re).astype(jnp.bfloat16)
            result_ref[0, 1] = (weight * out_im).astype(jnp.bfloat16)
        elif backward:
            source = extra_ref[0].astype(jnp.float32)
            passed_ref, term_ref = refs[0], refs[1]
            passed_ref[0, 0] = (patch_re * out_re + patch_im * out_im).astype(jnp.bfloat16)
            passed_ref[0, 1] = (patch_re * out_im - patch_im * out_re).astype(jnp.bfloat16)
            term_ref[0, 0] = source[0] * out_re + source[1] * out_im
            term_ref[0, 1] = source[0] * out_im - source[1] * out_re
        else:
            result_ref = refs[0]
            result_ref[0, 0] = out_re.astype(jnp.bfloat16)
            result_ref[0, 1] = out_im.astype(jnp.bfloat16)

    return kernel


def run_waves(waves, patches, chirps, blocks, extra=None, transmit_first=True, residual_after=False, backward=False):
    number, _, width, _ = waves.shape
    wave_spec = pl.BlockSpec((1, 2, width, width), lambda i: (i, 0, 0, 0))
    chirp_spec = pl.BlockSpec((2, width, width), lambda i: (0, 0, 0))
    in_specs = [wave_spec, wave_spec, chirp_spec] + [
        pl.BlockSpec((2 * width, width), lambda i: (0, 0)),
        pl.BlockSpec((width, 2 * width), lambda i: (0, 0)),
    ]
    args = [waves, patches, chirps] + list(blocks)
    if residual_after:
        in_specs.append(pl.BlockSpec((1, width, width), lambda i: (i, 0, 0)))
        args.append(extra)
    if backward:
        in_specs.append(wave_spec)
        args.append(extra)
        out_shape = (
            jax.ShapeDtypeStruct(waves.shape, jnp.bfloat16),
            jax.ShapeDtypeStruct(waves.shape, jnp.float32),
        )
        out_specs = (wave_spec, wave_spec)
    else:
        out_shape = jax.ShapeDtypeStruct(waves.shape, jnp.bfloat16)
        out_specs = wave_spec
    return pl.pallas_call(
        wave_kernel(transmit_first, residual_after, backward),
        grid=(number,),
        in_specs=in_specs,
        out_specs=out_specs,
        out_shape=out_shape,
    )(*args)


def scatter_kernel(rows_ref, columns_ref, live_ref, terms_ref, out_ref):
    index = pl.program_id(0)

    @pl.when(index == 0)
    def _():
        out_ref[...] = jnp.zeros(out_ref.shape, out_ref.dtype)

    width = terms_ref.shape[2]
    height = out_ref.shape[1]
    columns_all = out_ref.shape[2]
    row = rows_ref[index]
    column = columns_ref[index]
    alive = live_ref[index] > 0
    for part in range(2):
        term = jnp.where(alive, terms_ref[0, part], 0.0)
        wide = jnp.concatenate(
            [term, jnp.zeros((width, columns_all - width), jnp.float32)], axis=1
        )
        wide = pltpu.roll(wide, column, 1)
        tall = jnp.concatenate(
            [wide, jnp.zeros((height - width, columns_all), jnp.float32)], axis=0
        )
        tall = pltpu.roll(tall, row, 0)
        out_ref[part] = out_ref[part] + tall


def scatter_terms(terms, rows, columns, live, height, columns_all):
    number, _, width, _ = terms.shape
    grid_spec = pltpu.PrefetchScalarGridSpec(
        num_scalar_prefetch=3,
        grid=(number,),
        in_specs=[pl.BlockSpec((1, 2, width, width), lambda i, r, c, a: (i, 0, 0, 0))],
        out_specs=pl.BlockSpec((2, height, columns_all), lambda i, r, c, a: (0, 0, 0)),
    )
    return pl.pallas_call(
        scatter_kernel,
        grid_spec=grid_spec,
        out_shape=jax.ShapeDtypeStruct((2, height, columns_all), jnp.float32),
    )(rows, columns, live.astype(jnp.int32), terms)


def cut_kernel(rows_ref, columns_ref, order_ref, tile_ref, mine_ref, partner_ref, out_ref):
    index = pl.program_id(0)
    width = out_ref.shape[2]
    height = tile_ref.shape[2] + mine_ref.shape[2]
    columns_all = tile_ref.shape[3]
    row_shift = (height - rows_ref[index]) % height
    column_shift = (columns_all - columns_ref[index]) % columns_all
    first = order_ref[0] == 0
    for part in range(2):
        mine = mine_ref[0, part].astype(jnp.float32)
        partner = partner_ref[0, part].astype(jnp.float32)
        rim = jnp.concatenate(
            [jnp.where(first, mine, partner), jnp.where(first, partner, mine)], axis=1
        )
        full = jnp.concatenate([tile_ref[0, part], rim], axis=0)
        full = pltpu.roll(full, row_shift, 0)[:width]
        full = pltpu.roll(full, column_shift, 1)[:, :width]
        out_ref[0, part] = full


def cut_patches(tile, mine, partner, rows, columns, order, width):
    number = rows.shape[0]
    grid_spec = pltpu.PrefetchScalarGridSpec(
        num_scalar_prefetch=3,
        grid=(number,),
        in_specs=[
            pl.BlockSpec(tile.shape, lambda i, r, c, o: (0, 0, 0, 0)),
            pl.BlockSpec(mine.shape, lambda i, r, c, o: (0, 0, 0, 0)),
            pl.BlockSpec(partner.shape, lambda i, r, c, o: (0, 0, 0, 0)),
        ],
        out_specs=pl.BlockSpec((1, 2, width, width), lambda i, r, c, o: (i, 0, 0, 0)),
    )
    return pl.pallas_call(
        cut_kernel,
        grid_spec=grid_spec,
        out_shape=jax.ShapeDtypeStruct((number, 2, width, width), jnp.float32),
    )(rows, columns, order, tile, mine, partner)


def propagate_block(wave_re, wave_im, blocks, chirp_re, chirp_im):
    rows_ref, cols_ref = blocks
    width = wave_re.shape[0]
    dft_rows = rows_ref[...]
    dft_cols = cols_ref[...]

    def left(part_re, part_im):
        lanes = jnp.concatenate([part_re, part_im], axis=1).astype(jnp.bfloat16)
        return jnp.dot(dft_rows, lanes, preferred_element_type=jnp.float32)

    def right(part_re, part_im):
        rows = jnp.concatenate([part_re, part_im], axis=0).astype(jnp.bfloat16)
        return jnp.dot(rows, dft_cols, preferred_element_type=jnp.float32)

    first = left(wave_re, wave_im)
    z_re = (first[:width, :width] - first[width:, width:]).astype(jnp.bfloat16)
    z_im = (first[:width, width:] + first[width:, :width]).astype(jnp.bfloat16)
    second = right(z_re, z_im)
    spec_re = second[:width, :width] - second[width:, width:]
    spec_im = second[:width, width:] + second[width:, :width]
    w_re = spec_re * chirp_re - spec_im * chirp_im
    w_im = spec_re * chirp_im + spec_im * chirp_re
    third = right(w_re.astype(jnp.bfloat16), w_im.astype(jnp.bfloat16))
    v_re = (third[:width, :width] + third[width:, width:]).astype(jnp.bfloat16)
    v_im = (third[width:, :width] - third[:width, width:]).astype(jnp.bfloat16)
    fourth = left(v_re, v_im)
    out_re = (fourth[:width, :width] + fourth[width:, width:]).astype(jnp.bfloat16)
    out_im = (fourth[:width, width:] - fourth[width:, :width]).astype(jnp.bfloat16)
    return (out_re.astype(jnp.float32), out_im.astype(jnp.float32))


def place_term(term_re, term_im, row, column, alive, total_ref, direct_ref=None):
    width = term_re.shape[0]
    height = total_ref.shape[1]
    columns_all = total_ref.shape[2]
    row_shift = row % height
    column_shift = column % columns_all
    for part, term in enumerate((term_re, term_im)):
        term = jnp.where(alive, term, 0.0)
        wide = jnp.concatenate(
            [term, jnp.zeros((width, columns_all - width), jnp.float32)], axis=1
        )
        wide = pltpu.roll(wide, column_shift, 1)
        if height == 2 * width:
            rolled = pltpu.roll(wide, row % width, 0)
            below = lax.broadcasted_iota(jnp.int32, rolled.shape, 0) < row
            upper = jnp.where(below, 0.0, rolled)
            lower = jnp.where(below, rolled, 0.0)
            if direct_ref is None:
                total_ref[part, :width] = total_ref[part, :width] + upper
                total_ref[part, width:] = total_ref[part, width:] + lower
            else:
                direct_ref[part, :width] = upper.astype(direct_ref.dtype)
                direct_ref[part, width:] = lower.astype(direct_ref.dtype)
            continue
        tall = jnp.concatenate(
            [wide, jnp.zeros((height - width, columns_all), jnp.float32)], axis=0
        )
        if direct_ref is None:
            total_ref[part] = total_ref[part] + pltpu.roll(tall, row_shift, 0)
        else:
            direct_ref[part] = pltpu.roll(tall, row_shift, 0).astype(direct_ref.dtype)


def adjoint_kernel(last, single, opening=False):
    def kernel(rows_ref, columns_ref, live_ref, slot_ref, other_ref, *refs):
        refs = list(refs)
        wave_ref = refs.pop(0)
        patch_ref = None if opening else refs.pop(0)
        chirp_ref = refs.pop(0)
        blocks = refs[:2]
        refs = refs[2:]
        if last:
            own_ref = refs.pop(0)
            partner_ref = refs.pop(0)
        else:
            source_ref = refs.pop(0)
        if opening:
            grad_ref, total_ref = refs
            passed_ref = None
        else:
            passed_ref, grad_ref, total_ref = refs
        index = pl.program_id(0)

        if not single:
            @pl.when(index == 0)
            def _():
                total_ref[...] = jnp.zeros(total_ref.shape, total_ref.dtype)

        wave = wave_ref[0].astype(jnp.float32)
        if not opening:
            patch_re = patch_ref[0, 0]
            patch_im = patch_ref[0, 1]
        chirp_re = chirp_ref[0]
        chirp_im = chirp_ref[1]
        if last:
            source_re = wave[0]
            source_im = wave[1]
            lit_re = patch_re * wave[0] - patch_im * wave[1]
            lit_im = patch_re * wave[1] + patch_im * wave[0]
            out_re, out_im = propagate_block(lit_re, lit_im, blocks, chirp_re, chirp_im)
            measured = jnp.where(other_ref[index] > 0, partner_ref[0], own_ref[0])
            weight = RESIDUAL_SCALE * (out_re * out_re + out_im * out_im - measured)
            in_re = (weight * out_re).astype(jnp.bfloat16).astype(jnp.float32)
            in_im = (weight * out_im).astype(jnp.bfloat16).astype(jnp.float32)
        else:
            source = source_ref[0].astype(jnp.float32)
            source_re = source[0]
            source_im = source[1]
            in_re = wave[0]
            in_im = wave[1]
        spread_re, spread_im = propagate_block(in_re, in_im, blocks, chirp_re, -chirp_im)
        if not opening:
            passed_ref[0, 0] = (patch_re * spread_re + patch_im * spread_im).astype(jnp.bfloat16)
            passed_ref[0, 1] = (patch_re * spread_im - patch_im * spread_re).astype(jnp.bfloat16)
        term_re = source_re * spread_re + source_im * spread_im
        term_im = source_re * spread_im - source_im * spread_re
        place_term(
            term_re, term_im, rows_ref[index], columns_ref[index], live_ref[index] > 0,
            total_ref, grad_ref if single else None,
        )

        if not single:
            @pl.when(index == pl.num_programs(0) - 1)
            def _():
                grad_ref[...] = total_ref[...].astype(grad_ref.dtype)

    return kernel


def run_adjoint(waves, patches, chirps, blocks, scalars, extra, height, columns_all, last,
                opening=False):
    number, _, width, _ = waves.shape
    wave_spec = pl.BlockSpec((1, 2, width, width), lambda i, *s: (i, 0, 0, 0))
    chirp_spec = pl.BlockSpec((2, width, width), lambda i, *s: (0, 0, 0))
    in_specs = [wave_spec] + ([] if opening else [wave_spec]) + [chirp_spec] + [
        pl.BlockSpec((2 * width, width), lambda i, *s: (0, 0)),
        pl.BlockSpec((width, 2 * width), lambda i, *s: (0, 0)),
    ]
    if last:
        slot_spec = pl.BlockSpec((1, width, width), lambda i, r, c, a, s, o: (s[i], 0, 0))
        in_specs += [slot_spec, slot_spec]
    else:
        in_specs += [wave_spec]
    grid_spec = pltpu.PrefetchScalarGridSpec(
        num_scalar_prefetch=5,
        grid=(number,),
        in_specs=in_specs,
        out_specs=((() if opening else (wave_spec,))
                   + (pl.BlockSpec((2, height, columns_all), lambda i, *s: (0, 0, 0)),)),
        scratch_shapes=[pltpu.VMEM((2, height, columns_all), jnp.float32)],
    )
    return pl.pallas_call(
        adjoint_kernel(last, number == 1, opening),
        grid_spec=grid_spec,
        out_shape=((() if opening else (jax.ShapeDtypeStruct(waves.shape, jnp.bfloat16),))
                   + (jax.ShapeDtypeStruct((2, height, columns_all), jnp.bfloat16),)),
    )(*scalars, waves, *(() if opening else (patches,)), chirps, *blocks, *extra)


def first_kernel(rows_ref, columns_ref, order_ref, wave_ref, tile_ref, mine_ref, partner_ref,
                 chirp_ref, dft_rows_ref, dft_cols_ref, result_ref):
    index = pl.program_id(0)
    width = wave_ref.shape[2]
    height = tile_ref.shape[2] + mine_ref.shape[2]
    columns_all = tile_ref.shape[3]
    row_shift = (height - rows_ref[index]) % height
    column_shift = (columns_all - columns_ref[index]) % columns_all
    first = order_ref[0] == 0
    patch = []
    for part in range(2):
        mine = mine_ref[0, part].astype(jnp.float32)
        partner = partner_ref[0, part].astype(jnp.float32)
        rim = jnp.concatenate(
            [jnp.where(first, mine, partner), jnp.where(first, partner, mine)], axis=1
        )
        full = jnp.concatenate([tile_ref[0, part], rim], axis=0)
        full = pltpu.roll(full, row_shift, 0)[:width]
        patch.append(pltpu.roll(full, column_shift, 1)[:, :width])
    wave = wave_ref[0].astype(jnp.float32)
    wave_re = patch[0] * wave[0] - patch[1] * wave[1]
    wave_im = patch[0] * wave[1] + patch[1] * wave[0]
    out_re, out_im = propagate_block(
        wave_re, wave_im, (dft_rows_ref, dft_cols_ref), chirp_ref[0], chirp_ref[1]
    )
    result_ref[0, 0] = out_re.astype(jnp.bfloat16)
    result_ref[0, 1] = out_im.astype(jnp.bfloat16)


def run_first(waves, tile, mine, partner, rows, columns, order, chirps, blocks):
    number, _, width, _ = waves.shape
    wave_spec = pl.BlockSpec((1, 2, width, width), lambda i, r, c, o: (i, 0, 0, 0))
    whole = lambda shape: pl.BlockSpec(shape, lambda i, r, c, o: (0,) * len(shape))
    grid_spec = pltpu.PrefetchScalarGridSpec(
        num_scalar_prefetch=3,
        grid=(number,),
        in_specs=[
            wave_spec,
            whole(tile.shape),
            whole(mine.shape),
            whole(partner.shape),
            whole(chirps.shape),
            whole(blocks[0].shape),
            whole(blocks[1].shape),
        ],
        out_specs=wave_spec,
    )
    return pl.pallas_call(
        first_kernel,
        grid_spec=grid_spec,
        out_shape=jax.ShapeDtypeStruct(waves.shape, jnp.bfloat16),
    )(rows, columns, order, waves, tile, mine, partner, chirps, *blocks)


def local(object_field, probe, positions, counts, measured):
    width = probe.shape[1]
    tile_rows = object_field.shape[2]
    columns_all = object_field.shape[3]
    tile_index = lax.axis_index("tile")
    tile_count = lax.axis_size("tile")
    segment = lax.axis_index("depth")
    depth_count = lax.axis_size("depth")
    batch_index = lax.axis_index("batch")
    batch_count = lax.axis_size("batch")
    half = columns_all // batch_count
    wanted = lax.dynamic_slice_in_dim(object_field[:, :, :width, :], batch_index * half, half, 3)
    mine = from_behind(wanted.astype(jnp.bfloat16), "tile", -1)
    pairs = [(b, (b + 1) % batch_count) for b in range(batch_count)]
    partner = lax.ppermute(mine, "batch", pairs)
    capacity = positions.shape[0]
    share = -(-capacity // batch_count)
    first_core = batch_index == 0
    both_positions = lax.ppermute(positions, "batch", pairs)
    both_counts = lax.ppermute(counts, "batch", pairs)
    all_positions = jnp.where(
        first_core,
        jnp.concatenate([positions, both_positions]),
        jnp.concatenate([both_positions, positions]),
    )
    all_counts = jnp.where(
        first_core, jnp.concatenate([counts, both_counts]), jnp.concatenate([both_counts, counts])
    )
    entry = batch_index * share + jnp.arange(share, dtype=jnp.int32)
    live = entry < all_counts[0] + all_counts[1]
    later = entry >= all_counts[0]
    slot = jnp.clip(jnp.where(later, entry - all_counts[0], entry), 0, capacity - 1)
    flat = jnp.where(later, capacity, 0) + slot
    chosen = all_positions[flat]
    other = (later == first_core).astype(jnp.int32)
    local_rows = chosen[:, 0] - tile_index * tile_rows
    local_columns = chosen[:, 1]
    order = jnp.reshape(batch_index, (1,)).astype(jnp.int32)
    patches = cut_patches(object_field, mine, partner, local_rows, local_columns, order, width)
    number = patches.shape[0]
    coef = jnp.where(
        segment == depth_count - 1, jnp.float32(DETECTOR_COEF), jnp.float32(SLICE_COEF)
    )
    chirp_re, chirp_im = chirp_parts(width, coef)
    start = jnp.broadcast_to(probe[None], (number, 2, width, width))

    chirps = jnp.stack([chirp_re, chirp_im])
    dft_re, dft_im = dft_parts(width)
    blocks = (
        jnp.concatenate([dft_re, dft_im], axis=0),
        jnp.concatenate([dft_re, dft_im], axis=1),
    )

    def forward_all(waves):
        return run_first(
            waves, object_field, mine, partner, local_rows, local_columns, order, chirps, blocks
        )

    def silent(waves):
        return jnp.zeros_like(waves)

    carry = start
    inputs = start
    for turn in range(depth_count - 1):
        if turn > 0:
            carry = lax.ppermute(carry, "depth", [(turn - 1, turn)])
            inputs = jnp.where(segment == turn, carry, inputs)
        carry = lax.cond(segment == turn, forward_all, silent, carry)

    measured, carry = lax.optimization_barrier((measured, carry))
    both_measured = lax.ppermute(measured, "batch", pairs)
    height = tile_rows + width
    scalars = (local_rows, local_columns, live.astype(jnp.int32), slot, other)

    def last_pass(incoming):
        return run_adjoint(
            incoming, patches, chirps, blocks, scalars, (measured, both_measured),
            height, columns_all, True,
        )

    def last_silent(incoming):
        return (jnp.zeros_like(incoming), jnp.zeros((2, height, columns_all), jnp.bfloat16))

    if depth_count > 1:
        carry = lax.ppermute(carry, "depth", [(depth_count - 2, depth_count - 1)])
    carry, gradient = lax.cond(segment == depth_count - 1, last_pass, last_silent, carry)

    def back_pass(incoming, previous):
        return run_adjoint(
            incoming, patches, chirps, blocks, scalars, (inputs,), height, columns_all, False
        )

    def opening_pass(incoming, previous):
        (gradient,) = run_adjoint(
            incoming, patches, chirps, blocks, scalars, (inputs,), height, columns_all, False,
            opening=True,
        )
        return (incoming, gradient)

    def back_silent(incoming, previous):
        return (jnp.zeros_like(incoming), previous)

    for turn in reversed(range(depth_count - 1)):
        carry = lax.ppermute(carry, "depth", [(turn + 1, turn)])
        step = opening_pass if turn == 0 else back_pass
        carry, gradient = lax.cond(segment == turn, step, back_silent, carry, gradient)

    gradient = gradient.astype(jnp.bfloat16)
    spill = gradient[:, tile_rows:, :]
    keep = lax.dynamic_slice_in_dim(spill, batch_index * half, half, 2)
    give = lax.dynamic_slice_in_dim(spill, (1 - batch_index) * half, half, 2)
    got = lax.ppermute(give, "batch", pairs)
    spill_sum = (keep.astype(jnp.float32) + got.astype(jnp.float32)).astype(jnp.bfloat16)
    arrived = lax.ppermute(spill_sum, "tile", [(t, t + 1) for t in range(tile_count - 1)])
    own = gradient[:, :tile_rows, :]
    other = lax.ppermute(own, "batch", pairs)
    arrived_other = lax.ppermute(arrived, "batch", pairs)
    incoming = jnp.where(
        first_core,
        jnp.concatenate([arrived, arrived_other], axis=2),
        jnp.concatenate([arrived_other, arrived], axis=2),
    )
    summed = own.astype(jnp.float32) + other.astype(jnp.float32)
    summed = summed.at[:, :width, :].add(incoming.astype(jnp.float32))
    return summed[None]


def solution(mesh):
    placed = (
        P(("groups", "depth"), None, "tile", None),
        P("groups", None, None),
        P(("groups", "tile", "batch"), None),
        P(("groups", "tile", "batch")),
        P(("groups", "tile", "batch"), None, None),
    )
    return jax.shard_map(
        local,
        mesh=mesh,
        in_specs=placed,
        out_specs=P(("groups", "depth"), None, "tile", None),
        check_vma=False,
    )
```

```python
import math

import jax
import jax.numpy as jnp
from jax import lax
from jax.sharding import PartitionSpec as P
from jax.experimental import pallas as pl
from jax.experimental.pallas import tpu as pltpu

SLICE_COEF = 0.002
DETECTOR_COEF = 0.006
RESIDUAL_SCALE = 0.125


def from_behind(block, axis, distance):
    devices = range(lax.axis_size(axis))
    route = [(i - distance, i) for i in devices if i - distance in devices]
    return lax.ppermute(block, axis, route)


def dft_block(width, sign):
    freq = jnp.arange(width, dtype=jnp.int32)
    product = freq[:, None] * freq[None, :] % width
    angle = 2.0 * math.pi / width * product.astype(jnp.float32)
    scale = 1.0 / math.sqrt(width)
    real_part = (jnp.cos(angle) * scale).astype(jnp.bfloat16)
    imag_part = (sign * jnp.sin(angle) * scale).astype(jnp.bfloat16)
    upper = jnp.concatenate([real_part, -imag_part], axis=1)
    lower = jnp.concatenate([imag_part, real_part], axis=1)
    return jnp.concatenate([upper, lower], axis=0)


def dft_right(width, sign):
    freq = jnp.arange(width, dtype=jnp.int32)
    product = freq[:, None] * freq[None, :] % width
    angle = 2.0 * math.pi / width * product.astype(jnp.float32)
    scale = 1.0 / math.sqrt(width)
    real_part = (jnp.cos(angle) * scale).astype(jnp.bfloat16)
    imag_part = (sign * jnp.sin(angle) * scale).astype(jnp.bfloat16)
    upper = jnp.concatenate([real_part, imag_part], axis=1)
    lower = jnp.concatenate([-imag_part, real_part], axis=1)
    return jnp.concatenate([upper, lower], axis=0)


def dft_parts(width):
    freq = jnp.arange(width, dtype=jnp.int32)
    product = freq[:, None] * freq[None, :] % width
    angle = 2.0 * math.pi / width * product.astype(jnp.float32)
    scale = 1.0 / math.sqrt(width)
    real_part = (jnp.cos(angle) * scale).astype(jnp.bfloat16)
    imag_part = (-jnp.sin(angle) * scale).astype(jnp.bfloat16)
    return (real_part, imag_part)


def chirp_parts(width, coef):
    freq = jnp.arange(width, dtype=jnp.int32)
    shifted = (freq + width // 2) % width - width // 2
    square = shifted * shifted
    total = (square[:, None] + square[None, :]).astype(jnp.float32)
    phase = -coef * total
    return (jnp.cos(phase), jnp.sin(phase))


def left_apply(block, waves):
    number = waves.shape[0]
    width = waves.shape[2]
    stacked = waves.reshape(number, 2 * width, width)
    result = jnp.einsum("ij,gjk->gik", block, stacked, preferred_element_type=jnp.float32)
    return result.reshape(number, 2, width, width)


def propagate(waves, forward_block, inverse_block, chirp_re, chirp_im):
    first = left_apply(forward_block, waves).astype(jnp.bfloat16)
    spectrum = left_apply(forward_block, jnp.swapaxes(first, -1, -2))
    spec_re = spectrum[:, 0]
    spec_im = spectrum[:, 1]
    filtered = jnp.stack(
        [spec_re * chirp_re - spec_im * chirp_im, spec_re * chirp_im + spec_im * chirp_re], axis=1
    ).astype(jnp.bfloat16)
    back = left_apply(inverse_block, filtered).astype(jnp.bfloat16)
    return left_apply(inverse_block, jnp.swapaxes(back, -1, -2)).astype(jnp.bfloat16)


def transmit(waves, patch):
    values = waves.astype(jnp.float32)
    wave_re = values[:, 0]
    wave_im = values[:, 1]
    return jnp.stack(
        [
            patch[:, 0] * wave_re - patch[:, 1] * wave_im,
            patch[:, 0] * wave_im + patch[:, 1] * wave_re,
        ],
        axis=1,
    ).astype(jnp.bfloat16)


def residual_wave(waves, measured):
    values = waves.astype(jnp.float32)
    intensity = values[:, 0] * values[:, 0] + values[:, 1] * values[:, 1]
    weight = RESIDUAL_SCALE * (intensity - measured)
    return jnp.stack([weight * values[:, 0], weight * values[:, 1]], axis=1).astype(jnp.bfloat16)


def adjoint_terms(incoming, forward_block, inverse_block, chirp_re, chirp_im, inputs, patch):
    spread = propagate(incoming, forward_block, inverse_block, chirp_re, -chirp_im).astype(
        jnp.float32
    )
    source = inputs.astype(jnp.float32)
    term = jnp.stack(
        [
            source[:, 0] * spread[:, 0] + source[:, 1] * spread[:, 1],
            source[:, 0] * spread[:, 1] - source[:, 1] * spread[:, 0],
        ],
        axis=1,
    )
    passed = jnp.stack(
        [
            patch[:, 0] * spread[:, 0] + patch[:, 1] * spread[:, 1],
            patch[:, 0] * spread[:, 1] - patch[:, 1] * spread[:, 0],
        ],
        axis=1,
    ).astype(jnp.bfloat16)
    return (passed, term)


def wave_kernel(transmit_first, residual_after, backward):
    def kernel(*refs):
        refs = list(refs)
        wave_ref = refs.pop(0)
        patch_ref = refs.pop(0)
        chirp_ref = refs.pop(0)
        blocks = refs[:2]
        refs = refs[2:]
        extra_ref = refs.pop(0) if (residual_after or backward) else None
        wave = wave_ref[0].astype(jnp.float32)
        patch_re = patch_ref[0, 0]
        patch_im = patch_ref[0, 1]
        if transmit_first:
            wave_re = patch_re * wave[0] - patch_im * wave[1]
            wave_im = patch_re * wave[1] + patch_im * wave[0]
        else:
            wave_re = wave[0]
            wave_im = wave[1]
        chirp_re = chirp_ref[0]
        chirp_im = chirp_ref[1]
        if backward:
            chirp_im = -chirp_im
        out_re, out_im = propagate_block(wave_re, wave_im, blocks, chirp_re, chirp_im)
        if residual_after:
            measured = extra_ref[0]
            weight = RESIDUAL_SCALE * (out_re * out_re + out_im * out_im - measured)
            result_ref = refs[0]
            result_ref[0, 0] = (weight * out_re).astype(jnp.bfloat16)
            result_ref[0, 1] = (weight * out_im).astype(jnp.bfloat16)
        elif backward:
            source = extra_ref[0].astype(jnp.float32)
            passed_ref, term_ref = refs[0], refs[1]
            passed_ref[0, 0] = (patch_re * out_re + patch_im * out_im).astype(jnp.bfloat16)
            passed_ref[0, 1] = (patch_re * out_im - patch_im * out_re).astype(jnp.bfloat16)
            term_ref[0, 0] = source[0] * out_re + source[1] * out_im
            term_ref[0, 1] = source[0] * out_im - source[1] * out_re
        else:
            result_ref = refs[0]
            result_ref[0, 0] = out_re.astype(jnp.bfloat16)
            result_ref[0, 1] = out_im.astype(jnp.bfloat16)

    return kernel


def run_waves(waves, patches, chirps, blocks, extra=None, transmit_first=True, residual_after=False, backward=False):
    number, _, width, _ = waves.shape
    wave_spec = pl.BlockSpec((1, 2, width, width), lambda i: (i, 0, 0, 0))
    chirp_spec = pl.BlockSpec((2, width, width), lambda i: (0, 0, 0))
    in_specs = [wave_spec, wave_spec, chirp_spec] + [
        pl.BlockSpec((2 * width, width), lambda i: (0, 0)),
        pl.BlockSpec((width, 2 * width), lambda i: (0, 0)),
    ]
    args = [waves, patches, chirps] + list(blocks)
    if residual_after:
        in_specs.append(pl.BlockSpec((1, width, width), lambda i: (i, 0, 0)))
        args.append(extra)
    if backward:
        in_specs.append(wave_spec)
        args.append(extra)
        out_shape = (
            jax.ShapeDtypeStruct(waves.shape, jnp.bfloat16),
            jax.ShapeDtypeStruct(waves.shape, jnp.float32),
        )
        out_specs = (wave_spec, wave_spec)
    else:
        out_shape = jax.ShapeDtypeStruct(waves.shape, jnp.bfloat16)
        out_specs = wave_spec
    return pl.pallas_call(
        wave_kernel(transmit_first, residual_after, backward),
        grid=(number,),
        in_specs=in_specs,
        out_specs=out_specs,
        out_shape=out_shape,
    )(*args)


def scatter_kernel(rows_ref, columns_ref, live_ref, terms_ref, out_ref):
    index = pl.program_id(0)

    @pl.when(index == 0)
    def _():
        out_ref[...] = jnp.zeros(out_ref.shape, out_ref.dtype)

    width = terms_ref.shape[2]
    height = out_ref.shape[1]
    columns_all = out_ref.shape[2]
    row = rows_ref[index]
    column = columns_ref[index]
    alive = live_ref[index] > 0
    for part in range(2):
        term = jnp.where(alive, terms_ref[0, part], 0.0)
        wide = jnp.concatenate(
            [term, jnp.zeros((width, columns_all - width), jnp.float32)], axis=1
        )
        wide = pltpu.roll(wide, column, 1)
        tall = jnp.concatenate(
            [wide, jnp.zeros((height - width, columns_all), jnp.float32)], axis=0
        )
        tall = pltpu.roll(tall, row, 0)
        out_ref[part] = out_ref[part] + tall


def scatter_terms(terms, rows, columns, live, height, columns_all):
    number, _, width, _ = terms.shape
    grid_spec = pltpu.PrefetchScalarGridSpec(
        num_scalar_prefetch=3,
        grid=(number,),
        in_specs=[pl.BlockSpec((1, 2, width, width), lambda i, r, c, a: (i, 0, 0, 0))],
        out_specs=pl.BlockSpec((2, height, columns_all), lambda i, r, c, a: (0, 0, 0)),
    )
    return pl.pallas_call(
        scatter_kernel,
        grid_spec=grid_spec,
        out_shape=jax.ShapeDtypeStruct((2, height, columns_all), jnp.float32),
    )(rows, columns, live.astype(jnp.int32), terms)


def cut_kernel(rows_ref, columns_ref, order_ref, tile_ref, mine_ref, partner_ref, out_ref):
    index = pl.program_id(0)
    width = out_ref.shape[2]
    height = tile_ref.shape[2] + mine_ref.shape[2]
    columns_all = tile_ref.shape[3]
    row_shift = (height - rows_ref[index]) % height
    column_shift = (columns_all - columns_ref[index]) % columns_all
    first = order_ref[0] == 0
    for part in range(2):
        mine = mine_ref[0, part].astype(jnp.float32)
        partner = partner_ref[0, part].astype(jnp.float32)
        rim = jnp.concatenate(
            [jnp.where(first, mine, partner), jnp.where(first, partner, mine)], axis=1
        )
        full = jnp.concatenate([tile_ref[0, part], rim], axis=0)
        full = pltpu.roll(full, row_shift, 0)[:width]
        full = pltpu.roll(full, column_shift, 1)[:, :width]
        out_ref[0, part] = full


def cut_patches(tile, mine, partner, rows, columns, order, width):
    number = rows.shape[0]
    grid_spec = pltpu.PrefetchScalarGridSpec(
        num_scalar_prefetch=3,
        grid=(number,),
        in_specs=[
            pl.BlockSpec(tile.shape, lambda i, r, c, o: (0, 0, 0, 0)),
            pl.BlockSpec(mine.shape, lambda i, r, c, o: (0, 0, 0, 0)),
            pl.BlockSpec(partner.shape, lambda i, r, c, o: (0, 0, 0, 0)),
        ],
        out_specs=pl.BlockSpec((1, 2, width, width), lambda i, r, c, o: (i, 0, 0, 0)),
    )
    return pl.pallas_call(
        cut_kernel,
        grid_spec=grid_spec,
        out_shape=jax.ShapeDtypeStruct((number, 2, width, width), jnp.float32),
    )(rows, columns, order, tile, mine, partner)


def propagate_block(wave_re, wave_im, blocks, chirp_re, chirp_im):
    rows_ref, cols_ref = blocks
    width = wave_re.shape[0]
    dft_rows = rows_ref[...]
    dft_cols = cols_ref[...]

    def left(part_re, part_im):
        lanes = jnp.concatenate([part_re, part_im], axis=1).astype(jnp.bfloat16)
        return jnp.dot(dft_rows, lanes, preferred_element_type=jnp.float32)

    def right(part_re, part_im):
        rows = jnp.concatenate([part_re, part_im], axis=0).astype(jnp.bfloat16)
        return jnp.dot(rows, dft_cols, preferred_element_type=jnp.float32)

    first = left(wave_re, wave_im)
    z_re = (first[:width, :width] - first[width:, width:]).astype(jnp.bfloat16)
    z_im = (first[:width, width:] + first[width:, :width]).astype(jnp.bfloat16)
    second = right(z_re, z_im)
    spec_re = second[:width, :width] - second[width:, width:]
    spec_im = second[:width, width:] + second[width:, :width]
    w_re = spec_re * chirp_re - spec_im * chirp_im
    w_im = spec_re * chirp_im + spec_im * chirp_re
    third = right(w_re.astype(jnp.bfloat16), w_im.astype(jnp.bfloat16))
    v_re = (third[:width, :width] + third[width:, width:]).astype(jnp.bfloat16)
    v_im = (third[width:, :width] - third[:width, width:]).astype(jnp.bfloat16)
    fourth = left(v_re, v_im)
    out_re = (fourth[:width, :width] + fourth[width:, width:]).astype(jnp.bfloat16)
    out_im = (fourth[:width, width:] - fourth[width:, :width]).astype(jnp.bfloat16)
    return (out_re.astype(jnp.float32), out_im.astype(jnp.float32))


def place_term(term_re, term_im, row, column, alive, total_ref, direct_ref=None):
    width = term_re.shape[0]
    height = total_ref.shape[1]
    columns_all = total_ref.shape[2]
    row_shift = row % height
    column_shift = column % columns_all
    for part, term in enumerate((term_re, term_im)):
        term = jnp.where(alive, term, 0.0)
        wide = jnp.concatenate(
            [term, jnp.zeros((width, columns_all - width), jnp.float32)], axis=1
        )
        wide = pltpu.roll(wide, column_shift, 1)
        if height == 2 * width:
            rolled = pltpu.roll(wide, row % width, 0)
            below = lax.broadcasted_iota(jnp.int32, rolled.shape, 0) < row
            upper = jnp.where(below, 0.0, rolled)
            lower = jnp.where(below, rolled, 0.0)
            if direct_ref is None:
                total_ref[part, :width] = total_ref[part, :width] + upper
                total_ref[part, width:] = total_ref[part, width:] + lower
            else:
                direct_ref[part, :width] = upper.astype(direct_ref.dtype)
                direct_ref[part, width:] = lower.astype(direct_ref.dtype)
            continue
        tall = jnp.concatenate(
            [wide, jnp.zeros((height - width, columns_all), jnp.float32)], axis=0
        )
        if direct_ref is None:
            total_ref[part] = total_ref[part] + pltpu.roll(tall, row_shift, 0)
        else:
            direct_ref[part] = pltpu.roll(tall, row_shift, 0).astype(direct_ref.dtype)


def adjoint_kernel(last, single, opening=False):
    def kernel(rows_ref, columns_ref, live_ref, slot_ref, other_ref, *refs):
        refs = list(refs)
        wave_ref = refs.pop(0)
        patch_ref = None if opening else refs.pop(0)
        chirp_ref = refs.pop(0)
        blocks = refs[:2]
        refs = refs[2:]
        if last:
            own_ref = refs.pop(0)
            partner_ref = refs.pop(0)
        else:
            source_ref = refs.pop(0)
        if opening:
            grad_ref, total_ref = refs
            passed_ref = None
        else:
            passed_ref, grad_ref, total_ref = refs
        index = pl.program_id(0)

        if not single:
            @pl.when(index == 0)
            def _():
                total_ref[...] = jnp.zeros(total_ref.shape, total_ref.dtype)

        wave = wave_ref[0].astype(jnp.float32)
        if not opening:
            patch_re = patch_ref[0, 0]
            patch_im = patch_ref[0, 1]
        chirp_re = chirp_ref[0]
        chirp_im = chirp_ref[1]
        if last:
            source_re = wave[0]
            source_im = wave[1]
            lit_re = patch_re * wave[0] - patch_im * wave[1]
            lit_im = patch_re * wave[1] + patch_im * wave[0]
            out_re, out_im = propagate_block(lit_re, lit_im, blocks, chirp_re, chirp_im)
            measured = jnp.where(other_ref[index] > 0, partner_ref[0], own_ref[0])
            weight = RESIDUAL_SCALE * (out_re * out_re + out_im * out_im - measured)
            in_re = (weight * out_re).astype(jnp.bfloat16).astype(jnp.float32)
            in_im = (weight * out_im).astype(jnp.bfloat16).astype(jnp.float32)
        else:
            source = source_ref[0].astype(jnp.float32)
            source_re = source[0]
            source_im = source[1]
            in_re = wave[0]
            in_im = wave[1]
        spread_re, spread_im = propagate_block(in_re, in_im, blocks, chirp_re, -chirp_im)
        if not opening:
            passed_ref[0, 0] = (patch_re * spread_re + patch_im * spread_im).astype(jnp.bfloat16)
            passed_ref[0, 1] = (patch_re * spread_im - patch_im * spread_re).astype(jnp.bfloat16)
        if last:
            grad_ref[0, 0] = spread_re.astype(jnp.bfloat16)
            grad_ref[0, 1] = spread_im.astype(jnp.bfloat16)
            return
        term_re = source_re * spread_re + source_im * spread_im
        term_im = source_re * spread_im - source_im * spread_re
        place_term(
            term_re, term_im, rows_ref[index], columns_ref[index], live_ref[index] > 0,
            total_ref, grad_ref if single else None,
        )

        if not single:
            @pl.when(index == pl.num_programs(0) - 1)
            def _():
                grad_ref[...] = total_ref[...].astype(grad_ref.dtype)

    return kernel


def run_adjoint(waves, patches, chirps, blocks, scalars, extra, height, columns_all, last,
                opening=False):
    number, _, width, _ = waves.shape
    wave_spec = pl.BlockSpec((1, 2, width, width), lambda i, *s: (i, 0, 0, 0))
    chirp_spec = pl.BlockSpec((2, width, width), lambda i, *s: (0, 0, 0))
    in_specs = [wave_spec] + ([] if opening else [wave_spec]) + [chirp_spec] + [
        pl.BlockSpec((2 * width, width), lambda i, *s: (0, 0)),
        pl.BlockSpec((width, 2 * width), lambda i, *s: (0, 0)),
    ]
    if last:
        slot_spec = pl.BlockSpec((1, width, width), lambda i, r, c, a, s, o: (s[i], 0, 0))
        in_specs += [slot_spec, slot_spec]
    else:
        in_specs += [wave_spec]
    grid_spec = pltpu.PrefetchScalarGridSpec(
        num_scalar_prefetch=5,
        grid=(number,),
        in_specs=in_specs,
        out_specs=((() if opening else (wave_spec,))
                   + ((wave_spec,) if last else
                      (pl.BlockSpec((2, height, columns_all), lambda i, *s: (0, 0, 0)),))),
        scratch_shapes=[pltpu.VMEM((2, height, columns_all), jnp.float32)],
    )
    return pl.pallas_call(
        adjoint_kernel(last, number == 1, opening),
        grid_spec=grid_spec,
        out_shape=((() if opening else (jax.ShapeDtypeStruct(waves.shape, jnp.bfloat16),))
                   + ((jax.ShapeDtypeStruct(waves.shape, jnp.bfloat16),) if last else
                      (jax.ShapeDtypeStruct((2, height, columns_all), jnp.bfloat16),))),
    )(*scalars, waves, *(() if opening else (patches,)), chirps, *blocks, *extra)


def place_kernel(rows_ref, columns_ref, live_ref, spread_ref, source_ref, grad_ref, total_ref):
    index = pl.program_id(0)

    @pl.when(index == 0)
    def _():
        total_ref[...] = jnp.zeros(total_ref.shape, total_ref.dtype)

    spread = spread_ref[0].astype(jnp.float32)
    source = source_ref[0].astype(jnp.float32)
    term_re = source[0] * spread[0] + source[1] * spread[1]
    term_im = source[0] * spread[1] - source[1] * spread[0]
    place_term(
        term_re, term_im, rows_ref[index], columns_ref[index], live_ref[index] > 0, total_ref
    )

    @pl.when(index == pl.num_programs(0) - 1)
    def _():
        grad_ref[...] = total_ref[...].astype(grad_ref.dtype)


def run_place(spread, source, scalars, height, columns_all):
    number, _, width, _ = spread.shape
    wave_spec = pl.BlockSpec((1, 2, width, width), lambda i, *s: (i, 0, 0, 0))
    grid_spec = pltpu.PrefetchScalarGridSpec(
        num_scalar_prefetch=3,
        grid=(number,),
        in_specs=[wave_spec, wave_spec],
        out_specs=pl.BlockSpec((2, height, columns_all), lambda i, *s: (0, 0, 0)),
        scratch_shapes=[pltpu.VMEM((2, height, columns_all), jnp.float32)],
    )
    return pl.pallas_call(
        place_kernel,
        grid_spec=grid_spec,
        out_shape=jax.ShapeDtypeStruct((2, height, columns_all), jnp.bfloat16),
    )(*scalars[:3], spread, source)


def first_kernel(rows_ref, columns_ref, order_ref, wave_ref, tile_ref, mine_ref, partner_ref,
                 chirp_ref, dft_rows_ref, dft_cols_ref, result_ref):
    index = pl.program_id(0)
    width = wave_ref.shape[2]
    height = tile_ref.shape[2] + mine_ref.shape[2]
    columns_all = tile_ref.shape[3]
    row_shift = (height - rows_ref[index]) % height
    column_shift = (columns_all - columns_ref[index]) % columns_all
    first = order_ref[0] == 0
    patch = []
    for part in range(2):
        mine = mine_ref[0, part].astype(jnp.float32)
        partner = partner_ref[0, part].astype(jnp.float32)
        rim = jnp.concatenate(
            [jnp.where(first, mine, partner), jnp.where(first, partner, mine)], axis=1
        )
        full = jnp.concatenate([tile_ref[0, part], rim], axis=0)
        full = pltpu.roll(full, row_shift, 0)[:width]
        patch.append(pltpu.roll(full, column_shift, 1)[:, :width])
    wave = wave_ref[0].astype(jnp.float32)
    wave_re = patch[0] * wave[0] - patch[1] * wave[1]
    wave_im = patch[0] * wave[1] + patch[1] * wave[0]
    out_re, out_im = propagate_block(
        wave_re, wave_im, (dft_rows_ref, dft_cols_ref), chirp_ref[0], chirp_ref[1]
    )
    result_ref[0, 0] = out_re.astype(jnp.bfloat16)
    result_ref[0, 1] = out_im.astype(jnp.bfloat16)


def run_first(waves, tile, mine, partner, rows, columns, order, chirps, blocks):
    number, _, width, _ = waves.shape
    wave_spec = pl.BlockSpec((1, 2, width, width), lambda i, r, c, o: (i, 0, 0, 0))
    whole = lambda shape: pl.BlockSpec(shape, lambda i, r, c, o: (0,) * len(shape))
    grid_spec = pltpu.PrefetchScalarGridSpec(
        num_scalar_prefetch=3,
        grid=(number,),
        in_specs=[
            wave_spec,
            whole(tile.shape),
            whole(mine.shape),
            whole(partner.shape),
            whole(chirps.shape),
            whole(blocks[0].shape),
            whole(blocks[1].shape),
        ],
        out_specs=wave_spec,
    )
    return pl.pallas_call(
        first_kernel,
        grid_spec=grid_spec,
        out_shape=jax.ShapeDtypeStruct(waves.shape, jnp.bfloat16),
    )(rows, columns, order, waves, tile, mine, partner, chirps, *blocks)


def local(object_field, probe, positions, counts, measured):
    width = probe.shape[1]
    tile_rows = object_field.shape[2]
    columns_all = object_field.shape[3]
    tile_index = lax.axis_index("tile")
    tile_count = lax.axis_size("tile")
    segment = lax.axis_index("depth")
    depth_count = lax.axis_size("depth")
    batch_index = lax.axis_index("batch")
    batch_count = lax.axis_size("batch")
    half = columns_all // batch_count
    wanted = lax.dynamic_slice_in_dim(object_field[:, :, :width, :], batch_index * half, half, 3)
    mine = from_behind(wanted.astype(jnp.bfloat16), "tile", -1)
    pairs = [(b, (b + 1) % batch_count) for b in range(batch_count)]
    partner = lax.ppermute(mine, "batch", pairs)
    capacity = positions.shape[0]
    share = -(-capacity // batch_count)
    first_core = batch_index == 0
    both_positions = lax.ppermute(positions, "batch", pairs)
    both_counts = lax.ppermute(counts, "batch", pairs)
    all_positions = jnp.where(
        first_core,
        jnp.concatenate([positions, both_positions]),
        jnp.concatenate([both_positions, positions]),
    )
    all_counts = jnp.where(
        first_core, jnp.concatenate([counts, both_counts]), jnp.concatenate([both_counts, counts])
    )
    entry = batch_index * share + jnp.arange(share, dtype=jnp.int32)
    live = entry < all_counts[0] + all_counts[1]
    later = entry >= all_counts[0]
    slot = jnp.clip(jnp.where(later, entry - all_counts[0], entry), 0, capacity - 1)
    flat = jnp.where(later, capacity, 0) + slot
    chosen = all_positions[flat]
    other = (later == first_core).astype(jnp.int32)
    local_rows = chosen[:, 0] - tile_index * tile_rows
    local_columns = chosen[:, 1]
    order = jnp.reshape(batch_index, (1,)).astype(jnp.int32)
    patches = cut_patches(object_field, mine, partner, local_rows, local_columns, order, width)
    number = patches.shape[0]
    coef = jnp.where(
        segment == depth_count - 1, jnp.float32(DETECTOR_COEF), jnp.float32(SLICE_COEF)
    )
    chirp_re, chirp_im = chirp_parts(width, coef)
    start = jnp.broadcast_to(probe[None], (number, 2, width, width))

    chirps = jnp.stack([chirp_re, chirp_im])
    dft_re, dft_im = dft_parts(width)
    blocks = (
        jnp.concatenate([dft_re, dft_im], axis=0),
        jnp.concatenate([dft_re, dft_im], axis=1),
    )

    def forward_all(waves):
        return run_first(
            waves, object_field, mine, partner, local_rows, local_columns, order, chirps, blocks
        )

    def silent(waves):
        return jnp.zeros_like(waves)

    carry = start
    inputs = start
    for turn in range(depth_count - 1):
        if turn > 0:
            carry = lax.ppermute(carry, "depth", [(turn - 1, turn)])
            inputs = jnp.where(segment == turn, carry, inputs)
        carry = lax.cond(segment == turn, forward_all, silent, carry)

    measured, carry = lax.optimization_barrier((measured, carry))
    both_measured = lax.ppermute(measured, "batch", pairs)
    height = tile_rows + width
    scalars = (local_rows, local_columns, live.astype(jnp.int32), slot, other)

    def last_pass(incoming):
        return run_adjoint(
            incoming, patches, chirps, blocks, scalars, (measured, both_measured),
            height, columns_all, True,
        )

    def last_silent(incoming):
        return (jnp.zeros_like(incoming), jnp.zeros_like(incoming))

    if depth_count > 1:
        carry = lax.ppermute(carry, "depth", [(depth_count - 2, depth_count - 1)])
    arrived_last = carry
    carry, spread_last = lax.cond(segment == depth_count - 1, last_pass, last_silent, carry)
    gradient = lax.cond(
        segment == depth_count - 1,
        lambda s, a: run_place(s, a, scalars, height, columns_all),
        lambda s, a: jnp.zeros((2, height, columns_all), jnp.bfloat16),
        spread_last,
        arrived_last,
    )

    def back_pass(incoming, previous):
        return run_adjoint(
            incoming, patches, chirps, blocks, scalars, (inputs,), height, columns_all, False
        )

    def opening_pass(incoming, previous):
        (gradient,) = run_adjoint(
            incoming, patches, chirps, blocks, scalars, (inputs,), height, columns_all, False,
            opening=True,
        )
        return (incoming, gradient)

    def back_silent(incoming, previous):
        return (jnp.zeros_like(incoming), previous)

    for turn in reversed(range(depth_count - 1)):
        carry = lax.ppermute(carry, "depth", [(turn + 1, turn)])
        step = opening_pass if turn == 0 else back_pass
        carry, gradient = lax.cond(segment == turn, step, back_silent, carry, gradient)

    gradient = gradient.astype(jnp.bfloat16)
    spill = gradient[:, tile_rows:, :]
    keep = lax.dynamic_slice_in_dim(spill, batch_index * half, half, 2)
    give = lax.dynamic_slice_in_dim(spill, (1 - batch_index) * half, half, 2)
    got = lax.ppermute(give, "batch", pairs)
    spill_sum = (keep.astype(jnp.float32) + got.astype(jnp.float32)).astype(jnp.bfloat16)
    arrived = lax.ppermute(spill_sum, "tile", [(t, t + 1) for t in range(tile_count - 1)])
    own = gradient[:, :tile_rows, :]
    other = lax.ppermute(own, "batch", pairs)
    arrived_other = lax.ppermute(arrived, "batch", pairs)
    incoming = jnp.where(
        first_core,
        jnp.concatenate([arrived, arrived_other], axis=2),
        jnp.concatenate([arrived_other, arrived], axis=2),
    )
    summed = own.astype(jnp.float32) + other.astype(jnp.float32)
    summed = summed.at[:, :width, :].add(incoming.astype(jnp.float32))
    return summed[None]


def solution(mesh):
    placed = (
        P(("groups", "depth"), None, "tile", None),
        P("groups", None, None),
        P(("groups", "tile", "batch"), None),
        P(("groups", "tile", "batch")),
        P(("groups", "tile", "batch"), None, None),
    )
    return jax.shard_map(
        local,
        mesh=mesh,
        in_specs=placed,
        out_specs=P(("groups", "depth"), None, "tile", None),
        check_vma=False,
    )
```

```python
import math

import jax
import jax.numpy as jnp
from jax import lax
from jax.sharding import PartitionSpec as P
from jax.experimental import pallas as pl
from jax.experimental.pallas import tpu as pltpu

SLICE_COEF = 0.002
DETECTOR_COEF = 0.006
RESIDUAL_SCALE = 0.125


def from_behind(block, axis, distance):
    devices = range(lax.axis_size(axis))
    route = [(i - distance, i) for i in devices if i - distance in devices]
    return lax.ppermute(block, axis, route)


def dft_block(width, sign):
    freq = jnp.arange(width, dtype=jnp.int32)
    product = freq[:, None] * freq[None, :] % width
    angle = 2.0 * math.pi / width * product.astype(jnp.float32)
    scale = 1.0 / math.sqrt(width)
    real_part = (jnp.cos(angle) * scale).astype(jnp.bfloat16)
    imag_part = (sign * jnp.sin(angle) * scale).astype(jnp.bfloat16)
    upper = jnp.concatenate([real_part, -imag_part], axis=1)
    lower = jnp.concatenate([imag_part, real_part], axis=1)
    return jnp.concatenate([upper, lower], axis=0)


def dft_right(width, sign):
    freq = jnp.arange(width, dtype=jnp.int32)
    product = freq[:, None] * freq[None, :] % width
    angle = 2.0 * math.pi / width * product.astype(jnp.float32)
    scale = 1.0 / math.sqrt(width)
    real_part = (jnp.cos(angle) * scale).astype(jnp.bfloat16)
    imag_part = (sign * jnp.sin(angle) * scale).astype(jnp.bfloat16)
    upper = jnp.concatenate([real_part, imag_part], axis=1)
    lower = jnp.concatenate([-imag_part, real_part], axis=1)
    return jnp.concatenate([upper, lower], axis=0)


def dft_parts(width):
    freq = jnp.arange(width, dtype=jnp.int32)
    product = freq[:, None] * freq[None, :] % width
    angle = 2.0 * math.pi / width * product.astype(jnp.float32)
    scale = 1.0 / math.sqrt(width)
    real_part = (jnp.cos(angle) * scale).astype(jnp.bfloat16)
    imag_part = (-jnp.sin(angle) * scale).astype(jnp.bfloat16)
    return (real_part, imag_part)


def chirp_parts(width, coef):
    freq = jnp.arange(width, dtype=jnp.int32)
    shifted = (freq + width // 2) % width - width // 2
    square = shifted * shifted
    total = (square[:, None] + square[None, :]).astype(jnp.float32)
    phase = -coef * total
    return (jnp.cos(phase), jnp.sin(phase))


def left_apply(block, waves):
    number = waves.shape[0]
    width = waves.shape[2]
    stacked = waves.reshape(number, 2 * width, width)
    result = jnp.einsum("ij,gjk->gik", block, stacked, preferred_element_type=jnp.float32)
    return result.reshape(number, 2, width, width)


def propagate(waves, forward_block, inverse_block, chirp_re, chirp_im):
    first = left_apply(forward_block, waves).astype(jnp.bfloat16)
    spectrum = left_apply(forward_block, jnp.swapaxes(first, -1, -2))
    spec_re = spectrum[:, 0]
    spec_im = spectrum[:, 1]
    filtered = jnp.stack(
        [spec_re * chirp_re - spec_im * chirp_im, spec_re * chirp_im + spec_im * chirp_re], axis=1
    ).astype(jnp.bfloat16)
    back = left_apply(inverse_block, filtered).astype(jnp.bfloat16)
    return left_apply(inverse_block, jnp.swapaxes(back, -1, -2)).astype(jnp.bfloat16)


def transmit(waves, patch):
    values = waves.astype(jnp.float32)
    wave_re = values[:, 0]
    wave_im = values[:, 1]
    return jnp.stack(
        [
            patch[:, 0] * wave_re - patch[:, 1] * wave_im,
            patch[:, 0] * wave_im + patch[:, 1] * wave_re,
        ],
        axis=1,
    ).astype(jnp.bfloat16)


def residual_wave(waves, measured):
    values = waves.astype(jnp.float32)
    intensity = values[:, 0] * values[:, 0] + values[:, 1] * values[:, 1]
    weight = RESIDUAL_SCALE * (intensity - measured)
    return jnp.stack([weight * values[:, 0], weight * values[:, 1]], axis=1).astype(jnp.bfloat16)


def adjoint_terms(incoming, forward_block, inverse_block, chirp_re, chirp_im, inputs, patch):
    spread = propagate(incoming, forward_block, inverse_block, chirp_re, -chirp_im).astype(
        jnp.float32
    )
    source = inputs.astype(jnp.float32)
    term = jnp.stack(
        [
            source[:, 0] * spread[:, 0] + source[:, 1] * spread[:, 1],
            source[:, 0] * spread[:, 1] - source[:, 1] * spread[:, 0],
        ],
        axis=1,
    )
    passed = jnp.stack(
        [
            patch[:, 0] * spread[:, 0] + patch[:, 1] * spread[:, 1],
            patch[:, 0] * spread[:, 1] - patch[:, 1] * spread[:, 0],
        ],
        axis=1,
    ).astype(jnp.bfloat16)
    return (passed, term)


def wave_kernel(transmit_first, residual_after, backward):
    def kernel(*refs):
        refs = list(refs)
        wave_ref = refs.pop(0)
        patch_ref = refs.pop(0)
        chirp_ref = refs.pop(0)
        blocks = refs[:2]
        refs = refs[2:]
        extra_ref = refs.pop(0) if (residual_after or backward) else None
        wave = wave_ref[0].astype(jnp.float32)
        patch_re = patch_ref[0, 0]
        patch_im = patch_ref[0, 1]
        if transmit_first:
            wave_re = patch_re * wave[0] - patch_im * wave[1]
            wave_im = patch_re * wave[1] + patch_im * wave[0]
        else:
            wave_re = wave[0]
            wave_im = wave[1]
        chirp_re = chirp_ref[0]
        chirp_im = chirp_ref[1]
        if backward:
            chirp_im = -chirp_im
        out_re, out_im = propagate_block(wave_re, wave_im, blocks, chirp_re, chirp_im)
        if residual_after:
            measured = extra_ref[0]
            weight = RESIDUAL_SCALE * (out_re * out_re + out_im * out_im - measured)
            result_ref = refs[0]
            result_ref[0, 0] = (weight * out_re).astype(jnp.bfloat16)
            result_ref[0, 1] = (weight * out_im).astype(jnp.bfloat16)
        elif backward:
            source = extra_ref[0].astype(jnp.float32)
            passed_ref, term_ref = refs[0], refs[1]
            passed_ref[0, 0] = (patch_re * out_re + patch_im * out_im).astype(jnp.bfloat16)
            passed_ref[0, 1] = (patch_re * out_im - patch_im * out_re).astype(jnp.bfloat16)
            term_ref[0, 0] = source[0] * out_re + source[1] * out_im
            term_ref[0, 1] = source[0] * out_im - source[1] * out_re
        else:
            result_ref = refs[0]
            result_ref[0, 0] = out_re.astype(jnp.bfloat16)
            result_ref[0, 1] = out_im.astype(jnp.bfloat16)

    return kernel


def run_waves(waves, patches, chirps, blocks, extra=None, transmit_first=True, residual_after=False, backward=False):
    number, _, width, _ = waves.shape
    wave_spec = pl.BlockSpec((1, 2, width, width), lambda i: (i, 0, 0, 0))
    chirp_spec = pl.BlockSpec((2, width, width), lambda i: (0, 0, 0))
    in_specs = [wave_spec, wave_spec, chirp_spec] + [
        pl.BlockSpec((2 * width, width), lambda i: (0, 0)),
        pl.BlockSpec((width, 2 * width), lambda i: (0, 0)),
    ]
    args = [waves, patches, chirps] + list(blocks)
    if residual_after:
        in_specs.append(pl.BlockSpec((1, width, width), lambda i: (i, 0, 0)))
        args.append(extra)
    if backward:
        in_specs.append(wave_spec)
        args.append(extra)
        out_shape = (
            jax.ShapeDtypeStruct(waves.shape, jnp.bfloat16),
            jax.ShapeDtypeStruct(waves.shape, jnp.float32),
        )
        out_specs = (wave_spec, wave_spec)
    else:
        out_shape = jax.ShapeDtypeStruct(waves.shape, jnp.bfloat16)
        out_specs = wave_spec
    return pl.pallas_call(
        wave_kernel(transmit_first, residual_after, backward),
        grid=(number,),
        in_specs=in_specs,
        out_specs=out_specs,
        out_shape=out_shape,
    )(*args)


def scatter_kernel(rows_ref, columns_ref, live_ref, terms_ref, out_ref):
    index = pl.program_id(0)

    @pl.when(index == 0)
    def _():
        out_ref[...] = jnp.zeros(out_ref.shape, out_ref.dtype)

    width = terms_ref.shape[2]
    height = out_ref.shape[1]
    columns_all = out_ref.shape[2]
    row = rows_ref[index]
    column = columns_ref[index]
    alive = live_ref[index] > 0
    for part in range(2):
        term = jnp.where(alive, terms_ref[0, part], 0.0)
        wide = jnp.concatenate(
            [term, jnp.zeros((width, columns_all - width), jnp.float32)], axis=1
        )
        wide = pltpu.roll(wide, column, 1)
        tall = jnp.concatenate(
            [wide, jnp.zeros((height - width, columns_all), jnp.float32)], axis=0
        )
        tall = pltpu.roll(tall, row, 0)
        out_ref[part] = out_ref[part] + tall


def scatter_terms(terms, rows, columns, live, height, columns_all):
    number, _, width, _ = terms.shape
    grid_spec = pltpu.PrefetchScalarGridSpec(
        num_scalar_prefetch=3,
        grid=(number,),
        in_specs=[pl.BlockSpec((1, 2, width, width), lambda i, r, c, a: (i, 0, 0, 0))],
        out_specs=pl.BlockSpec((2, height, columns_all), lambda i, r, c, a: (0, 0, 0)),
    )
    return pl.pallas_call(
        scatter_kernel,
        grid_spec=grid_spec,
        out_shape=jax.ShapeDtypeStruct((2, height, columns_all), jnp.float32),
    )(rows, columns, live.astype(jnp.int32), terms)


def cut_kernel(rows_ref, columns_ref, order_ref, tile_ref, mine_ref, partner_ref, out_ref):
    index = pl.program_id(0)
    width = out_ref.shape[2]
    height = tile_ref.shape[2] + mine_ref.shape[2]
    columns_all = tile_ref.shape[3]
    row_shift = (height - rows_ref[index]) % height
    column_shift = (columns_all - columns_ref[index]) % columns_all
    first = order_ref[0] == 0
    for part in range(2):
        mine = mine_ref[0, part].astype(jnp.float32)
        partner = partner_ref[0, part].astype(jnp.float32)
        rim = jnp.concatenate(
            [jnp.where(first, mine, partner), jnp.where(first, partner, mine)], axis=1
        )
        full = jnp.concatenate([tile_ref[0, part], rim], axis=0)
        full = pltpu.roll(full, row_shift, 0)[:width]
        full = pltpu.roll(full, column_shift, 1)[:, :width]
        out_ref[0, part] = full


def cut_patches(tile, mine, partner, rows, columns, order, width):
    number = rows.shape[0]
    grid_spec = pltpu.PrefetchScalarGridSpec(
        num_scalar_prefetch=3,
        grid=(number,),
        in_specs=[
            pl.BlockSpec(tile.shape, lambda i, r, c, o: (0, 0, 0, 0)),
            pl.BlockSpec(mine.shape, lambda i, r, c, o: (0, 0, 0, 0)),
            pl.BlockSpec(partner.shape, lambda i, r, c, o: (0, 0, 0, 0)),
        ],
        out_specs=pl.BlockSpec((1, 2, width, width), lambda i, r, c, o: (i, 0, 0, 0)),
    )
    return pl.pallas_call(
        cut_kernel,
        grid_spec=grid_spec,
        out_shape=jax.ShapeDtypeStruct((number, 2, width, width), jnp.float32),
    )(rows, columns, order, tile, mine, partner)


def propagate_block(wave_re, wave_im, blocks, chirp_re, chirp_im):
    rows_ref, cols_ref = blocks
    width = wave_re.shape[0]
    dft_rows = rows_ref[...]
    dft_cols = cols_ref[...]

    def left(part_re, part_im):
        lanes = jnp.concatenate([part_re, part_im], axis=1).astype(jnp.bfloat16)
        return jnp.dot(dft_rows, lanes, preferred_element_type=jnp.float32)

    def right(part_re, part_im):
        rows = jnp.concatenate([part_re, part_im], axis=0).astype(jnp.bfloat16)
        return jnp.dot(rows, dft_cols, preferred_element_type=jnp.float32)

    first = left(wave_re, wave_im)
    z_re = (first[:width, :width] - first[width:, width:]).astype(jnp.bfloat16)
    z_im = (first[:width, width:] + first[width:, :width]).astype(jnp.bfloat16)
    second = right(z_re, z_im)
    spec_re = second[:width, :width] - second[width:, width:]
    spec_im = second[:width, width:] + second[width:, :width]
    w_re = spec_re * chirp_re - spec_im * chirp_im
    w_im = spec_re * chirp_im + spec_im * chirp_re
    third = right(w_re.astype(jnp.bfloat16), w_im.astype(jnp.bfloat16))
    v_re = (third[:width, :width] + third[width:, width:]).astype(jnp.bfloat16)
    v_im = (third[width:, :width] - third[:width, width:]).astype(jnp.bfloat16)
    fourth = left(v_re, v_im)
    out_re = (fourth[:width, :width] + fourth[width:, width:]).astype(jnp.bfloat16)
    out_im = (fourth[:width, width:] - fourth[width:, :width]).astype(jnp.bfloat16)
    return (out_re.astype(jnp.float32), out_im.astype(jnp.float32))


def place_term(term_re, term_im, row, column, alive, total_ref, direct_ref=None):
    width = term_re.shape[0]
    height = total_ref.shape[1]
    columns_all = total_ref.shape[2]
    row_shift = row % height
    column_shift = column % columns_all
    for part, term in enumerate((term_re, term_im)):
        term = jnp.where(alive, term, 0.0)
        wide = jnp.concatenate(
            [term, jnp.zeros((width, columns_all - width), jnp.float32)], axis=1
        )
        wide = pltpu.roll(wide, column_shift, 1)
        if height == 2 * width:
            rolled = pltpu.roll(wide, row % width, 0)
            below = lax.broadcasted_iota(jnp.int32, rolled.shape, 0) < row
            upper = jnp.where(below, 0.0, rolled)
            lower = jnp.where(below, rolled, 0.0)
            if direct_ref is None:
                total_ref[part, :width] = total_ref[part, :width] + upper
                total_ref[part, width:] = total_ref[part, width:] + lower
            else:
                direct_ref[part, :width] = upper.astype(direct_ref.dtype)
                direct_ref[part, width:] = lower.astype(direct_ref.dtype)
            continue
        tall = jnp.concatenate(
            [wide, jnp.zeros((height - width, columns_all), jnp.float32)], axis=0
        )
        if direct_ref is None:
            total_ref[part] = total_ref[part] + pltpu.roll(tall, row_shift, 0)
        else:
            direct_ref[part] = pltpu.roll(tall, row_shift, 0).astype(direct_ref.dtype)


def adjoint_kernel(last, single, opening=False):
    def kernel(rows_ref, columns_ref, live_ref, slot_ref, other_ref, *refs):
        refs = list(refs)
        wave_ref = refs.pop(0)
        patch_ref = None if opening else refs.pop(0)
        chirp_ref = refs.pop(0)
        blocks = refs[:2]
        refs = refs[2:]
        if last:
            own_ref = refs.pop(0)
            partner_ref = refs.pop(0)
        else:
            source_ref = refs.pop(0)
        if opening:
            grad_ref, total_ref = refs
            passed_ref = None
        else:
            passed_ref, grad_ref, total_ref = refs
        index = pl.program_id(0)

        if not single:
            @pl.when(index == 0)
            def _():
                total_ref[...] = jnp.zeros(total_ref.shape, total_ref.dtype)

        wave = wave_ref[0].astype(jnp.float32)
        if not opening:
            patch_re = patch_ref[0, 0]
            patch_im = patch_ref[0, 1]
        chirp_re = chirp_ref[0]
        chirp_im = chirp_ref[1]
        if last:
            source_re = wave[0]
            source_im = wave[1]
            lit_re = patch_re * wave[0] - patch_im * wave[1]
            lit_im = patch_re * wave[1] + patch_im * wave[0]
            out_re, out_im = propagate_block(lit_re, lit_im, blocks, chirp_re, chirp_im)
            measured = jnp.where(other_ref[index] > 0, partner_ref[0], own_ref[0])
            weight = RESIDUAL_SCALE * (out_re * out_re + out_im * out_im - measured)
            in_re = (weight * out_re).astype(jnp.bfloat16).astype(jnp.float32)
            in_im = (weight * out_im).astype(jnp.bfloat16).astype(jnp.float32)
        else:
            source = source_ref[0].astype(jnp.float32)
            source_re = source[0]
            source_im = source[1]
            in_re = wave[0]
            in_im = wave[1]
        spread_re, spread_im = propagate_block(in_re, in_im, blocks, chirp_re, -chirp_im)
        if not opening:
            passed_ref[0, 0] = (patch_re * spread_re + patch_im * spread_im).astype(jnp.bfloat16)
            passed_ref[0, 1] = (patch_re * spread_im - patch_im * spread_re).astype(jnp.bfloat16)
        if last:
            grad_ref[0, 0] = spread_re.astype(jnp.bfloat16)
            grad_ref[0, 1] = spread_im.astype(jnp.bfloat16)
            return
        term_re = source_re * spread_re + source_im * spread_im
        term_im = source_re * spread_im - source_im * spread_re
        place_term(
            term_re, term_im, rows_ref[index], columns_ref[index], live_ref[index] > 0,
            total_ref, grad_ref if single else None,
        )

        if not single:
            @pl.when(index == pl.num_programs(0) - 1)
            def _():
                grad_ref[...] = total_ref[...].astype(grad_ref.dtype)

    return kernel


def run_adjoint(waves, patches, chirps, blocks, scalars, extra, height, columns_all, last,
                opening=False):
    number, _, width, _ = waves.shape
    wave_spec = pl.BlockSpec((1, 2, width, width), lambda i, *s: (i, 0, 0, 0))
    chirp_spec = pl.BlockSpec((2, width, width), lambda i, *s: (0, 0, 0))
    in_specs = [wave_spec] + ([] if opening else [wave_spec]) + [chirp_spec] + [
        pl.BlockSpec((2 * width, width), lambda i, *s: (0, 0)),
        pl.BlockSpec((width, 2 * width), lambda i, *s: (0, 0)),
    ]
    if last:
        slot_spec = pl.BlockSpec((1, width, width), lambda i, r, c, a, s, o: (s[i], 0, 0))
        in_specs += [slot_spec, slot_spec]
    else:
        in_specs += [wave_spec]
    grid_spec = pltpu.PrefetchScalarGridSpec(
        num_scalar_prefetch=5,
        grid=(number,),
        in_specs=in_specs,
        out_specs=((() if opening else (wave_spec,))
                   + ((wave_spec,) if last else
                      (pl.BlockSpec((2, height, columns_all), lambda i, *s: (0, 0, 0)),))),
        scratch_shapes=[pltpu.VMEM((2, height, columns_all), jnp.float32)],
    )
    return pl.pallas_call(
        adjoint_kernel(last, number == 1, opening),
        grid_spec=grid_spec,
        out_shape=((() if opening else (jax.ShapeDtypeStruct(waves.shape, jnp.bfloat16),))
                   + ((jax.ShapeDtypeStruct(waves.shape, jnp.bfloat16),) if last else
                      (jax.ShapeDtypeStruct((2, height, columns_all), jnp.bfloat16),))),
    )(*scalars, waves, *(() if opening else (patches,)), chirps, *blocks, *extra)


def place_kernel(rows_ref, columns_ref, live_ref, spread_ref, source_ref, grad_ref, total_ref):
    index = pl.program_id(0)

    @pl.when(index == 0)
    def _():
        total_ref[...] = jnp.zeros(total_ref.shape, total_ref.dtype)

    spread = spread_ref[0].astype(jnp.float32)
    source = source_ref[0].astype(jnp.float32)
    term_re = source[0] * spread[0] + source[1] * spread[1]
    term_im = source[0] * spread[1] - source[1] * spread[0]
    place_term(
        term_re, term_im, rows_ref[index], columns_ref[index], live_ref[index] > 0, total_ref
    )

    @pl.when(index == pl.num_programs(0) - 1)
    def _():
        grad_ref[...] = total_ref[...].astype(grad_ref.dtype)


def run_place(spread, source, scalars, height, columns_all):
    number, _, width, _ = spread.shape
    wave_spec = pl.BlockSpec((1, 2, width, width), lambda i, *s: (i, 0, 0, 0))
    grid_spec = pltpu.PrefetchScalarGridSpec(
        num_scalar_prefetch=3,
        grid=(number,),
        in_specs=[wave_spec, wave_spec],
        out_specs=pl.BlockSpec((2, height, columns_all), lambda i, *s: (0, 0, 0)),
        scratch_shapes=[pltpu.VMEM((2, height, columns_all), jnp.float32)],
    )
    return pl.pallas_call(
        place_kernel,
        grid_spec=grid_spec,
        out_shape=jax.ShapeDtypeStruct((2, height, columns_all), jnp.bfloat16),
    )(*scalars[:3], spread, source)


def first_kernel(rows_ref, columns_ref, order_ref, wave_ref, tile_ref, mine_ref, partner_ref,
                 chirp_ref, dft_rows_ref, dft_cols_ref, result_ref):
    index = pl.program_id(0)
    width = wave_ref.shape[2]
    height = tile_ref.shape[2] + mine_ref.shape[2]
    columns_all = tile_ref.shape[3]
    row_shift = (height - rows_ref[index]) % height
    column_shift = (columns_all - columns_ref[index]) % columns_all
    first = order_ref[0] == 0
    patch = []
    for part in range(2):
        mine = mine_ref[0, part].astype(jnp.float32)
        partner = partner_ref[0, part].astype(jnp.float32)
        rim = jnp.concatenate(
            [jnp.where(first, mine, partner), jnp.where(first, partner, mine)], axis=1
        )
        full = jnp.concatenate([tile_ref[0, part], rim], axis=0)
        full = pltpu.roll(full, row_shift, 0)[:width]
        patch.append(pltpu.roll(full, column_shift, 1)[:, :width])
    wave = wave_ref[0].astype(jnp.float32)
    wave_re = patch[0] * wave[0] - patch[1] * wave[1]
    wave_im = patch[0] * wave[1] + patch[1] * wave[0]
    out_re, out_im = propagate_block(
        wave_re, wave_im, (dft_rows_ref, dft_cols_ref), chirp_ref[0], chirp_ref[1]
    )
    result_ref[0, 0] = out_re.astype(jnp.bfloat16)
    result_ref[0, 1] = out_im.astype(jnp.bfloat16)


def run_first(waves, tile, mine, partner, rows, columns, order, chirps, blocks):
    number, _, width, _ = waves.shape
    wave_spec = pl.BlockSpec((1, 2, width, width), lambda i, r, c, o: (i, 0, 0, 0))
    whole = lambda shape: pl.BlockSpec(shape, lambda i, r, c, o: (0,) * len(shape))
    grid_spec = pltpu.PrefetchScalarGridSpec(
        num_scalar_prefetch=3,
        grid=(number,),
        in_specs=[
            wave_spec,
            whole(tile.shape),
            whole(mine.shape),
            whole(partner.shape),
            whole(chirps.shape),
            whole(blocks[0].shape),
            whole(blocks[1].shape),
        ],
        out_specs=wave_spec,
    )
    return pl.pallas_call(
        first_kernel,
        grid_spec=grid_spec,
        out_shape=jax.ShapeDtypeStruct(waves.shape, jnp.bfloat16),
    )(rows, columns, order, waves, tile, mine, partner, chirps, *blocks)


def hop(block, axis, route):
    parts = [lax.ppermute(block[:, k], axis, route) for k in range(block.shape[1])]
    return jnp.stack(parts, axis=1)


def local(object_field, probe, positions, counts, measured):
    width = probe.shape[1]
    tile_rows = object_field.shape[2]
    columns_all = object_field.shape[3]
    tile_index = lax.axis_index("tile")
    tile_count = lax.axis_size("tile")
    segment = lax.axis_index("depth")
    depth_count = lax.axis_size("depth")
    batch_index = lax.axis_index("batch")
    batch_count = lax.axis_size("batch")
    half = columns_all // batch_count
    wanted = lax.dynamic_slice_in_dim(object_field[:, :, :width, :], batch_index * half, half, 3)
    mine = from_behind(wanted.astype(jnp.bfloat16), "tile", -1)
    pairs = [(b, (b + 1) % batch_count) for b in range(batch_count)]
    partner = lax.ppermute(mine, "batch", pairs)
    capacity = positions.shape[0]
    share = -(-capacity // batch_count)
    first_core = batch_index == 0
    both_positions = lax.ppermute(positions, "batch", pairs)
    both_counts = lax.ppermute(counts, "batch", pairs)
    all_positions = jnp.where(
        first_core,
        jnp.concatenate([positions, both_positions]),
        jnp.concatenate([both_positions, positions]),
    )
    all_counts = jnp.where(
        first_core, jnp.concatenate([counts, both_counts]), jnp.concatenate([both_counts, counts])
    )
    entry = batch_index * share + jnp.arange(share, dtype=jnp.int32)
    live = entry < all_counts[0] + all_counts[1]
    later = entry >= all_counts[0]
    slot = jnp.clip(jnp.where(later, entry - all_counts[0], entry), 0, capacity - 1)
    flat = jnp.where(later, capacity, 0) + slot
    chosen = all_positions[flat]
    other = (later == first_core).astype(jnp.int32)
    local_rows = chosen[:, 0] - tile_index * tile_rows
    local_columns = chosen[:, 1]
    order = jnp.reshape(batch_index, (1,)).astype(jnp.int32)
    patches = cut_patches(object_field, mine, partner, local_rows, local_columns, order, width)
    number = patches.shape[0]
    coef = jnp.where(
        segment == depth_count - 1, jnp.float32(DETECTOR_COEF), jnp.float32(SLICE_COEF)
    )
    chirp_re, chirp_im = chirp_parts(width, coef)
    start = jnp.broadcast_to(probe[None], (number, 2, width, width))

    chirps = jnp.stack([chirp_re, chirp_im])
    dft_re, dft_im = dft_parts(width)
    blocks = (
        jnp.concatenate([dft_re, dft_im], axis=0),
        jnp.concatenate([dft_re, dft_im], axis=1),
    )

    def forward_all(waves):
        return run_first(
            waves, object_field, mine, partner, local_rows, local_columns, order, chirps, blocks
        )

    def silent(waves):
        return jnp.zeros_like(waves)

    carry = start
    inputs = start
    for turn in range(depth_count - 1):
        if turn > 0:
            carry = hop(carry, "depth", [(turn - 1, turn)])
            inputs = jnp.where(segment == turn, carry, inputs)
        carry = lax.cond(segment == turn, forward_all, silent, carry)

    measured, carry = lax.optimization_barrier((measured, carry))
    both_measured = lax.ppermute(measured, "batch", pairs)
    height = tile_rows + width
    scalars = (local_rows, local_columns, live.astype(jnp.int32), slot, other)

    def last_pass(incoming):
        return run_adjoint(
            incoming, patches, chirps, blocks, scalars, (measured, both_measured),
            height, columns_all, True,
        )

    def last_silent(incoming):
        return (jnp.zeros_like(incoming), jnp.zeros_like(incoming))

    if depth_count > 1:
        carry = hop(carry, "depth", [(depth_count - 2, depth_count - 1)])
    arrived_last = carry
    carry, spread_last = lax.cond(segment == depth_count - 1, last_pass, last_silent, carry)
    gradient = lax.cond(
        segment == depth_count - 1,
        lambda s, a: run_place(s, a, scalars, height, columns_all),
        lambda s, a: jnp.zeros((2, height, columns_all), jnp.bfloat16),
        spread_last,
        arrived_last,
    )

    def back_pass(incoming, previous):
        return run_adjoint(
            incoming, patches, chirps, blocks, scalars, (inputs,), height, columns_all, False
        )

    def opening_pass(incoming, previous):
        (gradient,) = run_adjoint(
            incoming, patches, chirps, blocks, scalars, (inputs,), height, columns_all, False,
            opening=True,
        )
        return (incoming, gradient)

    def back_silent(incoming, previous):
        return (jnp.zeros_like(incoming), previous)

    for turn in reversed(range(depth_count - 1)):
        carry = hop(carry, "depth", [(turn + 1, turn)])
        step = opening_pass if turn == 0 else back_pass
        carry, gradient = lax.cond(segment == turn, step, back_silent, carry, gradient)

    gradient = gradient.astype(jnp.bfloat16)
    spill = gradient[:, tile_rows:, :]
    keep = lax.dynamic_slice_in_dim(spill, batch_index * half, half, 2)
    give = lax.dynamic_slice_in_dim(spill, (1 - batch_index) * half, half, 2)
    got = lax.ppermute(give, "batch", pairs)
    spill_sum = (keep.astype(jnp.float32) + got.astype(jnp.float32)).astype(jnp.bfloat16)
    arrived = lax.ppermute(spill_sum, "tile", [(t, t + 1) for t in range(tile_count - 1)])
    own = gradient[:, :tile_rows, :]
    other = lax.ppermute(own, "batch", pairs)
    arrived_other = lax.ppermute(arrived, "batch", pairs)
    incoming = jnp.where(
        first_core,
        jnp.concatenate([arrived, arrived_other], axis=2),
        jnp.concatenate([arrived_other, arrived], axis=2),
    )
    summed = own.astype(jnp.float32) + other.astype(jnp.float32)
    summed = summed.at[:, :width, :].add(incoming.astype(jnp.float32))
    return summed[None]


def solution(mesh):
    placed = (
        P(("groups", "depth"), None, "tile", None),
        P("groups", None, None),
        P(("groups", "tile", "batch"), None),
        P(("groups", "tile", "batch")),
        P(("groups", "tile", "batch"), None, None),
    )
    return jax.shard_map(
        local,
        mesh=mesh,
        in_specs=placed,
        out_specs=P(("groups", "depth"), None, "tile", None),
        check_vma=False,
    )
```

```python
import math

import jax
import jax.numpy as jnp
from jax import lax
from jax.sharding import PartitionSpec as P
from jax.experimental import pallas as pl
from jax.experimental.pallas import tpu as pltpu

SLICE_COEF = 0.002
DETECTOR_COEF = 0.006
RESIDUAL_SCALE = 0.125


def from_behind(block, axis, distance):
    devices = range(lax.axis_size(axis))
    route = [(i - distance, i) for i in devices if i - distance in devices]
    return lax.ppermute(block, axis, route)


def dft_block(width, sign):
    freq = jnp.arange(width, dtype=jnp.int32)
    product = freq[:, None] * freq[None, :] % width
    angle = 2.0 * math.pi / width * product.astype(jnp.float32)
    scale = 1.0 / math.sqrt(width)
    real_part = (jnp.cos(angle) * scale).astype(jnp.bfloat16)
    imag_part = (sign * jnp.sin(angle) * scale).astype(jnp.bfloat16)
    upper = jnp.concatenate([real_part, -imag_part], axis=1)
    lower = jnp.concatenate([imag_part, real_part], axis=1)
    return jnp.concatenate([upper, lower], axis=0)


def dft_right(width, sign):
    freq = jnp.arange(width, dtype=jnp.int32)
    product = freq[:, None] * freq[None, :] % width
    angle = 2.0 * math.pi / width * product.astype(jnp.float32)
    scale = 1.0 / math.sqrt(width)
    real_part = (jnp.cos(angle) * scale).astype(jnp.bfloat16)
    imag_part = (sign * jnp.sin(angle) * scale).astype(jnp.bfloat16)
    upper = jnp.concatenate([real_part, imag_part], axis=1)
    lower = jnp.concatenate([-imag_part, real_part], axis=1)
    return jnp.concatenate([upper, lower], axis=0)


def dft_parts(width):
    freq = jnp.arange(width, dtype=jnp.int32)
    product = freq[:, None] * freq[None, :] % width
    angle = 2.0 * math.pi / width * product.astype(jnp.float32)
    scale = 1.0 / math.sqrt(width)
    real_part = (jnp.cos(angle) * scale).astype(jnp.bfloat16)
    imag_part = (-jnp.sin(angle) * scale).astype(jnp.bfloat16)
    return (real_part, imag_part)


def chirp_parts(width, coef):
    freq = jnp.arange(width, dtype=jnp.int32)
    shifted = (freq + width // 2) % width - width // 2
    square = shifted * shifted
    total = (square[:, None] + square[None, :]).astype(jnp.float32)
    phase = -coef * total
    return (jnp.cos(phase), jnp.sin(phase))


def left_apply(block, waves):
    number = waves.shape[0]
    width = waves.shape[2]
    stacked = waves.reshape(number, 2 * width, width)
    result = jnp.einsum("ij,gjk->gik", block, stacked, preferred_element_type=jnp.float32)
    return result.reshape(number, 2, width, width)


def propagate(waves, forward_block, inverse_block, chirp_re, chirp_im):
    first = left_apply(forward_block, waves).astype(jnp.bfloat16)
    spectrum = left_apply(forward_block, jnp.swapaxes(first, -1, -2))
    spec_re = spectrum[:, 0]
    spec_im = spectrum[:, 1]
    filtered = jnp.stack(
        [spec_re * chirp_re - spec_im * chirp_im, spec_re * chirp_im + spec_im * chirp_re], axis=1
    ).astype(jnp.bfloat16)
    back = left_apply(inverse_block, filtered).astype(jnp.bfloat16)
    return left_apply(inverse_block, jnp.swapaxes(back, -1, -2)).astype(jnp.bfloat16)


def transmit(waves, patch):
    values = waves.astype(jnp.float32)
    wave_re = values[:, 0]
    wave_im = values[:, 1]
    return jnp.stack(
        [
            patch[:, 0] * wave_re - patch[:, 1] * wave_im,
            patch[:, 0] * wave_im + patch[:, 1] * wave_re,
        ],
        axis=1,
    ).astype(jnp.bfloat16)


def residual_wave(waves, measured):
    values = waves.astype(jnp.float32)
    intensity = values[:, 0] * values[:, 0] + values[:, 1] * values[:, 1]
    weight = RESIDUAL_SCALE * (intensity - measured)
    return jnp.stack([weight * values[:, 0], weight * values[:, 1]], axis=1).astype(jnp.bfloat16)


def adjoint_terms(incoming, forward_block, inverse_block, chirp_re, chirp_im, inputs, patch):
    spread = propagate(incoming, forward_block, inverse_block, chirp_re, -chirp_im).astype(
        jnp.float32
    )
    source = inputs.astype(jnp.float32)
    term = jnp.stack(
        [
            source[:, 0] * spread[:, 0] + source[:, 1] * spread[:, 1],
            source[:, 0] * spread[:, 1] - source[:, 1] * spread[:, 0],
        ],
        axis=1,
    )
    passed = jnp.stack(
        [
            patch[:, 0] * spread[:, 0] + patch[:, 1] * spread[:, 1],
            patch[:, 0] * spread[:, 1] - patch[:, 1] * spread[:, 0],
        ],
        axis=1,
    ).astype(jnp.bfloat16)
    return (passed, term)


def wave_kernel(transmit_first, residual_after, backward):
    def kernel(*refs):
        refs = list(refs)
        wave_ref = refs.pop(0)
        patch_ref = refs.pop(0)
        chirp_ref = refs.pop(0)
        blocks = refs[:2]
        refs = refs[2:]
        extra_ref = refs.pop(0) if (residual_after or backward) else None
        wave = wave_ref[0].astype(jnp.float32)
        patch_re = patch_ref[0, 0]
        patch_im = patch_ref[0, 1]
        if transmit_first:
            wave_re = patch_re * wave[0] - patch_im * wave[1]
            wave_im = patch_re * wave[1] + patch_im * wave[0]
        else:
            wave_re = wave[0]
            wave_im = wave[1]
        chirp_re = chirp_ref[0]
        chirp_im = chirp_ref[1]
        if backward:
            chirp_im = -chirp_im
        out_re, out_im = propagate_block(wave_re, wave_im, blocks, chirp_re, chirp_im)
        if residual_after:
            measured = extra_ref[0]
            weight = RESIDUAL_SCALE * (out_re * out_re + out_im * out_im - measured)
            result_ref = refs[0]
            result_ref[0, 0] = (weight * out_re).astype(jnp.bfloat16)
            result_ref[0, 1] = (weight * out_im).astype(jnp.bfloat16)
        elif backward:
            source = extra_ref[0].astype(jnp.float32)
            passed_ref, term_ref = refs[0], refs[1]
            passed_ref[0, 0] = (patch_re * out_re + patch_im * out_im).astype(jnp.bfloat16)
            passed_ref[0, 1] = (patch_re * out_im - patch_im * out_re).astype(jnp.bfloat16)
            term_ref[0, 0] = source[0] * out_re + source[1] * out_im
            term_ref[0, 1] = source[0] * out_im - source[1] * out_re
        else:
            result_ref = refs[0]
            result_ref[0, 0] = out_re.astype(jnp.bfloat16)
            result_ref[0, 1] = out_im.astype(jnp.bfloat16)

    return kernel


def run_waves(waves, patches, chirps, blocks, extra=None, transmit_first=True, residual_after=False, backward=False):
    number, _, width, _ = waves.shape
    wave_spec = pl.BlockSpec((1, 2, width, width), lambda i: (i, 0, 0, 0))
    chirp_spec = pl.BlockSpec((2, width, width), lambda i: (0, 0, 0))
    in_specs = [wave_spec, wave_spec, chirp_spec] + [
        pl.BlockSpec((2 * width, width), lambda i: (0, 0)),
        pl.BlockSpec((width, 2 * width), lambda i: (0, 0)),
    ]
    args = [waves, patches, chirps] + list(blocks)
    if residual_after:
        in_specs.append(pl.BlockSpec((1, width, width), lambda i: (i, 0, 0)))
        args.append(extra)
    if backward:
        in_specs.append(wave_spec)
        args.append(extra)
        out_shape = (
            jax.ShapeDtypeStruct(waves.shape, jnp.bfloat16),
            jax.ShapeDtypeStruct(waves.shape, jnp.float32),
        )
        out_specs = (wave_spec, wave_spec)
    else:
        out_shape = jax.ShapeDtypeStruct(waves.shape, jnp.bfloat16)
        out_specs = wave_spec
    return pl.pallas_call(
        wave_kernel(transmit_first, residual_after, backward),
        grid=(number,),
        in_specs=in_specs,
        out_specs=out_specs,
        out_shape=out_shape,
    )(*args)


def scatter_kernel(rows_ref, columns_ref, live_ref, terms_ref, out_ref):
    index = pl.program_id(0)

    @pl.when(index == 0)
    def _():
        out_ref[...] = jnp.zeros(out_ref.shape, out_ref.dtype)

    width = terms_ref.shape[2]
    height = out_ref.shape[1]
    columns_all = out_ref.shape[2]
    row = rows_ref[index]
    column = columns_ref[index]
    alive = live_ref[index] > 0
    for part in range(2):
        term = jnp.where(alive, terms_ref[0, part], 0.0)
        wide = jnp.concatenate(
            [term, jnp.zeros((width, columns_all - width), jnp.float32)], axis=1
        )
        wide = pltpu.roll(wide, column, 1)
        tall = jnp.concatenate(
            [wide, jnp.zeros((height - width, columns_all), jnp.float32)], axis=0
        )
        tall = pltpu.roll(tall, row, 0)
        out_ref[part] = out_ref[part] + tall


def scatter_terms(terms, rows, columns, live, height, columns_all):
    number, _, width, _ = terms.shape
    grid_spec = pltpu.PrefetchScalarGridSpec(
        num_scalar_prefetch=3,
        grid=(number,),
        in_specs=[pl.BlockSpec((1, 2, width, width), lambda i, r, c, a: (i, 0, 0, 0))],
        out_specs=pl.BlockSpec((2, height, columns_all), lambda i, r, c, a: (0, 0, 0)),
    )
    return pl.pallas_call(
        scatter_kernel,
        grid_spec=grid_spec,
        out_shape=jax.ShapeDtypeStruct((2, height, columns_all), jnp.float32),
    )(rows, columns, live.astype(jnp.int32), terms)


def cut_kernel(rows_ref, columns_ref, order_ref, tile_ref, mine_ref, partner_ref, out_ref):
    index = pl.program_id(0)
    width = out_ref.shape[2]
    height = tile_ref.shape[2] + mine_ref.shape[2]
    columns_all = tile_ref.shape[3]
    row_shift = (height - rows_ref[index]) % height
    column_shift = (columns_all - columns_ref[index]) % columns_all
    first = order_ref[0] == 0
    for part in range(2):
        mine = mine_ref[0, part].astype(jnp.float32)
        partner = partner_ref[0, part].astype(jnp.float32)
        rim = jnp.concatenate(
            [jnp.where(first, mine, partner), jnp.where(first, partner, mine)], axis=1
        )
        full = jnp.concatenate([tile_ref[0, part], rim], axis=0)
        full = pltpu.roll(full, row_shift, 0)[:width]
        full = pltpu.roll(full, column_shift, 1)[:, :width]
        out_ref[0, part] = full


def cut_patches(tile, mine, partner, rows, columns, order, width):
    number = rows.shape[0]
    grid_spec = pltpu.PrefetchScalarGridSpec(
        num_scalar_prefetch=3,
        grid=(number,),
        in_specs=[
            pl.BlockSpec(tile.shape, lambda i, r, c, o: (0, 0, 0, 0)),
            pl.BlockSpec(mine.shape, lambda i, r, c, o: (0, 0, 0, 0)),
            pl.BlockSpec(partner.shape, lambda i, r, c, o: (0, 0, 0, 0)),
        ],
        out_specs=pl.BlockSpec((1, 2, width, width), lambda i, r, c, o: (i, 0, 0, 0)),
    )
    return pl.pallas_call(
        cut_kernel,
        grid_spec=grid_spec,
        out_shape=jax.ShapeDtypeStruct((number, 2, width, width), jnp.float32),
    )(rows, columns, order, tile, mine, partner)


def propagate_block(wave_re, wave_im, blocks, chirp_re, chirp_im):
    rows_ref, cols_ref = blocks
    width = wave_re.shape[0]
    dft_rows = rows_ref[...]
    dft_cols = cols_ref[...]

    def left(part_re, part_im):
        lanes = jnp.concatenate([part_re, part_im], axis=1).astype(jnp.bfloat16)
        return jnp.dot(dft_rows, lanes, preferred_element_type=jnp.float32)

    def right(part_re, part_im):
        rows = jnp.concatenate([part_re, part_im], axis=0).astype(jnp.bfloat16)
        return jnp.dot(rows, dft_cols, preferred_element_type=jnp.float32)

    first = left(wave_re, wave_im)
    z_re = (first[:width, :width] - first[width:, width:]).astype(jnp.bfloat16)
    z_im = (first[:width, width:] + first[width:, :width]).astype(jnp.bfloat16)
    second = right(z_re, z_im)
    spec_re = second[:width, :width] - second[width:, width:]
    spec_im = second[:width, width:] + second[width:, :width]
    w_re = spec_re * chirp_re - spec_im * chirp_im
    w_im = spec_re * chirp_im + spec_im * chirp_re
    third = right(w_re.astype(jnp.bfloat16), w_im.astype(jnp.bfloat16))
    v_re = (third[:width, :width] + third[width:, width:]).astype(jnp.bfloat16)
    v_im = (third[width:, :width] - third[:width, width:]).astype(jnp.bfloat16)
    fourth = left(v_re, v_im)
    out_re = (fourth[:width, :width] + fourth[width:, width:]).astype(jnp.bfloat16)
    out_im = (fourth[:width, width:] - fourth[width:, :width]).astype(jnp.bfloat16)
    return (out_re.astype(jnp.float32), out_im.astype(jnp.float32))


def place_term(term_re, term_im, row, column, alive, total_ref, direct_ref=None):
    width = term_re.shape[0]
    height = total_ref.shape[1]
    columns_all = total_ref.shape[2]
    row_shift = row % height
    column_shift = column % columns_all
    for part, term in enumerate((term_re, term_im)):
        term = jnp.where(alive, term, 0.0)
        wide = jnp.concatenate(
            [term, jnp.zeros((width, columns_all - width), jnp.float32)], axis=1
        )
        wide = pltpu.roll(wide, column_shift, 1)
        if height == 2 * width:
            rolled = pltpu.roll(wide, row % width, 0)
            below = lax.broadcasted_iota(jnp.int32, rolled.shape, 0) < row
            upper = jnp.where(below, 0.0, rolled)
            lower = jnp.where(below, rolled, 0.0)
            if direct_ref is None:
                total_ref[part, :width] = total_ref[part, :width] + upper
                total_ref[part, width:] = total_ref[part, width:] + lower
            else:
                direct_ref[part, :width] = upper.astype(direct_ref.dtype)
                direct_ref[part, width:] = lower.astype(direct_ref.dtype)
            continue
        tall = jnp.concatenate(
            [wide, jnp.zeros((height - width, columns_all), jnp.float32)], axis=0
        )
        if direct_ref is None:
            total_ref[part] = total_ref[part] + pltpu.roll(tall, row_shift, 0)
        else:
            direct_ref[part] = pltpu.roll(tall, row_shift, 0).astype(direct_ref.dtype)


def adjoint_kernel(last, single, opening=False):
    def kernel(rows_ref, columns_ref, live_ref, slot_ref, other_ref, *refs):
        refs = list(refs)
        wave_ref = refs.pop(0)
        patch_ref = None if opening else refs.pop(0)
        chirp_ref = refs.pop(0)
        blocks = refs[:2]
        refs = refs[2:]
        if last:
            own_ref = refs.pop(0)
            partner_ref = refs.pop(0)
        else:
            source_ref = refs.pop(0)
        if opening:
            grad_ref, total_ref = refs
            passed_ref = None
        else:
            passed_ref, grad_ref, total_ref = refs
        index = pl.program_id(0)

        if not single:
            @pl.when(index == 0)
            def _():
                total_ref[...] = jnp.zeros(total_ref.shape, total_ref.dtype)

        wave = wave_ref[0].astype(jnp.float32)
        if not opening:
            patch_re = patch_ref[0, 0]
            patch_im = patch_ref[0, 1]
        chirp_re = chirp_ref[0]
        chirp_im = chirp_ref[1]
        if last:
            source_re = wave[0]
            source_im = wave[1]
            lit_re = patch_re * wave[0] - patch_im * wave[1]
            lit_im = patch_re * wave[1] + patch_im * wave[0]
            out_re, out_im = propagate_block(lit_re, lit_im, blocks, chirp_re, chirp_im)
            measured = jnp.where(other_ref[index] > 0, partner_ref[0], own_ref[0])
            weight = RESIDUAL_SCALE * (out_re * out_re + out_im * out_im - measured)
            in_re = (weight * out_re).astype(jnp.bfloat16).astype(jnp.float32)
            in_im = (weight * out_im).astype(jnp.bfloat16).astype(jnp.float32)
        else:
            source = source_ref[0].astype(jnp.float32)
            source_re = source[0]
            source_im = source[1]
            in_re = wave[0]
            in_im = wave[1]
        spread_re, spread_im = propagate_block(in_re, in_im, blocks, chirp_re, -chirp_im)
        if not opening:
            passed_ref[0, 0] = (patch_re * spread_re + patch_im * spread_im).astype(jnp.bfloat16)
            passed_ref[0, 1] = (patch_re * spread_im - patch_im * spread_re).astype(jnp.bfloat16)
        if last:
            grad_ref[0, 0] = spread_re.astype(jnp.bfloat16)
            grad_ref[0, 1] = spread_im.astype(jnp.bfloat16)
            return
        term_re = source_re * spread_re + source_im * spread_im
        term_im = source_re * spread_im - source_im * spread_re
        place_term(
            term_re, term_im, rows_ref[index], columns_ref[index], live_ref[index] > 0,
            total_ref, grad_ref if single else None,
        )

        if not single:
            @pl.when(index == pl.num_programs(0) - 1)
            def _():
                grad_ref[...] = total_ref[...].astype(grad_ref.dtype)

    return kernel


def run_adjoint(waves, patches, chirps, blocks, scalars, extra, height, columns_all, last,
                opening=False):
    number, _, width, _ = waves.shape
    wave_spec = pl.BlockSpec((1, 2, width, width), lambda i, *s: (i, 0, 0, 0))
    chirp_spec = pl.BlockSpec((2, width, width), lambda i, *s: (0, 0, 0))
    in_specs = [wave_spec] + ([] if opening else [wave_spec]) + [chirp_spec] + [
        pl.BlockSpec((2 * width, width), lambda i, *s: (0, 0)),
        pl.BlockSpec((width, 2 * width), lambda i, *s: (0, 0)),
    ]
    if last:
        slot_spec = pl.BlockSpec((1, width, width), lambda i, r, c, a, s, o: (s[i], 0, 0))
        in_specs += [slot_spec, slot_spec]
    else:
        in_specs += [wave_spec]
    grid_spec = pltpu.PrefetchScalarGridSpec(
        num_scalar_prefetch=5,
        grid=(number,),
        in_specs=in_specs,
        out_specs=((() if opening else (wave_spec,))
                   + ((wave_spec,) if last else
                      (pl.BlockSpec((2, height, columns_all), lambda i, *s: (0, 0, 0)),))),
        scratch_shapes=[pltpu.VMEM((2, height, columns_all), jnp.float32)],
    )
    return pl.pallas_call(
        adjoint_kernel(last, number == 1, opening),
        grid_spec=grid_spec,
        out_shape=((() if opening else (jax.ShapeDtypeStruct(waves.shape, jnp.bfloat16),))
                   + ((jax.ShapeDtypeStruct(waves.shape, jnp.bfloat16),) if last else
                      (jax.ShapeDtypeStruct((2, height, columns_all), jnp.bfloat16),))),
    )(*scalars, waves, *(() if opening else (patches,)), chirps, *blocks, *extra)


def place_kernel(rows_ref, columns_ref, live_ref, spread_ref, source_ref, grad_ref, total_ref):
    index = pl.program_id(0)

    @pl.when(index == 0)
    def _():
        total_ref[...] = jnp.zeros(total_ref.shape, total_ref.dtype)

    spread = spread_ref[0].astype(jnp.float32)
    source = source_ref[0].astype(jnp.float32)
    term_re = source[0] * spread[0] + source[1] * spread[1]
    term_im = source[0] * spread[1] - source[1] * spread[0]
    place_term(
        term_re, term_im, rows_ref[index], columns_ref[index], live_ref[index] > 0, total_ref
    )

    @pl.when(index == pl.num_programs(0) - 1)
    def _():
        grad_ref[...] = total_ref[...].astype(grad_ref.dtype)


def run_place(spread, source, scalars, height, columns_all):
    number, _, width, _ = spread.shape
    wave_spec = pl.BlockSpec((1, 2, width, width), lambda i, *s: (i, 0, 0, 0))
    grid_spec = pltpu.PrefetchScalarGridSpec(
        num_scalar_prefetch=3,
        grid=(number,),
        in_specs=[wave_spec, wave_spec],
        out_specs=pl.BlockSpec((2, height, columns_all), lambda i, *s: (0, 0, 0)),
        scratch_shapes=[pltpu.VMEM((2, height, columns_all), jnp.float32)],
    )
    return pl.pallas_call(
        place_kernel,
        grid_spec=grid_spec,
        out_shape=jax.ShapeDtypeStruct((2, height, columns_all), jnp.bfloat16),
    )(*scalars[:3], spread, source)


def first_kernel(rows_ref, columns_ref, order_ref, wave_ref, tile_ref, mine_ref, partner_ref,
                 chirp_ref, dft_rows_ref, dft_cols_ref, result_ref, rows_scratch):
    index = pl.program_id(0)
    width = wave_ref.shape[2]
    height = tile_ref.shape[2] + mine_ref.shape[2]
    columns_all = tile_ref.shape[3]
    column_shift = (columns_all - columns_ref[index]) % columns_all
    first = order_ref[0] == 0
    patch = []
    for part in range(2):
        mine = mine_ref[0, part].astype(jnp.float32)
        partner = partner_ref[0, part].astype(jnp.float32)
        rim = jnp.concatenate(
            [jnp.where(first, mine, partner), jnp.where(first, partner, mine)], axis=1
        )
        rows_tile = tile_ref.shape[2]
        rows_scratch[:rows_tile, :] = tile_ref[0, part]
        rows_scratch[rows_tile:, :] = rim
        row = rows_ref[index]
        aligned = pl.multiple_of((row // 8) * 8, 8)
        full = rows_scratch[pl.ds(aligned, width + 8), :]
        full = pltpu.roll(full, (width + 8 - row % 8) % (width + 8), 0)[:width]
        patch.append(pltpu.roll(full, column_shift, 1)[:, :width])
    wave = wave_ref[0].astype(jnp.float32)
    wave_re = patch[0] * wave[0] - patch[1] * wave[1]
    wave_im = patch[0] * wave[1] + patch[1] * wave[0]
    out_re, out_im = propagate_block(
        wave_re, wave_im, (dft_rows_ref, dft_cols_ref), chirp_ref[0], chirp_ref[1]
    )
    result_ref[0, 0] = out_re.astype(jnp.bfloat16)
    result_ref[0, 1] = out_im.astype(jnp.bfloat16)


def run_first(waves, tile, mine, partner, rows, columns, order, chirps, blocks):
    number, _, width, _ = waves.shape
    wave_spec = pl.BlockSpec((1, 2, width, width), lambda i, r, c, o: (i, 0, 0, 0))
    whole = lambda shape: pl.BlockSpec(shape, lambda i, r, c, o: (0,) * len(shape))
    grid_spec = pltpu.PrefetchScalarGridSpec(
        num_scalar_prefetch=3,
        grid=(number,),
        in_specs=[
            wave_spec,
            whole(tile.shape),
            whole(mine.shape),
            whole(partner.shape),
            whole(chirps.shape),
            whole(blocks[0].shape),
            whole(blocks[1].shape),
        ],
        out_specs=wave_spec,
        scratch_shapes=[pltpu.VMEM((tile.shape[2] + mine.shape[2], tile.shape[3]), jnp.float32)],
    )
    return pl.pallas_call(
        first_kernel,
        grid_spec=grid_spec,
        out_shape=jax.ShapeDtypeStruct(waves.shape, jnp.bfloat16),
    )(rows, columns, order, waves, tile, mine, partner, chirps, *blocks)


def local(object_field, probe, positions, counts, measured):
    width = probe.shape[1]
    tile_rows = object_field.shape[2]
    columns_all = object_field.shape[3]
    tile_index = lax.axis_index("tile")
    tile_count = lax.axis_size("tile")
    segment = lax.axis_index("depth")
    depth_count = lax.axis_size("depth")
    batch_index = lax.axis_index("batch")
    batch_count = lax.axis_size("batch")
    half = columns_all // batch_count
    wanted = lax.dynamic_slice_in_dim(object_field[:, :, :width, :], batch_index * half, half, 3)
    mine = from_behind(wanted.astype(jnp.bfloat16), "tile", -1)
    pairs = [(b, (b + 1) % batch_count) for b in range(batch_count)]
    partner = lax.ppermute(mine, "batch", pairs)
    capacity = positions.shape[0]
    share = -(-capacity // batch_count)
    first_core = batch_index == 0
    both_positions = lax.ppermute(positions, "batch", pairs)
    both_counts = lax.ppermute(counts, "batch", pairs)
    all_positions = jnp.where(
        first_core,
        jnp.concatenate([positions, both_positions]),
        jnp.concatenate([both_positions, positions]),
    )
    all_counts = jnp.where(
        first_core, jnp.concatenate([counts, both_counts]), jnp.concatenate([both_counts, counts])
    )
    entry = batch_index * share + jnp.arange(share, dtype=jnp.int32)
    live = entry < all_counts[0] + all_counts[1]
    later = entry >= all_counts[0]
    slot = jnp.clip(jnp.where(later, entry - all_counts[0], entry), 0, capacity - 1)
    flat = jnp.where(later, capacity, 0) + slot
    chosen = all_positions[flat]
    other = (later == first_core).astype(jnp.int32)
    local_rows = chosen[:, 0] - tile_index * tile_rows
    local_columns = chosen[:, 1]
    order = jnp.reshape(batch_index, (1,)).astype(jnp.int32)
    patches = cut_patches(object_field, mine, partner, local_rows, local_columns, order, width)
    number = patches.shape[0]
    coef = jnp.where(
        segment == depth_count - 1, jnp.float32(DETECTOR_COEF), jnp.float32(SLICE_COEF)
    )
    chirp_re, chirp_im = chirp_parts(width, coef)
    start = jnp.broadcast_to(probe[None], (number, 2, width, width))

    chirps = jnp.stack([chirp_re, chirp_im])
    dft_re, dft_im = dft_parts(width)
    blocks = (
        jnp.concatenate([dft_re, dft_im], axis=0),
        jnp.concatenate([dft_re, dft_im], axis=1),
    )

    def forward_all(waves):
        return run_first(
            waves, object_field, mine, partner, local_rows, local_columns, order, chirps, blocks
        )

    def silent(waves):
        return jnp.zeros_like(waves)

    carry = start
    inputs = start
    for turn in range(depth_count - 1):
        if turn > 0:
            carry = lax.ppermute(carry, "depth", [(turn - 1, turn)])
            inputs = jnp.where(segment == turn, carry, inputs)
        carry = lax.cond(segment == turn, forward_all, silent, carry)

    measured, carry = lax.optimization_barrier((measured, carry))
    both_measured = lax.ppermute(measured, "batch", pairs)
    height = tile_rows + width
    scalars = (local_rows, local_columns, live.astype(jnp.int32), slot, other)

    def last_pass(incoming):
        return run_adjoint(
            incoming, patches, chirps, blocks, scalars, (measured, both_measured),
            height, columns_all, True,
        )

    def last_silent(incoming):
        return (jnp.zeros_like(incoming), jnp.zeros_like(incoming))

    if depth_count > 1:
        carry = lax.ppermute(carry, "depth", [(depth_count - 2, depth_count - 1)])
    arrived_last = carry
    carry, spread_last = lax.cond(segment == depth_count - 1, last_pass, last_silent, carry)
    gradient = lax.cond(
        segment == depth_count - 1,
        lambda s, a: run_place(s, a, scalars, height, columns_all),
        lambda s, a: jnp.zeros((2, height, columns_all), jnp.bfloat16),
        spread_last,
        arrived_last,
    )

    def back_pass(incoming, previous):
        return run_adjoint(
            incoming, patches, chirps, blocks, scalars, (inputs,), height, columns_all, False
        )

    def opening_pass(incoming, previous):
        (gradient,) = run_adjoint(
            incoming, patches, chirps, blocks, scalars, (inputs,), height, columns_all, False,
            opening=True,
        )
        return (incoming, gradient)

    def back_silent(incoming, previous):
        return (jnp.zeros_like(incoming), previous)

    for turn in reversed(range(depth_count - 1)):
        carry = lax.ppermute(carry, "depth", [(turn + 1, turn)])
        step = opening_pass if turn == 0 else back_pass
        carry, gradient = lax.cond(segment == turn, step, back_silent, carry, gradient)

    gradient = gradient.astype(jnp.bfloat16)
    spill = gradient[:, tile_rows:, :]
    keep = lax.dynamic_slice_in_dim(spill, batch_index * half, half, 2)
    give = lax.dynamic_slice_in_dim(spill, (1 - batch_index) * half, half, 2)
    got = lax.ppermute(give, "batch", pairs)
    spill_sum = (keep.astype(jnp.float32) + got.astype(jnp.float32)).astype(jnp.bfloat16)
    arrived = lax.ppermute(spill_sum, "tile", [(t, t + 1) for t in range(tile_count - 1)])
    own = gradient[:, :tile_rows, :]
    other = lax.ppermute(own, "batch", pairs)
    arrived_other = lax.ppermute(arrived, "batch", pairs)
    incoming = jnp.where(
        first_core,
        jnp.concatenate([arrived, arrived_other], axis=2),
        jnp.concatenate([arrived_other, arrived], axis=2),
    )
    summed = own.astype(jnp.float32) + other.astype(jnp.float32)
    summed = summed.at[:, :width, :].add(incoming.astype(jnp.float32))
    return summed[None]


def solution(mesh):
    placed = (
        P(("groups", "depth"), None, "tile", None),
        P("groups", None, None),
        P(("groups", "tile", "batch"), None),
        P(("groups", "tile", "batch")),
        P(("groups", "tile", "batch"), None, None),
    )
    return jax.shard_map(
        local,
        mesh=mesh,
        in_specs=placed,
        out_specs=P(("groups", "depth"), None, "tile", None),
        check_vma=False,
    )
```

```python
import math

import jax
import jax.numpy as jnp
from jax import lax
from jax.sharding import PartitionSpec as P
from jax.experimental import pallas as pl
from jax.experimental.pallas import tpu as pltpu

SLICE_COEF = 0.002
DETECTOR_COEF = 0.006
RESIDUAL_SCALE = 0.125


def from_behind(block, axis, distance):
    devices = range(lax.axis_size(axis))
    route = [(i - distance, i) for i in devices if i - distance in devices]
    return lax.ppermute(block, axis, route)


def dft_block(width, sign):
    freq = jnp.arange(width, dtype=jnp.int32)
    product = freq[:, None] * freq[None, :] % width
    angle = 2.0 * math.pi / width * product.astype(jnp.float32)
    scale = 1.0 / math.sqrt(width)
    real_part = (jnp.cos(angle) * scale).astype(jnp.bfloat16)
    imag_part = (sign * jnp.sin(angle) * scale).astype(jnp.bfloat16)
    upper = jnp.concatenate([real_part, -imag_part], axis=1)
    lower = jnp.concatenate([imag_part, real_part], axis=1)
    return jnp.concatenate([upper, lower], axis=0)


def dft_right(width, sign):
    freq = jnp.arange(width, dtype=jnp.int32)
    product = freq[:, None] * freq[None, :] % width
    angle = 2.0 * math.pi / width * product.astype(jnp.float32)
    scale = 1.0 / math.sqrt(width)
    real_part = (jnp.cos(angle) * scale).astype(jnp.bfloat16)
    imag_part = (sign * jnp.sin(angle) * scale).astype(jnp.bfloat16)
    upper = jnp.concatenate([real_part, imag_part], axis=1)
    lower = jnp.concatenate([-imag_part, real_part], axis=1)
    return jnp.concatenate([upper, lower], axis=0)


def dft_parts(width):
    freq = jnp.arange(width, dtype=jnp.int32)
    product = freq[:, None] * freq[None, :] % width
    angle = 2.0 * math.pi / width * product.astype(jnp.float32)
    scale = 1.0 / math.sqrt(width)
    real_part = (jnp.cos(angle) * scale).astype(jnp.bfloat16)
    imag_part = (-jnp.sin(angle) * scale).astype(jnp.bfloat16)
    return (real_part, imag_part)


def chirp_parts(width, coef):
    freq = jnp.arange(width, dtype=jnp.int32)
    shifted = (freq + width // 2) % width - width // 2
    square = shifted * shifted
    total = (square[:, None] + square[None, :]).astype(jnp.float32)
    phase = -coef * total
    return (jnp.cos(phase), jnp.sin(phase))


def left_apply(block, waves):
    number = waves.shape[0]
    width = waves.shape[2]
    stacked = waves.reshape(number, 2 * width, width)
    result = jnp.einsum("ij,gjk->gik", block, stacked, preferred_element_type=jnp.float32)
    return result.reshape(number, 2, width, width)


def propagate(waves, forward_block, inverse_block, chirp_re, chirp_im):
    first = left_apply(forward_block, waves).astype(jnp.bfloat16)
    spectrum = left_apply(forward_block, jnp.swapaxes(first, -1, -2))
    spec_re = spectrum[:, 0]
    spec_im = spectrum[:, 1]
    filtered = jnp.stack(
        [spec_re * chirp_re - spec_im * chirp_im, spec_re * chirp_im + spec_im * chirp_re], axis=1
    ).astype(jnp.bfloat16)
    back = left_apply(inverse_block, filtered).astype(jnp.bfloat16)
    return left_apply(inverse_block, jnp.swapaxes(back, -1, -2)).astype(jnp.bfloat16)


def transmit(waves, patch):
    values = waves.astype(jnp.float32)
    wave_re = values[:, 0]
    wave_im = values[:, 1]
    return jnp.stack(
        [
            patch[:, 0] * wave_re - patch[:, 1] * wave_im,
            patch[:, 0] * wave_im + patch[:, 1] * wave_re,
        ],
        axis=1,
    ).astype(jnp.bfloat16)


def residual_wave(waves, measured):
    values = waves.astype(jnp.float32)
    intensity = values[:, 0] * values[:, 0] + values[:, 1] * values[:, 1]
    weight = RESIDUAL_SCALE * (intensity - measured)
    return jnp.stack([weight * values[:, 0], weight * values[:, 1]], axis=1).astype(jnp.bfloat16)


def adjoint_terms(incoming, forward_block, inverse_block, chirp_re, chirp_im, inputs, patch):
    spread = propagate(incoming, forward_block, inverse_block, chirp_re, -chirp_im).astype(
        jnp.float32
    )
    source = inputs.astype(jnp.float32)
    term = jnp.stack(
        [
            source[:, 0] * spread[:, 0] + source[:, 1] * spread[:, 1],
            source[:, 0] * spread[:, 1] - source[:, 1] * spread[:, 0],
        ],
        axis=1,
    )
    passed = jnp.stack(
        [
            patch[:, 0] * spread[:, 0] + patch[:, 1] * spread[:, 1],
            patch[:, 0] * spread[:, 1] - patch[:, 1] * spread[:, 0],
        ],
        axis=1,
    ).astype(jnp.bfloat16)
    return (passed, term)


def wave_kernel(transmit_first, residual_after, backward):
    def kernel(*refs):
        refs = list(refs)
        wave_ref = refs.pop(0)
        patch_ref = refs.pop(0)
        chirp_ref = refs.pop(0)
        blocks = refs[:2]
        refs = refs[2:]
        extra_ref = refs.pop(0) if (residual_after or backward) else None
        wave = wave_ref[0].astype(jnp.float32)
        patch_re = patch_ref[0, 0]
        patch_im = patch_ref[0, 1]
        if transmit_first:
            wave_re = patch_re * wave[0] - patch_im * wave[1]
            wave_im = patch_re * wave[1] + patch_im * wave[0]
        else:
            wave_re = wave[0]
            wave_im = wave[1]
        chirp_re = chirp_ref[0]
        chirp_im = chirp_ref[1]
        if backward:
            chirp_im = -chirp_im
        out_re, out_im = propagate_block(wave_re, wave_im, blocks, chirp_re, chirp_im)
        if residual_after:
            measured = extra_ref[0]
            weight = RESIDUAL_SCALE * (out_re * out_re + out_im * out_im - measured)
            result_ref = refs[0]
            result_ref[0, 0] = (weight * out_re).astype(jnp.bfloat16)
            result_ref[0, 1] = (weight * out_im).astype(jnp.bfloat16)
        elif backward:
            source = extra_ref[0].astype(jnp.float32)
            passed_ref, term_ref = refs[0], refs[1]
            passed_ref[0, 0] = (patch_re * out_re + patch_im * out_im).astype(jnp.bfloat16)
            passed_ref[0, 1] = (patch_re * out_im - patch_im * out_re).astype(jnp.bfloat16)
            term_ref[0, 0] = source[0] * out_re + source[1] * out_im
            term_ref[0, 1] = source[0] * out_im - source[1] * out_re
        else:
            result_ref = refs[0]
            result_ref[0, 0] = out_re.astype(jnp.bfloat16)
            result_ref[0, 1] = out_im.astype(jnp.bfloat16)

    return kernel


def run_waves(waves, patches, chirps, blocks, extra=None, transmit_first=True, residual_after=False, backward=False):
    number, _, width, _ = waves.shape
    wave_spec = pl.BlockSpec((1, 2, width, width), lambda i: (i, 0, 0, 0))
    chirp_spec = pl.BlockSpec((2, width, width), lambda i: (0, 0, 0))
    in_specs = [wave_spec, wave_spec, chirp_spec] + [
        pl.BlockSpec((2 * width, width), lambda i: (0, 0)),
        pl.BlockSpec((width, 2 * width), lambda i: (0, 0)),
    ]
    args = [waves, patches, chirps] + list(blocks)
    if residual_after:
        in_specs.append(pl.BlockSpec((1, width, width), lambda i: (i, 0, 0)))
        args.append(extra)
    if backward:
        in_specs.append(wave_spec)
        args.append(extra)
        out_shape = (
            jax.ShapeDtypeStruct(waves.shape, jnp.bfloat16),
            jax.ShapeDtypeStruct(waves.shape, jnp.float32),
        )
        out_specs = (wave_spec, wave_spec)
    else:
        out_shape = jax.ShapeDtypeStruct(waves.shape, jnp.bfloat16)
        out_specs = wave_spec
    return pl.pallas_call(
        wave_kernel(transmit_first, residual_after, backward),
        grid=(number,),
        in_specs=in_specs,
        out_specs=out_specs,
        out_shape=out_shape,
    )(*args)


def scatter_kernel(rows_ref, columns_ref, live_ref, terms_ref, out_ref):
    index = pl.program_id(0)

    @pl.when(index == 0)
    def _():
        out_ref[...] = jnp.zeros(out_ref.shape, out_ref.dtype)

    width = terms_ref.shape[2]
    height = out_ref.shape[1]
    columns_all = out_ref.shape[2]
    row = rows_ref[index]
    column = columns_ref[index]
    alive = live_ref[index] > 0
    for part in range(2):
        term = jnp.where(alive, terms_ref[0, part], 0.0)
        wide = jnp.concatenate(
            [term, jnp.zeros((width, columns_all - width), jnp.float32)], axis=1
        )
        wide = pltpu.roll(wide, column, 1)
        tall = jnp.concatenate(
            [wide, jnp.zeros((height - width, columns_all), jnp.float32)], axis=0
        )
        tall = pltpu.roll(tall, row, 0)
        out_ref[part] = out_ref[part] + tall


def scatter_terms(terms, rows, columns, live, height, columns_all):
    number, _, width, _ = terms.shape
    grid_spec = pltpu.PrefetchScalarGridSpec(
        num_scalar_prefetch=3,
        grid=(number,),
        in_specs=[pl.BlockSpec((1, 2, width, width), lambda i, r, c, a: (i, 0, 0, 0))],
        out_specs=pl.BlockSpec((2, height, columns_all), lambda i, r, c, a: (0, 0, 0)),
    )
    return pl.pallas_call(
        scatter_kernel,
        grid_spec=grid_spec,
        out_shape=jax.ShapeDtypeStruct((2, height, columns_all), jnp.float32),
    )(rows, columns, live.astype(jnp.int32), terms)


def cut_kernel(rows_ref, columns_ref, order_ref, tile_ref, mine_ref, partner_ref, out_ref):
    index = pl.program_id(0)
    width = out_ref.shape[2]
    height = tile_ref.shape[2] + mine_ref.shape[2]
    columns_all = tile_ref.shape[3]
    row_shift = (height - rows_ref[index]) % height
    column_shift = (columns_all - columns_ref[index]) % columns_all
    first = order_ref[0] == 0
    for part in range(2):
        mine = mine_ref[0, part].astype(jnp.float32)
        partner = partner_ref[0, part].astype(jnp.float32)
        rim = jnp.concatenate(
            [jnp.where(first, mine, partner), jnp.where(first, partner, mine)], axis=1
        )
        full = jnp.concatenate([tile_ref[0, part], rim], axis=0)
        full = pltpu.roll(full, row_shift, 0)[:width]
        full = pltpu.roll(full, column_shift, 1)[:, :width]
        out_ref[0, part] = full


def cut_patches(tile, mine, partner, rows, columns, order, width):
    number = rows.shape[0]
    grid_spec = pltpu.PrefetchScalarGridSpec(
        num_scalar_prefetch=3,
        grid=(number,),
        in_specs=[
            pl.BlockSpec(tile.shape, lambda i, r, c, o: (0, 0, 0, 0)),
            pl.BlockSpec(mine.shape, lambda i, r, c, o: (0, 0, 0, 0)),
            pl.BlockSpec(partner.shape, lambda i, r, c, o: (0, 0, 0, 0)),
        ],
        out_specs=pl.BlockSpec((1, 2, width, width), lambda i, r, c, o: (i, 0, 0, 0)),
    )
    return pl.pallas_call(
        cut_kernel,
        grid_spec=grid_spec,
        out_shape=jax.ShapeDtypeStruct((number, 2, width, width), jnp.float32),
    )(rows, columns, order, tile, mine, partner)


def propagate_block(wave_re, wave_im, blocks, chirp_re, chirp_im):
    rows_ref, cols_ref = blocks
    width = wave_re.shape[0]
    dft_rows = rows_ref[...]
    dft_cols = cols_ref[...]

    def left(part_re, part_im):
        lanes = jnp.concatenate([part_re, part_im], axis=1).astype(jnp.bfloat16)
        return jnp.dot(dft_rows, lanes, preferred_element_type=jnp.float32)

    def right(part_re, part_im):
        rows = jnp.concatenate([part_re, part_im], axis=0).astype(jnp.bfloat16)
        return jnp.dot(rows, dft_cols, preferred_element_type=jnp.float32)

    first = left(wave_re, wave_im)
    z_re = (first[:width, :width] - first[width:, width:]).astype(jnp.bfloat16)
    z_im = (first[:width, width:] + first[width:, :width]).astype(jnp.bfloat16)
    second = right(z_re, z_im)
    spec_re = second[:width, :width] - second[width:, width:]
    spec_im = second[:width, width:] + second[width:, :width]
    w_re = spec_re * chirp_re - spec_im * chirp_im
    w_im = spec_re * chirp_im + spec_im * chirp_re
    third = right(w_re.astype(jnp.bfloat16), w_im.astype(jnp.bfloat16))
    v_re = (third[:width, :width] + third[width:, width:]).astype(jnp.bfloat16)
    v_im = (third[width:, :width] - third[:width, width:]).astype(jnp.bfloat16)
    fourth = left(v_re, v_im)
    out_re = (fourth[:width, :width] + fourth[width:, width:]).astype(jnp.bfloat16)
    out_im = (fourth[:width, width:] - fourth[width:, :width]).astype(jnp.bfloat16)
    return (out_re.astype(jnp.float32), out_im.astype(jnp.float32))


def place_term(term_re, term_im, row, column, alive, total_ref, direct_ref=None):
    width = term_re.shape[0]
    height = total_ref.shape[1]
    columns_all = total_ref.shape[2]
    row_shift = row % height
    column_shift = column % columns_all
    for part, term in enumerate((term_re, term_im)):
        term = jnp.where(alive, term, 0.0)
        wide = jnp.concatenate(
            [term, jnp.zeros((width, columns_all - width), jnp.float32)], axis=1
        )
        wide = pltpu.roll(wide, column_shift, 1)
        if height == 2 * width:
            rolled = pltpu.roll(wide, row % width, 0)
            below = lax.broadcasted_iota(jnp.int32, rolled.shape, 0) < row
            upper = jnp.where(below, 0.0, rolled)
            lower = jnp.where(below, rolled, 0.0)
            if direct_ref is None:
                total_ref[part, :width] = total_ref[part, :width] + upper
                total_ref[part, width:] = total_ref[part, width:] + lower
            else:
                direct_ref[part, :width] = upper.astype(direct_ref.dtype)
                direct_ref[part, width:] = lower.astype(direct_ref.dtype)
            continue
        tall = jnp.concatenate(
            [wide, jnp.zeros((height - width, columns_all), jnp.float32)], axis=0
        )
        if direct_ref is None:
            total_ref[part] = total_ref[part] + pltpu.roll(tall, row_shift, 0)
        else:
            direct_ref[part] = pltpu.roll(tall, row_shift, 0).astype(direct_ref.dtype)


def adjoint_kernel(last, single, opening=False):
    def kernel(rows_ref, columns_ref, live_ref, slot_ref, other_ref, *refs):
        refs = list(refs)
        wave_ref = refs.pop(0)
        patch_ref = None if opening else refs.pop(0)
        chirp_ref = refs.pop(0)
        blocks = refs[:2]
        refs = refs[2:]
        if last:
            own_ref = refs.pop(0)
            partner_ref = refs.pop(0)
        else:
            source_ref = refs.pop(0)
        if opening:
            grad_ref, total_ref = refs
            passed_ref = None
        else:
            passed_ref, grad_ref, total_ref = refs
        index = pl.program_id(0)

        if not single:
            @pl.when(index == 0)
            def _():
                total_ref[...] = jnp.zeros(total_ref.shape, total_ref.dtype)

        wave = wave_ref[0].astype(jnp.float32)
        if not opening:
            patch_re = patch_ref[0, 0]
            patch_im = patch_ref[0, 1]
        chirp_re = chirp_ref[0]
        chirp_im = chirp_ref[1]
        if last:
            source_re = wave[0]
            source_im = wave[1]
            lit_re = patch_re * wave[0] - patch_im * wave[1]
            lit_im = patch_re * wave[1] + patch_im * wave[0]
            out_re, out_im = propagate_block(lit_re, lit_im, blocks, chirp_re, chirp_im)
            measured = jnp.where(other_ref[index] > 0, partner_ref[0], own_ref[0])
            weight = RESIDUAL_SCALE * (out_re * out_re + out_im * out_im - measured)
            in_re = (weight * out_re).astype(jnp.bfloat16).astype(jnp.float32)
            in_im = (weight * out_im).astype(jnp.bfloat16).astype(jnp.float32)
        else:
            source = source_ref[0].astype(jnp.float32)
            source_re = source[0]
            source_im = source[1]
            in_re = wave[0]
            in_im = wave[1]
        spread_re, spread_im = propagate_block(in_re, in_im, blocks, chirp_re, -chirp_im)
        if not opening:
            passed_ref[0, 0] = (patch_re * spread_re + patch_im * spread_im).astype(jnp.bfloat16)
            passed_ref[0, 1] = (patch_re * spread_im - patch_im * spread_re).astype(jnp.bfloat16)
        if last:
            grad_ref[0, 0] = spread_re.astype(jnp.bfloat16)
            grad_ref[0, 1] = spread_im.astype(jnp.bfloat16)
            return
        term_re = source_re * spread_re + source_im * spread_im
        term_im = source_re * spread_im - source_im * spread_re
        place_term(
            term_re, term_im, rows_ref[index], columns_ref[index], live_ref[index] > 0,
            total_ref, grad_ref if single else None,
        )

        if not single:
            @pl.when(index == pl.num_programs(0) - 1)
            def _():
                grad_ref[...] = total_ref[...].astype(grad_ref.dtype)

    return kernel


def run_adjoint(waves, patches, chirps, blocks, scalars, extra, height, columns_all, last,
                opening=False):
    number, _, width, _ = waves.shape
    wave_spec = pl.BlockSpec((1, 2, width, width), lambda i, *s: (i, 0, 0, 0))
    chirp_spec = pl.BlockSpec((2, width, width), lambda i, *s: (0, 0, 0))
    in_specs = [wave_spec] + ([] if opening else [wave_spec]) + [chirp_spec] + [
        pl.BlockSpec((2 * width, width), lambda i, *s: (0, 0)),
        pl.BlockSpec((width, 2 * width), lambda i, *s: (0, 0)),
    ]
    if last:
        slot_spec = pl.BlockSpec((1, width, width), lambda i, r, c, a, s, o: (s[i], 0, 0))
        in_specs += [slot_spec, slot_spec]
    else:
        in_specs += [wave_spec]
    grid_spec = pltpu.PrefetchScalarGridSpec(
        num_scalar_prefetch=5,
        grid=(number,),
        in_specs=in_specs,
        out_specs=((() if opening else (wave_spec,))
                   + ((wave_spec,) if last else
                      (pl.BlockSpec((2, height, columns_all), lambda i, *s: (0, 0, 0)),))),
        scratch_shapes=[pltpu.VMEM((2, height, columns_all), jnp.float32)],
    )
    return pl.pallas_call(
        adjoint_kernel(last, number == 1, opening),
        grid_spec=grid_spec,
        out_shape=((() if opening else (jax.ShapeDtypeStruct(waves.shape, jnp.bfloat16),))
                   + ((jax.ShapeDtypeStruct(waves.shape, jnp.bfloat16),) if last else
                      (jax.ShapeDtypeStruct((2, height, columns_all), jnp.bfloat16),))),
    )(*scalars, waves, *(() if opening else (patches,)), chirps, *blocks, *extra)


def place_kernel(rows_ref, columns_ref, live_ref, spread_ref, source_ref, grad_ref, total_ref):
    index = pl.program_id(0)

    @pl.when(index == 0)
    def _():
        total_ref[...] = jnp.zeros(total_ref.shape, total_ref.dtype)

    spread = spread_ref[0].astype(jnp.float32)
    source = source_ref[0].astype(jnp.float32)
    term_re = source[0] * spread[0] + source[1] * spread[1]
    term_im = source[0] * spread[1] - source[1] * spread[0]
    place_term(
        term_re, term_im, rows_ref[index], columns_ref[index], live_ref[index] > 0, total_ref
    )

    @pl.when(index == pl.num_programs(0) - 1)
    def _():
        grad_ref[...] = total_ref[...].astype(grad_ref.dtype)


def run_place(spread, source, scalars, height, columns_all):
    number, _, width, _ = spread.shape
    wave_spec = pl.BlockSpec((1, 2, width, width), lambda i, *s: (i, 0, 0, 0))
    grid_spec = pltpu.PrefetchScalarGridSpec(
        num_scalar_prefetch=3,
        grid=(number,),
        in_specs=[wave_spec, wave_spec],
        out_specs=pl.BlockSpec((2, height, columns_all), lambda i, *s: (0, 0, 0)),
        scratch_shapes=[pltpu.VMEM((2, height, columns_all), jnp.float32)],
    )
    return pl.pallas_call(
        place_kernel,
        grid_spec=grid_spec,
        out_shape=jax.ShapeDtypeStruct((2, height, columns_all), jnp.bfloat16),
    )(*scalars[:3], spread, source)


def first_kernel(rows_ref, columns_ref, order_ref, wave_ref, tile_ref, mine_ref, partner_ref,
                 chirp_ref, dft_rows_ref, dft_cols_ref, result_ref, rows_scratch):
    index = pl.program_id(0)
    width = wave_ref.shape[2]
    height = tile_ref.shape[2] + mine_ref.shape[2]
    columns_all = tile_ref.shape[3]
    first = order_ref[0] == 0
    patch = []
    for part in range(2):
        mine = mine_ref[0, part].astype(jnp.float32)
        partner = partner_ref[0, part].astype(jnp.float32)
        rim = jnp.concatenate(
            [jnp.where(first, mine, partner), jnp.where(first, partner, mine)], axis=1
        )
        rows_tile = tile_ref.shape[2]
        rows_scratch[:, columns_all:] = jnp.zeros(
            (rows_scratch.shape[0], rows_scratch.shape[1] - columns_all), jnp.float32
        )
        rows_scratch[:rows_tile, :columns_all] = tile_ref[0, part]
        rows_scratch[rows_tile:, :columns_all] = rim
        row = rows_ref[index]
        column = columns_ref[index]
        aligned = pl.multiple_of((row // 8) * 8, 8)
        across = pl.multiple_of((column // 128) * 128, 128)
        full = rows_scratch[pl.ds(aligned, width + 8), pl.ds(across, width + 128)]
        full = pltpu.roll(full, (width + 8 - row % 8) % (width + 8), 0)[:width]
        full = pltpu.roll(full, (width + 128 - column % 128) % (width + 128), 1)
        patch.append(full[:, :width])
    wave = wave_ref[0].astype(jnp.float32)
    wave_re = patch[0] * wave[0] - patch[1] * wave[1]
    wave_im = patch[0] * wave[1] + patch[1] * wave[0]
    out_re, out_im = propagate_block(
        wave_re, wave_im, (dft_rows_ref, dft_cols_ref), chirp_ref[0], chirp_ref[1]
    )
    result_ref[0, 0] = out_re.astype(jnp.bfloat16)
    result_ref[0, 1] = out_im.astype(jnp.bfloat16)


def run_first(waves, tile, mine, partner, rows, columns, order, chirps, blocks):
    number, _, width, _ = waves.shape
    wave_spec = pl.BlockSpec((1, 2, width, width), lambda i, r, c, o: (i, 0, 0, 0))
    whole = lambda shape: pl.BlockSpec(shape, lambda i, r, c, o: (0,) * len(shape))
    grid_spec = pltpu.PrefetchScalarGridSpec(
        num_scalar_prefetch=3,
        grid=(number,),
        in_specs=[
            wave_spec,
            whole(tile.shape),
            whole(mine.shape),
            whole(partner.shape),
            whole(chirps.shape),
            whole(blocks[0].shape),
            whole(blocks[1].shape),
        ],
        out_specs=wave_spec,
        scratch_shapes=[
            pltpu.VMEM((tile.shape[2] + mine.shape[2], tile.shape[3] + 128), jnp.float32)
        ],
    )
    return pl.pallas_call(
        first_kernel,
        grid_spec=grid_spec,
        out_shape=jax.ShapeDtypeStruct(waves.shape, jnp.bfloat16),
    )(rows, columns, order, waves, tile, mine, partner, chirps, *blocks)


def local(object_field, probe, positions, counts, measured):
    width = probe.shape[1]
    tile_rows = object_field.shape[2]
    columns_all = object_field.shape[3]
    tile_index = lax.axis_index("tile")
    tile_count = lax.axis_size("tile")
    segment = lax.axis_index("depth")
    depth_count = lax.axis_size("depth")
    batch_index = lax.axis_index("batch")
    batch_count = lax.axis_size("batch")
    half = columns_all // batch_count
    wanted = lax.dynamic_slice_in_dim(object_field[:, :, :width, :], batch_index * half, half, 3)
    mine = from_behind(wanted.astype(jnp.bfloat16), "tile", -1)
    pairs = [(b, (b + 1) % batch_count) for b in range(batch_count)]
    partner = lax.ppermute(mine, "batch", pairs)
    capacity = positions.shape[0]
    share = -(-capacity // batch_count)
    first_core = batch_index == 0
    both_positions = lax.ppermute(positions, "batch", pairs)
    both_counts = lax.ppermute(counts, "batch", pairs)
    all_positions = jnp.where(
        first_core,
        jnp.concatenate([positions, both_positions]),
        jnp.concatenate([both_positions, positions]),
    )
    all_counts = jnp.where(
        first_core, jnp.concatenate([counts, both_counts]), jnp.concatenate([both_counts, counts])
    )
    entry = batch_index * share + jnp.arange(share, dtype=jnp.int32)
    live = entry < all_counts[0] + all_counts[1]
    later = entry >= all_counts[0]
    slot = jnp.clip(jnp.where(later, entry - all_counts[0], entry), 0, capacity - 1)
    flat = jnp.where(later, capacity, 0) + slot
    chosen = all_positions[flat]
    other = (later == first_core).astype(jnp.int32)
    local_rows = chosen[:, 0] - tile_index * tile_rows
    local_columns = chosen[:, 1]
    order = jnp.reshape(batch_index, (1,)).astype(jnp.int32)
    patches = cut_patches(object_field, mine, partner, local_rows, local_columns, order, width)
    number = patches.shape[0]
    coef = jnp.where(
        segment == depth_count - 1, jnp.float32(DETECTOR_COEF), jnp.float32(SLICE_COEF)
    )
    chirp_re, chirp_im = chirp_parts(width, coef)
    start = jnp.broadcast_to(probe[None], (number, 2, width, width))

    chirps = jnp.stack([chirp_re, chirp_im])
    dft_re, dft_im = dft_parts(width)
    blocks = (
        jnp.concatenate([dft_re, dft_im], axis=0),
        jnp.concatenate([dft_re, dft_im], axis=1),
    )

    def forward_all(waves):
        return run_first(
            waves, object_field, mine, partner, local_rows, local_columns, order, chirps, blocks
        )

    def silent(waves):
        return jnp.zeros_like(waves)

    carry = start
    inputs = start
    for turn in range(depth_count - 1):
        if turn > 0:
            carry = lax.ppermute(carry, "depth", [(turn - 1, turn)])
            inputs = jnp.where(segment == turn, carry, inputs)
        carry = lax.cond(segment == turn, forward_all, silent, carry)

    measured, carry = lax.optimization_barrier((measured, carry))
    both_measured = lax.ppermute(measured, "batch", pairs)
    height = tile_rows + width
    scalars = (local_rows, local_columns, live.astype(jnp.int32), slot, other)

    def last_pass(incoming):
        return run_adjoint(
            incoming, patches, chirps, blocks, scalars, (measured, both_measured),
            height, columns_all, True,
        )

    def last_silent(incoming):
        return (jnp.zeros_like(incoming), jnp.zeros_like(incoming))

    if depth_count > 1:
        carry = lax.ppermute(carry, "depth", [(depth_count - 2, depth_count - 1)])
    arrived_last = carry
    carry, spread_last = lax.cond(segment == depth_count - 1, last_pass, last_silent, carry)
    gradient = lax.cond(
        segment == depth_count - 1,
        lambda s, a: run_place(s, a, scalars, height, columns_all),
        lambda s, a: jnp.zeros((2, height, columns_all), jnp.bfloat16),
        spread_last,
        arrived_last,
    )

    def back_pass(incoming, previous):
        return run_adjoint(
            incoming, patches, chirps, blocks, scalars, (inputs,), height, columns_all, False
        )

    def opening_pass(incoming, previous):
        (gradient,) = run_adjoint(
            incoming, patches, chirps, blocks, scalars, (inputs,), height, columns_all, False,
            opening=True,
        )
        return (incoming, gradient)

    def back_silent(incoming, previous):
        return (jnp.zeros_like(incoming), previous)

    for turn in reversed(range(depth_count - 1)):
        carry = lax.ppermute(carry, "depth", [(turn + 1, turn)])
        step = opening_pass if turn == 0 else back_pass
        carry, gradient = lax.cond(segment == turn, step, back_silent, carry, gradient)

    gradient = gradient.astype(jnp.bfloat16)
    spill = gradient[:, tile_rows:, :]
    keep = lax.dynamic_slice_in_dim(spill, batch_index * half, half, 2)
    give = lax.dynamic_slice_in_dim(spill, (1 - batch_index) * half, half, 2)
    got = lax.ppermute(give, "batch", pairs)
    spill_sum = (keep.astype(jnp.float32) + got.astype(jnp.float32)).astype(jnp.bfloat16)
    arrived = lax.ppermute(spill_sum, "tile", [(t, t + 1) for t in range(tile_count - 1)])
    own = gradient[:, :tile_rows, :]
    other = lax.ppermute(own, "batch", pairs)
    arrived_other = lax.ppermute(arrived, "batch", pairs)
    incoming = jnp.where(
        first_core,
        jnp.concatenate([arrived, arrived_other], axis=2),
        jnp.concatenate([arrived_other, arrived], axis=2),
    )
    summed = own.astype(jnp.float32) + other.astype(jnp.float32)
    summed = summed.at[:, :width, :].add(incoming.astype(jnp.float32))
    return summed[None]


def solution(mesh):
    placed = (
        P(("groups", "depth"), None, "tile", None),
        P("groups", None, None),
        P(("groups", "tile", "batch"), None),
        P(("groups", "tile", "batch")),
        P(("groups", "tile", "batch"), None, None),
    )
    return jax.shard_map(
        local,
        mesh=mesh,
        in_specs=placed,
        out_specs=P(("groups", "depth"), None, "tile", None),
        check_vma=False,
    )
```

```python
import math

import jax
import jax.numpy as jnp
from jax import lax
from jax.sharding import PartitionSpec as P
from jax.experimental import pallas as pl
from jax.experimental.pallas import tpu as pltpu

SLICE_COEF = 0.002
DETECTOR_COEF = 0.006
RESIDUAL_SCALE = 0.125


def from_behind(block, axis, distance):
    devices = range(lax.axis_size(axis))
    route = [(i - distance, i) for i in devices if i - distance in devices]
    return lax.ppermute(block, axis, route)


def dft_block(width, sign):
    freq = jnp.arange(width, dtype=jnp.int32)
    product = freq[:, None] * freq[None, :] % width
    angle = 2.0 * math.pi / width * product.astype(jnp.float32)
    scale = 1.0 / math.sqrt(width)
    real_part = (jnp.cos(angle) * scale).astype(jnp.bfloat16)
    imag_part = (sign * jnp.sin(angle) * scale).astype(jnp.bfloat16)
    upper = jnp.concatenate([real_part, -imag_part], axis=1)
    lower = jnp.concatenate([imag_part, real_part], axis=1)
    return jnp.concatenate([upper, lower], axis=0)


def dft_right(width, sign):
    freq = jnp.arange(width, dtype=jnp.int32)
    product = freq[:, None] * freq[None, :] % width
    angle = 2.0 * math.pi / width * product.astype(jnp.float32)
    scale = 1.0 / math.sqrt(width)
    real_part = (jnp.cos(angle) * scale).astype(jnp.bfloat16)
    imag_part = (sign * jnp.sin(angle) * scale).astype(jnp.bfloat16)
    upper = jnp.concatenate([real_part, imag_part], axis=1)
    lower = jnp.concatenate([-imag_part, real_part], axis=1)
    return jnp.concatenate([upper, lower], axis=0)


def dft_parts(width):
    freq = jnp.arange(width, dtype=jnp.int32)
    product = freq[:, None] * freq[None, :] % width
    angle = 2.0 * math.pi / width * product.astype(jnp.float32)
    scale = 1.0 / math.sqrt(width)
    real_part = (jnp.cos(angle) * scale).astype(jnp.bfloat16)
    imag_part = (-jnp.sin(angle) * scale).astype(jnp.bfloat16)
    return (real_part, imag_part)


def chirp_parts(width, coef):
    freq = jnp.arange(width, dtype=jnp.int32)
    shifted = (freq + width // 2) % width - width // 2
    square = shifted * shifted
    total = (square[:, None] + square[None, :]).astype(jnp.float32)
    phase = -coef * total
    return (jnp.cos(phase), jnp.sin(phase))


def left_apply(block, waves):
    number = waves.shape[0]
    width = waves.shape[2]
    stacked = waves.reshape(number, 2 * width, width)
    result = jnp.einsum("ij,gjk->gik", block, stacked, preferred_element_type=jnp.float32)
    return result.reshape(number, 2, width, width)


def propagate(waves, forward_block, inverse_block, chirp_re, chirp_im):
    first = left_apply(forward_block, waves).astype(jnp.bfloat16)
    spectrum = left_apply(forward_block, jnp.swapaxes(first, -1, -2))
    spec_re = spectrum[:, 0]
    spec_im = spectrum[:, 1]
    filtered = jnp.stack(
        [spec_re * chirp_re - spec_im * chirp_im, spec_re * chirp_im + spec_im * chirp_re], axis=1
    ).astype(jnp.bfloat16)
    back = left_apply(inverse_block, filtered).astype(jnp.bfloat16)
    return left_apply(inverse_block, jnp.swapaxes(back, -1, -2)).astype(jnp.bfloat16)


def transmit(waves, patch):
    values = waves.astype(jnp.float32)
    wave_re = values[:, 0]
    wave_im = values[:, 1]
    return jnp.stack(
        [
            patch[:, 0] * wave_re - patch[:, 1] * wave_im,
            patch[:, 0] * wave_im + patch[:, 1] * wave_re,
        ],
        axis=1,
    ).astype(jnp.bfloat16)


def residual_wave(waves, measured):
    values = waves.astype(jnp.float32)
    intensity = values[:, 0] * values[:, 0] + values[:, 1] * values[:, 1]
    weight = RESIDUAL_SCALE * (intensity - measured)
    return jnp.stack([weight * values[:, 0], weight * values[:, 1]], axis=1).astype(jnp.bfloat16)


def adjoint_terms(incoming, forward_block, inverse_block, chirp_re, chirp_im, inputs, patch):
    spread = propagate(incoming, forward_block, inverse_block, chirp_re, -chirp_im).astype(
        jnp.float32
    )
    source = inputs.astype(jnp.float32)
    term = jnp.stack(
        [
            source[:, 0] * spread[:, 0] + source[:, 1] * spread[:, 1],
            source[:, 0] * spread[:, 1] - source[:, 1] * spread[:, 0],
        ],
        axis=1,
    )
    passed = jnp.stack(
        [
            patch[:, 0] * spread[:, 0] + patch[:, 1] * spread[:, 1],
            patch[:, 0] * spread[:, 1] - patch[:, 1] * spread[:, 0],
        ],
        axis=1,
    ).astype(jnp.bfloat16)
    return (passed, term)


def wave_kernel(transmit_first, residual_after, backward):
    def kernel(*refs):
        refs = list(refs)
        wave_ref = refs.pop(0)
        patch_ref = refs.pop(0)
        chirp_ref = refs.pop(0)
        blocks = refs[:2]
        refs = refs[2:]
        extra_ref = refs.pop(0) if (residual_after or backward) else None
        wave = wave_ref[0].astype(jnp.float32)
        patch_re = patch_ref[0, 0]
        patch_im = patch_ref[0, 1]
        if transmit_first:
            wave_re = patch_re * wave[0] - patch_im * wave[1]
            wave_im = patch_re * wave[1] + patch_im * wave[0]
        else:
            wave_re = wave[0]
            wave_im = wave[1]
        chirp_re = chirp_ref[0]
        chirp_im = chirp_ref[1]
        if backward:
            chirp_im = -chirp_im
        out_re, out_im = propagate_block(wave_re, wave_im, blocks, chirp_re, chirp_im)
        if residual_after:
            measured = extra_ref[0]
            weight = RESIDUAL_SCALE * (out_re * out_re + out_im * out_im - measured)
            result_ref = refs[0]
            result_ref[0, 0] = (weight * out_re).astype(jnp.bfloat16)
            result_ref[0, 1] = (weight * out_im).astype(jnp.bfloat16)
        elif backward:
            source = extra_ref[0].astype(jnp.float32)
            passed_ref, term_ref = refs[0], refs[1]
            passed_ref[0, 0] = (patch_re * out_re + patch_im * out_im).astype(jnp.bfloat16)
            passed_ref[0, 1] = (patch_re * out_im - patch_im * out_re).astype(jnp.bfloat16)
            term_ref[0, 0] = source[0] * out_re + source[1] * out_im
            term_ref[0, 1] = source[0] * out_im - source[1] * out_re
        else:
            result_ref = refs[0]
            result_ref[0, 0] = out_re.astype(jnp.bfloat16)
            result_ref[0, 1] = out_im.astype(jnp.bfloat16)

    return kernel


def run_waves(waves, patches, chirps, blocks, extra=None, transmit_first=True, residual_after=False, backward=False):
    number, _, width, _ = waves.shape
    wave_spec = pl.BlockSpec((1, 2, width, width), lambda i: (i, 0, 0, 0))
    chirp_spec = pl.BlockSpec((2, width, width), lambda i: (0, 0, 0))
    in_specs = [wave_spec, wave_spec, chirp_spec] + [
        pl.BlockSpec((2 * width, width), lambda i: (0, 0)),
        pl.BlockSpec((width, 2 * width), lambda i: (0, 0)),
    ]
    args = [waves, patches, chirps] + list(blocks)
    if residual_after:
        in_specs.append(pl.BlockSpec((1, width, width), lambda i: (i, 0, 0)))
        args.append(extra)
    if backward:
        in_specs.append(wave_spec)
        args.append(extra)
        out_shape = (
            jax.ShapeDtypeStruct(waves.shape, jnp.bfloat16),
            jax.ShapeDtypeStruct(waves.shape, jnp.float32),
        )
        out_specs = (wave_spec, wave_spec)
    else:
        out_shape = jax.ShapeDtypeStruct(waves.shape, jnp.bfloat16)
        out_specs = wave_spec
    return pl.pallas_call(
        wave_kernel(transmit_first, residual_after, backward),
        grid=(number,),
        in_specs=in_specs,
        out_specs=out_specs,
        out_shape=out_shape,
    )(*args)


def scatter_kernel(rows_ref, columns_ref, live_ref, terms_ref, out_ref):
    index = pl.program_id(0)

    @pl.when(index == 0)
    def _():
        out_ref[...] = jnp.zeros(out_ref.shape, out_ref.dtype)

    width = terms_ref.shape[2]
    height = out_ref.shape[1]
    columns_all = out_ref.shape[2]
    row = rows_ref[index]
    column = columns_ref[index]
    alive = live_ref[index] > 0
    for part in range(2):
        term = jnp.where(alive, terms_ref[0, part], 0.0)
        wide = jnp.concatenate(
            [term, jnp.zeros((width, columns_all - width), jnp.float32)], axis=1
        )
        wide = pltpu.roll(wide, column, 1)
        tall = jnp.concatenate(
            [wide, jnp.zeros((height - width, columns_all), jnp.float32)], axis=0
        )
        tall = pltpu.roll(tall, row, 0)
        out_ref[part] = out_ref[part] + tall


def scatter_terms(terms, rows, columns, live, height, columns_all):
    number, _, width, _ = terms.shape
    grid_spec = pltpu.PrefetchScalarGridSpec(
        num_scalar_prefetch=3,
        grid=(number,),
        in_specs=[pl.BlockSpec((1, 2, width, width), lambda i, r, c, a: (i, 0, 0, 0))],
        out_specs=pl.BlockSpec((2, height, columns_all), lambda i, r, c, a: (0, 0, 0)),
    )
    return pl.pallas_call(
        scatter_kernel,
        grid_spec=grid_spec,
        out_shape=jax.ShapeDtypeStruct((2, height, columns_all), jnp.float32),
    )(rows, columns, live.astype(jnp.int32), terms)


def cut_kernel(rows_ref, columns_ref, order_ref, tile_ref, mine_ref, partner_ref, out_ref):
    index = pl.program_id(0)
    width = out_ref.shape[2]
    height = tile_ref.shape[2] + mine_ref.shape[2]
    columns_all = tile_ref.shape[3]
    row_shift = (height - rows_ref[index]) % height
    column_shift = (columns_all - columns_ref[index]) % columns_all
    first = order_ref[0] == 0
    for part in range(2):
        mine = mine_ref[0, part].astype(jnp.float32)
        partner = partner_ref[0, part].astype(jnp.float32)
        rim = jnp.concatenate(
            [jnp.where(first, mine, partner), jnp.where(first, partner, mine)], axis=1
        )
        full = jnp.concatenate([tile_ref[0, part], rim], axis=0)
        full = pltpu.roll(full, row_shift, 0)[:width]
        full = pltpu.roll(full, column_shift, 1)[:, :width]
        out_ref[0, part] = full


def cut_patches(tile, mine, partner, rows, columns, order, width):
    number = rows.shape[0]
    grid_spec = pltpu.PrefetchScalarGridSpec(
        num_scalar_prefetch=3,
        grid=(number,),
        in_specs=[
            pl.BlockSpec(tile.shape, lambda i, r, c, o: (0, 0, 0, 0)),
            pl.BlockSpec(mine.shape, lambda i, r, c, o: (0, 0, 0, 0)),
            pl.BlockSpec(partner.shape, lambda i, r, c, o: (0, 0, 0, 0)),
        ],
        out_specs=pl.BlockSpec((1, 2, width, width), lambda i, r, c, o: (i, 0, 0, 0)),
    )
    return pl.pallas_call(
        cut_kernel,
        grid_spec=grid_spec,
        out_shape=jax.ShapeDtypeStruct((number, 2, width, width), jnp.float32),
    )(rows, columns, order, tile, mine, partner)


def propagate_block(wave_re, wave_im, blocks, chirp_re, chirp_im):
    rows_ref, cols_ref = blocks
    width = wave_re.shape[0]
    dft_rows = rows_ref[...]
    dft_cols = cols_ref[...]

    def left(part_re, part_im):
        lanes = jnp.concatenate([part_re, part_im], axis=1).astype(jnp.bfloat16)
        return jnp.dot(dft_rows, lanes, preferred_element_type=jnp.float32)

    def right(part_re, part_im):
        rows = jnp.concatenate([part_re, part_im], axis=0).astype(jnp.bfloat16)
        return jnp.dot(rows, dft_cols, preferred_element_type=jnp.float32)

    first = left(wave_re, wave_im)
    z_re = (first[:width, :width] - first[width:, width:]).astype(jnp.bfloat16)
    z_im = (first[:width, width:] + first[width:, :width]).astype(jnp.bfloat16)
    second = right(z_re, z_im)
    spec_re = second[:width, :width] - second[width:, width:]
    spec_im = second[:width, width:] + second[width:, :width]
    w_re = spec_re * chirp_re - spec_im * chirp_im
    w_im = spec_re * chirp_im + spec_im * chirp_re
    third = right(w_re.astype(jnp.bfloat16), w_im.astype(jnp.bfloat16))
    v_re = (third[:width, :width] + third[width:, width:]).astype(jnp.bfloat16)
    v_im = (third[width:, :width] - third[:width, width:]).astype(jnp.bfloat16)
    fourth = left(v_re, v_im)
    out_re = (fourth[:width, :width] + fourth[width:, width:]).astype(jnp.bfloat16)
    out_im = (fourth[:width, width:] - fourth[width:, :width]).astype(jnp.bfloat16)
    return (out_re.astype(jnp.float32), out_im.astype(jnp.float32))


def place_term(term_re, term_im, row, column, alive, total_ref, direct_ref=None, pad_ref=None):
    width = term_re.shape[0]
    height = total_ref.shape[1]
    columns_all = total_ref.shape[2]
    row_shift = row % height
    column_shift = column % columns_all
    for part, term in enumerate((term_re, term_im)):
        term = jnp.where(alive, term, 0.0)
        if direct_ref is not None and pad_ref is not None:
            pad_ref[...] = jnp.zeros(pad_ref.shape, jnp.float32)
            block = jnp.concatenate([term, jnp.zeros((width, 128), jnp.float32)], axis=1)
            block = jnp.concatenate([block, jnp.zeros((8, width + 128), jnp.float32)], axis=0)
            block = pltpu.roll(pltpu.roll(block, row % 8, 0), column % 128, 1)
            aligned = pl.multiple_of((row // 8) * 8, 8)
            across = pl.multiple_of((column // 128) * 128, 128)
            pad_ref[pl.ds(aligned, width + 8), pl.ds(across, width + 128)] = block
            direct_ref[part] = pad_ref[:height, :columns_all].astype(direct_ref.dtype)
            continue
        wide = jnp.concatenate(
            [term, jnp.zeros((width, columns_all - width), jnp.float32)], axis=1
        )
        wide = pltpu.roll(wide, column_shift, 1)
        if height == 2 * width:
            rolled = pltpu.roll(wide, row % width, 0)
            below = lax.broadcasted_iota(jnp.int32, rolled.shape, 0) < row
            upper = jnp.where(below, 0.0, rolled)
            lower = jnp.where(below, rolled, 0.0)
            if direct_ref is None:
                total_ref[part, :width] = total_ref[part, :width] + upper
                total_ref[part, width:] = total_ref[part, width:] + lower
            else:
                direct_ref[part, :width] = upper.astype(direct_ref.dtype)
                direct_ref[part, width:] = lower.astype(direct_ref.dtype)
            continue
        tall = jnp.concatenate(
            [wide, jnp.zeros((height - width, columns_all), jnp.float32)], axis=0
        )
        if direct_ref is None:
            total_ref[part] = total_ref[part] + pltpu.roll(tall, row_shift, 0)
        else:
            direct_ref[part] = pltpu.roll(tall, row_shift, 0).astype(direct_ref.dtype)


def adjoint_kernel(last, single, opening=False):
    def kernel(rows_ref, columns_ref, live_ref, slot_ref, other_ref, *refs):
        refs = list(refs)
        wave_ref = refs.pop(0)
        patch_ref = None if opening else refs.pop(0)
        chirp_ref = refs.pop(0)
        blocks = refs[:2]
        refs = refs[2:]
        if last:
            own_ref = refs.pop(0)
            partner_ref = refs.pop(0)
        else:
            source_ref = refs.pop(0)
        if opening:
            grad_ref, total_ref, pad_ref = refs
            passed_ref = None
        else:
            passed_ref, grad_ref, total_ref, pad_ref = refs
        index = pl.program_id(0)

        if not single:
            @pl.when(index == 0)
            def _():
                total_ref[...] = jnp.zeros(total_ref.shape, total_ref.dtype)

        wave = wave_ref[0].astype(jnp.float32)
        if not opening:
            patch_re = patch_ref[0, 0]
            patch_im = patch_ref[0, 1]
        chirp_re = chirp_ref[0]
        chirp_im = chirp_ref[1]
        if last:
            source_re = wave[0]
            source_im = wave[1]
            lit_re = patch_re * wave[0] - patch_im * wave[1]
            lit_im = patch_re * wave[1] + patch_im * wave[0]
            out_re, out_im = propagate_block(lit_re, lit_im, blocks, chirp_re, chirp_im)
            measured = jnp.where(other_ref[index] > 0, partner_ref[0], own_ref[0])
            weight = RESIDUAL_SCALE * (out_re * out_re + out_im * out_im - measured)
            in_re = (weight * out_re).astype(jnp.bfloat16).astype(jnp.float32)
            in_im = (weight * out_im).astype(jnp.bfloat16).astype(jnp.float32)
        else:
            source = source_ref[0].astype(jnp.float32)
            source_re = source[0]
            source_im = source[1]
            in_re = wave[0]
            in_im = wave[1]
        spread_re, spread_im = propagate_block(in_re, in_im, blocks, chirp_re, -chirp_im)
        if not opening:
            passed_ref[0, 0] = (patch_re * spread_re + patch_im * spread_im).astype(jnp.bfloat16)
            passed_ref[0, 1] = (patch_re * spread_im - patch_im * spread_re).astype(jnp.bfloat16)
        if last:
            grad_ref[0, 0] = spread_re.astype(jnp.bfloat16)
            grad_ref[0, 1] = spread_im.astype(jnp.bfloat16)
            return
        term_re = source_re * spread_re + source_im * spread_im
        term_im = source_re * spread_im - source_im * spread_re
        place_term(
            term_re, term_im, rows_ref[index], columns_ref[index], live_ref[index] > 0,
            total_ref, grad_ref if single else None, pad_ref,
        )

        if not single:
            @pl.when(index == pl.num_programs(0) - 1)
            def _():
                grad_ref[...] = total_ref[...].astype(grad_ref.dtype)

    return kernel


def run_adjoint(waves, patches, chirps, blocks, scalars, extra, height, columns_all, last,
                opening=False):
    number, _, width, _ = waves.shape
    wave_spec = pl.BlockSpec((1, 2, width, width), lambda i, *s: (i, 0, 0, 0))
    chirp_spec = pl.BlockSpec((2, width, width), lambda i, *s: (0, 0, 0))
    in_specs = [wave_spec] + ([] if opening else [wave_spec]) + [chirp_spec] + [
        pl.BlockSpec((2 * width, width), lambda i, *s: (0, 0)),
        pl.BlockSpec((width, 2 * width), lambda i, *s: (0, 0)),
    ]
    if last:
        slot_spec = pl.BlockSpec((1, width, width), lambda i, r, c, a, s, o: (s[i], 0, 0))
        in_specs += [slot_spec, slot_spec]
    else:
        in_specs += [wave_spec]
    grid_spec = pltpu.PrefetchScalarGridSpec(
        num_scalar_prefetch=5,
        grid=(number,),
        in_specs=in_specs,
        out_specs=((() if opening else (wave_spec,))
                   + ((wave_spec,) if last else
                      (pl.BlockSpec((2, height, columns_all), lambda i, *s: (0, 0, 0)),))),
        scratch_shapes=[
            pltpu.VMEM((2, height, columns_all), jnp.float32),
            pltpu.VMEM((height + 8, columns_all + 128), jnp.float32),
        ],
    )
    return pl.pallas_call(
        adjoint_kernel(last, number == 1, opening),
        grid_spec=grid_spec,
        out_shape=((() if opening else (jax.ShapeDtypeStruct(waves.shape, jnp.bfloat16),))
                   + ((jax.ShapeDtypeStruct(waves.shape, jnp.bfloat16),) if last else
                      (jax.ShapeDtypeStruct((2, height, columns_all), jnp.bfloat16),))),
    )(*scalars, waves, *(() if opening else (patches,)), chirps, *blocks, *extra)


def place_kernel(rows_ref, columns_ref, live_ref, spread_ref, source_ref, grad_ref, total_ref):
    index = pl.program_id(0)

    @pl.when(index == 0)
    def _():
        total_ref[...] = jnp.zeros(total_ref.shape, total_ref.dtype)

    spread = spread_ref[0].astype(jnp.float32)
    source = source_ref[0].astype(jnp.float32)
    term_re = source[0] * spread[0] + source[1] * spread[1]
    term_im = source[0] * spread[1] - source[1] * spread[0]
    place_term(
        term_re, term_im, rows_ref[index], columns_ref[index], live_ref[index] > 0, total_ref
    )

    @pl.when(index == pl.num_programs(0) - 1)
    def _():
        grad_ref[...] = total_ref[...].astype(grad_ref.dtype)


def run_place(spread, source, scalars, height, columns_all):
    number, _, width, _ = spread.shape
    wave_spec = pl.BlockSpec((1, 2, width, width), lambda i, *s: (i, 0, 0, 0))
    grid_spec = pltpu.PrefetchScalarGridSpec(
        num_scalar_prefetch=3,
        grid=(number,),
        in_specs=[wave_spec, wave_spec],
        out_specs=pl.BlockSpec((2, height, columns_all), lambda i, *s: (0, 0, 0)),
        scratch_shapes=[pltpu.VMEM((2, height, columns_all), jnp.float32)],
    )
    return pl.pallas_call(
        place_kernel,
        grid_spec=grid_spec,
        out_shape=jax.ShapeDtypeStruct((2, height, columns_all), jnp.bfloat16),
    )(*scalars[:3], spread, source)


def first_kernel(rows_ref, columns_ref, order_ref, wave_ref, tile_ref, mine_ref, partner_ref,
                 chirp_ref, dft_rows_ref, dft_cols_ref, result_ref, rows_scratch):
    index = pl.program_id(0)
    width = wave_ref.shape[2]
    height = tile_ref.shape[2] + mine_ref.shape[2]
    columns_all = tile_ref.shape[3]
    first = order_ref[0] == 0
    patch = []
    for part in range(2):
        mine = mine_ref[0, part].astype(jnp.float32)
        partner = partner_ref[0, part].astype(jnp.float32)
        rim = jnp.concatenate(
            [jnp.where(first, mine, partner), jnp.where(first, partner, mine)], axis=1
        )
        rows_tile = tile_ref.shape[2]
        rows_scratch[:, columns_all:] = jnp.zeros(
            (rows_scratch.shape[0], rows_scratch.shape[1] - columns_all), jnp.float32
        )
        rows_scratch[:rows_tile, :columns_all] = tile_ref[0, part]
        rows_scratch[rows_tile:, :columns_all] = rim
        row = rows_ref[index]
        column = columns_ref[index]
        aligned = pl.multiple_of((row // 8) * 8, 8)
        across = pl.multiple_of((column // 128) * 128, 128)
        full = rows_scratch[pl.ds(aligned, width + 8), pl.ds(across, width + 128)]
        full = pltpu.roll(full, (width + 8 - row % 8) % (width + 8), 0)[:width]
        full = pltpu.roll(full, (width + 128 - column % 128) % (width + 128), 1)
        patch.append(full[:, :width])
    wave = wave_ref[0].astype(jnp.float32)
    wave_re = patch[0] * wave[0] - patch[1] * wave[1]
    wave_im = patch[0] * wave[1] + patch[1] * wave[0]
    out_re, out_im = propagate_block(
        wave_re, wave_im, (dft_rows_ref, dft_cols_ref), chirp_ref[0], chirp_ref[1]
    )
    result_ref[0, 0] = out_re.astype(jnp.bfloat16)
    result_ref[0, 1] = out_im.astype(jnp.bfloat16)


def run_first(waves, tile, mine, partner, rows, columns, order, chirps, blocks):
    number, _, width, _ = waves.shape
    wave_spec = pl.BlockSpec((1, 2, width, width), lambda i, r, c, o: (i, 0, 0, 0))
    whole = lambda shape: pl.BlockSpec(shape, lambda i, r, c, o: (0,) * len(shape))
    grid_spec = pltpu.PrefetchScalarGridSpec(
        num_scalar_prefetch=3,
        grid=(number,),
        in_specs=[
            wave_spec,
            whole(tile.shape),
            whole(mine.shape),
            whole(partner.shape),
            whole(chirps.shape),
            whole(blocks[0].shape),
            whole(blocks[1].shape),
        ],
        out_specs=wave_spec,
        scratch_shapes=[
            pltpu.VMEM((tile.shape[2] + mine.shape[2], tile.shape[3] + 128), jnp.float32)
        ],
    )
    return pl.pallas_call(
        first_kernel,
        grid_spec=grid_spec,
        out_shape=jax.ShapeDtypeStruct(waves.shape, jnp.bfloat16),
    )(rows, columns, order, waves, tile, mine, partner, chirps, *blocks)


def local(object_field, probe, positions, counts, measured):
    width = probe.shape[1]
    tile_rows = object_field.shape[2]
    columns_all = object_field.shape[3]
    tile_index = lax.axis_index("tile")
    tile_count = lax.axis_size("tile")
    segment = lax.axis_index("depth")
    depth_count = lax.axis_size("depth")
    batch_index = lax.axis_index("batch")
    batch_count = lax.axis_size("batch")
    half = columns_all // batch_count
    wanted = lax.dynamic_slice_in_dim(object_field[:, :, :width, :], batch_index * half, half, 3)
    mine = from_behind(wanted.astype(jnp.bfloat16), "tile", -1)
    pairs = [(b, (b + 1) % batch_count) for b in range(batch_count)]
    partner = lax.ppermute(mine, "batch", pairs)
    capacity = positions.shape[0]
    share = -(-capacity // batch_count)
    first_core = batch_index == 0
    both_positions = lax.ppermute(positions, "batch", pairs)
    both_counts = lax.ppermute(counts, "batch", pairs)
    all_positions = jnp.where(
        first_core,
        jnp.concatenate([positions, both_positions]),
        jnp.concatenate([both_positions, positions]),
    )
    all_counts = jnp.where(
        first_core, jnp.concatenate([counts, both_counts]), jnp.concatenate([both_counts, counts])
    )
    entry = batch_index * share + jnp.arange(share, dtype=jnp.int32)
    live = entry < all_counts[0] + all_counts[1]
    later = entry >= all_counts[0]
    slot = jnp.clip(jnp.where(later, entry - all_counts[0], entry), 0, capacity - 1)
    flat = jnp.where(later, capacity, 0) + slot
    chosen = all_positions[flat]
    other = (later == first_core).astype(jnp.int32)
    local_rows = chosen[:, 0] - tile_index * tile_rows
    local_columns = chosen[:, 1]
    order = jnp.reshape(batch_index, (1,)).astype(jnp.int32)
    patches = cut_patches(object_field, mine, partner, local_rows, local_columns, order, width)
    number = patches.shape[0]
    coef = jnp.where(
        segment == depth_count - 1, jnp.float32(DETECTOR_COEF), jnp.float32(SLICE_COEF)
    )
    chirp_re, chirp_im = chirp_parts(width, coef)
    start = jnp.broadcast_to(probe[None], (number, 2, width, width))

    chirps = jnp.stack([chirp_re, chirp_im])
    dft_re, dft_im = dft_parts(width)
    blocks = (
        jnp.concatenate([dft_re, dft_im], axis=0),
        jnp.concatenate([dft_re, dft_im], axis=1),
    )

    def forward_all(waves):
        return run_first(
            waves, object_field, mine, partner, local_rows, local_columns, order, chirps, blocks
        )

    def silent(waves):
        return jnp.zeros_like(waves)

    carry = start
    inputs = start
    for turn in range(depth_count - 1):
        if turn > 0:
            carry = lax.ppermute(carry, "depth", [(turn - 1, turn)])
            inputs = jnp.where(segment == turn, carry, inputs)
        carry = lax.cond(segment == turn, forward_all, silent, carry)

    measured, carry = lax.optimization_barrier((measured, carry))
    both_measured = lax.ppermute(measured, "batch", pairs)
    height = tile_rows + width
    scalars = (local_rows, local_columns, live.astype(jnp.int32), slot, other)

    def last_pass(incoming):
        return run_adjoint(
            incoming, patches, chirps, blocks, scalars, (measured, both_measured),
            height, columns_all, True,
        )

    def last_silent(incoming):
        return (jnp.zeros_like(incoming), jnp.zeros_like(incoming))

    if depth_count > 1:
        carry = lax.ppermute(carry, "depth", [(depth_count - 2, depth_count - 1)])
    arrived_last = carry
    carry, spread_last = lax.cond(segment == depth_count - 1, last_pass, last_silent, carry)
    gradient = lax.cond(
        segment == depth_count - 1,
        lambda s, a: run_place(s, a, scalars, height, columns_all),
        lambda s, a: jnp.zeros((2, height, columns_all), jnp.bfloat16),
        spread_last,
        arrived_last,
    )

    def back_pass(incoming, previous):
        return run_adjoint(
            incoming, patches, chirps, blocks, scalars, (inputs,), height, columns_all, False
        )

    def opening_pass(incoming, previous):
        (gradient,) = run_adjoint(
            incoming, patches, chirps, blocks, scalars, (inputs,), height, columns_all, False,
            opening=True,
        )
        return (incoming, gradient)

    def back_silent(incoming, previous):
        return (jnp.zeros_like(incoming), previous)

    for turn in reversed(range(depth_count - 1)):
        carry = lax.ppermute(carry, "depth", [(turn + 1, turn)])
        step = opening_pass if turn == 0 else back_pass
        carry, gradient = lax.cond(segment == turn, step, back_silent, carry, gradient)

    gradient = gradient.astype(jnp.bfloat16)
    spill = gradient[:, tile_rows:, :]
    keep = lax.dynamic_slice_in_dim(spill, batch_index * half, half, 2)
    give = lax.dynamic_slice_in_dim(spill, (1 - batch_index) * half, half, 2)
    got = lax.ppermute(give, "batch", pairs)
    spill_sum = (keep.astype(jnp.float32) + got.astype(jnp.float32)).astype(jnp.bfloat16)
    arrived = lax.ppermute(spill_sum, "tile", [(t, t + 1) for t in range(tile_count - 1)])
    own = gradient[:, :tile_rows, :]
    other = lax.ppermute(own, "batch", pairs)
    arrived_other = lax.ppermute(arrived, "batch", pairs)
    incoming = jnp.where(
        first_core,
        jnp.concatenate([arrived, arrived_other], axis=2),
        jnp.concatenate([arrived_other, arrived], axis=2),
    )
    summed = own.astype(jnp.float32) + other.astype(jnp.float32)
    summed = summed.at[:, :width, :].add(incoming.astype(jnp.float32))
    return summed[None]


def solution(mesh):
    placed = (
        P(("groups", "depth"), None, "tile", None),
        P("groups", None, None),
        P(("groups", "tile", "batch"), None),
        P(("groups", "tile", "batch")),
        P(("groups", "tile", "batch"), None, None),
    )
    return jax.shard_map(
        local,
        mesh=mesh,
        in_specs=placed,
        out_specs=P(("groups", "depth"), None, "tile", None),
        check_vma=False,
    )
```

```python
import math

import jax
import jax.numpy as jnp
from jax import lax
from jax.sharding import PartitionSpec as P
from jax.experimental import pallas as pl
from jax.experimental.pallas import tpu as pltpu

SLICE_COEF = 0.002
DETECTOR_COEF = 0.006
RESIDUAL_SCALE = 0.125


def from_behind(block, axis, distance):
    devices = range(lax.axis_size(axis))
    route = [(i - distance, i) for i in devices if i - distance in devices]
    return lax.ppermute(block, axis, route)


def dft_block(width, sign):
    freq = jnp.arange(width, dtype=jnp.int32)
    product = freq[:, None] * freq[None, :] % width
    angle = 2.0 * math.pi / width * product.astype(jnp.float32)
    scale = 1.0 / math.sqrt(width)
    real_part = (jnp.cos(angle) * scale).astype(jnp.bfloat16)
    imag_part = (sign * jnp.sin(angle) * scale).astype(jnp.bfloat16)
    upper = jnp.concatenate([real_part, -imag_part], axis=1)
    lower = jnp.concatenate([imag_part, real_part], axis=1)
    return jnp.concatenate([upper, lower], axis=0)


def dft_right(width, sign):
    freq = jnp.arange(width, dtype=jnp.int32)
    product = freq[:, None] * freq[None, :] % width
    angle = 2.0 * math.pi / width * product.astype(jnp.float32)
    scale = 1.0 / math.sqrt(width)
    real_part = (jnp.cos(angle) * scale).astype(jnp.bfloat16)
    imag_part = (sign * jnp.sin(angle) * scale).astype(jnp.bfloat16)
    upper = jnp.concatenate([real_part, imag_part], axis=1)
    lower = jnp.concatenate([-imag_part, real_part], axis=1)
    return jnp.concatenate([upper, lower], axis=0)


def dft_parts(width):
    freq = jnp.arange(width, dtype=jnp.int32)
    product = freq[:, None] * freq[None, :] % width
    angle = 2.0 * math.pi / width * product.astype(jnp.float32)
    scale = 1.0 / math.sqrt(width)
    real_part = (jnp.cos(angle) * scale).astype(jnp.bfloat16)
    imag_part = (-jnp.sin(angle) * scale).astype(jnp.bfloat16)
    return (real_part, imag_part)


def chirp_parts(width, coef):
    freq = jnp.arange(width, dtype=jnp.int32)
    shifted = (freq + width // 2) % width - width // 2
    square = shifted * shifted
    total = (square[:, None] + square[None, :]).astype(jnp.float32)
    phase = -coef * total
    return (jnp.cos(phase), jnp.sin(phase))


def left_apply(block, waves):
    number = waves.shape[0]
    width = waves.shape[2]
    stacked = waves.reshape(number, 2 * width, width)
    result = jnp.einsum("ij,gjk->gik", block, stacked, preferred_element_type=jnp.float32)
    return result.reshape(number, 2, width, width)


def propagate(waves, forward_block, inverse_block, chirp_re, chirp_im):
    first = left_apply(forward_block, waves).astype(jnp.bfloat16)
    spectrum = left_apply(forward_block, jnp.swapaxes(first, -1, -2))
    spec_re = spectrum[:, 0]
    spec_im = spectrum[:, 1]
    filtered = jnp.stack(
        [spec_re * chirp_re - spec_im * chirp_im, spec_re * chirp_im + spec_im * chirp_re], axis=1
    ).astype(jnp.bfloat16)
    back = left_apply(inverse_block, filtered).astype(jnp.bfloat16)
    return left_apply(inverse_block, jnp.swapaxes(back, -1, -2)).astype(jnp.bfloat16)


def transmit(waves, patch):
    values = waves.astype(jnp.float32)
    wave_re = values[:, 0]
    wave_im = values[:, 1]
    return jnp.stack(
        [
            patch[:, 0] * wave_re - patch[:, 1] * wave_im,
            patch[:, 0] * wave_im + patch[:, 1] * wave_re,
        ],
        axis=1,
    ).astype(jnp.bfloat16)


def residual_wave(waves, measured):
    values = waves.astype(jnp.float32)
    intensity = values[:, 0] * values[:, 0] + values[:, 1] * values[:, 1]
    weight = RESIDUAL_SCALE * (intensity - measured)
    return jnp.stack([weight * values[:, 0], weight * values[:, 1]], axis=1).astype(jnp.bfloat16)


def adjoint_terms(incoming, forward_block, inverse_block, chirp_re, chirp_im, inputs, patch):
    spread = propagate(incoming, forward_block, inverse_block, chirp_re, -chirp_im).astype(
        jnp.float32
    )
    source = inputs.astype(jnp.float32)
    term = jnp.stack(
        [
            source[:, 0] * spread[:, 0] + source[:, 1] * spread[:, 1],
            source[:, 0] * spread[:, 1] - source[:, 1] * spread[:, 0],
        ],
        axis=1,
    )
    passed = jnp.stack(
        [
            patch[:, 0] * spread[:, 0] + patch[:, 1] * spread[:, 1],
            patch[:, 0] * spread[:, 1] - patch[:, 1] * spread[:, 0],
        ],
        axis=1,
    ).astype(jnp.bfloat16)
    return (passed, term)


def wave_kernel(transmit_first, residual_after, backward):
    def kernel(*refs):
        refs = list(refs)
        wave_ref = refs.pop(0)
        patch_ref = refs.pop(0)
        chirp_ref = refs.pop(0)
        blocks = refs[:2]
        refs = refs[2:]
        extra_ref = refs.pop(0) if (residual_after or backward) else None
        wave = wave_ref[0].astype(jnp.float32)
        patch_re = patch_ref[0, 0]
        patch_im = patch_ref[0, 1]
        if transmit_first:
            wave_re = patch_re * wave[0] - patch_im * wave[1]
            wave_im = patch_re * wave[1] + patch_im * wave[0]
        else:
            wave_re = wave[0]
            wave_im = wave[1]
        chirp_re = chirp_ref[0]
        chirp_im = chirp_ref[1]
        if backward:
            chirp_im = -chirp_im
        out_re, out_im = propagate_block(wave_re, wave_im, blocks, chirp_re, chirp_im)
        if residual_after:
            measured = extra_ref[0]
            weight = RESIDUAL_SCALE * (out_re * out_re + out_im * out_im - measured)
            result_ref = refs[0]
            result_ref[0, 0] = (weight * out_re).astype(jnp.bfloat16)
            result_ref[0, 1] = (weight * out_im).astype(jnp.bfloat16)
        elif backward:
            source = extra_ref[0].astype(jnp.float32)
            passed_ref, term_ref = refs[0], refs[1]
            passed_ref[0, 0] = (patch_re * out_re + patch_im * out_im).astype(jnp.bfloat16)
            passed_ref[0, 1] = (patch_re * out_im - patch_im * out_re).astype(jnp.bfloat16)
            term_ref[0, 0] = source[0] * out_re + source[1] * out_im
            term_ref[0, 1] = source[0] * out_im - source[1] * out_re
        else:
            result_ref = refs[0]
            result_ref[0, 0] = out_re.astype(jnp.bfloat16)
            result_ref[0, 1] = out_im.astype(jnp.bfloat16)

    return kernel


def run_waves(waves, patches, chirps, blocks, extra=None, transmit_first=True, residual_after=False, backward=False):
    number, _, width, _ = waves.shape
    wave_spec = pl.BlockSpec((1, 2, width, width), lambda i: (i, 0, 0, 0))
    chirp_spec = pl.BlockSpec((2, width, width), lambda i: (0, 0, 0))
    in_specs = [wave_spec, wave_spec, chirp_spec] + [
        pl.BlockSpec((2 * width, width), lambda i: (0, 0)),
        pl.BlockSpec((width, 2 * width), lambda i: (0, 0)),
    ]
    args = [waves, patches, chirps] + list(blocks)
    if residual_after:
        in_specs.append(pl.BlockSpec((1, width, width), lambda i: (i, 0, 0)))
        args.append(extra)
    if backward:
        in_specs.append(wave_spec)
        args.append(extra)
        out_shape = (
            jax.ShapeDtypeStruct(waves.shape, jnp.bfloat16),
            jax.ShapeDtypeStruct(waves.shape, jnp.float32),
        )
        out_specs = (wave_spec, wave_spec)
    else:
        out_shape = jax.ShapeDtypeStruct(waves.shape, jnp.bfloat16)
        out_specs = wave_spec
    return pl.pallas_call(
        wave_kernel(transmit_first, residual_after, backward),
        grid=(number,),
        in_specs=in_specs,
        out_specs=out_specs,
        out_shape=out_shape,
    )(*args)


def scatter_kernel(rows_ref, columns_ref, live_ref, terms_ref, out_ref):
    index = pl.program_id(0)

    @pl.when(index == 0)
    def _():
        out_ref[...] = jnp.zeros(out_ref.shape, out_ref.dtype)

    width = terms_ref.shape[2]
    height = out_ref.shape[1]
    columns_all = out_ref.shape[2]
    row = rows_ref[index]
    column = columns_ref[index]
    alive = live_ref[index] > 0
    for part in range(2):
        term = jnp.where(alive, terms_ref[0, part], 0.0)
        wide = jnp.concatenate(
            [term, jnp.zeros((width, columns_all - width), jnp.float32)], axis=1
        )
        wide = pltpu.roll(wide, column, 1)
        tall = jnp.concatenate(
            [wide, jnp.zeros((height - width, columns_all), jnp.float32)], axis=0
        )
        tall = pltpu.roll(tall, row, 0)
        out_ref[part] = out_ref[part] + tall


def scatter_terms(terms, rows, columns, live, height, columns_all):
    number, _, width, _ = terms.shape
    grid_spec = pltpu.PrefetchScalarGridSpec(
        num_scalar_prefetch=3,
        grid=(number,),
        in_specs=[pl.BlockSpec((1, 2, width, width), lambda i, r, c, a: (i, 0, 0, 0))],
        out_specs=pl.BlockSpec((2, height, columns_all), lambda i, r, c, a: (0, 0, 0)),
    )
    return pl.pallas_call(
        scatter_kernel,
        grid_spec=grid_spec,
        out_shape=jax.ShapeDtypeStruct((2, height, columns_all), jnp.float32),
    )(rows, columns, live.astype(jnp.int32), terms)


def cut_kernel(rows_ref, columns_ref, order_ref, tile_ref, mine_ref, partner_ref, out_ref):
    index = pl.program_id(0)
    width = out_ref.shape[2]
    height = tile_ref.shape[2] + mine_ref.shape[2]
    columns_all = tile_ref.shape[3]
    row_shift = (height - rows_ref[index]) % height
    column_shift = (columns_all - columns_ref[index]) % columns_all
    first = order_ref[0] == 0
    for part in range(2):
        mine = mine_ref[0, part].astype(jnp.float32)
        partner = partner_ref[0, part].astype(jnp.float32)
        rim = jnp.concatenate(
            [jnp.where(first, mine, partner), jnp.where(first, partner, mine)], axis=1
        )
        full = jnp.concatenate([tile_ref[0, part], rim], axis=0)
        full = pltpu.roll(full, row_shift, 0)[:width]
        full = pltpu.roll(full, column_shift, 1)[:, :width]
        out_ref[0, part] = full


def cut_patches(tile, mine, partner, rows, columns, order, width):
    number = rows.shape[0]
    grid_spec = pltpu.PrefetchScalarGridSpec(
        num_scalar_prefetch=3,
        grid=(number,),
        in_specs=[
            pl.BlockSpec(tile.shape, lambda i, r, c, o: (0, 0, 0, 0)),
            pl.BlockSpec(mine.shape, lambda i, r, c, o: (0, 0, 0, 0)),
            pl.BlockSpec(partner.shape, lambda i, r, c, o: (0, 0, 0, 0)),
        ],
        out_specs=pl.BlockSpec((1, 2, width, width), lambda i, r, c, o: (i, 0, 0, 0)),
    )
    return pl.pallas_call(
        cut_kernel,
        grid_spec=grid_spec,
        out_shape=jax.ShapeDtypeStruct((number, 2, width, width), jnp.float32),
    )(rows, columns, order, tile, mine, partner)


def propagate_block(wave_re, wave_im, blocks, chirp_re, chirp_im):
    rows_ref, cols_ref = blocks
    width = wave_re.shape[0]
    dft_rows = rows_ref[...]
    dft_cols = cols_ref[...]

    def left(part_re, part_im):
        lanes = jnp.concatenate([part_re, part_im], axis=1).astype(jnp.bfloat16)
        return jnp.dot(dft_rows, lanes, preferred_element_type=jnp.float32)

    def right(part_re, part_im):
        rows = jnp.concatenate([part_re, part_im], axis=0).astype(jnp.bfloat16)
        return jnp.dot(rows, dft_cols, preferred_element_type=jnp.float32)

    first = left(wave_re, wave_im)
    z_re = (first[:width, :width] - first[width:, width:]).astype(jnp.bfloat16)
    z_im = (first[:width, width:] + first[width:, :width]).astype(jnp.bfloat16)
    second = right(z_re, z_im)
    spec_re = second[:width, :width] - second[width:, width:]
    spec_im = second[:width, width:] + second[width:, :width]
    w_re = spec_re * chirp_re - spec_im * chirp_im
    w_im = spec_re * chirp_im + spec_im * chirp_re
    third = right(w_re.astype(jnp.bfloat16), w_im.astype(jnp.bfloat16))
    v_re = (third[:width, :width] + third[width:, width:]).astype(jnp.bfloat16)
    v_im = (third[width:, :width] - third[:width, width:]).astype(jnp.bfloat16)
    fourth = left(v_re, v_im)
    out_re = (fourth[:width, :width] + fourth[width:, width:]).astype(jnp.bfloat16)
    out_im = (fourth[:width, width:] - fourth[width:, :width]).astype(jnp.bfloat16)
    return (out_re.astype(jnp.float32), out_im.astype(jnp.float32))


def place_term(term_re, term_im, row, column, alive, total_ref, direct_ref=None, pad_ref=None):
    width = term_re.shape[0]
    height = total_ref.shape[1]
    columns_all = total_ref.shape[2]
    row_shift = row % height
    column_shift = column % columns_all
    for part, term in enumerate((term_re, term_im)):
        term = jnp.where(alive, term, 0.0)
        if direct_ref is not None and pad_ref is not None:
            pad_ref[...] = jnp.zeros(pad_ref.shape, jnp.float32)
            block = jnp.concatenate([term, jnp.zeros((width, 128), jnp.float32)], axis=1)
            block = jnp.concatenate([block, jnp.zeros((8, width + 128), jnp.float32)], axis=0)
            block = pltpu.roll(pltpu.roll(block, row % 8, 0), column % 128, 1)
            aligned = pl.multiple_of((row // 8) * 8, 8)
            across = pl.multiple_of((column // 128) * 128, 128)
            pad_ref[pl.ds(aligned, width + 8), pl.ds(across, width + 128)] = block
            direct_ref[part] = pad_ref[:height, :columns_all].astype(direct_ref.dtype)
            continue
        wide = jnp.concatenate(
            [term, jnp.zeros((width, columns_all - width), jnp.float32)], axis=1
        )
        wide = pltpu.roll(wide, column_shift, 1)
        if height == 2 * width:
            rolled = pltpu.roll(wide, row % width, 0)
            below = lax.broadcasted_iota(jnp.int32, rolled.shape, 0) < row
            upper = jnp.where(below, 0.0, rolled)
            lower = jnp.where(below, rolled, 0.0)
            if direct_ref is None:
                total_ref[part, :width] = total_ref[part, :width] + upper
                total_ref[part, width:] = total_ref[part, width:] + lower
            else:
                direct_ref[part, :width] = upper.astype(direct_ref.dtype)
                direct_ref[part, width:] = lower.astype(direct_ref.dtype)
            continue
        tall = jnp.concatenate(
            [wide, jnp.zeros((height - width, columns_all), jnp.float32)], axis=0
        )
        if direct_ref is None:
            total_ref[part] = total_ref[part] + pltpu.roll(tall, row_shift, 0)
        else:
            direct_ref[part] = pltpu.roll(tall, row_shift, 0).astype(direct_ref.dtype)


def adjoint_kernel(last, single, opening=False):
    def kernel(rows_ref, columns_ref, live_ref, slot_ref, other_ref, *refs):
        refs = list(refs)
        wave_ref = refs.pop(0)
        patch_ref = None if opening else refs.pop(0)
        chirp_ref = refs.pop(0)
        blocks = refs[:2]
        refs = refs[2:]
        if last:
            own_ref = refs.pop(0)
            partner_ref = refs.pop(0)
        else:
            source_ref = refs.pop(0)
        if opening:
            grad_ref, total_ref, pad_ref = refs
            passed_ref = None
        else:
            passed_ref, grad_ref, total_ref, pad_ref = refs
        index = pl.program_id(0)

        if not single:
            @pl.when(index == 0)
            def _():
                total_ref[...] = jnp.zeros(total_ref.shape, total_ref.dtype)

        wave = wave_ref[0].astype(jnp.float32)
        if not opening:
            patch_re = patch_ref[0, 0]
            patch_im = patch_ref[0, 1]
        chirp_re = chirp_ref[0]
        chirp_im = chirp_ref[1]
        if last:
            source_re = wave[0]
            source_im = wave[1]
            lit_re = patch_re * wave[0] - patch_im * wave[1]
            lit_im = patch_re * wave[1] + patch_im * wave[0]
            out_re, out_im = propagate_block(lit_re, lit_im, blocks, chirp_re, chirp_im)
            measured = jnp.where(other_ref[index] > 0, partner_ref[0], own_ref[0])
            weight = RESIDUAL_SCALE * (out_re * out_re + out_im * out_im - measured)
            in_re = (weight * out_re).astype(jnp.bfloat16).astype(jnp.float32)
            in_im = (weight * out_im).astype(jnp.bfloat16).astype(jnp.float32)
        else:
            source = source_ref[0].astype(jnp.float32)
            source_re = source[0]
            source_im = source[1]
            in_re = wave[0]
            in_im = wave[1]
        spread_re, spread_im = propagate_block(in_re, in_im, blocks, chirp_re, -chirp_im)
        if not opening:
            passed_ref[0, 0] = (patch_re * spread_re + patch_im * spread_im).astype(jnp.bfloat16)
            passed_ref[0, 1] = (patch_re * spread_im - patch_im * spread_re).astype(jnp.bfloat16)
        if last:
            grad_ref[0, 0] = spread_re.astype(jnp.bfloat16)
            grad_ref[0, 1] = spread_im.astype(jnp.bfloat16)
            return
        term_re = source_re * spread_re + source_im * spread_im
        term_im = source_re * spread_im - source_im * spread_re
        place_term(
            term_re, term_im, rows_ref[index], columns_ref[index], live_ref[index] > 0,
            total_ref, grad_ref if single else None, pad_ref,
        )

        if not single:
            @pl.when(index == pl.num_programs(0) - 1)
            def _():
                grad_ref[...] = total_ref[...].astype(grad_ref.dtype)

    return kernel


def run_adjoint(waves, patches, chirps, blocks, scalars, extra, height, columns_all, last,
                opening=False):
    number, _, width, _ = waves.shape
    wave_spec = pl.BlockSpec((1, 2, width, width), lambda i, *s: (i, 0, 0, 0))
    chirp_spec = pl.BlockSpec((2, width, width), lambda i, *s: (0, 0, 0))
    in_specs = [wave_spec] + ([] if opening else [wave_spec]) + [chirp_spec] + [
        pl.BlockSpec((2 * width, width), lambda i, *s: (0, 0)),
        pl.BlockSpec((width, 2 * width), lambda i, *s: (0, 0)),
    ]
    if last:
        slot_spec = pl.BlockSpec((1, width, width), lambda i, r, c, a, s, o: (s[i], 0, 0))
        in_specs += [slot_spec, slot_spec]
    else:
        in_specs += [wave_spec]
    grid_spec = pltpu.PrefetchScalarGridSpec(
        num_scalar_prefetch=5,
        grid=(number,),
        in_specs=in_specs,
        out_specs=((() if opening else (wave_spec,))
                   + ((wave_spec,) if last else
                      (pl.BlockSpec((2, height, columns_all), lambda i, *s: (0, 0, 0)),))),
        scratch_shapes=[
            pltpu.VMEM((2, height, columns_all), jnp.float32),
            pltpu.VMEM((height + 8, columns_all + 128), jnp.float32),
        ],
    )
    return pl.pallas_call(
        adjoint_kernel(last, number == 1, opening),
        grid_spec=grid_spec,
        out_shape=((() if opening else (jax.ShapeDtypeStruct(waves.shape, jnp.bfloat16),))
                   + ((jax.ShapeDtypeStruct(waves.shape, jnp.bfloat16),) if last else
                      (jax.ShapeDtypeStruct((2, height, columns_all), jnp.bfloat16),))),
    )(*scalars, waves, *(() if opening else (patches,)), chirps, *blocks, *extra)


def place_kernel(rows_ref, columns_ref, live_ref, spread_ref, source_ref, grad_ref, total_ref):
    index = pl.program_id(0)

    @pl.when(index == 0)
    def _():
        total_ref[...] = jnp.zeros(total_ref.shape, total_ref.dtype)

    spread = spread_ref[0].astype(jnp.float32)
    source = source_ref[0].astype(jnp.float32)
    term_re = source[0] * spread[0] + source[1] * spread[1]
    term_im = source[0] * spread[1] - source[1] * spread[0]
    place_term(
        term_re, term_im, rows_ref[index], columns_ref[index], live_ref[index] > 0, total_ref
    )

    @pl.when(index == pl.num_programs(0) - 1)
    def _():
        grad_ref[...] = total_ref[...].astype(grad_ref.dtype)


def run_place(spread, source, scalars, height, columns_all):
    number, _, width, _ = spread.shape
    wave_spec = pl.BlockSpec((1, 2, width, width), lambda i, *s: (i, 0, 0, 0))
    grid_spec = pltpu.PrefetchScalarGridSpec(
        num_scalar_prefetch=3,
        grid=(number,),
        in_specs=[wave_spec, wave_spec],
        out_specs=pl.BlockSpec((2, height, columns_all), lambda i, *s: (0, 0, 0)),
        scratch_shapes=[pltpu.VMEM((2, height, columns_all), jnp.float32)],
    )
    return pl.pallas_call(
        place_kernel,
        grid_spec=grid_spec,
        out_shape=jax.ShapeDtypeStruct((2, height, columns_all), jnp.bfloat16),
    )(*scalars[:3], spread, source)


def first_kernel(rows_ref, columns_ref, order_ref, wave_ref, tile_ref, mine_ref, partner_ref,
                 chirp_ref, dft_rows_ref, dft_cols_ref, result_ref, rows_scratch):
    index = pl.program_id(0)
    width = wave_ref.shape[2]
    height = tile_ref.shape[2] + mine_ref.shape[2]
    columns_all = tile_ref.shape[3]
    first = order_ref[0] == 0
    patch = []
    for part in range(2):
        mine = mine_ref[0, part].astype(jnp.float32)
        partner = partner_ref[0, part].astype(jnp.float32)
        rim = jnp.concatenate(
            [jnp.where(first, mine, partner), jnp.where(first, partner, mine)], axis=1
        )
        rows_tile = tile_ref.shape[2]
        rows_scratch[:, columns_all:] = jnp.zeros(
            (rows_scratch.shape[0], rows_scratch.shape[1] - columns_all), jnp.float32
        )
        rows_scratch[:rows_tile, :columns_all] = tile_ref[0, part]
        rows_scratch[rows_tile:, :columns_all] = rim
        row = rows_ref[index]
        column = columns_ref[index]
        aligned = pl.multiple_of((row // 8) * 8, 8)
        across = pl.multiple_of((column // 128) * 128, 128)
        full = rows_scratch[pl.ds(aligned, width + 8), pl.ds(across, width + 128)]
        full = pltpu.roll(full, (width + 8 - row % 8) % (width + 8), 0)[:width]
        full = pltpu.roll(full, (width + 128 - column % 128) % (width + 128), 1)
        patch.append(full[:, :width])
    wave = wave_ref[0].astype(jnp.float32)
    wave_re = patch[0] * wave[0] - patch[1] * wave[1]
    wave_im = patch[0] * wave[1] + patch[1] * wave[0]
    out_re, out_im = propagate_block(
        wave_re, wave_im, (dft_rows_ref, dft_cols_ref), chirp_ref[0], chirp_ref[1]
    )
    result_ref[0, 0] = out_re.astype(jnp.bfloat16)
    result_ref[0, 1] = out_im.astype(jnp.bfloat16)


def run_first(waves, tile, mine, partner, rows, columns, order, chirps, blocks):
    number, _, width, _ = waves.shape
    wave_spec = pl.BlockSpec((1, 2, width, width), lambda i, r, c, o: (i, 0, 0, 0))
    whole = lambda shape: pl.BlockSpec(shape, lambda i, r, c, o: (0,) * len(shape))
    grid_spec = pltpu.PrefetchScalarGridSpec(
        num_scalar_prefetch=3,
        grid=(number,),
        in_specs=[
            wave_spec,
            whole(tile.shape),
            whole(mine.shape),
            whole(partner.shape),
            whole(chirps.shape),
            whole(blocks[0].shape),
            whole(blocks[1].shape),
        ],
        out_specs=wave_spec,
        scratch_shapes=[
            pltpu.VMEM((tile.shape[2] + mine.shape[2], tile.shape[3] + 128), jnp.float32)
        ],
    )
    return pl.pallas_call(
        first_kernel,
        grid_spec=grid_spec,
        out_shape=jax.ShapeDtypeStruct(waves.shape, jnp.bfloat16),
    )(rows, columns, order, waves, tile, mine, partner, chirps, *blocks)


def local(object_field, probe, positions, counts, measured):
    width = probe.shape[1]
    tile_rows = object_field.shape[2]
    columns_all = object_field.shape[3]
    tile_index = lax.axis_index("tile")
    tile_count = lax.axis_size("tile")
    segment = lax.axis_index("depth")
    depth_count = lax.axis_size("depth")
    batch_index = lax.axis_index("batch")
    batch_count = lax.axis_size("batch")
    half = columns_all // batch_count
    wanted = lax.dynamic_slice_in_dim(object_field[:, :, :width, :], batch_index * half, half, 3)
    mine = from_behind(wanted.astype(jnp.bfloat16), "tile", -1)
    pairs = [(b, (b + 1) % batch_count) for b in range(batch_count)]
    partner = lax.ppermute(mine, "batch", pairs)
    capacity = positions.shape[0]
    share = -(-capacity // batch_count)
    first_core = batch_index == 0
    packed = jnp.concatenate([positions, jnp.broadcast_to(counts[:, None], (1, 2))])
    both_packed = lax.ppermute(packed, "batch", pairs)
    both_positions = both_packed[:-1]
    both_counts = both_packed[-1, :1]
    all_positions = jnp.where(
        first_core,
        jnp.concatenate([positions, both_positions]),
        jnp.concatenate([both_positions, positions]),
    )
    all_counts = jnp.where(
        first_core, jnp.concatenate([counts, both_counts]), jnp.concatenate([both_counts, counts])
    )
    entry = batch_index * share + jnp.arange(share, dtype=jnp.int32)
    live = entry < all_counts[0] + all_counts[1]
    later = entry >= all_counts[0]
    slot = jnp.clip(jnp.where(later, entry - all_counts[0], entry), 0, capacity - 1)
    flat = jnp.where(later, capacity, 0) + slot
    chosen = all_positions[flat]
    other = (later == first_core).astype(jnp.int32)
    local_rows = chosen[:, 0] - tile_index * tile_rows
    local_columns = chosen[:, 1]
    order = jnp.reshape(batch_index, (1,)).astype(jnp.int32)
    patches = cut_patches(object_field, mine, partner, local_rows, local_columns, order, width)
    number = patches.shape[0]
    coef = jnp.where(
        segment == depth_count - 1, jnp.float32(DETECTOR_COEF), jnp.float32(SLICE_COEF)
    )
    chirp_re, chirp_im = chirp_parts(width, coef)
    start = jnp.broadcast_to(probe[None], (number, 2, width, width))

    chirps = jnp.stack([chirp_re, chirp_im])
    dft_re, dft_im = dft_parts(width)
    blocks = (
        jnp.concatenate([dft_re, dft_im], axis=0),
        jnp.concatenate([dft_re, dft_im], axis=1),
    )

    def forward_all(waves):
        return run_first(
            waves, object_field, mine, partner, local_rows, local_columns, order, chirps, blocks
        )

    def silent(waves):
        return jnp.zeros_like(waves)

    carry = start
    inputs = start
    for turn in range(depth_count - 1):
        if turn > 0:
            carry = lax.ppermute(carry, "depth", [(turn - 1, turn)])
            inputs = jnp.where(segment == turn, carry, inputs)
        carry = lax.cond(segment == turn, forward_all, silent, carry)

    measured, carry = lax.optimization_barrier((measured, carry))
    both_measured = lax.ppermute(measured, "batch", pairs)
    height = tile_rows + width
    scalars = (local_rows, local_columns, live.astype(jnp.int32), slot, other)

    def last_pass(incoming):
        return run_adjoint(
            incoming, patches, chirps, blocks, scalars, (measured, both_measured),
            height, columns_all, True,
        )

    def last_silent(incoming):
        return (jnp.zeros_like(incoming), jnp.zeros_like(incoming))

    if depth_count > 1:
        carry = lax.ppermute(carry, "depth", [(depth_count - 2, depth_count - 1)])
    arrived_last = carry
    carry, spread_last = lax.cond(segment == depth_count - 1, last_pass, last_silent, carry)
    gradient = lax.cond(
        segment == depth_count - 1,
        lambda s, a: run_place(s, a, scalars, height, columns_all),
        lambda s, a: jnp.zeros((2, height, columns_all), jnp.bfloat16),
        spread_last,
        arrived_last,
    )

    def back_pass(incoming, previous):
        return run_adjoint(
            incoming, patches, chirps, blocks, scalars, (inputs,), height, columns_all, False
        )

    def opening_pass(incoming, previous):
        (gradient,) = run_adjoint(
            incoming, patches, chirps, blocks, scalars, (inputs,), height, columns_all, False,
            opening=True,
        )
        return (incoming, gradient)

    def back_silent(incoming, previous):
        return (jnp.zeros_like(incoming), previous)

    for turn in reversed(range(depth_count - 1)):
        carry = lax.ppermute(carry, "depth", [(turn + 1, turn)])
        step = opening_pass if turn == 0 else back_pass
        carry, gradient = lax.cond(segment == turn, step, back_silent, carry, gradient)

    gradient = gradient.astype(jnp.bfloat16)
    spill = gradient[:, tile_rows:, :]
    keep = lax.dynamic_slice_in_dim(spill, batch_index * half, half, 2)
    give = lax.dynamic_slice_in_dim(spill, (1 - batch_index) * half, half, 2)
    got = lax.ppermute(give, "batch", pairs)
    spill_sum = (keep.astype(jnp.float32) + got.astype(jnp.float32)).astype(jnp.bfloat16)
    arrived = lax.ppermute(spill_sum, "tile", [(t, t + 1) for t in range(tile_count - 1)])
    own = gradient[:, :tile_rows, :]
    other = lax.ppermute(own, "batch", pairs)
    arrived_other = lax.ppermute(arrived, "batch", pairs)
    incoming = jnp.where(
        first_core,
        jnp.concatenate([arrived, arrived_other], axis=2),
        jnp.concatenate([arrived_other, arrived], axis=2),
    )
    summed = own.astype(jnp.float32) + other.astype(jnp.float32)
    summed = summed.at[:, :width, :].add(incoming.astype(jnp.float32))
    return summed[None]


def solution(mesh):
    placed = (
        P(("groups", "depth"), None, "tile", None),
        P("groups", None, None),
        P(("groups", "tile", "batch"), None),
        P(("groups", "tile", "batch")),
        P(("groups", "tile", "batch"), None, None),
    )
    return jax.shard_map(
        local,
        mesh=mesh,
        in_specs=placed,
        out_specs=P(("groups", "depth"), None, "tile", None),
        check_vma=False,
    )
```

```python
import math

import jax
import jax.numpy as jnp
from jax import lax
from jax.sharding import PartitionSpec as P
from jax.experimental import pallas as pl
from jax.experimental.pallas import tpu as pltpu

SLICE_COEF = 0.002
DETECTOR_COEF = 0.006
RESIDUAL_SCALE = 0.125


def from_behind(block, axis, distance):
    devices = range(lax.axis_size(axis))
    route = [(i - distance, i) for i in devices if i - distance in devices]
    return lax.ppermute(block, axis, route)


def dft_block(width, sign):
    freq = jnp.arange(width, dtype=jnp.int32)
    product = freq[:, None] * freq[None, :] % width
    angle = 2.0 * math.pi / width * product.astype(jnp.float32)
    scale = 1.0 / math.sqrt(width)
    real_part = (jnp.cos(angle) * scale).astype(jnp.bfloat16)
    imag_part = (sign * jnp.sin(angle) * scale).astype(jnp.bfloat16)
    upper = jnp.concatenate([real_part, -imag_part], axis=1)
    lower = jnp.concatenate([imag_part, real_part], axis=1)
    return jnp.concatenate([upper, lower], axis=0)


def dft_right(width, sign):
    freq = jnp.arange(width, dtype=jnp.int32)
    product = freq[:, None] * freq[None, :] % width
    angle = 2.0 * math.pi / width * product.astype(jnp.float32)
    scale = 1.0 / math.sqrt(width)
    real_part = (jnp.cos(angle) * scale).astype(jnp.bfloat16)
    imag_part = (sign * jnp.sin(angle) * scale).astype(jnp.bfloat16)
    upper = jnp.concatenate([real_part, imag_part], axis=1)
    lower = jnp.concatenate([-imag_part, real_part], axis=1)
    return jnp.concatenate([upper, lower], axis=0)


def dft_parts(width):
    freq = jnp.arange(width, dtype=jnp.int32)
    product = freq[:, None] * freq[None, :] % width
    angle = 2.0 * math.pi / width * product.astype(jnp.float32)
    scale = 1.0 / math.sqrt(width)
    real_part = (jnp.cos(angle) * scale).astype(jnp.bfloat16)
    imag_part = (-jnp.sin(angle) * scale).astype(jnp.bfloat16)
    return (real_part, imag_part)


def chirp_parts(width, coef):
    freq = jnp.arange(width, dtype=jnp.int32)
    shifted = (freq + width // 2) % width - width // 2
    square = shifted * shifted
    total = (square[:, None] + square[None, :]).astype(jnp.float32)
    phase = -coef * total
    return (jnp.cos(phase), jnp.sin(phase))


def left_apply(block, waves):
    number = waves.shape[0]
    width = waves.shape[2]
    stacked = waves.reshape(number, 2 * width, width)
    result = jnp.einsum("ij,gjk->gik", block, stacked, preferred_element_type=jnp.float32)
    return result.reshape(number, 2, width, width)


def propagate(waves, forward_block, inverse_block, chirp_re, chirp_im):
    first = left_apply(forward_block, waves).astype(jnp.bfloat16)
    spectrum = left_apply(forward_block, jnp.swapaxes(first, -1, -2))
    spec_re = spectrum[:, 0]
    spec_im = spectrum[:, 1]
    filtered = jnp.stack(
        [spec_re * chirp_re - spec_im * chirp_im, spec_re * chirp_im + spec_im * chirp_re], axis=1
    ).astype(jnp.bfloat16)
    back = left_apply(inverse_block, filtered).astype(jnp.bfloat16)
    return left_apply(inverse_block, jnp.swapaxes(back, -1, -2)).astype(jnp.bfloat16)


def transmit(waves, patch):
    values = waves.astype(jnp.float32)
    wave_re = values[:, 0]
    wave_im = values[:, 1]
    return jnp.stack(
        [
            patch[:, 0] * wave_re - patch[:, 1] * wave_im,
            patch[:, 0] * wave_im + patch[:, 1] * wave_re,
        ],
        axis=1,
    ).astype(jnp.bfloat16)


def residual_wave(waves, measured):
    values = waves.astype(jnp.float32)
    intensity = values[:, 0] * values[:, 0] + values[:, 1] * values[:, 1]
    weight = RESIDUAL_SCALE * (intensity - measured)
    return jnp.stack([weight * values[:, 0], weight * values[:, 1]], axis=1).astype(jnp.bfloat16)


def adjoint_terms(incoming, forward_block, inverse_block, chirp_re, chirp_im, inputs, patch):
    spread = propagate(incoming, forward_block, inverse_block, chirp_re, -chirp_im).astype(
        jnp.float32
    )
    source = inputs.astype(jnp.float32)
    term = jnp.stack(
        [
            source[:, 0] * spread[:, 0] + source[:, 1] * spread[:, 1],
            source[:, 0] * spread[:, 1] - source[:, 1] * spread[:, 0],
        ],
        axis=1,
    )
    passed = jnp.stack(
        [
            patch[:, 0] * spread[:, 0] + patch[:, 1] * spread[:, 1],
            patch[:, 0] * spread[:, 1] - patch[:, 1] * spread[:, 0],
        ],
        axis=1,
    ).astype(jnp.bfloat16)
    return (passed, term)


def wave_kernel(transmit_first, residual_after, backward):
    def kernel(*refs):
        refs = list(refs)
        wave_ref = refs.pop(0)
        patch_ref = refs.pop(0)
        chirp_ref = refs.pop(0)
        blocks = refs[:2]
        refs = refs[2:]
        extra_ref = refs.pop(0) if (residual_after or backward) else None
        wave = wave_ref[0].astype(jnp.float32)
        patch_re = patch_ref[0, 0]
        patch_im = patch_ref[0, 1]
        if transmit_first:
            wave_re = patch_re * wave[0] - patch_im * wave[1]
            wave_im = patch_re * wave[1] + patch_im * wave[0]
        else:
            wave_re = wave[0]
            wave_im = wave[1]
        chirp_re = chirp_ref[0]
        chirp_im = chirp_ref[1]
        if backward:
            chirp_im = -chirp_im
        out_re, out_im = propagate_block(wave_re, wave_im, blocks, chirp_re, chirp_im)
        if residual_after:
            measured = extra_ref[0]
            weight = RESIDUAL_SCALE * (out_re * out_re + out_im * out_im - measured)
            result_ref = refs[0]
            result_ref[0, 0] = (weight * out_re).astype(jnp.bfloat16)
            result_ref[0, 1] = (weight * out_im).astype(jnp.bfloat16)
        elif backward:
            source = extra_ref[0].astype(jnp.float32)
            passed_ref, term_ref = refs[0], refs[1]
            passed_ref[0, 0] = (patch_re * out_re + patch_im * out_im).astype(jnp.bfloat16)
            passed_ref[0, 1] = (patch_re * out_im - patch_im * out_re).astype(jnp.bfloat16)
            term_ref[0, 0] = source[0] * out_re + source[1] * out_im
            term_ref[0, 1] = source[0] * out_im - source[1] * out_re
        else:
            result_ref = refs[0]
            result_ref[0, 0] = out_re.astype(jnp.bfloat16)
            result_ref[0, 1] = out_im.astype(jnp.bfloat16)

    return kernel


def run_waves(waves, patches, chirps, blocks, extra=None, transmit_first=True, residual_after=False, backward=False):
    number, _, width, _ = waves.shape
    wave_spec = pl.BlockSpec((1, 2, width, width), lambda i: (i, 0, 0, 0))
    chirp_spec = pl.BlockSpec((2, width, width), lambda i: (0, 0, 0))
    in_specs = [wave_spec, wave_spec, chirp_spec] + [
        pl.BlockSpec((2 * width, width), lambda i: (0, 0)),
        pl.BlockSpec((width, 2 * width), lambda i: (0, 0)),
    ]
    args = [waves, patches, chirps] + list(blocks)
    if residual_after:
        in_specs.append(pl.BlockSpec((1, width, width), lambda i: (i, 0, 0)))
        args.append(extra)
    if backward:
        in_specs.append(wave_spec)
        args.append(extra)
        out_shape = (
            jax.ShapeDtypeStruct(waves.shape, jnp.bfloat16),
            jax.ShapeDtypeStruct(waves.shape, jnp.float32),
        )
        out_specs = (wave_spec, wave_spec)
    else:
        out_shape = jax.ShapeDtypeStruct(waves.shape, jnp.bfloat16)
        out_specs = wave_spec
    return pl.pallas_call(
        wave_kernel(transmit_first, residual_after, backward),
        grid=(number,),
        in_specs=in_specs,
        out_specs=out_specs,
        out_shape=out_shape,
    )(*args)


def scatter_kernel(rows_ref, columns_ref, live_ref, terms_ref, out_ref):
    index = pl.program_id(0)

    @pl.when(index == 0)
    def _():
        out_ref[...] = jnp.zeros(out_ref.shape, out_ref.dtype)

    width = terms_ref.shape[2]
    height = out_ref.shape[1]
    columns_all = out_ref.shape[2]
    row = rows_ref[index]
    column = columns_ref[index]
    alive = live_ref[index] > 0
    for part in range(2):
        term = jnp.where(alive, terms_ref[0, part], 0.0)
        wide = jnp.concatenate(
            [term, jnp.zeros((width, columns_all - width), jnp.float32)], axis=1
        )
        wide = pltpu.roll(wide, column, 1)
        tall = jnp.concatenate(
            [wide, jnp.zeros((height - width, columns_all), jnp.float32)], axis=0
        )
        tall = pltpu.roll(tall, row, 0)
        out_ref[part] = out_ref[part] + tall


def scatter_terms(terms, rows, columns, live, height, columns_all):
    number, _, width, _ = terms.shape
    grid_spec = pltpu.PrefetchScalarGridSpec(
        num_scalar_prefetch=3,
        grid=(number,),
        in_specs=[pl.BlockSpec((1, 2, width, width), lambda i, r, c, a: (i, 0, 0, 0))],
        out_specs=pl.BlockSpec((2, height, columns_all), lambda i, r, c, a: (0, 0, 0)),
    )
    return pl.pallas_call(
        scatter_kernel,
        grid_spec=grid_spec,
        out_shape=jax.ShapeDtypeStruct((2, height, columns_all), jnp.float32),
    )(rows, columns, live.astype(jnp.int32), terms)


def cut_kernel(rows_ref, columns_ref, order_ref, tile_ref, mine_ref, partner_ref, out_ref):
    index = pl.program_id(0)
    width = out_ref.shape[2]
    height = tile_ref.shape[2] + mine_ref.shape[2]
    columns_all = tile_ref.shape[3]
    row_shift = (height - rows_ref[index]) % height
    column_shift = (columns_all - columns_ref[index]) % columns_all
    first = order_ref[0] == 0
    for part in range(2):
        mine = mine_ref[0, part].astype(jnp.float32)
        partner = partner_ref[0, part].astype(jnp.float32)
        rim = jnp.concatenate(
            [jnp.where(first, mine, partner), jnp.where(first, partner, mine)], axis=1
        )
        full = jnp.concatenate([tile_ref[0, part], rim], axis=0)
        full = pltpu.roll(full, row_shift, 0)[:width]
        full = pltpu.roll(full, column_shift, 1)[:, :width]
        out_ref[0, part] = full


def cut_patches(tile, mine, partner, rows, columns, order, width):
    number = rows.shape[0]
    grid_spec = pltpu.PrefetchScalarGridSpec(
        num_scalar_prefetch=3,
        grid=(number,),
        in_specs=[
            pl.BlockSpec(tile.shape, lambda i, r, c, o: (0, 0, 0, 0)),
            pl.BlockSpec(mine.shape, lambda i, r, c, o: (0, 0, 0, 0)),
            pl.BlockSpec(partner.shape, lambda i, r, c, o: (0, 0, 0, 0)),
        ],
        out_specs=pl.BlockSpec((1, 2, width, width), lambda i, r, c, o: (i, 0, 0, 0)),
    )
    return pl.pallas_call(
        cut_kernel,
        grid_spec=grid_spec,
        out_shape=jax.ShapeDtypeStruct((number, 2, width, width), jnp.float32),
    )(rows, columns, order, tile, mine, partner)


def propagate_block(wave_re, wave_im, blocks, chirp_re, chirp_im):
    rows_ref, cols_ref = blocks
    width = wave_re.shape[0]
    dft_rows = rows_ref[...]
    dft_cols = cols_ref[...]

    def left(part_re, part_im):
        lanes = jnp.concatenate([part_re, part_im], axis=1).astype(jnp.bfloat16)
        return jnp.dot(dft_rows, lanes, preferred_element_type=jnp.float32)

    def right(part_re, part_im):
        rows = jnp.concatenate([part_re, part_im], axis=0).astype(jnp.bfloat16)
        return jnp.dot(rows, dft_cols, preferred_element_type=jnp.float32)

    first = left(wave_re, wave_im)
    z_re = (first[:width, :width] - first[width:, width:]).astype(jnp.bfloat16)
    z_im = (first[:width, width:] + first[width:, :width]).astype(jnp.bfloat16)
    second = right(z_re, z_im)
    spec_re = second[:width, :width] - second[width:, width:]
    spec_im = second[:width, width:] + second[width:, :width]
    w_re = spec_re * chirp_re - spec_im * chirp_im
    w_im = spec_re * chirp_im + spec_im * chirp_re
    third = right(w_re.astype(jnp.bfloat16), w_im.astype(jnp.bfloat16))
    v_re = (third[:width, :width] + third[width:, width:]).astype(jnp.bfloat16)
    v_im = (third[width:, :width] - third[:width, width:]).astype(jnp.bfloat16)
    fourth = left(v_re, v_im)
    out_re = (fourth[:width, :width] + fourth[width:, width:]).astype(jnp.bfloat16)
    out_im = (fourth[:width, width:] - fourth[width:, :width]).astype(jnp.bfloat16)
    return (out_re.astype(jnp.float32), out_im.astype(jnp.float32))


def place_term(term_re, term_im, row, column, alive, total_ref, direct_ref=None, pad_ref=None):
    width = term_re.shape[0]
    height = total_ref.shape[1]
    columns_all = total_ref.shape[2]
    row_shift = row % height
    column_shift = column % columns_all
    for part, term in enumerate((term_re, term_im)):
        term = jnp.where(alive, term, 0.0)
        if direct_ref is not None and pad_ref is not None:
            pad_ref[...] = jnp.zeros(pad_ref.shape, jnp.float32)
            block = jnp.concatenate([term, jnp.zeros((width, 128), jnp.float32)], axis=1)
            block = jnp.concatenate([block, jnp.zeros((8, width + 128), jnp.float32)], axis=0)
            block = pltpu.roll(pltpu.roll(block, row % 8, 0), column % 128, 1)
            aligned = pl.multiple_of((row // 8) * 8, 8)
            across = pl.multiple_of((column // 128) * 128, 128)
            pad_ref[pl.ds(aligned, width + 8), pl.ds(across, width + 128)] = block
            direct_ref[part] = pad_ref[:height, :columns_all].astype(direct_ref.dtype)
            continue
        wide = jnp.concatenate(
            [term, jnp.zeros((width, columns_all - width), jnp.float32)], axis=1
        )
        wide = pltpu.roll(wide, column_shift, 1)
        if height == 2 * width:
            rolled = pltpu.roll(wide, row % width, 0)
            below = lax.broadcasted_iota(jnp.int32, rolled.shape, 0) < row
            upper = jnp.where(below, 0.0, rolled)
            lower = jnp.where(below, rolled, 0.0)
            if direct_ref is None:
                total_ref[part, :width] = total_ref[part, :width] + upper
                total_ref[part, width:] = total_ref[part, width:] + lower
            else:
                direct_ref[part, :width] = upper.astype(direct_ref.dtype)
                direct_ref[part, width:] = lower.astype(direct_ref.dtype)
            continue
        tall = jnp.concatenate(
            [wide, jnp.zeros((height - width, columns_all), jnp.float32)], axis=0
        )
        if direct_ref is None:
            total_ref[part] = total_ref[part] + pltpu.roll(tall, row_shift, 0)
        else:
            direct_ref[part] = pltpu.roll(tall, row_shift, 0).astype(direct_ref.dtype)


def adjoint_kernel(last, single, opening=False):
    def kernel(rows_ref, columns_ref, live_ref, slot_ref, other_ref, *refs):
        refs = list(refs)
        wave_ref = refs.pop(0)
        patch_ref = None if opening else refs.pop(0)
        chirp_ref = refs.pop(0)
        blocks = refs[:2]
        refs = refs[2:]
        if last:
            own_ref = refs.pop(0)
            partner_ref = refs.pop(0)
        else:
            source_ref = refs.pop(0)
        if opening:
            grad_ref, total_ref, pad_ref = refs
            passed_ref = None
        else:
            passed_ref, grad_ref, total_ref, pad_ref = refs
        index = pl.program_id(0)

        if not single:
            @pl.when(index == 0)
            def _():
                total_ref[...] = jnp.zeros(total_ref.shape, total_ref.dtype)

        wave = wave_ref[0].astype(jnp.float32)
        if not opening:
            patch_re = patch_ref[0, 0]
            patch_im = patch_ref[0, 1]
        chirp_re = chirp_ref[0]
        chirp_im = chirp_ref[1]
        if last:
            source_re = wave[0]
            source_im = wave[1]
            lit_re = patch_re * wave[0] - patch_im * wave[1]
            lit_im = patch_re * wave[1] + patch_im * wave[0]
            out_re, out_im = propagate_block(lit_re, lit_im, blocks, chirp_re, chirp_im)
            measured = jnp.where(other_ref[index] > 0, partner_ref[0], own_ref[0])
            weight = RESIDUAL_SCALE * (out_re * out_re + out_im * out_im - measured)
            in_re = (weight * out_re).astype(jnp.bfloat16).astype(jnp.float32)
            in_im = (weight * out_im).astype(jnp.bfloat16).astype(jnp.float32)
        else:
            source = source_ref[0].astype(jnp.float32)
            source_re = source[0]
            source_im = source[1]
            in_re = wave[0]
            in_im = wave[1]
        spread_re, spread_im = propagate_block(in_re, in_im, blocks, chirp_re, -chirp_im)
        if not opening:
            passed_ref[0, 0] = (patch_re * spread_re + patch_im * spread_im).astype(jnp.bfloat16)
            passed_ref[0, 1] = (patch_re * spread_im - patch_im * spread_re).astype(jnp.bfloat16)
        if last:
            grad_ref[0, 0] = spread_re.astype(jnp.bfloat16)
            grad_ref[0, 1] = spread_im.astype(jnp.bfloat16)
            return
        term_re = source_re * spread_re + source_im * spread_im
        term_im = source_re * spread_im - source_im * spread_re
        place_term(
            term_re, term_im, rows_ref[index], columns_ref[index], live_ref[index] > 0,
            total_ref, grad_ref if single else None, pad_ref,
        )

        if not single:
            @pl.when(index == pl.num_programs(0) - 1)
            def _():
                grad_ref[...] = total_ref[...].astype(grad_ref.dtype)

    return kernel


def run_adjoint(waves, patches, chirps, blocks, scalars, extra, height, columns_all, last,
                opening=False):
    number, _, width, _ = waves.shape
    wave_spec = pl.BlockSpec((1, 2, width, width), lambda i, *s: (i, 0, 0, 0))
    chirp_spec = pl.BlockSpec((2, width, width), lambda i, *s: (0, 0, 0))
    in_specs = [wave_spec] + ([] if opening else [wave_spec]) + [chirp_spec] + [
        pl.BlockSpec((2 * width, width), lambda i, *s: (0, 0)),
        pl.BlockSpec((width, 2 * width), lambda i, *s: (0, 0)),
    ]
    if last:
        slot_spec = pl.BlockSpec((1, width, width), lambda i, r, c, a, s, o: (s[i], 0, 0))
        in_specs += [slot_spec, slot_spec]
    else:
        in_specs += [wave_spec]
    grid_spec = pltpu.PrefetchScalarGridSpec(
        num_scalar_prefetch=5,
        grid=(number,),
        in_specs=in_specs,
        out_specs=((() if opening else (wave_spec,))
                   + ((wave_spec,) if last else
                      (pl.BlockSpec((2, height, columns_all), lambda i, *s: (0, 0, 0)),))),
        scratch_shapes=[
            pltpu.VMEM((2, height, columns_all), jnp.float32),
            pltpu.VMEM((height + 8, columns_all + 128), jnp.float32),
        ],
    )
    return pl.pallas_call(
        adjoint_kernel(last, number == 1, opening),
        grid_spec=grid_spec,
        out_shape=((() if opening else (jax.ShapeDtypeStruct(waves.shape, jnp.bfloat16),))
                   + ((jax.ShapeDtypeStruct(waves.shape, jnp.bfloat16),) if last else
                      (jax.ShapeDtypeStruct((2, height, columns_all), jnp.bfloat16),))),
    )(*scalars, waves, *(() if opening else (patches,)), chirps, *blocks, *extra)


def place_kernel(rows_ref, columns_ref, live_ref, spread_ref, source_ref, grad_ref, total_ref):
    index = pl.program_id(0)

    @pl.when(index == 0)
    def _():
        total_ref[...] = jnp.zeros(total_ref.shape, total_ref.dtype)

    spread = spread_ref[0].astype(jnp.float32)
    source = source_ref[0].astype(jnp.float32)
    term_re = source[0] * spread[0] + source[1] * spread[1]
    term_im = source[0] * spread[1] - source[1] * spread[0]
    place_term(
        term_re, term_im, rows_ref[index], columns_ref[index], live_ref[index] > 0, total_ref
    )

    @pl.when(index == pl.num_programs(0) - 1)
    def _():
        grad_ref[...] = total_ref[...].astype(grad_ref.dtype)


def run_place(spread, source, scalars, height, columns_all):
    number, _, width, _ = spread.shape
    wave_spec = pl.BlockSpec((1, 2, width, width), lambda i, *s: (i, 0, 0, 0))
    grid_spec = pltpu.PrefetchScalarGridSpec(
        num_scalar_prefetch=3,
        grid=(number,),
        in_specs=[wave_spec, wave_spec],
        out_specs=pl.BlockSpec((2, height, columns_all), lambda i, *s: (0, 0, 0)),
        scratch_shapes=[pltpu.VMEM((2, height, columns_all), jnp.float32)],
    )
    return pl.pallas_call(
        place_kernel,
        grid_spec=grid_spec,
        out_shape=jax.ShapeDtypeStruct((2, height, columns_all), jnp.bfloat16),
    )(*scalars[:3], spread, source)


def first_kernel(rows_ref, columns_ref, order_ref, wave_ref, tile_ref, mine_ref, partner_ref,
                 chirp_ref, dft_rows_ref, dft_cols_ref, result_ref, rows_scratch):
    index = pl.program_id(0)
    width = wave_ref.shape[2]
    height = tile_ref.shape[2] + mine_ref.shape[2]
    columns_all = tile_ref.shape[3]
    first = order_ref[0] == 0
    patch = []
    for part in range(2):
        mine = mine_ref[0, part].astype(jnp.float32)
        partner = partner_ref[0, part].astype(jnp.float32)
        rim = jnp.concatenate(
            [jnp.where(first, mine, partner), jnp.where(first, partner, mine)], axis=1
        )
        rows_tile = tile_ref.shape[2]
        rows_scratch[:, columns_all:] = jnp.zeros(
            (rows_scratch.shape[0], rows_scratch.shape[1] - columns_all), jnp.float32
        )
        rows_scratch[:rows_tile, :columns_all] = tile_ref[0, part]
        rows_scratch[rows_tile:, :columns_all] = rim
        row = rows_ref[index]
        column = columns_ref[index]
        aligned = pl.multiple_of((row // 8) * 8, 8)
        across = pl.multiple_of((column // 128) * 128, 128)
        full = rows_scratch[pl.ds(aligned, width + 8), pl.ds(across, width + 128)]
        full = pltpu.roll(full, (width + 8 - row % 8) % (width + 8), 0)[:width]
        full = pltpu.roll(full, (width + 128 - column % 128) % (width + 128), 1)
        patch.append(full[:, :width])
    wave = wave_ref[0].astype(jnp.float32)
    wave_re = patch[0] * wave[0] - patch[1] * wave[1]
    wave_im = patch[0] * wave[1] + patch[1] * wave[0]
    out_re, out_im = propagate_block(
        wave_re, wave_im, (dft_rows_ref, dft_cols_ref), chirp_ref[0], chirp_ref[1]
    )
    result_ref[0, 0] = out_re.astype(jnp.bfloat16)
    result_ref[0, 1] = out_im.astype(jnp.bfloat16)


def run_first(waves, tile, mine, partner, rows, columns, order, chirps, blocks):
    number, _, width, _ = waves.shape
    wave_spec = pl.BlockSpec((1, 2, width, width), lambda i, r, c, o: (i, 0, 0, 0))
    whole = lambda shape: pl.BlockSpec(shape, lambda i, r, c, o: (0,) * len(shape))
    grid_spec = pltpu.PrefetchScalarGridSpec(
        num_scalar_prefetch=3,
        grid=(number,),
        in_specs=[
            wave_spec,
            whole(tile.shape),
            whole(mine.shape),
            whole(partner.shape),
            whole(chirps.shape),
            whole(blocks[0].shape),
            whole(blocks[1].shape),
        ],
        out_specs=wave_spec,
        scratch_shapes=[
            pltpu.VMEM((tile.shape[2] + mine.shape[2], tile.shape[3] + 128), jnp.float32)
        ],
    )
    return pl.pallas_call(
        first_kernel,
        grid_spec=grid_spec,
        out_shape=jax.ShapeDtypeStruct(waves.shape, jnp.bfloat16),
    )(rows, columns, order, waves, tile, mine, partner, chirps, *blocks)


def local(object_field, probe, positions, counts, measured):
    width = probe.shape[1]
    tile_rows = object_field.shape[2]
    columns_all = object_field.shape[3]
    tile_index = lax.axis_index("tile")
    tile_count = lax.axis_size("tile")
    segment = lax.axis_index("depth")
    depth_count = lax.axis_size("depth")
    batch_index = lax.axis_index("batch")
    batch_count = lax.axis_size("batch")
    half = columns_all // batch_count
    wanted = lax.dynamic_slice_in_dim(object_field[:, :, :width, :], batch_index * half, half, 3)
    mine = from_behind(wanted.astype(jnp.bfloat16), "tile", -1)
    pairs = [(b, (b + 1) % batch_count) for b in range(batch_count)]
    partner = lax.ppermute(mine, "batch", pairs)
    capacity = positions.shape[0]
    share = -(-capacity // batch_count)
    first_core = batch_index == 0
    both_positions = lax.ppermute(positions, "batch", pairs)
    both_counts = lax.ppermute(counts, "batch", pairs)
    all_positions = jnp.where(
        first_core,
        jnp.concatenate([positions, both_positions]),
        jnp.concatenate([both_positions, positions]),
    )
    all_counts = jnp.where(
        first_core, jnp.concatenate([counts, both_counts]), jnp.concatenate([both_counts, counts])
    )
    entry = batch_index * share + jnp.arange(share, dtype=jnp.int32)
    live = entry < all_counts[0] + all_counts[1]
    later = entry >= all_counts[0]
    slot = jnp.clip(jnp.where(later, entry - all_counts[0], entry), 0, capacity - 1)
    flat = jnp.where(later, capacity, 0) + slot
    chosen = all_positions[flat]
    other = (later == first_core).astype(jnp.int32)
    local_rows = chosen[:, 0] - tile_index * tile_rows
    local_columns = chosen[:, 1]
    order = jnp.reshape(batch_index, (1,)).astype(jnp.int32)
    patches = cut_patches(object_field, mine, partner, local_rows, local_columns, order, width)
    number = patches.shape[0]
    coef = jnp.where(
        segment == depth_count - 1, jnp.float32(DETECTOR_COEF), jnp.float32(SLICE_COEF)
    )
    chirp_re, chirp_im = chirp_parts(width, coef)
    start = jnp.broadcast_to(probe[None], (number, 2, width, width))

    chirps = jnp.stack([chirp_re, chirp_im])
    dft_re, dft_im = dft_parts(width)
    blocks = (
        jnp.concatenate([dft_re, dft_im], axis=0),
        jnp.concatenate([dft_re, dft_im], axis=1),
    )

    def forward_all(waves):
        return run_first(
            waves, object_field, mine, partner, local_rows, local_columns, order, chirps, blocks
        )

    def silent(waves):
        return jnp.zeros_like(waves)

    carry = start
    inputs = start
    for turn in range(depth_count - 1):
        if turn > 0:
            carry = lax.ppermute(carry, "depth", [(turn - 1, turn)])
            inputs = jnp.where(segment == turn, carry, inputs)
        carry = lax.cond(segment == turn, forward_all, silent, carry)

    both_measured = lax.ppermute(measured, "batch", pairs)
    height = tile_rows + width
    scalars = (local_rows, local_columns, live.astype(jnp.int32), slot, other)

    def last_pass(incoming):
        return run_adjoint(
            incoming, patches, chirps, blocks, scalars, (measured, both_measured),
            height, columns_all, True,
        )

    def last_silent(incoming):
        return (jnp.zeros_like(incoming), jnp.zeros_like(incoming))

    if depth_count > 1:
        carry = lax.ppermute(carry, "depth", [(depth_count - 2, depth_count - 1)])
    arrived_last = carry
    carry, spread_last = lax.cond(segment == depth_count - 1, last_pass, last_silent, carry)
    gradient = lax.cond(
        segment == depth_count - 1,
        lambda s, a: run_place(s, a, scalars, height, columns_all),
        lambda s, a: jnp.zeros((2, height, columns_all), jnp.bfloat16),
        spread_last,
        arrived_last,
    )

    def back_pass(incoming, previous):
        return run_adjoint(
            incoming, patches, chirps, blocks, scalars, (inputs,), height, columns_all, False
        )

    def opening_pass(incoming, previous):
        (gradient,) = run_adjoint(
            incoming, patches, chirps, blocks, scalars, (inputs,), height, columns_all, False,
            opening=True,
        )
        return (incoming, gradient)

    def back_silent(incoming, previous):
        return (jnp.zeros_like(incoming), previous)

    for turn in reversed(range(depth_count - 1)):
        carry = lax.ppermute(carry, "depth", [(turn + 1, turn)])
        step = opening_pass if turn == 0 else back_pass
        carry, gradient = lax.cond(segment == turn, step, back_silent, carry, gradient)

    gradient = gradient.astype(jnp.bfloat16)
    spill = gradient[:, tile_rows:, :]
    keep = lax.dynamic_slice_in_dim(spill, batch_index * half, half, 2)
    give = lax.dynamic_slice_in_dim(spill, (1 - batch_index) * half, half, 2)
    got = lax.ppermute(give, "batch", pairs)
    spill_sum = (keep.astype(jnp.float32) + got.astype(jnp.float32)).astype(jnp.bfloat16)
    arrived = lax.ppermute(spill_sum, "tile", [(t, t + 1) for t in range(tile_count - 1)])
    own = gradient[:, :tile_rows, :]
    other = lax.ppermute(own, "batch", pairs)
    arrived_other = lax.ppermute(arrived, "batch", pairs)
    incoming = jnp.where(
        first_core,
        jnp.concatenate([arrived, arrived_other], axis=2),
        jnp.concatenate([arrived_other, arrived], axis=2),
    )
    summed = own.astype(jnp.float32) + other.astype(jnp.float32)
    summed = summed.at[:, :width, :].add(incoming.astype(jnp.float32))
    return summed[None]


def solution(mesh):
    placed = (
        P(("groups", "depth"), None, "tile", None),
        P("groups", None, None),
        P(("groups", "tile", "batch"), None),
        P(("groups", "tile", "batch")),
        P(("groups", "tile", "batch"), None, None),
    )
    return jax.shard_map(
        local,
        mesh=mesh,
        in_specs=placed,
        out_specs=P(("groups", "depth"), None, "tile", None),
        check_vma=False,
    )
```

```python
import math

import jax
import jax.numpy as jnp
from jax import lax
from jax.sharding import PartitionSpec as P
from jax.experimental import pallas as pl
from jax.experimental.pallas import tpu as pltpu

SLICE_COEF = 0.002
DETECTOR_COEF = 0.006
RESIDUAL_SCALE = 0.125


def from_behind(block, axis, distance):
    devices = range(lax.axis_size(axis))
    route = [(i - distance, i) for i in devices if i - distance in devices]
    return lax.ppermute(block, axis, route)


def dft_block(width, sign):
    freq = jnp.arange(width, dtype=jnp.int32)
    product = freq[:, None] * freq[None, :] % width
    angle = 2.0 * math.pi / width * product.astype(jnp.float32)
    scale = 1.0 / math.sqrt(width)
    real_part = (jnp.cos(angle) * scale).astype(jnp.bfloat16)
    imag_part = (sign * jnp.sin(angle) * scale).astype(jnp.bfloat16)
    upper = jnp.concatenate([real_part, -imag_part], axis=1)
    lower = jnp.concatenate([imag_part, real_part], axis=1)
    return jnp.concatenate([upper, lower], axis=0)


def dft_right(width, sign):
    freq = jnp.arange(width, dtype=jnp.int32)
    product = freq[:, None] * freq[None, :] % width
    angle = 2.0 * math.pi / width * product.astype(jnp.float32)
    scale = 1.0 / math.sqrt(width)
    real_part = (jnp.cos(angle) * scale).astype(jnp.bfloat16)
    imag_part = (sign * jnp.sin(angle) * scale).astype(jnp.bfloat16)
    upper = jnp.concatenate([real_part, imag_part], axis=1)
    lower = jnp.concatenate([-imag_part, real_part], axis=1)
    return jnp.concatenate([upper, lower], axis=0)


def dft_parts(width):
    freq = jnp.arange(width, dtype=jnp.int32)
    product = freq[:, None] * freq[None, :] % width
    angle = 2.0 * math.pi / width * product.astype(jnp.float32)
    scale = 1.0 / math.sqrt(width)
    real_part = (jnp.cos(angle) * scale).astype(jnp.bfloat16)
    imag_part = (-jnp.sin(angle) * scale).astype(jnp.bfloat16)
    return (real_part, imag_part)


def chirp_parts(width, coef):
    freq = jnp.arange(width, dtype=jnp.int32)
    shifted = (freq + width // 2) % width - width // 2
    square = shifted * shifted
    total = (square[:, None] + square[None, :]).astype(jnp.float32)
    phase = -coef * total
    return (jnp.cos(phase), jnp.sin(phase))


def left_apply(block, waves):
    number = waves.shape[0]
    width = waves.shape[2]
    stacked = waves.reshape(number, 2 * width, width)
    result = jnp.einsum("ij,gjk->gik", block, stacked, preferred_element_type=jnp.float32)
    return result.reshape(number, 2, width, width)


def propagate(waves, forward_block, inverse_block, chirp_re, chirp_im):
    first = left_apply(forward_block, waves).astype(jnp.bfloat16)
    spectrum = left_apply(forward_block, jnp.swapaxes(first, -1, -2))
    spec_re = spectrum[:, 0]
    spec_im = spectrum[:, 1]
    filtered = jnp.stack(
        [spec_re * chirp_re - spec_im * chirp_im, spec_re * chirp_im + spec_im * chirp_re], axis=1
    ).astype(jnp.bfloat16)
    back = left_apply(inverse_block, filtered).astype(jnp.bfloat16)
    return left_apply(inverse_block, jnp.swapaxes(back, -1, -2)).astype(jnp.bfloat16)


def transmit(waves, patch):
    values = waves.astype(jnp.float32)
    wave_re = values[:, 0]
    wave_im = values[:, 1]
    return jnp.stack(
        [
            patch[:, 0] * wave_re - patch[:, 1] * wave_im,
            patch[:, 0] * wave_im + patch[:, 1] * wave_re,
        ],
        axis=1,
    ).astype(jnp.bfloat16)


def residual_wave(waves, measured):
    values = waves.astype(jnp.float32)
    intensity = values[:, 0] * values[:, 0] + values[:, 1] * values[:, 1]
    weight = RESIDUAL_SCALE * (intensity - measured)
    return jnp.stack([weight * values[:, 0], weight * values[:, 1]], axis=1).astype(jnp.bfloat16)


def adjoint_terms(incoming, forward_block, inverse_block, chirp_re, chirp_im, inputs, patch):
    spread = propagate(incoming, forward_block, inverse_block, chirp_re, -chirp_im).astype(
        jnp.float32
    )
    source = inputs.astype(jnp.float32)
    term = jnp.stack(
        [
            source[:, 0] * spread[:, 0] + source[:, 1] * spread[:, 1],
            source[:, 0] * spread[:, 1] - source[:, 1] * spread[:, 0],
        ],
        axis=1,
    )
    passed = jnp.stack(
        [
            patch[:, 0] * spread[:, 0] + patch[:, 1] * spread[:, 1],
            patch[:, 0] * spread[:, 1] - patch[:, 1] * spread[:, 0],
        ],
        axis=1,
    ).astype(jnp.bfloat16)
    return (passed, term)


def wave_kernel(transmit_first, residual_after, backward):
    def kernel(*refs):
        refs = list(refs)
        wave_ref = refs.pop(0)
        patch_ref = refs.pop(0)
        chirp_ref = refs.pop(0)
        blocks = refs[:2]
        refs = refs[2:]
        extra_ref = refs.pop(0) if (residual_after or backward) else None
        wave = wave_ref[0].astype(jnp.float32)
        patch_re = patch_ref[0, 0]
        patch_im = patch_ref[0, 1]
        if transmit_first:
            wave_re = patch_re * wave[0] - patch_im * wave[1]
            wave_im = patch_re * wave[1] + patch_im * wave[0]
        else:
            wave_re = wave[0]
            wave_im = wave[1]
        chirp_re = chirp_ref[0]
        chirp_im = chirp_ref[1]
        if backward:
            chirp_im = -chirp_im
        out_re, out_im = propagate_block(wave_re, wave_im, blocks, chirp_re, chirp_im)
        if residual_after:
            measured = extra_ref[0]
            weight = RESIDUAL_SCALE * (out_re * out_re + out_im * out_im - measured)
            result_ref = refs[0]
            result_ref[0, 0] = (weight * out_re).astype(jnp.bfloat16)
            result_ref[0, 1] = (weight * out_im).astype(jnp.bfloat16)
        elif backward:
            source = extra_ref[0].astype(jnp.float32)
            passed_ref, term_ref = refs[0], refs[1]
            passed_ref[0, 0] = (patch_re * out_re + patch_im * out_im).astype(jnp.bfloat16)
            passed_ref[0, 1] = (patch_re * out_im - patch_im * out_re).astype(jnp.bfloat16)
            term_ref[0, 0] = source[0] * out_re + source[1] * out_im
            term_ref[0, 1] = source[0] * out_im - source[1] * out_re
        else:
            result_ref = refs[0]
            result_ref[0, 0] = out_re.astype(jnp.bfloat16)
            result_ref[0, 1] = out_im.astype(jnp.bfloat16)

    return kernel


def run_waves(waves, patches, chirps, blocks, extra=None, transmit_first=True, residual_after=False, backward=False):
    number, _, width, _ = waves.shape
    wave_spec = pl.BlockSpec((1, 2, width, width), lambda i: (i, 0, 0, 0))
    chirp_spec = pl.BlockSpec((2, width, width), lambda i: (0, 0, 0))
    in_specs = [wave_spec, wave_spec, chirp_spec] + [
        pl.BlockSpec((2 * width, width), lambda i: (0, 0)),
        pl.BlockSpec((width, 2 * width), lambda i: (0, 0)),
    ]
    args = [waves, patches, chirps] + list(blocks)
    if residual_after:
        in_specs.append(pl.BlockSpec((1, width, width), lambda i: (i, 0, 0)))
        args.append(extra)
    if backward:
        in_specs.append(wave_spec)
        args.append(extra)
        out_shape = (
            jax.ShapeDtypeStruct(waves.shape, jnp.bfloat16),
            jax.ShapeDtypeStruct(waves.shape, jnp.float32),
        )
        out_specs = (wave_spec, wave_spec)
    else:
        out_shape = jax.ShapeDtypeStruct(waves.shape, jnp.bfloat16)
        out_specs = wave_spec
    return pl.pallas_call(
        wave_kernel(transmit_first, residual_after, backward),
        grid=(number,),
        in_specs=in_specs,
        out_specs=out_specs,
        out_shape=out_shape,
    )(*args)


def scatter_kernel(rows_ref, columns_ref, live_ref, terms_ref, out_ref):
    index = pl.program_id(0)

    @pl.when(index == 0)
    def _():
        out_ref[...] = jnp.zeros(out_ref.shape, out_ref.dtype)

    width = terms_ref.shape[2]
    height = out_ref.shape[1]
    columns_all = out_ref.shape[2]
    row = rows_ref[index]
    column = columns_ref[index]
    alive = live_ref[index] > 0
    for part in range(2):
        term = jnp.where(alive, terms_ref[0, part], 0.0)
        wide = jnp.concatenate(
            [term, jnp.zeros((width, columns_all - width), jnp.float32)], axis=1
        )
        wide = pltpu.roll(wide, column, 1)
        tall = jnp.concatenate(
            [wide, jnp.zeros((height - width, columns_all), jnp.float32)], axis=0
        )
        tall = pltpu.roll(tall, row, 0)
        out_ref[part] = out_ref[part] + tall


def scatter_terms(terms, rows, columns, live, height, columns_all):
    number, _, width, _ = terms.shape
    grid_spec = pltpu.PrefetchScalarGridSpec(
        num_scalar_prefetch=3,
        grid=(number,),
        in_specs=[pl.BlockSpec((1, 2, width, width), lambda i, r, c, a: (i, 0, 0, 0))],
        out_specs=pl.BlockSpec((2, height, columns_all), lambda i, r, c, a: (0, 0, 0)),
    )
    return pl.pallas_call(
        scatter_kernel,
        grid_spec=grid_spec,
        out_shape=jax.ShapeDtypeStruct((2, height, columns_all), jnp.float32),
    )(rows, columns, live.astype(jnp.int32), terms)


def cut_kernel(rows_ref, columns_ref, order_ref, tile_ref, mine_ref, partner_ref, out_ref):
    index = pl.program_id(0)
    width = out_ref.shape[2]
    height = tile_ref.shape[2] + mine_ref.shape[2]
    columns_all = tile_ref.shape[3]
    row_shift = (height - rows_ref[index]) % height
    column_shift = (columns_all - columns_ref[index]) % columns_all
    first = order_ref[0] == 0
    for part in range(2):
        mine = mine_ref[0, part].astype(jnp.float32)
        partner = partner_ref[0, part].astype(jnp.float32)
        rim = jnp.concatenate(
            [jnp.where(first, mine, partner), jnp.where(first, partner, mine)], axis=1
        )
        full = jnp.concatenate([tile_ref[0, part], rim], axis=0)
        full = pltpu.roll(full, row_shift, 0)[:width]
        full = pltpu.roll(full, column_shift, 1)[:, :width]
        out_ref[0, part] = full


def cut_patches(tile, mine, partner, rows, columns, order, width):
    number = rows.shape[0]
    grid_spec = pltpu.PrefetchScalarGridSpec(
        num_scalar_prefetch=3,
        grid=(number,),
        in_specs=[
            pl.BlockSpec(tile.shape, lambda i, r, c, o: (0, 0, 0, 0)),
            pl.BlockSpec(mine.shape, lambda i, r, c, o: (0, 0, 0, 0)),
            pl.BlockSpec(partner.shape, lambda i, r, c, o: (0, 0, 0, 0)),
        ],
        out_specs=pl.BlockSpec((1, 2, width, width), lambda i, r, c, o: (i, 0, 0, 0)),
    )
    return pl.pallas_call(
        cut_kernel,
        grid_spec=grid_spec,
        out_shape=jax.ShapeDtypeStruct((number, 2, width, width), jnp.float32),
    )(rows, columns, order, tile, mine, partner)


def propagate_block(wave_re, wave_im, blocks, chirp_re, chirp_im):
    rows_ref, cols_ref = blocks
    width = wave_re.shape[0]
    dft_rows = rows_ref[...]
    dft_cols = cols_ref[...]

    def left(part_re, part_im):
        lanes = jnp.concatenate([part_re, part_im], axis=1).astype(jnp.bfloat16)
        return jnp.dot(dft_rows, lanes, preferred_element_type=jnp.float32)

    def right(part_re, part_im):
        rows = jnp.concatenate([part_re, part_im], axis=0).astype(jnp.bfloat16)
        return jnp.dot(rows, dft_cols, preferred_element_type=jnp.float32)

    first = left(wave_re, wave_im)
    z_re = (first[:width, :width] - first[width:, width:]).astype(jnp.bfloat16)
    z_im = (first[:width, width:] + first[width:, :width]).astype(jnp.bfloat16)
    second = right(z_re, z_im)
    spec_re = second[:width, :width] - second[width:, width:]
    spec_im = second[:width, width:] + second[width:, :width]
    w_re = spec_re * chirp_re - spec_im * chirp_im
    w_im = spec_re * chirp_im + spec_im * chirp_re
    third = right(w_re.astype(jnp.bfloat16), w_im.astype(jnp.bfloat16))
    v_re = (third[:width, :width] + third[width:, width:]).astype(jnp.bfloat16)
    v_im = (third[width:, :width] - third[:width, width:]).astype(jnp.bfloat16)
    fourth = left(v_re, v_im)
    out_re = (fourth[:width, :width] + fourth[width:, width:]).astype(jnp.bfloat16)
    out_im = (fourth[:width, width:] - fourth[width:, :width]).astype(jnp.bfloat16)
    return (out_re.astype(jnp.float32), out_im.astype(jnp.float32))


def place_term(term_re, term_im, row, column, alive, total_ref, direct_ref=None, pad_ref=None):
    width = term_re.shape[0]
    height = total_ref.shape[1]
    columns_all = total_ref.shape[2]
    row_shift = row % height
    column_shift = column % columns_all
    for part, term in enumerate((term_re, term_im)):
        term = jnp.where(alive, term, 0.0)
        if direct_ref is not None and pad_ref is not None:
            pad_ref[...] = jnp.zeros(pad_ref.shape, jnp.float32)
            block = jnp.concatenate([term, jnp.zeros((width, 128), jnp.float32)], axis=1)
            block = jnp.concatenate([block, jnp.zeros((8, width + 128), jnp.float32)], axis=0)
            block = pltpu.roll(pltpu.roll(block, row % 8, 0), column % 128, 1)
            aligned = pl.multiple_of((row // 8) * 8, 8)
            across = pl.multiple_of((column // 128) * 128, 128)
            pad_ref[pl.ds(aligned, width + 8), pl.ds(across, width + 128)] = block
            direct_ref[part] = pad_ref[:height, :columns_all].astype(direct_ref.dtype)
            continue
        wide = jnp.concatenate(
            [term, jnp.zeros((width, columns_all - width), jnp.float32)], axis=1
        )
        wide = pltpu.roll(wide, column_shift, 1)
        if height == 2 * width:
            rolled = pltpu.roll(wide, row % width, 0)
            below = lax.broadcasted_iota(jnp.int32, rolled.shape, 0) < row
            upper = jnp.where(below, 0.0, rolled)
            lower = jnp.where(below, rolled, 0.0)
            if direct_ref is None:
                total_ref[part, :width] = total_ref[part, :width] + upper
                total_ref[part, width:] = total_ref[part, width:] + lower
            else:
                direct_ref[part, :width] = upper.astype(direct_ref.dtype)
                direct_ref[part, width:] = lower.astype(direct_ref.dtype)
            continue
        tall = jnp.concatenate(
            [wide, jnp.zeros((height - width, columns_all), jnp.float32)], axis=0
        )
        if direct_ref is None:
            total_ref[part] = total_ref[part] + pltpu.roll(tall, row_shift, 0)
        else:
            direct_ref[part] = pltpu.roll(tall, row_shift, 0).astype(direct_ref.dtype)


def adjoint_kernel(last, single, opening=False):
    def kernel(rows_ref, columns_ref, live_ref, slot_ref, other_ref, *refs):
        refs = list(refs)
        wave_ref = refs.pop(0)
        patch_ref = None if opening else refs.pop(0)
        chirp_ref = refs.pop(0)
        blocks = refs[:2]
        refs = refs[2:]
        if last:
            own_ref = refs.pop(0)
        else:
            source_ref = refs.pop(0)
        if opening:
            grad_ref, total_ref, pad_ref = refs
            passed_ref = None
        else:
            passed_ref, grad_ref, total_ref, pad_ref = refs
        index = pl.program_id(0)

        if not single:
            @pl.when(index == 0)
            def _():
                total_ref[...] = jnp.zeros(total_ref.shape, total_ref.dtype)

        wave = wave_ref[0].astype(jnp.float32)
        if not opening:
            patch_re = patch_ref[0, 0]
            patch_im = patch_ref[0, 1]
        chirp_re = chirp_ref[0]
        chirp_im = chirp_ref[1]
        if last:
            source_re = wave[0]
            source_im = wave[1]
            lit_re = patch_re * wave[0] - patch_im * wave[1]
            lit_im = patch_re * wave[1] + patch_im * wave[0]
            out_re, out_im = propagate_block(lit_re, lit_im, blocks, chirp_re, chirp_im)
            measured = own_ref[0]
            weight = RESIDUAL_SCALE * (out_re * out_re + out_im * out_im - measured)
            in_re = (weight * out_re).astype(jnp.bfloat16).astype(jnp.float32)
            in_im = (weight * out_im).astype(jnp.bfloat16).astype(jnp.float32)
        else:
            source = source_ref[0].astype(jnp.float32)
            source_re = source[0]
            source_im = source[1]
            in_re = wave[0]
            in_im = wave[1]
        spread_re, spread_im = propagate_block(in_re, in_im, blocks, chirp_re, -chirp_im)
        if not opening:
            passed_ref[0, 0] = (patch_re * spread_re + patch_im * spread_im).astype(jnp.bfloat16)
            passed_ref[0, 1] = (patch_re * spread_im - patch_im * spread_re).astype(jnp.bfloat16)
        if last:
            grad_ref[0, 0] = spread_re.astype(jnp.bfloat16)
            grad_ref[0, 1] = spread_im.astype(jnp.bfloat16)
            return
        term_re = source_re * spread_re + source_im * spread_im
        term_im = source_re * spread_im - source_im * spread_re
        place_term(
            term_re, term_im, rows_ref[index], columns_ref[index], live_ref[index] > 0,
            total_ref, grad_ref if single else None, pad_ref,
        )

        if not single:
            @pl.when(index == pl.num_programs(0) - 1)
            def _():
                grad_ref[...] = total_ref[...].astype(grad_ref.dtype)

    return kernel


def run_adjoint(waves, patches, chirps, blocks, scalars, extra, height, columns_all, last,
                opening=False):
    number, _, width, _ = waves.shape
    wave_spec = pl.BlockSpec((1, 2, width, width), lambda i, *s: (i, 0, 0, 0))
    chirp_spec = pl.BlockSpec((2, width, width), lambda i, *s: (0, 0, 0))
    in_specs = [wave_spec] + ([] if opening else [wave_spec]) + [chirp_spec] + [
        pl.BlockSpec((2 * width, width), lambda i, *s: (0, 0)),
        pl.BlockSpec((width, 2 * width), lambda i, *s: (0, 0)),
    ]
    if last:
        in_specs += [pl.BlockSpec((1, width, width), lambda i, *s: (i, 0, 0))]
    else:
        in_specs += [wave_spec]
    grid_spec = pltpu.PrefetchScalarGridSpec(
        num_scalar_prefetch=5,
        grid=(number,),
        in_specs=in_specs,
        out_specs=((() if opening else (wave_spec,))
                   + ((wave_spec,) if last else
                      (pl.BlockSpec((2, height, columns_all), lambda i, *s: (0, 0, 0)),))),
        scratch_shapes=[
            pltpu.VMEM((2, height, columns_all), jnp.float32),
            pltpu.VMEM((height + 8, columns_all + 128), jnp.float32),
        ],
    )
    return pl.pallas_call(
        adjoint_kernel(last, number == 1, opening),
        grid_spec=grid_spec,
        out_shape=((() if opening else (jax.ShapeDtypeStruct(waves.shape, jnp.bfloat16),))
                   + ((jax.ShapeDtypeStruct(waves.shape, jnp.bfloat16),) if last else
                      (jax.ShapeDtypeStruct((2, height, columns_all), jnp.bfloat16),))),
    )(*scalars, waves, *(() if opening else (patches,)), chirps, *blocks, *extra)


def place_kernel(rows_ref, columns_ref, live_ref, spread_ref, source_ref, grad_ref, total_ref):
    index = pl.program_id(0)

    @pl.when(index == 0)
    def _():
        total_ref[...] = jnp.zeros(total_ref.shape, total_ref.dtype)

    spread = spread_ref[0].astype(jnp.float32)
    source = source_ref[0].astype(jnp.float32)
    term_re = source[0] * spread[0] + source[1] * spread[1]
    term_im = source[0] * spread[1] - source[1] * spread[0]
    place_term(
        term_re, term_im, rows_ref[index], columns_ref[index], live_ref[index] > 0, total_ref
    )

    @pl.when(index == pl.num_programs(0) - 1)
    def _():
        grad_ref[...] = total_ref[...].astype(grad_ref.dtype)


def run_place(spread, source, scalars, height, columns_all):
    number, _, width, _ = spread.shape
    wave_spec = pl.BlockSpec((1, 2, width, width), lambda i, *s: (i, 0, 0, 0))
    grid_spec = pltpu.PrefetchScalarGridSpec(
        num_scalar_prefetch=3,
        grid=(number,),
        in_specs=[wave_spec, wave_spec],
        out_specs=pl.BlockSpec((2, height, columns_all), lambda i, *s: (0, 0, 0)),
        scratch_shapes=[pltpu.VMEM((2, height, columns_all), jnp.float32)],
    )
    return pl.pallas_call(
        place_kernel,
        grid_spec=grid_spec,
        out_shape=jax.ShapeDtypeStruct((2, height, columns_all), jnp.bfloat16),
    )(*scalars[:3], spread, source)


def first_kernel(rows_ref, columns_ref, order_ref, wave_ref, tile_ref, mine_ref, partner_ref,
                 chirp_ref, dft_rows_ref, dft_cols_ref, result_ref, rows_scratch):
    index = pl.program_id(0)
    width = wave_ref.shape[2]
    height = tile_ref.shape[2] + mine_ref.shape[2]
    columns_all = tile_ref.shape[3]
    first = order_ref[0] == 0
    patch = []
    for part in range(2):
        mine = mine_ref[0, part].astype(jnp.float32)
        partner = partner_ref[0, part].astype(jnp.float32)
        rim = jnp.concatenate(
            [jnp.where(first, mine, partner), jnp.where(first, partner, mine)], axis=1
        )
        rows_tile = tile_ref.shape[2]
        rows_scratch[:, columns_all:] = jnp.zeros(
            (rows_scratch.shape[0], rows_scratch.shape[1] - columns_all), jnp.float32
        )
        rows_scratch[:rows_tile, :columns_all] = tile_ref[0, part]
        rows_scratch[rows_tile:, :columns_all] = rim
        row = rows_ref[index]
        column = columns_ref[index]
        aligned = pl.multiple_of((row // 8) * 8, 8)
        across = pl.multiple_of((column // 128) * 128, 128)
        full = rows_scratch[pl.ds(aligned, width + 8), pl.ds(across, width + 128)]
        full = pltpu.roll(full, (width + 8 - row % 8) % (width + 8), 0)[:width]
        full = pltpu.roll(full, (width + 128 - column % 128) % (width + 128), 1)
        patch.append(full[:, :width])
    wave = wave_ref[0].astype(jnp.float32)
    wave_re = patch[0] * wave[0] - patch[1] * wave[1]
    wave_im = patch[0] * wave[1] + patch[1] * wave[0]
    out_re, out_im = propagate_block(
        wave_re, wave_im, (dft_rows_ref, dft_cols_ref), chirp_ref[0], chirp_ref[1]
    )
    result_ref[0, 0] = out_re.astype(jnp.bfloat16)
    result_ref[0, 1] = out_im.astype(jnp.bfloat16)


def run_first(waves, tile, mine, partner, rows, columns, order, chirps, blocks):
    number, _, width, _ = waves.shape
    wave_spec = pl.BlockSpec((1, 2, width, width), lambda i, r, c, o: (i, 0, 0, 0))
    whole = lambda shape: pl.BlockSpec(shape, lambda i, r, c, o: (0,) * len(shape))
    grid_spec = pltpu.PrefetchScalarGridSpec(
        num_scalar_prefetch=3,
        grid=(number,),
        in_specs=[
            wave_spec,
            whole(tile.shape),
            whole(mine.shape),
            whole(partner.shape),
            whole(chirps.shape),
            whole(blocks[0].shape),
            whole(blocks[1].shape),
        ],
        out_specs=wave_spec,
        scratch_shapes=[
            pltpu.VMEM((tile.shape[2] + mine.shape[2], tile.shape[3] + 128), jnp.float32)
        ],
    )
    return pl.pallas_call(
        first_kernel,
        grid_spec=grid_spec,
        out_shape=jax.ShapeDtypeStruct(waves.shape, jnp.bfloat16),
    )(rows, columns, order, waves, tile, mine, partner, chirps, *blocks)


def local(object_field, probe, positions, counts, measured):
    width = probe.shape[1]
    tile_rows = object_field.shape[2]
    columns_all = object_field.shape[3]
    tile_index = lax.axis_index("tile")
    tile_count = lax.axis_size("tile")
    segment = lax.axis_index("depth")
    depth_count = lax.axis_size("depth")
    batch_index = lax.axis_index("batch")
    batch_count = lax.axis_size("batch")
    half = columns_all // batch_count
    wanted = lax.dynamic_slice_in_dim(object_field[:, :, :width, :], batch_index * half, half, 3)
    mine = from_behind(wanted.astype(jnp.bfloat16), "tile", -1)
    pairs = [(b, (b + 1) % batch_count) for b in range(batch_count)]
    partner = lax.ppermute(mine, "batch", pairs)
    capacity = positions.shape[0]
    share = -(-capacity // batch_count)
    first_core = batch_index == 0
    both_positions = lax.ppermute(positions, "batch", pairs)
    both_counts = lax.ppermute(counts, "batch", pairs)
    all_positions = jnp.where(
        first_core,
        jnp.concatenate([positions, both_positions]),
        jnp.concatenate([both_positions, positions]),
    )
    all_counts = jnp.where(
        first_core, jnp.concatenate([counts, both_counts]), jnp.concatenate([both_counts, counts])
    )
    entry = batch_index * share + jnp.arange(share, dtype=jnp.int32)
    live = entry < all_counts[0] + all_counts[1]
    later = entry >= all_counts[0]
    slot = jnp.clip(jnp.where(later, entry - all_counts[0], entry), 0, capacity - 1)
    flat = jnp.where(later, capacity, 0) + slot
    chosen = all_positions[flat]
    other = (later == first_core).astype(jnp.int32)
    local_rows = chosen[:, 0] - tile_index * tile_rows
    local_columns = chosen[:, 1]
    order = jnp.reshape(batch_index, (1,)).astype(jnp.int32)
    patches = cut_patches(object_field, mine, partner, local_rows, local_columns, order, width)
    number = patches.shape[0]
    coef = jnp.where(
        segment == depth_count - 1, jnp.float32(DETECTOR_COEF), jnp.float32(SLICE_COEF)
    )
    chirp_re, chirp_im = chirp_parts(width, coef)
    start = jnp.broadcast_to(probe[None], (number, 2, width, width))

    chirps = jnp.stack([chirp_re, chirp_im])
    dft_re, dft_im = dft_parts(width)
    blocks = (
        jnp.concatenate([dft_re, dft_im], axis=0),
        jnp.concatenate([dft_re, dft_im], axis=1),
    )

    def forward_all(waves):
        return run_first(
            waves, object_field, mine, partner, local_rows, local_columns, order, chirps, blocks
        )

    def silent(waves):
        return jnp.zeros_like(waves)

    carry = start
    inputs = start
    for turn in range(depth_count - 1):
        if turn > 0:
            carry = lax.ppermute(carry, "depth", [(turn - 1, turn)])
            inputs = jnp.where(segment == turn, carry, inputs)
        carry = lax.cond(segment == turn, forward_all, silent, carry)

    both_measured = lax.ppermute(measured, "batch", pairs)
    chosen_measured = jnp.where(
        (other > 0)[:, None, None], both_measured[slot], measured[slot]
    )
    height = tile_rows + width
    scalars = (local_rows, local_columns, live.astype(jnp.int32), slot, other)

    def last_pass(incoming):
        return run_adjoint(
            incoming, patches, chirps, blocks, scalars, (chosen_measured,),
            height, columns_all, True,
        )

    def last_silent(incoming):
        return (jnp.zeros_like(incoming), jnp.zeros_like(incoming))

    if depth_count > 1:
        carry = lax.ppermute(carry, "depth", [(depth_count - 2, depth_count - 1)])
    arrived_last = carry
    carry, spread_last = lax.cond(segment == depth_count - 1, last_pass, last_silent, carry)
    gradient = lax.cond(
        segment == depth_count - 1,
        lambda s, a: run_place(s, a, scalars, height, columns_all),
        lambda s, a: jnp.zeros((2, height, columns_all), jnp.bfloat16),
        spread_last,
        arrived_last,
    )

    def back_pass(incoming, previous):
        return run_adjoint(
            incoming, patches, chirps, blocks, scalars, (inputs,), height, columns_all, False
        )

    def opening_pass(incoming, previous):
        (gradient,) = run_adjoint(
            incoming, patches, chirps, blocks, scalars, (inputs,), height, columns_all, False,
            opening=True,
        )
        return (incoming, gradient)

    def back_silent(incoming, previous):
        return (jnp.zeros_like(incoming), previous)

    for turn in reversed(range(depth_count - 1)):
        carry = lax.ppermute(carry, "depth", [(turn + 1, turn)])
        step = opening_pass if turn == 0 else back_pass
        carry, gradient = lax.cond(segment == turn, step, back_silent, carry, gradient)

    gradient = gradient.astype(jnp.bfloat16)
    spill = gradient[:, tile_rows:, :]
    keep = lax.dynamic_slice_in_dim(spill, batch_index * half, half, 2)
    give = lax.dynamic_slice_in_dim(spill, (1 - batch_index) * half, half, 2)
    got = lax.ppermute(give, "batch", pairs)
    spill_sum = (keep.astype(jnp.float32) + got.astype(jnp.float32)).astype(jnp.bfloat16)
    arrived = lax.ppermute(spill_sum, "tile", [(t, t + 1) for t in range(tile_count - 1)])
    own = gradient[:, :tile_rows, :]
    other = lax.ppermute(own, "batch", pairs)
    arrived_other = lax.ppermute(arrived, "batch", pairs)
    incoming = jnp.where(
        first_core,
        jnp.concatenate([arrived, arrived_other], axis=2),
        jnp.concatenate([arrived_other, arrived], axis=2),
    )
    summed = own.astype(jnp.float32) + other.astype(jnp.float32)
    summed = summed.at[:, :width, :].add(incoming.astype(jnp.float32))
    return summed[None]


def solution(mesh):
    placed = (
        P(("groups", "depth"), None, "tile", None),
        P("groups", None, None),
        P(("groups", "tile", "batch"), None),
        P(("groups", "tile", "batch")),
        P(("groups", "tile", "batch"), None, None),
    )
    return jax.shard_map(
        local,
        mesh=mesh,
        in_specs=placed,
        out_specs=P(("groups", "depth"), None, "tile", None),
        check_vma=False,
    )
```
